128 devices in a mesh: gx: 8 (over z, core), gy: 16 (over x, y).
Axes of the slice: x: 4, y: 4, z: 4, core: 2. Of those that a mesh axis runs over, the one named last changes fastest.
Arguments:
- pixel_adjoint: float32 [4, 32, 16384], P(None, None, ('gx', 'gy')), may hold values from -6 to 6
- pixel_owner: int32 [4, 16384, 1], P(None, ('gx', 'gy')), may hold values from 0 to 127; in each aligned block of 128 rows (0 to 127, 128 to 255, ..., all dimensions but the last counted through in order) at most 2 rows name the same one
- pixel_column: int32 [4, 16384], P(None, ('gx', 'gy')), may hold values from 0 to 1023
- pixel_level: int32 [4, 16384], P(None, ('gx', 'gy')), may hold values from 0 to 24
- wind_x: float32 [4, 64, 2048], P(None, 'gx', 'gy'), may hold values from -0.45 to 0.45
- wind_y: float32 [4, 64, 2048], P(None, 'gx', 'gy'), may hold values from -0.45 to 0.45
- diffusivity: float32 [39, 64, 2048], P(None, 'gx', 'gy'), may hold values from 0.1 to 10
- prior_emission: float32 [2, 64, 2048], P(None, 'gx', 'gy'), may hold values from 0.01 to 0.1
- region_map: int32 [64, 2048], P('gx', 'gy'), may hold values from 0 to 1023, as said below
Outputs:
- adjoint_out: float32 [2, 40, 64, 2048], P(None, None, 'gx', 'gy')
- emission_gradient: float32 [2, 1024], P(None, ('gx', 'gy'))
The draws below stay inside these ranges and needn't reach their ends.
Inputs may be any that keep to these rules, and one draw needn't show every extreme that they name: `pixel_owner`: within the 128 entries of one device in one step no owner is named more than 2 times, a bound that some block reaches. `region_map`: constant on aligned blocks of 2 rows by 4 columns; every region covers exactly 16 such blocks.
All inputs are finite; a program needn't handle non-finite values.
Results may differ from the reference program's by a relative error of at most 0.00014.
Values sent between devices are 32-bit elements; how exact they have to be, the bound alone decides.
No kernel may reach another device: no remote copies, remote signals or barrier semaphores. Data moves between devices by JAX's collectives and lax.ppermute only.
A program may use at most 64 MiB of HBM per device.

```python
import math
import jax
import jax.numpy as jnp
import numpy as np
from jax import lax

CX = 8
CY = 128
LEV = 40
S = 2
AKL = 16
STEPS = 4
PIX = 128
NX = 64
NY = 2048
NPIX = 16384
CAP = 2
NREG = 1024
N_GY = 16
DEVICES = 128


def draw_region_map(key, part):
    rows_blk = NX // 2
    cols_blk = NY // 4
    order = jax.random.permutation(key, rows_blk * cols_blk) % NREG
    blocks = order.reshape(rows_blk, cols_blk).astype(jnp.int32)
    return jnp.repeat(jnp.repeat(blocks, 2, axis=0), 4, axis=1)


def plant(values, key, smallest, top_value):
    longest = values.shape.index(max(values.shape))
    spots = []
    for shift in (0, 1):
        where = [jax.random.randint(jax.random.fold_in(key, axis), (), 0, length) for axis, length in enumerate(values.shape)]
        where[longest] = (where[longest] + shift) % values.shape[longest]
        spots.append(tuple(where))
    return values.at[spots[0]].set(smallest).at[spots[1]].set(top_value)


def steps_of(rng, extent, split, low, largest):
    level, own = 1.0, jax.random.fold_in(rng, 6)
    for position, blocks in split:
        draws = jnp.exp(jax.random.uniform(jax.random.fold_in(own, position), (blocks,), jnp.float32, low / len(split), largest / len(split)))
        level = level * jnp.repeat(draws, extent[position] // blocks).reshape([-1 if axis == position else 1 for axis in range(len(extent))])
    return level


def shared_out(stream_key, own, number, rows, count, top, most, skew):
    order = jax.random.permutation(stream_key, count)
    packed, usual = portions_of(count, rows * top, most, skew, True), portions_of(count, rows * top, most, skew, False)
    places = jnp.arange(count)

    def named(lengths, rotation):
        used = int((lengths > 0).sum())
        fixed = max(1, used // 4)
        passed = fixed + (places - fixed + rotation * (used - fixed)) % max(1, count - fixed)
        return jnp.zeros((count,), jnp.int32).at[order[jnp.where(places < fixed, places, passed)]].set(jnp.asarray(lengths, jnp.int32))

    lengths = jnp.where(number % 4 == 0, named(packed, number // 4), named(usual, number - number // 4 - 1))
    mixed = jax.random.permutation(jax.random.fold_in(own, 3), count)
    giver, receiver = mixed[0:count // 2 * 2:2], mixed[1:count // 2 * 2:2]
    room = jnp.minimum(lengths[giver] - 1, most - lengths[receiver]) // 2
    room = jnp.where((giver == order[0]) | (receiver == order[0]) | (lengths[receiver] == 0), 0, jnp.maximum(room, 0))
    passed = jax.random.randint(jax.random.fold_in(own, 4), (count // 2,), 0, 1 << 20) % (room + 1)
    lengths = lengths.at[giver].add(-passed).at[receiver].add(passed)
    items = jnp.searchsorted(jnp.cumsum(lengths), jnp.arange(rows * top), side="right").astype(jnp.int32)
    grid = items.reshape(top, rows).T
    grid = grid[jax.random.permutation(jax.random.fold_in(own, 1), rows)]
    rotation = jax.random.randint(jax.random.fold_in(own, 2), (rows, 1), 0, top)
    return jnp.take_along_axis(grid, (jnp.arange(top)[None, :] + rotation) % top, axis=1)


def portions_of(amount, total, reach, skew, full):
    weights = [(1 << 20) // math.isqrt(rank ** skew) + 1 for rank in range(1, amount + 1)]
    largest = reach if full else min(reach, max(-(-total // amount), total * weights[0] // sum(weights)))
    least = 1 if total - largest >= amount - 1 else 0
    given, surplus = [largest] + [least] * (amount - 1), total - largest - least * (amount - 1)
    while surplus > 0:
        candidates = [i for i in range(1, amount) if given[i] < largest] or [i for i in range(1, amount) if given[i] < reach]
        whole, remaining = sum([weights[i] for i in candidates]), surplus
        for i in candidates:
            more = min(reach - given[i], max(1, remaining * weights[i] // whole), surplus)
            given[i] = given[i] + more
            surplus = surplus - more
    return np.array(given)


def gaussian(stream_key, shape, deviation, bound, split=(), held_as=jnp.bfloat16):
    entries = deviation * jax.random.normal(stream_key, shape, jnp.float32)
    if split:
        entries = entries * steps_of(stream_key, shape, split, -0.22, 0.18)
    return jnp.clip(entries, -bound, bound).astype(held_as)


def setup_inputs(seed: int = 0) -> dict:
    keys = jax.random.split(jax.random.key(seed), 10)
    pixel_adjoint = gaussian(keys[0], (STEPS, S * AKL, NPIX), 1.0, 6.0, ((2, 128),), jnp.float32)
    pixel_owner_keys = jax.random.split(jax.random.fold_in(keys[1], 1), STEPS * NPIX // PIX)
    pixel_owner_turns = jax.random.permutation(jax.random.fold_in(keys[1], 3), STEPS * NPIX // PIX)
    pixel_owner = jax.vmap(lambda own, number: shared_out(jax.random.fold_in(keys[1], 2), own, number, PIX, DEVICES, 1, CAP, 2))(pixel_owner_keys, pixel_owner_turns).reshape((STEPS, NPIX, 1))
    pixel_column = plant(jax.random.randint(keys[2], (STEPS, NPIX), 0, CX * CY), jax.random.fold_in(keys[2], 1), 0, (CX * CY) - 1).astype(jnp.int32)
    pixel_level = plant(jax.random.randint(keys[3], (STEPS, NPIX), 0, LEV - AKL + 1), jax.random.fold_in(keys[3], 1), 0, LEV - AKL).astype(jnp.int32)
    wind_x = jnp.clip(jax.random.uniform(keys[4], (STEPS, NX, NY), jnp.float32, -0.45, 0.45) * steps_of(keys[4], (STEPS, NX, NY), ((1, 8), (2, 16)), -0.4, 0.0), -0.45, 0.45)
    wind_y = jnp.clip(jax.random.uniform(keys[5], (STEPS, NX, NY), jnp.float32, -0.45, 0.45) * steps_of(keys[5], (STEPS, NX, NY), ((1, 8), (2, 16)), -0.4, 0.0), -0.45, 0.45)
    diffusivity = jnp.clip(jnp.exp(math.log(10.0) - 4.6051702 * jax.random.uniform(keys[6], (LEV - 1, NX, NY), jnp.float32) ** steps_of(keys[6], (LEV - 1, NX, NY), ((1, 8), (2, 16)), -0.2, 0.2)), 0.1, 10.0)
    prior_emission = jnp.clip(jnp.exp(math.log(0.1) - 2.3025851 * jax.random.uniform(keys[7], (S, NX, NY), jnp.float32) ** steps_of(keys[7], (S, NX, NY), ((1, 8), (2, 16)), -0.2, 0.2)), 0.01, 0.1)
    region_map = draw_region_map(jax.random.fold_in(keys[9], 71), 0)
    return {"pixel_adjoint": pixel_adjoint, "pixel_owner": pixel_owner, "pixel_column": pixel_column, "pixel_level": pixel_level, "wind_x": wind_x, "wind_y": wind_y, "diffusivity": diffusivity, "prior_emission": prior_emission, "region_map": region_map}


def spread(payload, column, start, species, levels, kernel, cells):
    offset = jnp.arange(levels, dtype=jnp.int32)[:, None] - start[None, :]
    inside = (offset >= 0) & (offset < kernel)
    kernel_row = jnp.clip(offset, 0, kernel - 1)
    values = payload.reshape(species, kernel, -1)
    picked = jnp.take_along_axis(values, jnp.broadcast_to(kernel_row[None], (species, levels, kernel_row.shape[1])), axis=1)
    profile = jnp.where(inside[None], picked, 0.0)
    forcing = jnp.zeros((species * levels, cells), jnp.float32)
    return forcing.at[:, column].add(profile.reshape(species * levels, -1))


def transpose_advect(padded, wind_pad):
    eastward = jnp.maximum(wind_pad[0], 0.0)
    westward = jnp.maximum(-wind_pad[0], 0.0)
    northward = jnp.maximum(wind_pad[1], 0.0)
    southward = jnp.maximum(-wind_pad[1], 0.0)
    remain = 1.0 - (eastward + westward + northward + southward)[1:-1, 1:-1]
    moved = padded[:, :, 1:-1, 1:-1] * remain
    moved = moved + (eastward * padded)[:, :, 2:, 1:-1] + (westward * padded)[:, :, :-2, 1:-1]
    moved = moved + (northward * padded)[:, :, 1:-1, 2:] + (southward * padded)[:, :, 1:-1, :-2]
    return moved


def factor(diffusivity):
    edge = jnp.zeros_like(diffusivity[:1])
    below = jnp.concatenate([edge, diffusivity], axis=0)
    above = jnp.concatenate([diffusivity, edge], axis=0)

    def sweep(carried, inputs):
        below_row, above_row = inputs
        inverse_row = 1.0 / (1.0 + below_row + above_row + below_row * carried)
        ratio_row = -above_row * inverse_row
        return ratio_row, (ratio_row, inverse_row)

    end_state, (ratios, inverses) = lax.scan(sweep, jnp.zeros_like(edge[0]), (below, above))
    return below, ratios, inverses


def solve(rhs, below, ratios, inverses):
    stacked = jnp.moveaxis(rhs, 1, 0)

    def forward(carried, inputs):
        rhs_row, below_row, inverse_row = inputs
        reduced = (rhs_row + below_row * carried) * inverse_row
        return reduced, reduced

    end_state, reduced_all = lax.scan(forward, jnp.zeros_like(stacked[0]), (stacked, below, inverses))

    def backward(carried, inputs):
        reduced_row, ratio_row = inputs
        result = reduced_row - ratio_row * carried
        return result, result

    top_state, solved = lax.scan(backward, jnp.zeros_like(stacked[0]), (reduced_all, ratios), reverse=True)
    return jnp.moveaxis(solved, 0, 1)


def reference(pixel_adjoint, pixel_owner, pixel_column, pixel_level, wind_x, wind_y, diffusivity, prior_emission, region_map):
    cells = NX * NY
    below, ratios, inverses = factor(diffusivity)
    winds = jnp.pad(jnp.stack([wind_x, wind_y]), ((0, 0), (0, 0), (1, 1), (1, 1)))
    adjoint = jnp.zeros((S, LEV, NX, NY), jnp.float32)
    surface_sum = jnp.zeros((S, NX, NY), jnp.float32)
    for moment in reversed(range(STEPS)):
        owners = pixel_owner[moment, :, 0]
        column = pixel_column[moment]
        grid_row = (owners // N_GY) * CX + column // CY
        grid_col = (owners % N_GY) * CY + column % CY
        flat = (grid_row * NY + grid_col).astype(jnp.int32)
        forcing = spread(pixel_adjoint[moment], flat, pixel_level[moment], S, LEV, AKL, cells).reshape(S, LEV, NX, NY)
        forced = adjoint + forcing
        padded = jnp.pad(forced, ((0, 0), (0, 0), (1, 1), (1, 1)))
        moved = transpose_advect(padded, winds[:, moment])
        adjoint = solve(moved, below, ratios, inverses)
        surface_sum = surface_sum + prior_emission * adjoint[:, 0]
    gradient = jax.ops.segment_sum(surface_sum.reshape(S, -1).T, region_map.reshape(-1), num_segments=NREG).T
    return (adjoint, gradient)
```

```python
import functools

import jax
import jax.numpy as jnp
from jax import lax
from jax.experimental import pallas as pl
from jax.experimental.pallas import tpu as pltpu
from jax.sharding import PartitionSpec as P

HI = lax.Precision.HIGHEST
REG_DEV = 8


def _full(shape):
    nd = len(shape)
    return pl.BlockSpec(shape, lambda i, _n=nd: (0,) * _n)


def _fluxes(forced_ref, wx, wy, e_ref, w_ref, n_ref, s_ref):
    east = jnp.maximum(wx, 0.0)
    west = jnp.maximum(-wx, 0.0)
    north = jnp.maximum(wy, 0.0)
    south = jnp.maximum(-wy, 0.0)
    species, levels = forced_ref.shape[0], forced_ref.shape[1]
    rows, cols = wx.shape
    for s in range(species):

        def body(l, carry):
            f = forced_ref[s, l]
            e_ref[s, l] = (east * f)[0:1, :]
            w_ref[s, l] = (west * f)[rows - 1:rows, :]
            n_ref[s, l] = (north * f)[:, 0:1]
            s_ref[s, l] = (south * f)[:, cols - 1:cols]
            return carry

        lax.fori_loop(0, levels, body, 0, unroll=8)


def _init_kernel(diff_ref, forcing_ref, wx_ref, wy_ref,
                 ratio_ref, inv_ref, e_ref, w_ref, n_ref, s_ref):
    levels = ratio_ref.shape[0]
    zero = jnp.zeros(ratio_ref.shape[1:], jnp.float32)
    carried = zero
    for l in range(levels):
        below = diff_ref[l - 1] if l > 0 else zero
        above = diff_ref[l] if l < levels - 1 else zero
        inverse = 1.0 / (1.0 + below + above + below * carried)
        ratio = -above * inverse
        ratio_ref[l] = ratio
        inv_ref[l] = inverse
        carried = ratio
    k = wx_ref.shape[0] - 1
    _fluxes(forcing_ref, wx_ref[k], wy_ref[k], e_ref, w_ref, n_ref, s_ref)


def _step_kernel(k, first, *refs):
    last = k == 0
    if last:
        (forced_ref, he_ref, hw_ref, hn_ref, hs_ref, wx_ref, wy_ref, diff_ref,
         ratio_ref, inv_ref, prior_ref, ss_ref,
         adj_ref, ss_out_ref, red_ref) = refs
    else:
        (forced_ref, he_ref, hw_ref, hn_ref, hs_ref, wx_ref, wy_ref, diff_ref,
         ratio_ref, inv_ref, prior_ref, ss_ref, next_forcing_ref,
         adj_ref, e_ref, w_ref, n_ref, s_ref, ss_out_ref, red_ref) = refs
    species, levels, rows, cols = forced_ref.shape
    wx = wx_ref[k]
    wy = wy_ref[k]
    east = jnp.maximum(wx, 0.0)
    west = jnp.maximum(-wx, 0.0)
    north = jnp.maximum(wy, 0.0)
    south = jnp.maximum(-wy, 0.0)
    remain = 1.0 - (east + west + north + south)
    row = lax.broadcasted_iota(jnp.int32, (rows, cols), 0)
    col = lax.broadcasted_iota(jnp.int32, (rows, cols), 1)
    top_row = row == rows - 1
    bottom_row = row == 0
    last_col = col == cols - 1
    first_col = col == 0
    zero = jnp.zeros((rows, cols), jnp.float32)

    for s in range(species):

        def forward(l, reduced):
            f = forced_ref[s, l]
            from_east = jnp.where(
                top_row, jnp.broadcast_to(he_ref[s, l], (rows, cols)),
                pltpu.roll(east * f, rows - 1, 0))
            from_west = jnp.where(
                bottom_row, jnp.broadcast_to(hw_ref[s, l], (rows, cols)),
                pltpu.roll(west * f, 1, 0))
            from_north = jnp.where(
                last_col, jnp.broadcast_to(hn_ref[s, l], (rows, cols)),
                pltpu.roll(north * f, cols - 1, 1))
            from_south = jnp.where(
                first_col, jnp.broadcast_to(hs_ref[s, l], (rows, cols)),
                pltpu.roll(south * f, 1, 1))
            moved = f * remain
            moved = moved + from_east + from_west
            moved = moved + from_north + from_south
            below = jnp.where(l > 0, diff_ref[jnp.maximum(l - 1, 0)], zero)
            reduced = (moved + below * reduced) * inv_ref[l]
            red_ref[l] = reduced
            return reduced

        lax.fori_loop(0, levels, forward, zero, unroll=8)

        def backward(i, result):
            l = levels - 1 - i
            result = red_ref[l] - ratio_ref[l] * result
            adj_ref[s, l] = result
            return result

        lax.fori_loop(0, levels, backward, zero, unroll=8)
        if first:
            ss_out_ref[s] = prior_ref[s] * adj_ref[s, 0]
        else:
            ss_out_ref[s] = ss_ref[s] + prior_ref[s] * adj_ref[s, 0]

    if not last:
        for s in range(species):

            def add(l, carry):
                adj_ref[s, l] = adj_ref[s, l] + next_forcing_ref[s, l]
                return carry

            lax.fori_loop(0, levels, add, 0, unroll=8)
        _fluxes(adj_ref, wx_ref[k - 1], wy_ref[k - 1], e_ref, w_ref, n_ref, s_ref)


def _halo_shapes(species, levels, rows, cols):
    row_halo = jax.ShapeDtypeStruct((species, levels, 1, cols), jnp.float32)
    col_halo = jax.ShapeDtypeStruct((species, levels, rows, 1), jnp.float32)
    return [row_halo, row_halo, col_halo, col_halo]


def init_call(diffusivity, forcing, wind_x, wind_y):
    steps, species, levels, rows, cols = forcing.shape
    k = steps - 1
    plane = jax.ShapeDtypeStruct((levels, rows, cols), jnp.float32)
    halos = _halo_shapes(species, levels, rows, cols)
    return pl.pallas_call(
        _init_kernel,
        grid=(1,),
        in_specs=[
            _full(diffusivity.shape),
            pl.BlockSpec((None, species, levels, rows, cols), lambda i: (k, 0, 0, 0, 0)),
            _full(wind_x.shape),
            _full(wind_y.shape),
        ],
        out_specs=[_full(plane.shape), _full(plane.shape)] + [_full(h.shape) for h in halos],
        out_shape=[plane, plane] + halos,
    )(diffusivity, forcing, wind_x, wind_y)


def step_call(k, first, forced, halos, wind_x, wind_y, diffusivity, ratios, inverses,
              prior, surface_sum, forcing):
    species, levels, rows, cols = forced.shape
    last = k == 0
    state = jax.ShapeDtypeStruct((species, levels, rows, cols), jnp.float32)
    surf = jax.ShapeDtypeStruct(prior.shape, jnp.float32)
    in_specs = [_full(forced.shape)] + [_full(h.shape) for h in halos]
    args = [forced] + list(halos)
    in_specs += [_full(wind_x.shape), _full(wind_y.shape)]
    args += [wind_x, wind_y]
    in_specs += [_full(diffusivity.shape), _full(ratios.shape), _full(inverses.shape),
                 _full(prior.shape), _full(surface_sum.shape)]
    args += [diffusivity, ratios, inverses, prior, surface_sum]
    out_shape = [state]
    if not last:
        in_specs.append(
            pl.BlockSpec((None, species, levels, rows, cols), lambda i: (k - 1, 0, 0, 0, 0)))
        args.append(forcing)
        out_shape += _halo_shapes(species, levels, rows, cols)
    out_shape.append(surf)
    return pl.pallas_call(
        functools.partial(_step_kernel, k, first),
        grid=(1,),
        in_specs=in_specs,
        out_specs=[_full(o.shape) for o in out_shape],
        out_shape=out_shape,
        scratch_shapes=[pltpu.VMEM((levels, rows, cols), jnp.float32)],
    )(*args)


def exchange(halos):
    east, west, north, south = halos
    gx = lax.axis_size("gx")
    gy = lax.axis_size("gy")
    up_x = [(i, i + 1) for i in range(gx - 1)]
    down_x = [(i + 1, i) for i in range(gx - 1)]
    up_y = [(i, i + 1) for i in range(gy - 1)]
    down_y = [(i + 1, i) for i in range(gy - 1)]
    east = lax.ppermute(east, "gx", down_x)
    west = lax.ppermute(west, "gx", up_x)
    north = lax.ppermute(north, "gy", down_y)
    south = lax.ppermute(south, "gy", up_y)
    return [east, west, north, south]


def local(pixel_adjoint, pixel_owner, pixel_column, pixel_level, wind_x, wind_y,
          diffusivity, prior_emission, region_map):
    devices = lax.axis_size("gx") * lax.axis_size("gy")
    steps, rows, cols = wind_x.shape
    levels = diffusivity.shape[0] + 1
    species = prior_emission.shape[0]
    kernel = pixel_adjoint.shape[1] // species
    pixels = pixel_adjoint.shape[2]
    capacity = 2 * pixels // devices
    cells = rows * cols
    slots = devices * capacity

    owners = pixel_owner[:, :, 0]
    matches = (owners[:, :, None] == jnp.arange(devices, dtype=jnp.int32)).astype(jnp.int32)
    rank = jnp.sum(jnp.cumsum(matches, axis=1) * matches, axis=2) - 1
    position = owners * capacity + rank
    rows_out = jnp.concatenate(
        [pixel_adjoint, pixel_column.astype(jnp.float32)[:, None, :],
         pixel_level.astype(jnp.float32)[:, None, :]], axis=1)
    place = (position[:, :, None] == jnp.arange(slots, dtype=jnp.int32)).astype(jnp.float32)
    placed = jnp.einsum("kap,kpq->kaq", rows_out, place, precision=HI)
    received = lax.all_to_all(placed, ("gx", "gy"), 2, 2, tiled=True)

    payload = received[:, :species * kernel].reshape(steps, species, kernel, slots)
    column = jnp.round(received[:, species * kernel]).astype(jnp.int32)
    start = jnp.round(received[:, species * kernel + 1]).astype(jnp.int32)
    offset = jnp.arange(levels, dtype=jnp.int32)[None, :, None] - start[:, None, :]
    profile = jnp.zeros((steps, species, levels, slots), jnp.float32)
    for j in range(kernel):
        profile = profile + jnp.where((offset == j)[:, None], payload[:, :, j][:, :, None, :], 0.0)
    hits = (column[:, :, None] == jnp.arange(cells, dtype=jnp.int32)).astype(jnp.float32)
    forcing = jnp.einsum("ksq,kqc->ksc", profile.reshape(steps, species * levels, slots), hits,
                         precision=HI)
    forcing = forcing.reshape(steps, species, levels, rows, cols)

    ratios, inverses, *halos = init_call(diffusivity, forcing, wind_x, wind_y)
    forced = forcing[steps - 1]
    surface_sum = jnp.zeros(prior_emission.shape, jnp.float32)
    for k in reversed(range(steps)):
        halos = exchange(halos)
        outs = step_call(k, k == steps - 1, forced, halos, wind_x, wind_y, diffusivity,
                         ratios, inverses, prior_emission, surface_sum, forcing)
        if k > 0:
            forced, *halos, surface_sum = outs
        else:
            adjoint, surface_sum = outs

    nreg = REG_DEV * devices
    member = (region_map.reshape(-1)[:, None] == jnp.arange(nreg, dtype=jnp.int32)).astype(jnp.float32)
    partial = jnp.dot(surface_sum.reshape(species, cells), member, precision=HI)
    pieces = lax.all_to_all(partial.reshape(species, devices, nreg // devices), ("gx", "gy"), 1, 1,
                            tiled=True)
    gradient = jnp.sum(pieces, axis=1)
    return adjoint, gradient


def solution(mesh):
    in_specs = (
        P(None, None, ("gx", "gy")),
        P(None, ("gx", "gy"), None),
        P(None, ("gx", "gy")),
        P(None, ("gx", "gy")),
        P(None, "gx", "gy"),
        P(None, "gx", "gy"),
        P(None, "gx", "gy"),
        P(None, "gx", "gy"),
        P("gx", "gy"),
    )
    out_specs = (P(None, None, "gx", "gy"), P(None, ("gx", "gy")))
    return jax.shard_map(local, mesh=mesh, in_specs=in_specs, out_specs=out_specs, check_vma=False)
```

```python
import functools

import jax
import jax.numpy as jnp
from jax import lax
from jax.experimental import pallas as pl
from jax.experimental.pallas import tpu as pltpu
from jax.sharding import PartitionSpec as P

HI = lax.Precision.HIGHEST
REG_DEV = 8


def _full(shape):
    nd = len(shape)
    return pl.BlockSpec(shape, lambda i, _n=nd: (0,) * _n)


def _step_kernel(k, first, last, *refs):
    refs = list(refs)
    forced_ref = refs.pop(0)
    mask_ref, wx_ref, wy_ref, diff_ref, prior_ref = refs[:5]
    refs = refs[5:]
    if not first:
        ratio_in, inv_in, ss_ref = refs[:3]
        refs = refs[3:]
    if not last:
        next_forcing_ref = refs.pop(0)
    if first:
        ratio_ref, inv_ref = refs[:2]
        refs = refs[2:]
    else:
        ratio_ref, inv_ref = ratio_in, inv_in
    out_ref, ss_out_ref, red_ref = refs

    species, levels, rows, lanes = out_ref.shape
    zero = jnp.zeros((rows, lanes), jnp.float32)

    if first:
        carried = zero
        for l in range(levels):
            below = diff_ref[l - 1] if l > 0 else zero
            above = diff_ref[l] if l < levels - 1 else zero
            inverse = 1.0 / (1.0 + below + above + below * carried)
            ratio = -above * inverse
            ratio_ref[l] = ratio
            inv_ref[l] = inverse
            carried = ratio

    inside = mask_ref[...] > 0.5
    wx = wx_ref[k]
    wy = wy_ref[k]
    east = jnp.maximum(wx, 0.0)
    west = jnp.maximum(-wx, 0.0)
    north = jnp.maximum(wy, 0.0)
    south = jnp.maximum(-wy, 0.0)
    remain = 1.0 - (east + west + north + south)

    for s in range(species):

        def forward(l, reduced):
            f = forced_ref[s, l]
            if first:
                f = jnp.where(inside, f, 0.0)
            from_east = pltpu.roll(east * f, rows - 1, 0)
            from_west = pltpu.roll(west * f, 1, 0)
            from_north = pltpu.roll(north * f, lanes - 1, 1)
            from_south = pltpu.roll(south * f, 1, 1)
            moved = f * remain
            moved = moved + from_east + from_west
            moved = moved + from_north + from_south
            below = jnp.where(l > 0, diff_ref[jnp.maximum(l - 1, 0)], zero)
            reduced = (moved + below * reduced) * inv_ref[l]
            red_ref[l] = reduced
            return reduced

        lax.fori_loop(0, levels, forward, zero, unroll=4)

        def backward(i, result):
            l = levels - 1 - i
            result = red_ref[l] - ratio_ref[l] * result
            if last:
                out_ref[s, l] = result
            else:
                out_ref[s, l] = jnp.where(inside, result + next_forcing_ref[s, l], 0.0)
            return result

        surface = lax.fori_loop(0, levels, backward, zero, unroll=4)
        if first:
            ss_out_ref[s] = prior_ref[s] * surface
        else:
            ss_out_ref[s] = ss_ref[s] + prior_ref[s] * surface


def step_call(k, steps, forced, mask, wind_x, wind_y, diffusivity, prior, ratios, inverses,
              surface_sum, forcing):
    first = k == steps - 1
    last = k == 0
    species, levels, rows, lanes = forcing.shape[1:]
    state = jax.ShapeDtypeStruct((species, levels, rows, lanes), jnp.float32)
    plane = jax.ShapeDtypeStruct((levels, rows, lanes), jnp.float32)
    surf = jax.ShapeDtypeStruct(prior.shape, jnp.float32)
    block = (None, species, levels, rows, lanes)
    if first:
        in_specs = [pl.BlockSpec(block, lambda i: (k, 0, 0, 0, 0))]
        args = [forcing]
    else:
        in_specs = [_full(forced.shape)]
        args = [forced]
    for a in (mask, wind_x, wind_y, diffusivity, prior):
        in_specs.append(_full(a.shape))
        args.append(a)
    if not first:
        for a in (ratios, inverses, surface_sum):
            in_specs.append(_full(a.shape))
            args.append(a)
    if not last:
        in_specs.append(pl.BlockSpec(block, lambda i: (k - 1, 0, 0, 0, 0)))
        args.append(forcing)
    out_shape = [plane, plane] if first else []
    out_shape += [state, surf]
    return pl.pallas_call(
        functools.partial(_step_kernel, k, first, last),
        grid=(1,),
        in_specs=in_specs,
        out_specs=[_full(o.shape) for o in out_shape],
        out_shape=out_shape,
        scratch_shapes=[pltpu.VMEM((levels, rows, lanes), jnp.float32)],
    )(*args)


def extend(chans, halo, lanes):
    gx = lax.axis_size("gx")
    gy = lax.axis_size("gy")
    up_x = [(i, i + 1) for i in range(gx - 1)]
    down_x = [(i + 1, i) for i in range(gx - 1)]
    up_y = [(i, i + 1) for i in range(gy - 1)]
    down_y = [(i + 1, i) for i in range(gy - 1)]
    channels, rows, cols = chans.shape
    top = lax.ppermute(jnp.swapaxes(chans[:, rows - halo:], 0, 1), "gx", up_x)
    bottom = lax.ppermute(jnp.swapaxes(chans[:, :halo], 0, 1), "gx", down_x)
    ext = jnp.concatenate([jnp.swapaxes(top, 0, 1), chans, jnp.swapaxes(bottom, 0, 1)], axis=1)
    left = lax.ppermute(jnp.transpose(ext[:, :, cols - halo:], (2, 1, 0)), "gy", up_y)
    right = lax.ppermute(jnp.transpose(ext[:, :, :halo], (2, 1, 0)), "gy", down_y)
    gap = jnp.zeros((channels, rows + 2 * halo, lanes - cols - 2 * halo), jnp.float32)
    return jnp.concatenate(
        [ext, jnp.transpose(right, (2, 1, 0)), gap, jnp.transpose(left, (2, 1, 0))], axis=2)


def local(pixel_adjoint, pixel_owner, pixel_column, pixel_level, wind_x, wind_y,
          diffusivity, prior_emission, region_map):
    gx_n = lax.axis_size("gx")
    gy_n = lax.axis_size("gy")
    devices = gx_n * gy_n
    steps, rows, cols = wind_x.shape
    levels = diffusivity.shape[0] + 1
    species = prior_emission.shape[0]
    kernel = pixel_adjoint.shape[1] // species
    pixels = pixel_adjoint.shape[2]
    capacity = 2 * pixels // devices
    cells = rows * cols
    slots = devices * capacity
    halo = steps
    lanes = 2 * cols
    ext_rows = rows + 2 * halo

    owners = pixel_owner[:, :, 0]
    matches = (owners[:, :, None] == jnp.arange(devices, dtype=jnp.int32)).astype(jnp.int32)
    rank = jnp.sum(jnp.cumsum(matches, axis=1) * matches, axis=2) - 1
    position = owners * capacity + rank
    rows_out = jnp.concatenate(
        [pixel_adjoint, pixel_column.astype(jnp.float32)[:, None, :],
         pixel_level.astype(jnp.float32)[:, None, :]], axis=1)
    place = (position[:, :, None] == jnp.arange(slots, dtype=jnp.int32)).astype(jnp.float32)
    placed = jnp.einsum("kap,kpq->kaq", rows_out, place, precision=HI)
    received = lax.all_to_all(placed, ("gx", "gy"), 2, 2, tiled=True)

    payload = received[:, :species * kernel].reshape(steps, species, kernel, slots)
    column = jnp.round(received[:, species * kernel]).astype(jnp.int32)
    start = jnp.round(received[:, species * kernel + 1]).astype(jnp.int32)
    offset = jnp.arange(levels, dtype=jnp.int32)[None, :, None] - start[:, None, :]
    profile = jnp.zeros((steps, species, levels, slots), jnp.float32)
    for j in range(kernel):
        profile = profile + jnp.where((offset == j)[:, None], payload[:, :, j][:, :, None, :], 0.0)
    hits = (column[:, :, None] == jnp.arange(cells, dtype=jnp.int32)).astype(jnp.float32)
    forcing = jnp.einsum("ksq,kqc->ksc", profile.reshape(steps, species * levels, slots), hits,
                         precision=HI)

    chans = jnp.concatenate(
        [forcing.reshape(steps * species * levels, rows, cols), wind_x, wind_y, diffusivity],
        axis=0)
    ext = extend(chans, halo, lanes)
    n_f = steps * species * levels
    forcing_ext = ext[:n_f].reshape(steps, species, levels, ext_rows, lanes)
    wx_ext = ext[n_f:n_f + steps]
    wy_ext = ext[n_f + steps:n_f + 2 * steps]
    diff_ext = ext[n_f + 2 * steps:]

    gxi = lax.axis_index("gx")
    gyi = lax.axis_index("gy")
    r = jnp.arange(ext_rows, dtype=jnp.int32)[:, None]
    c = jnp.arange(lanes, dtype=jnp.int32)[None, :]
    grow = gxi * rows + r - halo
    ccol = jnp.where(c < cols + halo, c, c - lanes)
    gcol = gyi * cols + ccol
    inside = ((grow >= 0) & (grow < gx_n * rows) & (gcol >= 0) & (gcol < gy_n * cols)
              & ((c < cols + halo) | (c >= lanes - halo)))
    mask = inside.astype(jnp.float32)
    prior_ext = jnp.pad(prior_emission, ((0, 0), (halo, halo), (0, lanes - cols)))

    forced = None
    ratios = inverses = surface_sum = None
    for k in reversed(range(steps)):
        outs = step_call(k, steps, forced, mask, wx_ext, wy_ext, diff_ext, prior_ext, ratios,
                         inverses, surface_sum, forcing_ext)
        if k == steps - 1:
            ratios, inverses, forced, surface_sum = outs
        else:
            forced, surface_sum = outs
    adjoint = forced[:, :, halo:halo + rows, :cols]
    surface_sum = surface_sum[:, halo:halo + rows, :cols]

    nreg = REG_DEV * devices
    member = (region_map.reshape(-1)[:, None] == jnp.arange(nreg, dtype=jnp.int32)).astype(jnp.float32)
    partial = jnp.dot(surface_sum.reshape(species, cells), member, precision=HI)
    pieces = lax.all_to_all(partial.reshape(species, devices, nreg // devices), ("gx", "gy"), 1, 1,
                            tiled=True)
    gradient = jnp.sum(pieces, axis=1)
    return adjoint, gradient


def solution(mesh):
    in_specs = (
        P(None, None, ("gx", "gy")),
        P(None, ("gx", "gy"), None),
        P(None, ("gx", "gy")),
        P(None, ("gx", "gy")),
        P(None, "gx", "gy"),
        P(None, "gx", "gy"),
        P(None, "gx", "gy"),
        P(None, "gx", "gy"),
        P("gx", "gy"),
    )
    out_specs = (P(None, None, "gx", "gy"), P(None, ("gx", "gy")))
    return jax.shard_map(local, mesh=mesh, in_specs=in_specs, out_specs=out_specs, check_vma=False)
```

```python
import functools

import jax
import jax.numpy as jnp
from jax import lax
from jax.experimental import pallas as pl
from jax.experimental.pallas import tpu as pltpu
from jax.sharding import PartitionSpec as P

HI = lax.Precision.HIGHEST
REG_DEV = 8


def _full(shape):
    nd = len(shape)
    return pl.BlockSpec(shape, lambda i, _n=nd: (0,) * _n)


def _step_kernel(k, first, last, *refs):
    refs = list(refs)
    if first:
        own_ref, xh_ref, yh_ref = refs[:3]
        refs = refs[3:]
    else:
        forced_ref = refs.pop(0)
    mask_ref, wx_ref, wy_ref, diff_ref, prior_ref = refs[:5]
    refs = refs[5:]
    if not first:
        ratio_in, inv_in, ss_ref = refs[:3]
        refs = refs[3:]
    if not last:
        nown_ref, nxh_ref, nyh_ref = refs[:3]
        refs = refs[3:]
    if first:
        ratio_ref, inv_ref = refs[:2]
        refs = refs[2:]
    else:
        ratio_ref, inv_ref = ratio_in, inv_in
    out_ref, ss_out_ref, red_ref = refs[:3]
    if first:
        forced_ref = refs[3]

    species, levels = ss_out_ref.shape[0], red_ref.shape[0]
    rows, lanes = red_ref.shape[1:]
    tr, tc = ss_out_ref.shape[1:]
    zero = jnp.zeros((rows, lanes), jnp.float32)
    inside = mask_ref[...] > 0.5

    if first:
        carried = zero
        for l in range(levels):
            below = diff_ref[l - 1] if l > 0 else zero
            above = diff_ref[l] if l < levels - 1 else zero
            inverse = 1.0 / (1.0 + below + above + below * carried)
            ratio = -above * inverse
            ratio_ref[l] = ratio
            inv_ref[l] = inverse
            carried = ratio
        for s in range(species):

            def assemble(l, carry):
                forced_ref[s, l, :tr, :tc] = own_ref[s, l]
                forced_ref[s, l, tr:, :tc] = xh_ref[s, l]
                forced_ref[s, l, :, tc:] = yh_ref[s, l]
                forced_ref[s, l] = jnp.where(inside, forced_ref[s, l], 0.0)
                return carry

            lax.fori_loop(0, levels, assemble, 0, unroll=4)

    wx = wx_ref[k]
    wy = wy_ref[k]
    east = jnp.maximum(wx, 0.0)
    west = jnp.maximum(-wx, 0.0)
    north = jnp.maximum(wy, 0.0)
    south = jnp.maximum(-wy, 0.0)
    remain = 1.0 - (east + west + north + south)

    for s in range(species):

        def forward(l, reduced):
            f = forced_ref[s, l]
            from_east = pltpu.roll(east * f, rows - 1, 0)
            from_west = pltpu.roll(west * f, 1, 0)
            from_north = pltpu.roll(north * f, lanes - 1, 1)
            from_south = pltpu.roll(south * f, 1, 1)
            moved = f * remain
            moved = moved + from_east + from_west
            moved = moved + from_north + from_south
            below = jnp.where(l > 0, diff_ref[jnp.maximum(l - 1, 0)], zero)
            reduced = (moved + below * reduced) * inv_ref[l]
            red_ref[l] = reduced
            return reduced

        lax.fori_loop(0, levels, forward, zero, unroll=4)

        def backward(i, result):
            l = levels - 1 - i
            result = red_ref[l] - ratio_ref[l] * result
            if last:
                out_ref[s, l] = result[:tr, :tc]
            else:
                out_ref[s, l, :tr, :tc] = jnp.where(
                    inside[:tr, :tc], result[:tr, :tc] + nown_ref[s, l], 0.0)
                out_ref[s, l, tr:, :tc] = jnp.where(
                    inside[tr:, :tc], result[tr:, :tc] + nxh_ref[s, l], 0.0)
                out_ref[s, l, :, tc:] = jnp.where(
                    inside[:, tc:], result[:, tc:] + nyh_ref[s, l], 0.0)
            return result

        surface = lax.fori_loop(0, levels, backward, zero, unroll=4)
        if first:
            ss_out_ref[s] = prior_ref[s] * surface[:tr, :tc]
        else:
            ss_out_ref[s] = ss_ref[s] + prior_ref[s] * surface[:tr, :tc]


def step_call(k, steps, forced, mask, wind_x, wind_y, diffusivity, prior, ratios, inverses,
              surface_sum, own, xh, yh):
    first = k == steps - 1
    last = k == 0
    species, levels, rows, cols = own.shape[1:]
    rows_e, lanes = mask.shape
    ext = jax.ShapeDtypeStruct((species, levels, rows_e, lanes), jnp.float32)
    tile = jax.ShapeDtypeStruct((species, levels, rows, cols), jnp.float32)
    plane = jax.ShapeDtypeStruct((levels, rows_e, lanes), jnp.float32)
    surf = jax.ShapeDtypeStruct(prior.shape, jnp.float32)

    def blocks(step):
        return [pl.BlockSpec((None,) + a.shape[1:], lambda i, _s=step: (_s, 0, 0, 0, 0))
                for a in (own, xh, yh)]

    in_specs, args = [], []
    if first:
        in_specs += blocks(k)
        args += [own, xh, yh]
    else:
        in_specs.append(_full(forced.shape))
        args.append(forced)
    for a in (mask, wind_x, wind_y, diffusivity, prior):
        in_specs.append(_full(a.shape))
        args.append(a)
    if not first:
        for a in (ratios, inverses, surface_sum):
            in_specs.append(_full(a.shape))
            args.append(a)
    if not last:
        in_specs += blocks(k - 1)
        args += [own, xh, yh]
    out_shape = [plane, plane] if first else []
    out_shape += [tile if last else ext, surf]
    scratch = [pltpu.VMEM((levels, rows_e, lanes), jnp.float32)]
    if first:
        scratch.append(pltpu.VMEM((species, levels, rows_e, lanes), jnp.float32))
    return pl.pallas_call(
        functools.partial(_step_kernel, k, first, last),
        grid=(1,),
        in_specs=in_specs,
        out_specs=[_full(o.shape) for o in out_shape],
        out_shape=out_shape,
        scratch_shapes=scratch,
    )(*args)


def _pairs(axis):
    n = lax.axis_size(axis)
    return [(i, i + 1) for i in range(n - 1)], [(i + 1, i) for i in range(n - 1)]


def extend(tile, halo):
    up_x, down_x = _pairs("gx")
    up_y, down_y = _pairs("gy")
    rows, cols = tile.shape[-2:]
    below = lax.ppermute(tile[..., :halo, :], "gx", down_x)
    above = lax.ppermute(tile[..., rows - halo:, :], "gx", up_x)
    xh = jnp.concatenate([below, jnp.zeros_like(below)[..., :rows - 2 * halo, :], above], axis=-2)
    tall = jnp.concatenate([tile, xh], axis=-2)
    right = lax.ppermute(jnp.swapaxes(tall[..., :halo], -1, -3), "gy", down_y)
    left = lax.ppermute(jnp.swapaxes(tall[..., cols - halo:], -1, -3), "gy", up_y)
    right = jnp.swapaxes(right, -1, -3)
    left = jnp.swapaxes(left, -1, -3)
    gap = jnp.zeros(right.shape[:-1] + (cols - 2 * halo,), jnp.float32)
    yh = jnp.concatenate([right, gap, left], axis=-1)
    return xh, yh


def local(pixel_adjoint, pixel_owner, pixel_column, pixel_level, wind_x, wind_y,
          diffusivity, prior_emission, region_map):
    gx_n = lax.axis_size("gx")
    gy_n = lax.axis_size("gy")
    devices = gx_n * gy_n
    steps, rows, cols = wind_x.shape
    levels = diffusivity.shape[0] + 1
    species = prior_emission.shape[0]
    kernel = pixel_adjoint.shape[1] // species
    pixels = pixel_adjoint.shape[2]
    capacity = 2 * pixels // devices
    cells = rows * cols
    slots = devices * capacity
    halo = steps
    lanes = 2 * cols
    ext_rows = 2 * rows

    owners = pixel_owner[:, :, 0]
    matches = (owners[:, :, None] == jnp.arange(devices, dtype=jnp.int32)).astype(jnp.int32)
    rank = jnp.sum(jnp.cumsum(matches, axis=1) * matches, axis=2) - 1
    position = owners * capacity + rank
    rows_out = jnp.concatenate(
        [pixel_adjoint, pixel_column.astype(jnp.float32)[:, None, :],
         pixel_level.astype(jnp.float32)[:, None, :]], axis=1)
    place = (position[:, :, None] == jnp.arange(slots, dtype=jnp.int32)).astype(jnp.float32)
    placed = jnp.einsum("kap,kpq->kaq", rows_out, place, precision=HI)
    received = lax.all_to_all(placed, ("gx", "gy"), 2, 2, tiled=True)

    payload = received[:, :species * kernel].reshape(steps, species, kernel, slots)
    column = jnp.round(received[:, species * kernel]).astype(jnp.int32)
    start = jnp.round(received[:, species * kernel + 1]).astype(jnp.int32)
    offset = jnp.arange(levels, dtype=jnp.int32)[None, :, None] - start[:, None, :]
    profile = jnp.zeros((steps, species, levels, slots), jnp.float32)
    for j in range(kernel):
        profile = profile + jnp.where((offset == j)[:, None], payload[:, :, j][:, :, None, :], 0.0)
    hits = (column[:, :, None] == jnp.arange(cells, dtype=jnp.int32)).astype(jnp.float32)
    forcing = jnp.einsum("ksq,kqc->ksc", profile.reshape(steps, species * levels, slots), hits,
                         precision=HI)

    own = forcing.reshape(steps, species, levels, rows, cols)
    xh, yh = extend(own, halo)
    statics = jnp.concatenate([wind_x, wind_y, diffusivity], axis=0)
    sxh, syh = extend(statics, halo)
    statics = jnp.concatenate([jnp.concatenate([statics, sxh], axis=1), syh], axis=2)
    wx_ext = statics[:steps]
    wy_ext = statics[steps:2 * steps]
    diff_ext = statics[2 * steps:]

    gxi = lax.axis_index("gx")
    gyi = lax.axis_index("gy")
    r = jnp.arange(ext_rows, dtype=jnp.int32)[:, None]
    c = jnp.arange(lanes, dtype=jnp.int32)[None, :]
    grow = gxi * rows + jnp.where(r < rows + halo, r, r - ext_rows)
    ccol = jnp.where(c < cols + halo, c, c - lanes)
    gcol = gyi * cols + ccol
    inside = ((grow >= 0) & (grow < gx_n * rows) & (gcol >= 0) & (gcol < gy_n * cols)
              & ((c < cols + halo) | (c >= lanes - halo)))
    mask = inside.astype(jnp.float32)

    forced = None
    ratios = inverses = surface_sum = None
    for k in reversed(range(steps)):
        outs = step_call(k, steps, forced, mask, wx_ext, wy_ext, diff_ext, prior_emission,
                         ratios, inverses, surface_sum, own, xh, yh)
        if k == steps - 1:
            ratios, inverses, forced, surface_sum = outs
        else:
            forced, surface_sum = outs
    adjoint = forced

    nreg = REG_DEV * devices
    member = (region_map.reshape(-1)[:, None] == jnp.arange(nreg, dtype=jnp.int32)).astype(jnp.float32)
    partial = jnp.dot(surface_sum.reshape(species, cells), member, precision=HI)
    pieces = lax.all_to_all(partial.reshape(species, devices, nreg // devices), ("gx", "gy"), 1, 1,
                            tiled=True)
    gradient = jnp.sum(pieces, axis=1)
    return adjoint, gradient


def solution(mesh):
    in_specs = (
        P(None, None, ("gx", "gy")),
        P(None, ("gx", "gy"), None),
        P(None, ("gx", "gy")),
        P(None, ("gx", "gy")),
        P(None, "gx", "gy"),
        P(None, "gx", "gy"),
        P(None, "gx", "gy"),
        P(None, "gx", "gy"),
        P("gx", "gy"),
    )
    out_specs = (P(None, None, "gx", "gy"), P(None, ("gx", "gy")))
    return jax.shard_map(local, mesh=mesh, in_specs=in_specs, out_specs=out_specs, check_vma=False)
```

```python
import functools

import jax
import jax.numpy as jnp
from jax import lax
from jax.experimental import pallas as pl
from jax.experimental.pallas import tpu as pltpu
from jax.sharding import PartitionSpec as P

HI = lax.Precision.HIGHEST
REG_DEV = 8


def _full(shape):
    nd = len(shape)
    return pl.BlockSpec(shape, lambda i, _n=nd: (0,) * _n)


def _step_kernel(k, steps, first, last, *refs):
    refs = list(refs)
    if first:
        own_ref, xh_ref, yh_ref = refs[:3]
        refs = refs[3:]
    else:
        forced_ref = refs.pop(0)
    mask_ref, se_ref, prior_ref = refs[:3]
    refs = refs[3:]
    if not first:
        ratio_in, inv_in, ss_ref = refs[:3]
        refs = refs[3:]
    if not last:
        nown_ref, nxh_ref, nyh_ref = refs[:3]
        refs = refs[3:]
    if first:
        ratio_ref, inv_ref = refs[:2]
        refs = refs[2:]
    else:
        ratio_ref, inv_ref = ratio_in, inv_in
    out_ref, ss_out_ref, red_ref = refs[:3]
    if first:
        forced_ref = refs[3]

    species, levels = ss_out_ref.shape[0], red_ref.shape[0]
    rows, lanes = red_ref.shape[1:]
    tr, tc = ss_out_ref.shape[1:]
    d0 = 2 * steps
    zero = jnp.zeros((rows, lanes), jnp.float32)
    inside = mask_ref[...] > 0.5

    if first:
        carried = zero
        for l in range(levels):
            below = se_ref[d0 + l - 1] if l > 0 else zero
            above = se_ref[d0 + l] if l < levels - 1 else zero
            inverse = 1.0 / (1.0 + below + above + below * carried)
            ratio = -above * inverse
            ratio_ref[l] = ratio
            inv_ref[l] = inverse
            carried = ratio
        for s in range(species):

            def assemble(l, carry):
                c = s * levels + l
                forced_ref[s, l, :tr, :tc] = own_ref[c]
                forced_ref[s, l, tr:, :tc] = xh_ref[c]
                forced_ref[s, l, :, tc:] = yh_ref[c]
                forced_ref[s, l] = jnp.where(inside, forced_ref[s, l], 0.0)
                return carry

            lax.fori_loop(0, levels, assemble, 0, unroll=4)

    wx = se_ref[k]
    wy = se_ref[steps + k]
    east = jnp.maximum(wx, 0.0)
    west = jnp.maximum(-wx, 0.0)
    north = jnp.maximum(wy, 0.0)
    south = jnp.maximum(-wy, 0.0)
    remain = 1.0 - (east + west + north + south)

    for s in range(species):

        def forward(l, reduced):
            f = forced_ref[s, l]
            from_east = pltpu.roll(east * f, rows - 1, 0)
            from_west = pltpu.roll(west * f, 1, 0)
            from_north = pltpu.roll(north * f, lanes - 1, 1)
            from_south = pltpu.roll(south * f, 1, 1)
            moved = f * remain
            moved = moved + from_east + from_west
            moved = moved + from_north + from_south
            below = jnp.where(l > 0, se_ref[d0 + jnp.maximum(l - 1, 0)], zero)
            reduced = (moved + below * reduced) * inv_ref[l]
            red_ref[l] = reduced
            return reduced

        lax.fori_loop(0, levels, forward, zero, unroll=4)

        def backward(i, result):
            l = levels - 1 - i
            c = s * levels + l
            result = red_ref[l] - ratio_ref[l] * result
            if last:
                out_ref[s, l] = result[:tr, :tc]
            else:
                out_ref[s, l, :tr, :tc] = jnp.where(
                    inside[:tr, :tc], result[:tr, :tc] + nown_ref[c], 0.0)
                out_ref[s, l, tr:, :tc] = jnp.where(
                    inside[tr:, :tc], result[tr:, :tc] + nxh_ref[c], 0.0)
                out_ref[s, l, :, tc:] = jnp.where(
                    inside[:, tc:], result[:, tc:] + nyh_ref[c], 0.0)
            return result

        surface = lax.fori_loop(0, levels, backward, zero, unroll=4)
        if first:
            ss_out_ref[s] = prior_ref[s] * surface[:tr, :tc]
        else:
            ss_out_ref[s] = ss_ref[s] + prior_ref[s] * surface[:tr, :tc]


def step_call(k, steps, species, levels, forced, mask, statics, prior, ratios, inverses,
              surface_sum, chans, xh, yh):
    first = k == steps - 1
    last = k == 0
    rows, cols = chans.shape[1:]
    rows_e, lanes = mask.shape
    planes = species * levels
    ext = jax.ShapeDtypeStruct((species, levels, rows_e, lanes), jnp.float32)
    tile = jax.ShapeDtypeStruct((species, levels, rows, cols), jnp.float32)
    plane = jax.ShapeDtypeStruct((levels, rows_e, lanes), jnp.float32)
    surf = jax.ShapeDtypeStruct(prior.shape, jnp.float32)

    def blocks(step):
        return [pl.BlockSpec((planes,) + a.shape[1:], lambda i, _s=step: (_s, 0, 0))
                for a in (chans, xh, yh)]

    in_specs, args = [], []
    if first:
        in_specs += blocks(k)
        args += [chans, xh, yh]
    else:
        in_specs.append(_full(forced.shape))
        args.append(forced)
    for a in (mask, statics, prior):
        in_specs.append(_full(a.shape))
        args.append(a)
    if not first:
        for a in (ratios, inverses, surface_sum):
            in_specs.append(_full(a.shape))
            args.append(a)
    if not last:
        in_specs += blocks(k - 1)
        args += [chans, xh, yh]
    out_shape = [plane, plane] if first else []
    out_shape += [tile if last else ext, surf]
    scratch = [pltpu.VMEM((levels, rows_e, lanes), jnp.float32)]
    if first:
        scratch.append(pltpu.VMEM((species, levels, rows_e, lanes), jnp.float32))
    return pl.pallas_call(
        functools.partial(_step_kernel, k, steps, first, last),
        grid=(1,),
        in_specs=in_specs,
        out_specs=[_full(o.shape) for o in out_shape],
        out_shape=out_shape,
        scratch_shapes=scratch,
    )(*args)


def _pairs(axis):
    n = lax.axis_size(axis)
    return [(i, i + 1) for i in range(n - 1)], [(i + 1, i) for i in range(n - 1)]


def _whole(shapes):
    return [pl.BlockSpec(memory_space=pltpu.VMEM) for _ in shapes]


def _xpack_kernel(chans_ref, lo_ref, hi_ref):
    rows = chans_ref.shape[1]
    half = rows // 2
    row = lax.broadcasted_iota(jnp.int32, chans_ref.shape[1:], 0)

    def body(i, carry):
        a = chans_ref[2 * i]
        b = chans_ref[2 * i + 1]
        lo_ref[i] = jnp.where(row < half, a, pltpu.roll(b, half, 0))
        hi_ref[i] = jnp.where(row < half, pltpu.roll(a, half, 0), b)
        return carry

    lax.fori_loop(0, lo_ref.shape[0], body, 0, unroll=4)


def _ypack_kernel(chans_ref, below_ref, above_ref, xh_ref, right_ref, left_ref):
    rows, cols = chans_ref.shape[1:]
    half = rows // 2
    group = cols // half
    row = lax.broadcasted_iota(jnp.int32, (rows, cols), 0)
    lane = lax.broadcasted_iota(jnp.int32, (rows, cols), 1)
    zero = jnp.zeros((rows, cols), jnp.float32)

    def body(g, carry):
        acc = [zero, zero, zero, zero]
        for q2 in range(group // 2):
            i = g * (group // 2) + q2
            b = below_ref[i]
            a = above_ref[i]
            xh0 = jnp.where(row < half, b, pltpu.roll(a, half, 0))
            xh1 = jnp.where(row < half, pltpu.roll(b, half, 0), a)
            xh_ref[2 * i] = xh0
            xh_ref[2 * i + 1] = xh1
            for off, top, bot in ((0, chans_ref[2 * i], xh0), (1, chans_ref[2 * i + 1], xh1)):
                q = 2 * q2 + off
                sel = (lane >= half * q) & (lane < half * q + half)
                rs = (half * q) % cols
                ls = (half * q + half) % cols
                acc[0] = jnp.where(sel, pltpu.roll(top, rs, 1) if rs else top, acc[0])
                acc[1] = jnp.where(sel, pltpu.roll(bot, rs, 1) if rs else bot, acc[1])
                acc[2] = jnp.where(sel, pltpu.roll(top, ls, 1) if ls else top, acc[2])
                acc[3] = jnp.where(sel, pltpu.roll(bot, ls, 1) if ls else bot, acc[3])
        right_ref[g, :rows] = acc[0]
        right_ref[g, rows:] = acc[1]
        left_ref[g, :rows] = acc[2]
        left_ref[g, rows:] = acc[3]
        return carry

    lax.fori_loop(0, right_ref.shape[0], body, 0)


def _yunpack_kernel(first_static, chans_ref, xh_ref, right_ref, left_ref, yh_ref, se_ref):
    rows, cols = chans_ref.shape[1:]
    half = rows // 2
    group = cols // half
    lane = lax.broadcasted_iota(jnp.int32, (2 * rows, cols), 1)

    def body(g, carry):
        r = right_ref[g]
        l = left_ref[g]
        for q in range(group):
            rs = (cols - half * q) % cols
            ls = (cols - half - half * q) % cols
            yh = jnp.where(lane < half, pltpu.roll(r, rs, 1) if rs else r,
                           jnp.where(lane >= cols - half, pltpu.roll(l, ls, 1) if ls else l, 0.0))
            yh_ref[g * group + q] = yh
        return carry

    lax.fori_loop(0, right_ref.shape[0], body, 0)
    for c in range(se_ref.shape[0]):
        se_ref[c, :rows, :cols] = chans_ref[first_static + c]
        se_ref[c, rows:, :cols] = xh_ref[first_static + c]
        se_ref[c, :, cols:] = yh_ref[first_static + c]


def extend(chans, first_static, n_statics):
    up_x, down_x = _pairs("gx")
    up_y, down_y = _pairs("gy")
    channels, rows, cols = chans.shape
    halo = rows // 2
    group = cols // halo
    pairs = jax.ShapeDtypeStruct((channels // 2, rows, cols), jnp.float32)
    lo, hi = pl.pallas_call(
        _xpack_kernel, out_shape=[pairs, pairs],
        in_specs=_whole([chans]), out_specs=_whole([0, 0]))(chans)
    below = lax.ppermute(lo, "gx", down_x)
    above = lax.ppermute(hi, "gx", up_x)
    packed = jax.ShapeDtypeStruct((channels // group, 2 * rows, cols), jnp.float32)
    xh, right, left = pl.pallas_call(
        _ypack_kernel,
        out_shape=[jax.ShapeDtypeStruct(chans.shape, jnp.float32), packed, packed],
        in_specs=_whole([0, 0, 0]), out_specs=_whole([0, 0, 0]))(chans, below, above)
    right = lax.ppermute(right, "gy", down_y)
    left = lax.ppermute(left, "gy", up_y)
    yh, statics = pl.pallas_call(
        functools.partial(_yunpack_kernel, first_static),
        out_shape=[jax.ShapeDtypeStruct((channels, 2 * rows, cols), jnp.float32),
                   jax.ShapeDtypeStruct((n_statics, 2 * rows, 2 * cols), jnp.float32)],
        in_specs=_whole([0, 0, 0, 0]), out_specs=_whole([0, 0]))(chans, xh, right, left)
    return xh, yh, statics


def local(pixel_adjoint, pixel_owner, pixel_column, pixel_level, wind_x, wind_y,
          diffusivity, prior_emission, region_map):
    gx_n = lax.axis_size("gx")
    gy_n = lax.axis_size("gy")
    devices = gx_n * gy_n
    steps, rows, cols = wind_x.shape
    levels = diffusivity.shape[0] + 1
    species = prior_emission.shape[0]
    kernel = pixel_adjoint.shape[1] // species
    pixels = pixel_adjoint.shape[2]
    capacity = 2 * pixels // devices
    cells = rows * cols
    slots = devices * capacity
    halo = rows // 2
    assert steps <= halo
    lanes = 2 * cols
    ext_rows = 2 * rows

    owners = pixel_owner[:, :, 0]
    matches = (owners[:, :, None] == jnp.arange(devices, dtype=jnp.int32)).astype(jnp.int32)
    rank = jnp.sum(jnp.cumsum(matches, axis=1) * matches, axis=2) - 1
    position = owners * capacity + rank
    rows_out = jnp.concatenate(
        [pixel_adjoint, pixel_column.astype(jnp.float32)[:, None, :],
         pixel_level.astype(jnp.float32)[:, None, :]], axis=1)
    place = (position[:, :, None] == jnp.arange(slots, dtype=jnp.int32)).astype(jnp.float32)
    placed = jnp.einsum("kap,kpq->kaq", rows_out, place, precision=HI)
    received = lax.all_to_all(placed, ("gx", "gy"), 2, 2, tiled=True)

    payload = received[:, :species * kernel].reshape(steps, species, kernel, slots)
    column = jnp.round(received[:, species * kernel]).astype(jnp.int32)
    start = jnp.round(received[:, species * kernel + 1]).astype(jnp.int32)
    offset = jnp.arange(levels, dtype=jnp.int32)[None, :, None] - start[:, None, :]
    profile = jnp.zeros((steps, species, levels, slots), jnp.float32)
    for j in range(kernel):
        profile = profile + jnp.where((offset == j)[:, None], payload[:, :, j][:, :, None, :], 0.0)
    hits = (column[:, :, None] == jnp.arange(cells, dtype=jnp.int32)).astype(jnp.float32)
    forcing = jnp.einsum("ksq,kqc->ksc", profile.reshape(steps, species * levels, slots), hits,
                         precision=HI)

    n_f = steps * species * levels
    n_s = 2 * steps + levels - 1
    group = cols // halo
    channels = -(-(n_f + n_s) // group) * group
    chans = jnp.concatenate(
        [forcing.reshape(n_f, rows, cols), wind_x, wind_y, diffusivity,
         jnp.zeros((channels - n_f - n_s, rows, cols), jnp.float32)], axis=0)
    xh, yh, statics = extend(chans, n_f, n_s)

    gxi = lax.axis_index("gx")
    gyi = lax.axis_index("gy")
    r = jnp.arange(ext_rows, dtype=jnp.int32)[:, None]
    c = jnp.arange(lanes, dtype=jnp.int32)[None, :]
    grow = gxi * rows + jnp.where(r < rows + halo, r, r - ext_rows)
    ccol = jnp.where(c < cols + halo, c, c - lanes)
    gcol = gyi * cols + ccol
    inside = ((grow >= 0) & (grow < gx_n * rows) & (gcol >= 0) & (gcol < gy_n * cols)
              & ((c < cols + halo) | (c >= lanes - halo)))
    mask = inside.astype(jnp.float32)

    forced = None
    ratios = inverses = surface_sum = None
    for k in reversed(range(steps)):
        outs = step_call(k, steps, species, levels, forced, mask, statics, prior_emission,
                         ratios, inverses, surface_sum, chans, xh, yh)
        if k == steps - 1:
            ratios, inverses, forced, surface_sum = outs
        else:
            forced, surface_sum = outs
    adjoint = forced

    nreg = REG_DEV * devices
    member = (region_map.reshape(-1)[:, None] == jnp.arange(nreg, dtype=jnp.int32)).astype(jnp.float32)
    partial = jnp.dot(surface_sum.reshape(species, cells), member, precision=HI)
    pieces = lax.all_to_all(partial.reshape(species, devices, nreg // devices), ("gx", "gy"), 1, 1,
                            tiled=True)
    gradient = jnp.sum(pieces, axis=1)
    return adjoint, gradient


def solution(mesh):
    in_specs = (
        P(None, None, ("gx", "gy")),
        P(None, ("gx", "gy"), None),
        P(None, ("gx", "gy")),
        P(None, ("gx", "gy")),
        P(None, "gx", "gy"),
        P(None, "gx", "gy"),
        P(None, "gx", "gy"),
        P(None, "gx", "gy"),
        P("gx", "gy"),
    )
    out_specs = (P(None, None, "gx", "gy"), P(None, ("gx", "gy")))
    return jax.shard_map(local, mesh=mesh, in_specs=in_specs, out_specs=out_specs, check_vma=False)
```

```python
import functools

import jax
import jax.numpy as jnp
from jax import lax
from jax.experimental import pallas as pl
from jax.experimental.pallas import tpu as pltpu
from jax.sharding import PartitionSpec as P

HI = lax.Precision.HIGHEST
REG_DEV = 8


def _full(shape):
    nd = len(shape)
    return pl.BlockSpec(shape, lambda i, _n=nd: (0,) * _n)


def _step_kernel(k, steps, first, last, *refs):
    refs = list(refs)
    if first:
        own_ref, xh_ref, yh_ref = refs[:3]
        refs = refs[3:]
    else:
        forced_ref = refs.pop(0)
    mask_ref, se_ref, prior_ref = refs[:3]
    refs = refs[3:]
    if not first:
        ratio_in, inv_in, ss_ref = refs[:3]
        refs = refs[3:]
    if not last:
        nown_ref, nxh_ref, nyh_ref = refs[:3]
        refs = refs[3:]
    if first:
        ratio_ref, inv_ref = refs[:2]
        refs = refs[2:]
    else:
        ratio_ref, inv_ref = ratio_in, inv_in
    out_ref, ss_out_ref, red_ref = refs[:3]
    if first:
        forced_ref = refs[3]

    species, levels = ss_out_ref.shape[0], red_ref.shape[0]
    rows, lanes = red_ref.shape[1:]
    tr, tc = ss_out_ref.shape[1:]
    d0 = 2 * steps
    zero = jnp.zeros((rows, lanes), jnp.float32)
    inside = mask_ref[...] > 0.5

    if first:
        carried = zero
        for l in range(levels):
            below = se_ref[d0 + l - 1] if l > 0 else zero
            above = se_ref[d0 + l] if l < levels - 1 else zero
            inverse = 1.0 / (1.0 + below + above + below * carried)
            ratio = -above * inverse
            ratio_ref[l] = ratio
            inv_ref[l] = inverse
            carried = ratio
        for s in range(species):

            def assemble(l, carry):
                c = s * levels + l
                forced_ref[s, l, :tr, :tc] = own_ref[c]
                forced_ref[s, l, tr:, :tc] = xh_ref[c]
                forced_ref[s, l, :, tc:] = yh_ref[c]
                forced_ref[s, l] = jnp.where(inside, forced_ref[s, l], 0.0)
                return carry

            lax.fori_loop(0, levels, assemble, 0, unroll=4)

    wx = se_ref[k]
    wy = se_ref[steps + k]
    east = jnp.maximum(wx, 0.0)
    west = jnp.maximum(-wx, 0.0)
    north = jnp.maximum(wy, 0.0)
    south = jnp.maximum(-wy, 0.0)
    remain = 1.0 - (east + west + north + south)

    for s in range(species):

        def forward(l, reduced):
            f = forced_ref[s, l]
            from_east = pltpu.roll(east * f, rows - 1, 0)
            from_west = pltpu.roll(west * f, 1, 0)
            from_north = pltpu.roll(north * f, lanes - 1, 1)
            from_south = pltpu.roll(south * f, 1, 1)
            moved = f * remain
            moved = moved + from_east + from_west
            moved = moved + from_north + from_south
            below = jnp.where(l > 0, se_ref[d0 + jnp.maximum(l - 1, 0)], zero)
            reduced = (moved + below * reduced) * inv_ref[l]
            red_ref[l] = reduced
            return reduced

        lax.fori_loop(0, levels, forward, zero, unroll=4)

        def backward(i, result):
            l = levels - 1 - i
            c = s * levels + l
            result = red_ref[l] - ratio_ref[l] * result
            if last:
                out_ref[s, l] = result[:tr, :tc]
            else:
                out_ref[s, l, :tr, :tc] = jnp.where(
                    inside[:tr, :tc], result[:tr, :tc] + nown_ref[c], 0.0)
                out_ref[s, l, tr:, :tc] = jnp.where(
                    inside[tr:, :tc], result[tr:, :tc] + nxh_ref[c], 0.0)
                out_ref[s, l, :, tc:] = jnp.where(
                    inside[:, tc:], result[:, tc:] + nyh_ref[c], 0.0)
            return result

        surface = lax.fori_loop(0, levels, backward, zero, unroll=4)
        if first:
            ss_out_ref[s] = prior_ref[s] * surface[:tr, :tc]
        else:
            ss_out_ref[s] = ss_ref[s] + prior_ref[s] * surface[:tr, :tc]


def step_call(k, steps, species, levels, forced, mask, statics, prior, ratios, inverses,
              surface_sum, chans, xh, yh):
    first = k == steps - 1
    last = k == 0
    rows, cols = chans.shape[1:]
    rows_e, lanes = mask.shape
    planes = species * levels
    ext = jax.ShapeDtypeStruct((species, levels, rows_e, lanes), jnp.float32)
    tile = jax.ShapeDtypeStruct((species, levels, rows, cols), jnp.float32)
    plane = jax.ShapeDtypeStruct((levels, rows_e, lanes), jnp.float32)
    surf = jax.ShapeDtypeStruct(prior.shape, jnp.float32)

    def blocks(step):
        return [pl.BlockSpec((planes,) + a.shape[1:], lambda i, _s=step: (_s, 0, 0))
                for a in (chans, xh, yh)]

    in_specs, args = [], []
    if first:
        in_specs += blocks(k)
        args += [chans, xh, yh]
    else:
        in_specs.append(_full(forced.shape))
        args.append(forced)
    for a in (mask, statics, prior):
        in_specs.append(_full(a.shape))
        args.append(a)
    if not first:
        for a in (ratios, inverses, surface_sum):
            in_specs.append(_full(a.shape))
            args.append(a)
    if not last:
        in_specs += blocks(k - 1)
        args += [chans, xh, yh]
    out_shape = [plane, plane] if first else []
    out_shape += [tile if last else ext, surf]
    scratch = [pltpu.VMEM((levels, rows_e, lanes), jnp.float32)]
    if first:
        scratch.append(pltpu.VMEM((species, levels, rows_e, lanes), jnp.float32))
    return pl.pallas_call(
        functools.partial(_step_kernel, k, steps, first, last),
        grid=(1,),
        in_specs=in_specs,
        out_specs=[_full(o.shape) for o in out_shape],
        out_shape=out_shape,
        scratch_shapes=scratch,
    )(*args)


def _pairs(axis):
    n = lax.axis_size(axis)
    return [(i, i + 1) for i in range(n - 1)], [(i + 1, i) for i in range(n - 1)]


def _whole(shapes):
    return [pl.BlockSpec(memory_space=pltpu.VMEM) for _ in shapes]


def _xpack_kernel(chans_ref, lo_ref, hi_ref):
    rows = chans_ref.shape[1]
    half = rows // 2
    row = lax.broadcasted_iota(jnp.int32, chans_ref.shape[1:], 0)

    def body(i, carry):
        a = chans_ref[2 * i]
        b = chans_ref[2 * i + 1]
        lo_ref[i] = jnp.where(row < half, a, pltpu.roll(b, half, 0))
        hi_ref[i] = jnp.where(row < half, pltpu.roll(a, half, 0), b)
        return carry

    lax.fori_loop(0, lo_ref.shape[0], body, 0, unroll=4)


def _ypack_kernel(chans_ref, below_ref, above_ref, xh_ref, right_ref, left_ref):
    rows, cols = chans_ref.shape[1:]
    half = rows // 2
    group = cols // half
    row = lax.broadcasted_iota(jnp.int32, (rows, cols), 0)
    lane = lax.broadcasted_iota(jnp.int32, (rows, cols), 1)
    zero = jnp.zeros((rows, cols), jnp.float32)

    def body(g, carry):
        acc = [zero, zero, zero, zero]
        for q2 in range(group // 2):
            i = g * (group // 2) + q2
            b = below_ref[i]
            a = above_ref[i]
            xh0 = jnp.where(row < half, b, pltpu.roll(a, half, 0))
            xh1 = jnp.where(row < half, pltpu.roll(b, half, 0), a)
            xh_ref[2 * i] = xh0
            xh_ref[2 * i + 1] = xh1
            for off, top, bot in ((0, chans_ref[2 * i], xh0), (1, chans_ref[2 * i + 1], xh1)):
                q = 2 * q2 + off
                sel = (lane >= half * q) & (lane < half * q + half)
                rs = (half * q) % cols
                ls = (half * q + half) % cols
                acc[0] = jnp.where(sel, pltpu.roll(top, rs, 1) if rs else top, acc[0])
                acc[1] = jnp.where(sel, pltpu.roll(bot, rs, 1) if rs else bot, acc[1])
                acc[2] = jnp.where(sel, pltpu.roll(top, ls, 1) if ls else top, acc[2])
                acc[3] = jnp.where(sel, pltpu.roll(bot, ls, 1) if ls else bot, acc[3])
        right_ref[g, :rows] = acc[0]
        right_ref[g, rows:] = acc[1]
        left_ref[g, :rows] = acc[2]
        left_ref[g, rows:] = acc[3]
        return carry

    lax.fori_loop(0, right_ref.shape[0], body, 0)


def _yunpack_kernel(first_static, chans_ref, xh_ref, right_ref, left_ref, yh_ref, se_ref):
    rows, cols = chans_ref.shape[1:]
    half = rows // 2
    group = cols // half
    lane = lax.broadcasted_iota(jnp.int32, (2 * rows, cols), 1)

    def body(g, carry):
        r = right_ref[g]
        l = left_ref[g]
        for q in range(group):
            rs = (cols - half * q) % cols
            ls = (cols - half - half * q) % cols
            yh = jnp.where(lane < half, pltpu.roll(r, rs, 1) if rs else r,
                           jnp.where(lane >= cols - half, pltpu.roll(l, ls, 1) if ls else l, 0.0))
            yh_ref[g * group + q] = yh
        return carry

    lax.fori_loop(0, right_ref.shape[0], body, 0)
    for c in range(se_ref.shape[0]):
        se_ref[c, :rows, :cols] = chans_ref[first_static + c]
        se_ref[c, rows:, :cols] = xh_ref[first_static + c]
        se_ref[c, :, cols:] = yh_ref[first_static + c]


def extend(chans, first_static, n_statics):
    up_x, down_x = _pairs("gx")
    up_y, down_y = _pairs("gy")
    channels, rows, cols = chans.shape
    halo = rows // 2
    group = cols // halo
    pairs = jax.ShapeDtypeStruct((channels // 2, rows, cols), jnp.float32)
    lo, hi = pl.pallas_call(
        _xpack_kernel, out_shape=[pairs, pairs],
        in_specs=_whole([chans]), out_specs=_whole([0, 0]))(chans)
    below = lax.ppermute(lo, "gx", down_x)
    above = lax.ppermute(hi, "gx", up_x)
    packed = jax.ShapeDtypeStruct((channels // group, 2 * rows, cols), jnp.float32)
    xh, right, left = pl.pallas_call(
        _ypack_kernel,
        out_shape=[jax.ShapeDtypeStruct(chans.shape, jnp.float32), packed, packed],
        in_specs=_whole([0, 0, 0]), out_specs=_whole([0, 0, 0]))(chans, below, above)
    right = lax.ppermute(right, "gy", down_y)
    left = lax.ppermute(left, "gy", up_y)
    yh, statics = pl.pallas_call(
        functools.partial(_yunpack_kernel, first_static),
        out_shape=[jax.ShapeDtypeStruct((channels, 2 * rows, cols), jnp.float32),
                   jax.ShapeDtypeStruct((n_statics, 2 * rows, 2 * cols), jnp.float32)],
        in_specs=_whole([0, 0, 0, 0]), out_specs=_whole([0, 0]))(chans, xh, right, left)
    return xh, yh, statics


def local(pixel_adjoint, pixel_owner, pixel_column, pixel_level, wind_x, wind_y,
          diffusivity, prior_emission, region_map):
    gx_n = lax.axis_size("gx")
    gy_n = lax.axis_size("gy")
    devices = gx_n * gy_n
    steps, rows, cols = wind_x.shape
    levels = diffusivity.shape[0] + 1
    species = prior_emission.shape[0]
    kernel = pixel_adjoint.shape[1] // species
    pixels = pixel_adjoint.shape[2]
    capacity = 2 * pixels // devices
    cells = rows * cols
    slots = devices * capacity
    halo = rows // 2
    assert steps <= halo
    lanes = 2 * cols
    ext_rows = 2 * rows

    owners = pixel_owner[:, :, 0]
    matches = (owners[:, :, None] == jnp.arange(devices, dtype=jnp.int32)).astype(jnp.int32)
    rank = jnp.sum(jnp.cumsum(matches, axis=1) * matches, axis=2) - 1
    position = owners * capacity + rank
    rows_out = jnp.concatenate(
        [pixel_adjoint, pixel_column.astype(jnp.float32)[:, None, :],
         pixel_level.astype(jnp.float32)[:, None, :]], axis=1)
    place = (position[:, :, None] == jnp.arange(slots, dtype=jnp.int32)).astype(jnp.float32)
    placed = jnp.einsum("kap,kpq->kaq", rows_out, place, precision=HI)
    received = lax.all_to_all(placed, ("gx", "gy"), 2, 2, tiled=True)

    payload = received[:, :species * kernel].reshape(steps, species, kernel, slots)
    column = jnp.round(received[:, species * kernel]).astype(jnp.int32)
    start = jnp.round(received[:, species * kernel + 1]).astype(jnp.int32)
    offset = jnp.arange(levels, dtype=jnp.int32)[None, :, None] - start[:, None, :]
    profile = jnp.zeros((steps, species, levels, slots), jnp.float32)
    for j in range(kernel):
        profile = profile + jnp.where((offset == j)[:, None], payload[:, :, j][:, :, None, :], 0.0)
    hits = (column[:, :, None] == jnp.arange(cells, dtype=jnp.int32)).astype(jnp.float32)
    forcing = jnp.einsum("ksq,kqc->ksc", profile.reshape(steps, species * levels, slots), hits,
                         precision=HI)

    n_f = steps * species * levels
    n_s = 2 * steps + levels - 1
    group = cols // halo
    channels = -(-(n_f + n_s) // group) * group
    chans = jnp.concatenate(
        [forcing.reshape(n_f, rows, cols), wind_x, wind_y, diffusivity,
         jnp.zeros((channels - n_f - n_s, rows, cols), jnp.float32)], axis=0)
    xh, yh, statics = extend(chans, n_f, n_s)

    gxi = lax.axis_index("gx")
    gyi = lax.axis_index("gy")
    r = jnp.arange(ext_rows, dtype=jnp.int32)[:, None]
    c = jnp.arange(lanes, dtype=jnp.int32)[None, :]
    grow = gxi * rows + jnp.where(r < rows + halo, r, r - ext_rows)
    ccol = jnp.where(c < cols + halo, c, c - lanes)
    gcol = gyi * cols + ccol
    inside = ((grow >= 0) & (grow < gx_n * rows) & (gcol >= 0) & (gcol < gy_n * cols)
              & ((c < cols + halo) | (c >= lanes - halo)))
    mask = inside.astype(jnp.float32)

    forced = None
    ratios = inverses = surface_sum = None
    for k in reversed(range(steps)):
        outs = step_call(k, steps, species, levels, forced, mask, statics, prior_emission,
                         ratios, inverses, surface_sum, chans, xh, yh)
        if k == steps - 1:
            ratios, inverses, forced, surface_sum = outs
        else:
            forced, surface_sum = outs
    adjoint = forced

    nreg = REG_DEV * devices
    member = (region_map.reshape(-1)[:, None] == jnp.arange(nreg, dtype=jnp.int32)).astype(jnp.float32)
    partial = jnp.dot(surface_sum.reshape(species, cells), member, precision=HI)
    per_dev = nreg // devices
    pieces = lax.all_to_all(partial.reshape(species, gx_n, gy_n, per_dev), "gy", 2, 2, tiled=True)
    pieces = lax.all_to_all(jnp.sum(pieces, axis=2), "gx", 1, 1, tiled=True)
    gradient = jnp.sum(pieces, axis=1)
    return adjoint, gradient


def solution(mesh):
    in_specs = (
        P(None, None, ("gx", "gy")),
        P(None, ("gx", "gy"), None),
        P(None, ("gx", "gy")),
        P(None, ("gx", "gy")),
        P(None, "gx", "gy"),
        P(None, "gx", "gy"),
        P(None, "gx", "gy"),
        P(None, "gx", "gy"),
        P("gx", "gy"),
    )
    out_specs = (P(None, None, "gx", "gy"), P(None, ("gx", "gy")))
    return jax.shard_map(local, mesh=mesh, in_specs=in_specs, out_specs=out_specs, check_vma=False)
```

```python
import functools

import jax
import jax.numpy as jnp
from jax import lax
from jax.experimental import pallas as pl
from jax.experimental.pallas import tpu as pltpu
from jax.sharding import PartitionSpec as P

HI = lax.Precision.HIGHEST
REG_DEV = 8


def _full(shape):
    nd = len(shape)
    return pl.BlockSpec(shape, lambda i, _n=nd: (0,) * _n)


def _step_kernel(k, steps, first, last, *refs):
    refs = list(refs)
    if first:
        own_ref, xh_ref, yh_ref = refs[:3]
        refs = refs[3:]
    else:
        forced_ref = refs.pop(0)
    mask_ref, se_ref, prior_ref = refs[:3]
    refs = refs[3:]
    if not first:
        ratio_in, inv_in, ss_ref = refs[:3]
        refs = refs[3:]
    if not last:
        nown_ref, nxh_ref, nyh_ref = refs[:3]
        refs = refs[3:]
    if first:
        ratio_ref, inv_ref = refs[:2]
        refs = refs[2:]
    else:
        ratio_ref, inv_ref = ratio_in, inv_in
    out_ref, ss_out_ref, red_ref = refs[:3]
    if first:
        forced_ref = refs[3]

    species, levels = ss_out_ref.shape[0], red_ref.shape[0]
    rows, lanes = red_ref.shape[1:]
    tr, tc = ss_out_ref.shape[1:]
    d0 = 2 * steps
    zero = jnp.zeros((rows, lanes), jnp.float32)
    inside = mask_ref[...] > 0.5

    if first:
        carried = zero
        for l in range(levels):
            below = se_ref[d0 + l - 1] if l > 0 else zero
            above = se_ref[d0 + l] if l < levels - 1 else zero
            inverse = 1.0 / (1.0 + below + above + below * carried)
            ratio = -above * inverse
            ratio_ref[l] = ratio
            inv_ref[l] = inverse
            carried = ratio
        for s in range(species):

            def assemble(l, carry):
                c = s * levels + l
                forced_ref[s, l, :tr, :tc] = own_ref[c]
                forced_ref[s, l, tr:, :tc] = xh_ref[c]
                forced_ref[s, l, :, tc:] = yh_ref[c]
                forced_ref[s, l] = jnp.where(inside, forced_ref[s, l], 0.0)
                return carry

            lax.fori_loop(0, levels, assemble, 0, unroll=4)

    wx = se_ref[k]
    wy = se_ref[steps + k]
    east = jnp.maximum(wx, 0.0)
    west = jnp.maximum(-wx, 0.0)
    north = jnp.maximum(wy, 0.0)
    south = jnp.maximum(-wy, 0.0)
    remain = 1.0 - (east + west + north + south)

    if last:
        _last_step(species, levels, tr, tc, forced_ref, east, west, north, south, remain,
                   se_ref, d0, inv_ref, ratio_ref, red_ref, out_ref, ss_ref, ss_out_ref,
                   prior_ref)
        return

    for s in range(species):

        def forward(l, reduced):
            f = forced_ref[s, l]
            from_east = pltpu.roll(east * f, rows - 1, 0)
            from_west = pltpu.roll(west * f, 1, 0)
            from_north = pltpu.roll(north * f, lanes - 1, 1)
            from_south = pltpu.roll(south * f, 1, 1)
            moved = f * remain
            moved = moved + from_east + from_west
            moved = moved + from_north + from_south
            below = jnp.where(l > 0, se_ref[d0 + jnp.maximum(l - 1, 0)], zero)
            reduced = (moved + below * reduced) * inv_ref[l]
            red_ref[l] = reduced
            return reduced

        lax.fori_loop(0, levels, forward, zero, unroll=4)

        def backward(i, result):
            l = levels - 1 - i
            c = s * levels + l
            result = red_ref[l] - ratio_ref[l] * result
            out_ref[s, l, :tr, :tc] = jnp.where(
                inside[:tr, :tc], result[:tr, :tc] + nown_ref[c], 0.0)
            out_ref[s, l, tr:, :tc] = jnp.where(
                inside[tr:, :tc], result[tr:, :tc] + nxh_ref[c], 0.0)
            out_ref[s, l, :, tc:] = jnp.where(
                inside[:, tc:], result[:, tc:] + nyh_ref[c], 0.0)
            return result

        surface = lax.fori_loop(0, levels, backward, zero, unroll=4)
        if first:
            ss_out_ref[s] = prior_ref[s] * surface[:tr, :tc]
        else:
            ss_out_ref[s] = ss_ref[s] + prior_ref[s] * surface[:tr, :tc]


def _last_step(species, levels, tr, tc, forced_ref, east, west, north, south, remain, se_ref,
               d0, inv_ref, ratio_ref, red_ref, out_ref, ss_ref, ss_out_ref, prior_ref):
    row = lax.broadcasted_iota(jnp.int32, (tr, tc), 0)
    lane = lax.broadcasted_iota(jnp.int32, (tr, tc), 1)
    last_row = row == tr - 1
    first_row = row == 0
    last_lane = lane == tc - 1
    first_lane = lane == 0
    e_a, e_b = east[:tr, :tc], east[tr:, :tc]
    w_a, w_b = west[:tr, :tc], west[tr:, :tc]
    n_a, n_c = north[:tr, :tc], north[:tr, tc:]
    s_a, s_c = south[:tr, :tc], south[:tr, tc:]
    rem = remain[:tr, :tc]
    zero = jnp.zeros((tr, tc), jnp.float32)
    for s in range(species):

        def forward(l, reduced):
            f_a = forced_ref[s, l, :tr, :tc]
            f_b = forced_ref[s, l, tr:, :tc]
            f_c = forced_ref[s, l, :tr, tc:]
            from_east = jnp.where(last_row, pltpu.roll(e_b * f_b, tr - 1, 0),
                                  pltpu.roll(e_a * f_a, tr - 1, 0))
            from_west = jnp.where(first_row, pltpu.roll(w_b * f_b, 1, 0),
                                  pltpu.roll(w_a * f_a, 1, 0))
            from_north = jnp.where(last_lane, pltpu.roll(n_c * f_c, tc - 1, 1),
                                   pltpu.roll(n_a * f_a, tc - 1, 1))
            from_south = jnp.where(first_lane, pltpu.roll(s_c * f_c, 1, 1),
                                   pltpu.roll(s_a * f_a, 1, 1))
            moved = f_a * rem
            moved = moved + from_east + from_west
            moved = moved + from_north + from_south
            below = jnp.where(l > 0, se_ref[d0 + jnp.maximum(l - 1, 0), :tr, :tc], zero)
            reduced = (moved + below * reduced) * inv_ref[l, :tr, :tc]
            red_ref[l, :tr, :tc] = reduced
            return reduced

        lax.fori_loop(0, levels, forward, zero, unroll=4)

        def backward(i, result):
            l = levels - 1 - i
            result = red_ref[l, :tr, :tc] - ratio_ref[l, :tr, :tc] * result
            out_ref[s, l] = result
            return result

        surface = lax.fori_loop(0, levels, backward, zero, unroll=4)
        ss_out_ref[s] = ss_ref[s] + prior_ref[s] * surface


def step_call(k, steps, species, levels, forced, mask, statics, prior, ratios, inverses,
              surface_sum, chans, xh, yh):
    first = k == steps - 1
    last = k == 0
    rows, cols = chans.shape[1:]
    rows_e, lanes = mask.shape
    planes = species * levels
    ext = jax.ShapeDtypeStruct((species, levels, rows_e, lanes), jnp.float32)
    tile = jax.ShapeDtypeStruct((species, levels, rows, cols), jnp.float32)
    plane = jax.ShapeDtypeStruct((levels, rows_e, lanes), jnp.float32)
    surf = jax.ShapeDtypeStruct(prior.shape, jnp.float32)

    def blocks(step):
        return [pl.BlockSpec((planes,) + a.shape[1:], lambda i, _s=step: (_s, 0, 0))
                for a in (chans, xh, yh)]

    in_specs, args = [], []
    if first:
        in_specs += blocks(k)
        args += [chans, xh, yh]
    else:
        in_specs.append(_full(forced.shape))
        args.append(forced)
    for a in (mask, statics, prior):
        in_specs.append(_full(a.shape))
        args.append(a)
    if not first:
        for a in (ratios, inverses, surface_sum):
            in_specs.append(_full(a.shape))
            args.append(a)
    if not last:
        in_specs += blocks(k - 1)
        args += [chans, xh, yh]
    out_shape = [plane, plane] if first else []
    out_shape += [tile if last else ext, surf]
    scratch = [pltpu.VMEM((levels, rows_e, lanes), jnp.float32)]
    if first:
        scratch.append(pltpu.VMEM((species, levels, rows_e, lanes), jnp.float32))
    return pl.pallas_call(
        functools.partial(_step_kernel, k, steps, first, last),
        grid=(1,),
        in_specs=in_specs,
        out_specs=[_full(o.shape) for o in out_shape],
        out_shape=out_shape,
        scratch_shapes=scratch,
    )(*args)


def _pairs(axis):
    n = lax.axis_size(axis)
    return [(i, i + 1) for i in range(n - 1)], [(i + 1, i) for i in range(n - 1)]


def _whole(shapes):
    return [pl.BlockSpec(memory_space=pltpu.VMEM) for _ in shapes]


def _xpack_kernel(chans_ref, lo_ref, hi_ref):
    rows = chans_ref.shape[1]
    half = rows // 2
    row = lax.broadcasted_iota(jnp.int32, chans_ref.shape[1:], 0)

    def body(i, carry):
        a = chans_ref[2 * i]
        b = chans_ref[2 * i + 1]
        lo_ref[i] = jnp.where(row < half, a, pltpu.roll(b, half, 0))
        hi_ref[i] = jnp.where(row < half, pltpu.roll(a, half, 0), b)
        return carry

    lax.fori_loop(0, lo_ref.shape[0], body, 0, unroll=4)


def _ypack_kernel(chans_ref, below_ref, above_ref, xh_ref, right_ref, left_ref):
    rows, cols = chans_ref.shape[1:]
    half = rows // 2
    group = cols // half
    row = lax.broadcasted_iota(jnp.int32, (rows, cols), 0)
    lane = lax.broadcasted_iota(jnp.int32, (rows, cols), 1)
    zero = jnp.zeros((rows, cols), jnp.float32)

    def body(g, carry):
        acc = [zero, zero, zero, zero]
        for q2 in range(group // 2):
            i = g * (group // 2) + q2
            b = below_ref[i]
            a = above_ref[i]
            xh0 = jnp.where(row < half, b, pltpu.roll(a, half, 0))
            xh1 = jnp.where(row < half, pltpu.roll(b, half, 0), a)
            xh_ref[2 * i] = xh0
            xh_ref[2 * i + 1] = xh1
            for off, top, bot in ((0, chans_ref[2 * i], xh0), (1, chans_ref[2 * i + 1], xh1)):
                q = 2 * q2 + off
                sel = (lane >= half * q) & (lane < half * q + half)
                rs = (half * q) % cols
                ls = (half * q + half) % cols
                acc[0] = jnp.where(sel, pltpu.roll(top, rs, 1) if rs else top, acc[0])
                acc[1] = jnp.where(sel, pltpu.roll(bot, rs, 1) if rs else bot, acc[1])
                acc[2] = jnp.where(sel, pltpu.roll(top, ls, 1) if ls else top, acc[2])
                acc[3] = jnp.where(sel, pltpu.roll(bot, ls, 1) if ls else bot, acc[3])
        right_ref[g, :rows] = acc[0]
        right_ref[g, rows:] = acc[1]
        left_ref[g, :rows] = acc[2]
        left_ref[g, rows:] = acc[3]
        return carry

    lax.fori_loop(0, right_ref.shape[0], body, 0)


def _yunpack_kernel(first_static, chans_ref, xh_ref, right_ref, left_ref, yh_ref, se_ref):
    rows, cols = chans_ref.shape[1:]
    half = rows // 2
    group = cols // half
    lane = lax.broadcasted_iota(jnp.int32, (2 * rows, cols), 1)

    def body(g, carry):
        r = right_ref[g]
        l = left_ref[g]
        for q in range(group):
            rs = (cols - half * q) % cols
            ls = (cols - half - half * q) % cols
            yh = jnp.where(lane < half, pltpu.roll(r, rs, 1) if rs else r,
                           jnp.where(lane >= cols - half, pltpu.roll(l, ls, 1) if ls else l, 0.0))
            yh_ref[g * group + q] = yh
        return carry

    lax.fori_loop(0, right_ref.shape[0], body, 0)
    for c in range(se_ref.shape[0]):
        se_ref[c, :rows, :cols] = chans_ref[first_static + c]
        se_ref[c, rows:, :cols] = xh_ref[first_static + c]
        se_ref[c, :, cols:] = yh_ref[first_static + c]


def extend(chans, first_static, n_statics):
    up_x, down_x = _pairs("gx")
    up_y, down_y = _pairs("gy")
    channels, rows, cols = chans.shape
    halo = rows // 2
    group = cols // halo
    pairs = jax.ShapeDtypeStruct((channels // 2, rows, cols), jnp.float32)
    lo, hi = pl.pallas_call(
        _xpack_kernel, out_shape=[pairs, pairs],
        in_specs=_whole([chans]), out_specs=_whole([0, 0]))(chans)
    below = lax.ppermute(lo, "gx", down_x)
    above = lax.ppermute(hi, "gx", up_x)
    packed = jax.ShapeDtypeStruct((channels // group, 2 * rows, cols), jnp.float32)
    xh, right, left = pl.pallas_call(
        _ypack_kernel,
        out_shape=[jax.ShapeDtypeStruct(chans.shape, jnp.float32), packed, packed],
        in_specs=_whole([0, 0, 0]), out_specs=_whole([0, 0, 0]))(chans, below, above)
    right = lax.ppermute(right, "gy", down_y)
    left = lax.ppermute(left, "gy", up_y)
    yh, statics = pl.pallas_call(
        functools.partial(_yunpack_kernel, first_static),
        out_shape=[jax.ShapeDtypeStruct((channels, 2 * rows, cols), jnp.float32),
                   jax.ShapeDtypeStruct((n_statics, 2 * rows, 2 * cols), jnp.float32)],
        in_specs=_whole([0, 0, 0, 0]), out_specs=_whole([0, 0]))(chans, xh, right, left)
    return xh, yh, statics


def local(pixel_adjoint, pixel_owner, pixel_column, pixel_level, wind_x, wind_y,
          diffusivity, prior_emission, region_map):
    gx_n = lax.axis_size("gx")
    gy_n = lax.axis_size("gy")
    devices = gx_n * gy_n
    steps, rows, cols = wind_x.shape
    levels = diffusivity.shape[0] + 1
    species = prior_emission.shape[0]
    kernel = pixel_adjoint.shape[1] // species
    pixels = pixel_adjoint.shape[2]
    capacity = 2 * pixels // devices
    cells = rows * cols
    slots = devices * capacity
    halo = rows // 2
    assert steps <= halo
    lanes = 2 * cols
    ext_rows = 2 * rows

    owners = pixel_owner[:, :, 0]
    matches = (owners[:, :, None] == jnp.arange(devices, dtype=jnp.int32)).astype(jnp.int32)
    rank = jnp.sum(jnp.cumsum(matches, axis=1) * matches, axis=2) - 1
    position = owners * capacity + rank
    rows_out = jnp.concatenate(
        [pixel_adjoint, pixel_column.astype(jnp.float32)[:, None, :],
         pixel_level.astype(jnp.float32)[:, None, :]], axis=1)
    place = (position[:, :, None] == jnp.arange(slots, dtype=jnp.int32)).astype(jnp.float32)
    placed = jnp.einsum("kap,kpq->kaq", rows_out, place, precision=HI)
    received = lax.all_to_all(placed, ("gx", "gy"), 2, 2, tiled=True)

    payload = received[:, :species * kernel].reshape(steps, species, kernel, slots)
    column = jnp.round(received[:, species * kernel]).astype(jnp.int32)
    start = jnp.round(received[:, species * kernel + 1]).astype(jnp.int32)
    offset = jnp.arange(levels, dtype=jnp.int32)[None, :, None] - start[:, None, :]
    profile = jnp.zeros((steps, species, levels, slots), jnp.float32)
    for j in range(kernel):
        profile = profile + jnp.where((offset == j)[:, None], payload[:, :, j][:, :, None, :], 0.0)
    hits = (column[:, :, None] == jnp.arange(cells, dtype=jnp.int32)).astype(jnp.float32)
    forcing = jnp.einsum("ksq,kqc->ksc", profile.reshape(steps, species * levels, slots), hits,
                         precision=HI)

    n_f = steps * species * levels
    n_s = 2 * steps + levels - 1
    group = cols // halo
    channels = -(-(n_f + n_s) // group) * group
    chans = jnp.concatenate(
        [forcing.reshape(n_f, rows, cols), wind_x, wind_y, diffusivity,
         jnp.zeros((channels - n_f - n_s, rows, cols), jnp.float32)], axis=0)
    xh, yh, statics = extend(chans, n_f, n_s)

    gxi = lax.axis_index("gx")
    gyi = lax.axis_index("gy")
    r = jnp.arange(ext_rows, dtype=jnp.int32)[:, None]
    c = jnp.arange(lanes, dtype=jnp.int32)[None, :]
    grow = gxi * rows + jnp.where(r < rows + halo, r, r - ext_rows)
    ccol = jnp.where(c < cols + halo, c, c - lanes)
    gcol = gyi * cols + ccol
    inside = ((grow >= 0) & (grow < gx_n * rows) & (gcol >= 0) & (gcol < gy_n * cols)
              & ((c < cols + halo) | (c >= lanes - halo)))
    mask = inside.astype(jnp.float32)

    forced = None
    ratios = inverses = surface_sum = None
    for k in reversed(range(steps)):
        outs = step_call(k, steps, species, levels, forced, mask, statics, prior_emission,
                         ratios, inverses, surface_sum, chans, xh, yh)
        if k == steps - 1:
            ratios, inverses, forced, surface_sum = outs
        else:
            forced, surface_sum = outs
    adjoint = forced

    nreg = REG_DEV * devices
    member = (region_map.reshape(-1)[:, None] == jnp.arange(nreg, dtype=jnp.int32)).astype(jnp.float32)
    partial = jnp.dot(surface_sum.reshape(species, cells), member, precision=HI)
    pieces = lax.all_to_all(partial.reshape(species, devices, nreg // devices), ("gx", "gy"), 1, 1,
                            tiled=True)
    gradient = jnp.sum(pieces, axis=1)
    return adjoint, gradient


def solution(mesh):
    in_specs = (
        P(None, None, ("gx", "gy")),
        P(None, ("gx", "gy"), None),
        P(None, ("gx", "gy")),
        P(None, ("gx", "gy")),
        P(None, "gx", "gy"),
        P(None, "gx", "gy"),
        P(None, "gx", "gy"),
        P(None, "gx", "gy"),
        P("gx", "gy"),
    )
    out_specs = (P(None, None, "gx", "gy"), P(None, ("gx", "gy")))
    return jax.shard_map(local, mesh=mesh, in_specs=in_specs, out_specs=out_specs, check_vma=False)
```

```python
import functools

import jax
import jax.numpy as jnp
from jax import lax
from jax.experimental import pallas as pl
from jax.experimental.pallas import tpu as pltpu
from jax.sharding import PartitionSpec as P

HI = lax.Precision.HIGHEST
REG_DEV = 8


def _full(shape):
    nd = len(shape)
    return pl.BlockSpec(shape, lambda i, _n=nd: (0,) * _n)


def _unpack(r, l, q, cols, half):
    lane = lax.broadcasted_iota(jnp.int32, r.shape, 1)
    rs = (cols - half * q) % cols
    ls = (cols - half - half * q) % cols
    return jnp.where(lane < half, pltpu.roll(r, rs, 1) if rs else r,
                     jnp.where(lane >= cols - half, pltpu.roll(l, ls, 1) if ls else l, 0.0))


def _steps_kernel(steps, species, levels, first_static, n_statics,
                  right_ref, left_ref, mask_ref, prior_ref, chans_hbm, xh_hbm,
                  adj_ref, ss_ref,
                  own_buf, xhb_buf, yh_buf, st_own, st_xh, se_ref, state_ref, red_ref,
                  ratio_ref, inv_ref, sems):
    planes = species * levels
    rows, lanes = mask_ref.shape
    tr, tc = adj_ref.shape[2:]
    half = tr // 2
    group = tc // half
    d0 = 2 * steps

    statics_o = pltpu.make_async_copy(chans_hbm.at[pl.ds(first_static, n_statics)], st_own,
                                      sems.at[0])
    statics_x = pltpu.make_async_copy(xh_hbm.at[pl.ds(first_static, n_statics)], st_xh,
                                      sems.at[1])
    statics_o.start()
    statics_x.start()
    loads = {}
    for k in reversed(range(steps)):
        co = pltpu.make_async_copy(chans_hbm.at[pl.ds(k * planes, planes)], own_buf.at[k],
                                   sems.at[2 + 2 * k])
        cx = pltpu.make_async_copy(xh_hbm.at[pl.ds(k * planes, planes)], xhb_buf.at[k],
                                   sems.at[3 + 2 * k])
        co.start()
        cx.start()
        loads[k] = (co, cx)

    n_fgroups = first_static // group

    def unpack_group(g, carry):
        r = right_ref[g]
        l = left_ref[g]
        for q in range(group):
            yh_buf[g * group + q] = _unpack(r, l, q, tc, half)
        return carry

    lax.fori_loop(0, n_fgroups, unpack_group, 0)
    for c in range(n_statics):
        ch = first_static + c
        se_ref[c, :, tc:] = _unpack(right_ref[ch // group], left_ref[ch // group], ch % group,
                                    tc, half)
    statics_o.wait()
    statics_x.wait()

    def assemble_static(c, carry):
        se_ref[c, :tr, :tc] = st_own[c]
        se_ref[c, tr:, :tc] = st_xh[c]
        return carry

    lax.fori_loop(0, n_statics, assemble_static, 0)

    zero = jnp.zeros((rows, lanes), jnp.float32)
    inside = mask_ref[...] > 0.5
    carried = zero
    for l in range(levels):
        below = se_ref[d0 + l - 1] if l > 0 else zero
        above = se_ref[d0 + l] if l < levels - 1 else zero
        inverse = 1.0 / (1.0 + below + above + below * carried)
        ratio = -above * inverse
        ratio_ref[l] = ratio
        inv_ref[l] = inverse
        carried = ratio

    for k in reversed(range(steps)):
        first = k == steps - 1
        last = k == 0
        if first:
            loads[k][0].wait()
            loads[k][1].wait()
            for s in range(species):

                def assemble(l, carry, s=s, k=k):
                    c = s * levels + l
                    state_ref[s, l, :tr, :tc] = own_buf[k, c]
                    state_ref[s, l, tr:, :tc] = xhb_buf[k, c]
                    state_ref[s, l, :, tc:] = yh_buf[k * planes + c]
                    state_ref[s, l] = jnp.where(inside, state_ref[s, l], 0.0)
                    return carry

                lax.fori_loop(0, levels, assemble, 0, unroll=4)
        if not last:
            loads[k - 1][0].wait()
            loads[k - 1][1].wait()

        wx = se_ref[k]
        wy = se_ref[steps + k]
        east = jnp.maximum(wx, 0.0)
        west = jnp.maximum(-wx, 0.0)
        north = jnp.maximum(wy, 0.0)
        south = jnp.maximum(-wy, 0.0)
        remain = 1.0 - (east + west + north + south)
        if last:
            _last_step(species, levels, tr, tc, state_ref, east, west, north, south, remain,
                       se_ref, d0, inv_ref, ratio_ref, red_ref, adj_ref, ss_ref, prior_ref)
            continue

        for s in range(species):

            def forward(l, reduced, s=s):
                f = state_ref[s, l]
                from_east = pltpu.roll(east * f, rows - 1, 0)
                from_west = pltpu.roll(west * f, 1, 0)
                from_north = pltpu.roll(north * f, lanes - 1, 1)
                from_south = pltpu.roll(south * f, 1, 1)
                moved = f * remain
                moved = moved + from_east + from_west
                moved = moved + from_north + from_south
                below = jnp.where(l > 0, se_ref[d0 + jnp.maximum(l - 1, 0)], zero)
                reduced = (moved + below * reduced) * inv_ref[l]
                red_ref[l] = reduced
                return reduced

            lax.fori_loop(0, levels, forward, zero, unroll=4)

            def backward(i, result, s=s, k=k):
                l = levels - 1 - i
                c = s * levels + l
                result = red_ref[l] - ratio_ref[l] * result
                state_ref[s, l, :tr, :tc] = jnp.where(
                    inside[:tr, :tc], result[:tr, :tc] + own_buf[k - 1, c], 0.0)
                state_ref[s, l, tr:, :tc] = jnp.where(
                    inside[tr:, :tc], result[tr:, :tc] + xhb_buf[k - 1, c], 0.0)
                state_ref[s, l, :, tc:] = jnp.where(
                    inside[:, tc:], result[:, tc:] + yh_buf[(k - 1) * planes + c], 0.0)
                return result

            surface = lax.fori_loop(0, levels, backward, zero, unroll=4)
            if first:
                ss_ref[s] = prior_ref[s] * surface[:tr, :tc]
            else:
                ss_ref[s] = ss_ref[s] + prior_ref[s] * surface[:tr, :tc]


def _last_step(species, levels, tr, tc, forced_ref, east, west, north, south, remain, se_ref,
               d0, inv_ref, ratio_ref, red_ref, out_ref, ss_ref, prior_ref):
    row = lax.broadcasted_iota(jnp.int32, (tr, tc), 0)
    lane = lax.broadcasted_iota(jnp.int32, (tr, tc), 1)
    last_row = row == tr - 1
    first_row = row == 0
    last_lane = lane == tc - 1
    first_lane = lane == 0
    e_a, e_b = east[:tr, :tc], east[tr:, :tc]
    w_a, w_b = west[:tr, :tc], west[tr:, :tc]
    n_a, n_c = north[:tr, :tc], north[:tr, tc:]
    s_a, s_c = south[:tr, :tc], south[:tr, tc:]
    rem = remain[:tr, :tc]
    zero = jnp.zeros((tr, tc), jnp.float32)
    for s in range(species):

        def forward(l, reduced, s=s):
            f_a = forced_ref[s, l, :tr, :tc]
            f_b = forced_ref[s, l, tr:, :tc]
            f_c = forced_ref[s, l, :tr, tc:]
            from_east = jnp.where(last_row, pltpu.roll(e_b * f_b, tr - 1, 0),
                                  pltpu.roll(e_a * f_a, tr - 1, 0))
            from_west = jnp.where(first_row, pltpu.roll(w_b * f_b, 1, 0),
                                  pltpu.roll(w_a * f_a, 1, 0))
            from_north = jnp.where(last_lane, pltpu.roll(n_c * f_c, tc - 1, 1),
                                   pltpu.roll(n_a * f_a, tc - 1, 1))
            from_south = jnp.where(first_lane, pltpu.roll(s_c * f_c, 1, 1),
                                   pltpu.roll(s_a * f_a, 1, 1))
            moved = f_a * rem
            moved = moved + from_east + from_west
            moved = moved + from_north + from_south
            below = jnp.where(l > 0, se_ref[d0 + jnp.maximum(l - 1, 0), :tr, :tc], zero)
            reduced = (moved + below * reduced) * inv_ref[l, :tr, :tc]
            red_ref[l, :tr, :tc] = reduced
            return reduced

        lax.fori_loop(0, levels, forward, zero, unroll=4)

        def backward(i, result, s=s):
            l = levels - 1 - i
            result = red_ref[l, :tr, :tc] - ratio_ref[l, :tr, :tc] * result
            out_ref[s, l] = result
            return result

        surface = lax.fori_loop(0, levels, backward, zero, unroll=4)
        ss_ref[s] = ss_ref[s] + prior_ref[s] * surface


def steps_call(steps, species, levels, first_static, n_statics, right, left, mask, prior,
               chans, xh):
    channels, tr, tc = chans.shape
    rows, lanes = mask.shape
    planes = species * levels
    vmem = pl.BlockSpec(memory_space=pltpu.VMEM)
    anyspace = pl.BlockSpec(memory_space=pl.ANY)
    return pl.pallas_call(
        functools.partial(_steps_kernel, steps, species, levels, first_static, n_statics),
        in_specs=[vmem, vmem, vmem, vmem, anyspace, anyspace],
        out_specs=[vmem, vmem],
        out_shape=[jax.ShapeDtypeStruct((species, levels, tr, tc), jnp.float32),
                   jax.ShapeDtypeStruct(prior.shape, jnp.float32)],
        scratch_shapes=[
            pltpu.VMEM((steps, planes, tr, tc), jnp.float32),
            pltpu.VMEM((steps, planes, tr, tc), jnp.float32),
            pltpu.VMEM((first_static, rows, tc), jnp.float32),
            pltpu.VMEM((n_statics, tr, tc), jnp.float32),
            pltpu.VMEM((n_statics, tr, tc), jnp.float32),
            pltpu.VMEM((n_statics, rows, lanes), jnp.float32),
            pltpu.VMEM((species, levels, rows, lanes), jnp.float32),
            pltpu.VMEM((levels, rows, lanes), jnp.float32),
            pltpu.VMEM((levels, rows, lanes), jnp.float32),
            pltpu.VMEM((levels, rows, lanes), jnp.float32),
            pltpu.SemaphoreType.DMA((2 + 2 * steps,)),
        ],
        compiler_params=pltpu.CompilerParams(vmem_limit_bytes=48 * 1024 * 1024),
    )(right, left, mask, prior, chans, xh)


def _pairs(axis):
    n = lax.axis_size(axis)
    return [(i, i + 1) for i in range(n - 1)], [(i + 1, i) for i in range(n - 1)]


def _whole(shapes):
    return [pl.BlockSpec(memory_space=pltpu.VMEM) for _ in shapes]


def _xpack_kernel(chans_ref, lo_ref, hi_ref):
    rows = chans_ref.shape[1]
    half = rows // 2
    row = lax.broadcasted_iota(jnp.int32, chans_ref.shape[1:], 0)

    def body(i, carry):
        a = chans_ref[2 * i]
        b = chans_ref[2 * i + 1]
        lo_ref[i] = jnp.where(row < half, a, pltpu.roll(b, half, 0))
        hi_ref[i] = jnp.where(row < half, pltpu.roll(a, half, 0), b)
        return carry

    lax.fori_loop(0, lo_ref.shape[0], body, 0, unroll=4)


def _ypack_kernel(chans_ref, below_ref, above_ref, xh_ref, right_ref, left_ref):
    rows, cols = chans_ref.shape[1:]
    half = rows // 2
    group = cols // half
    row = lax.broadcasted_iota(jnp.int32, (rows, cols), 0)
    lane = lax.broadcasted_iota(jnp.int32, (rows, cols), 1)
    zero = jnp.zeros((rows, cols), jnp.float32)

    def body(g, carry):
        acc = [zero, zero, zero, zero]
        for q2 in range(group // 2):
            i = g * (group // 2) + q2
            b = below_ref[i]
            a = above_ref[i]
            xh0 = jnp.where(row < half, b, pltpu.roll(a, half, 0))
            xh1 = jnp.where(row < half, pltpu.roll(b, half, 0), a)
            xh_ref[2 * i] = xh0
            xh_ref[2 * i + 1] = xh1
            for off, top, bot in ((0, chans_ref[2 * i], xh0), (1, chans_ref[2 * i + 1], xh1)):
                q = 2 * q2 + off
                sel = (lane >= half * q) & (lane < half * q + half)
                rs = (half * q) % cols
                ls = (half * q + half) % cols
                acc[0] = jnp.where(sel, pltpu.roll(top, rs, 1) if rs else top, acc[0])
                acc[1] = jnp.where(sel, pltpu.roll(bot, rs, 1) if rs else bot, acc[1])
                acc[2] = jnp.where(sel, pltpu.roll(top, ls, 1) if ls else top, acc[2])
                acc[3] = jnp.where(sel, pltpu.roll(bot, ls, 1) if ls else bot, acc[3])
        right_ref[g, :rows] = acc[0]
        right_ref[g, rows:] = acc[1]
        left_ref[g, :rows] = acc[2]
        left_ref[g, rows:] = acc[3]
        return carry

    lax.fori_loop(0, right_ref.shape[0], body, 0)


def extend(chans, first_static, n_statics):
    up_x, down_x = _pairs("gx")
    up_y, down_y = _pairs("gy")
    channels, rows, cols = chans.shape
    halo = rows // 2
    group = cols // halo
    pairs = jax.ShapeDtypeStruct((channels // 2, rows, cols), jnp.float32)
    lo, hi = pl.pallas_call(
        _xpack_kernel, out_shape=[pairs, pairs],
        in_specs=_whole([chans]), out_specs=_whole([0, 0]))(chans)
    below = lax.ppermute(lo, "gx", down_x)
    above = lax.ppermute(hi, "gx", up_x)
    packed = jax.ShapeDtypeStruct((channels // group, 2 * rows, cols), jnp.float32)
    xh, right, left = pl.pallas_call(
        _ypack_kernel,
        out_shape=[jax.ShapeDtypeStruct(chans.shape, jnp.float32), packed, packed],
        in_specs=_whole([0, 0, 0]), out_specs=_whole([0, 0, 0]))(chans, below, above)
    right = lax.ppermute(right, "gy", down_y)
    left = lax.ppermute(left, "gy", up_y)
    return xh, right, left


def local(pixel_adjoint, pixel_owner, pixel_column, pixel_level, wind_x, wind_y,
          diffusivity, prior_emission, region_map):
    gx_n = lax.axis_size("gx")
    gy_n = lax.axis_size("gy")
    devices = gx_n * gy_n
    steps, rows, cols = wind_x.shape
    levels = diffusivity.shape[0] + 1
    species = prior_emission.shape[0]
    kernel = pixel_adjoint.shape[1] // species
    pixels = pixel_adjoint.shape[2]
    capacity = 2 * pixels // devices
    cells = rows * cols
    slots = devices * capacity
    halo = rows // 2
    assert steps <= halo
    lanes = 2 * cols
    ext_rows = 2 * rows

    owners = pixel_owner[:, :, 0]
    matches = (owners[:, :, None] == jnp.arange(devices, dtype=jnp.int32)).astype(jnp.int32)
    rank = jnp.sum(jnp.cumsum(matches, axis=1) * matches, axis=2) - 1
    position = owners * capacity + rank
    rows_out = jnp.concatenate(
        [pixel_adjoint, pixel_column.astype(jnp.float32)[:, None, :],
         pixel_level.astype(jnp.float32)[:, None, :]], axis=1)
    place = (position[:, :, None] == jnp.arange(slots, dtype=jnp.int32)).astype(jnp.float32)
    placed = jnp.einsum("kap,kpq->kaq", rows_out, place, precision=HI)
    received = lax.all_to_all(placed, ("gx", "gy"), 2, 2, tiled=True)

    payload = received[:, :species * kernel].reshape(steps, species, kernel, slots)
    column = jnp.round(received[:, species * kernel]).astype(jnp.int32)
    start = jnp.round(received[:, species * kernel + 1]).astype(jnp.int32)
    offset = jnp.arange(levels, dtype=jnp.int32)[None, :, None] - start[:, None, :]
    profile = jnp.zeros((steps, species, levels, slots), jnp.float32)
    for j in range(kernel):
        profile = profile + jnp.where((offset == j)[:, None], payload[:, :, j][:, :, None, :], 0.0)
    hits = (column[:, :, None] == jnp.arange(cells, dtype=jnp.int32)).astype(jnp.float32)
    forcing = jnp.einsum("ksq,kqc->ksc", profile.reshape(steps, species * levels, slots), hits,
                         precision=HI)

    n_f = steps * species * levels
    n_s = 2 * steps + levels - 1
    group = cols // halo
    channels = -(-(n_f + n_s) // group) * group
    chans = jnp.concatenate(
        [forcing.reshape(n_f, rows, cols), wind_x, wind_y, diffusivity,
         jnp.zeros((channels - n_f - n_s, rows, cols), jnp.float32)], axis=0)
    xh, right, left = extend(chans, n_f, n_s)

    gxi = lax.axis_index("gx")
    gyi = lax.axis_index("gy")
    r = jnp.arange(ext_rows, dtype=jnp.int32)[:, None]
    c = jnp.arange(lanes, dtype=jnp.int32)[None, :]
    grow = gxi * rows + jnp.where(r < rows + halo, r, r - ext_rows)
    ccol = jnp.where(c < cols + halo, c, c - lanes)
    gcol = gyi * cols + ccol
    inside = ((grow >= 0) & (grow < gx_n * rows) & (gcol >= 0) & (gcol < gy_n * cols)
              & ((c < cols + halo) | (c >= lanes - halo)))
    mask = inside.astype(jnp.float32)

    adjoint, surface_sum = steps_call(steps, species, levels, n_f, n_s, right, left, mask,
                                      prior_emission, chans, xh)

    nreg = REG_DEV * devices
    member = (region_map.reshape(-1)[:, None] == jnp.arange(nreg, dtype=jnp.int32)).astype(jnp.float32)
    partial = jnp.dot(surface_sum.reshape(species, cells), member, precision=HI)
    pieces = lax.all_to_all(partial.reshape(species, devices, nreg // devices), ("gx", "gy"), 1, 1,
                            tiled=True)
    gradient = jnp.sum(pieces, axis=1)
    return adjoint, gradient


def solution(mesh):
    in_specs = (
        P(None, None, ("gx", "gy")),
        P(None, ("gx", "gy"), None),
        P(None, ("gx", "gy")),
        P(None, ("gx", "gy")),
        P(None, "gx", "gy"),
        P(None, "gx", "gy"),
        P(None, "gx", "gy"),
        P(None, "gx", "gy"),
        P("gx", "gy"),
    )
    out_specs = (P(None, None, "gx", "gy"), P(None, ("gx", "gy")))
    return jax.shard_map(local, mesh=mesh, in_specs=in_specs, out_specs=out_specs, check_vma=False)
```

```python
import functools

import jax
import jax.numpy as jnp
from jax import lax
from jax.experimental import pallas as pl
from jax.experimental.pallas import tpu as pltpu
from jax.sharding import PartitionSpec as P

HI = lax.Precision.HIGHEST
REG_DEV = 8


def _full(shape):
    nd = len(shape)
    return pl.BlockSpec(shape, lambda i, _n=nd: (0,) * _n)


def _unpack(r, l, q, cols, half):
    lane = lax.broadcasted_iota(jnp.int32, r.shape, 1)
    rs = (cols - half * q) % cols
    ls = (cols - half - half * q) % cols
    return jnp.where(lane < half, pltpu.roll(r, rs, 1) if rs else r,
                     jnp.where(lane >= cols - half, pltpu.roll(l, ls, 1) if ls else l, 0.0))


def _exact_dot(a, b):
    dims = (((1,), (1,)), ((), ()))
    hi = a.astype(jnp.bfloat16)
    rest = a - hi.astype(jnp.float32)
    mid = rest.astype(jnp.bfloat16)
    lo = (rest - mid.astype(jnp.float32)).astype(jnp.bfloat16)
    out = lax.dot_general(hi, b, dims, preferred_element_type=jnp.float32)
    out = out + lax.dot_general(mid, b, dims, preferred_element_type=jnp.float32)
    return out + lax.dot_general(lo, b, dims, preferred_element_type=jnp.float32)


def _forcing_kernel(species, kernel, levels, own_ref, below_ref, above_ref,
                    tall_ref, right_ref, left_ref, lown_ref, lnb_ref):
    steps, _, slots = own_ref.shape
    tr2, tc = tall_ref.shape[2:]
    tr = tr2 // 2
    half = tr // 2
    group = tc // half
    n_pay = species * kernel
    lane_t = lax.broadcasted_iota(jnp.int32, (tc, slots), 0)
    row_i = lax.broadcasted_iota(jnp.int32, (tr, slots), 0)
    lev_i = lax.broadcasted_iota(jnp.int32, (levels, slots), 0)
    lane16 = lax.broadcasted_iota(jnp.int32, (tr2, tc), 1)
    right_ref[...] = jnp.zeros(right_ref.shape, jnp.float32)
    left_ref[...] = jnp.zeros(left_ref.shape, jnp.float32)
    for k in range(steps):
        hts = []
        for src, ref in enumerate((own_ref, below_ref, above_ref)):
            blk = ref[k]
            col = blk[n_pay:n_pay + 1].astype(jnp.int32)
            lev = blk[n_pay + 1:n_pay + 2].astype(jnp.int32)
            row_q = col // tc
            lane_q = col % tc
            if src == 1:
                row_q = jnp.where(row_q < half, row_q, -1)
            elif src == 2:
                row_q = jnp.where(row_q >= half, row_q, -1)
            rmask = row_i == row_q
            hts.append((lane_t == lane_q).astype(jnp.bfloat16))
            offset = lev_i - lev
            dst = lown_ref if src == 0 else lnb_ref
            c0 = 0 if src < 2 else slots
            for s in range(species):
                prof = jnp.zeros((levels, slots), jnp.float32)
                for j in range(kernel):
                    prof = prof + jnp.where(offset == j, blk[s * kernel + j:s * kernel + j + 1], 0.0)
                for l in range(levels):
                    c = s * levels + l
                    dst[c * tr:(c + 1) * tr, c0:c0 + slots] = jnp.where(
                        rmask, jnp.broadcast_to(prof[l:l + 1], (tr, slots)), 0.0)
        own = _exact_dot(lown_ref[...], hts[0])
        xh = _exact_dot(lnb_ref[...], jnp.concatenate([hts[1], hts[2]], axis=1))
        planes = own.shape[0] // tr
        tall_ref[k, :, :tr, :] = own.reshape(planes, tr, tc)
        tall_ref[k, :, tr:, :] = xh.reshape(planes, tr, tc)
        for c in range(planes):
            g, q = divmod(k * planes + c, group)
            plane = tall_ref[k, c]
            sel = (lane16 >= half * q) & (lane16 < half * q + half)
            rs = (half * q) % tc
            ls = (half * q + half) % tc
            right_ref[g] = jnp.where(sel, pltpu.roll(plane, rs, 1) if rs else plane, right_ref[g])
            left_ref[g] = jnp.where(sel, pltpu.roll(plane, ls, 1) if ls else plane, left_ref[g])


def forcing_call(species, kernel, levels, own, below, above, cols):
    steps, _, slots = own.shape
    tr = 8
    planes = species * levels
    group = cols // (tr // 2)
    packed = jax.ShapeDtypeStruct((steps * planes // group, 2 * tr, cols), jnp.float32)
    vmem = pl.BlockSpec(memory_space=pltpu.VMEM)
    return pl.pallas_call(
        functools.partial(_forcing_kernel, species, kernel, levels),
        in_specs=[vmem, vmem, vmem],
        out_specs=[vmem, vmem, vmem],
        out_shape=[jax.ShapeDtypeStruct((steps, planes, 2 * tr, cols), jnp.float32), packed,
                   packed],
        scratch_shapes=[pltpu.VMEM((planes * tr, slots), jnp.float32),
                        pltpu.VMEM((planes * tr, 2 * slots), jnp.float32)],
    )(own, below, above)


def _steps_kernel(steps, species, levels, n_statics,
                  right_ref, left_ref, sright_ref, sleft_ref, st_own, st_xh, mask_ref, prior_ref,
                  tall_hbm, adj_ref, ss_ref,
                  tall_buf, yh_buf, se_ref, state_ref, red_ref, ratio_ref, inv_ref, sems):
    planes = species * levels
    rows, lanes = mask_ref.shape
    tr, tc = adj_ref.shape[2:]
    half = tr // 2
    group = tc // half
    d0 = 2 * steps

    loads = {}
    for k in reversed(range(steps)):
        copy = pltpu.make_async_copy(tall_hbm.at[k], tall_buf.at[k], sems.at[k])
        copy.start()
        loads[k] = copy

    n_fgroups = right_ref.shape[0]

    def unpack_group(g, carry):
        r = right_ref[g]
        l = left_ref[g]
        for q in range(group):
            yh_buf[g * group + q] = _unpack(r, l, q, tc, half)
        return carry

    lax.fori_loop(0, n_fgroups, unpack_group, 0)
    for c in range(n_statics):
        se_ref[c, :, tc:] = _unpack(sright_ref[c // group], sleft_ref[c // group], c % group,
                                    tc, half)

    def assemble_static(c, carry):
        se_ref[c, :tr, :tc] = st_own[c]
        se_ref[c, tr:, :tc] = st_xh[c]
        return carry

    lax.fori_loop(0, n_statics, assemble_static, 0)

    zero = jnp.zeros((rows, lanes), jnp.float32)
    inside = mask_ref[...] > 0.5
    carried = zero
    for l in range(levels):
        below = se_ref[d0 + l - 1] if l > 0 else zero
        above = se_ref[d0 + l] if l < levels - 1 else zero
        inverse = 1.0 / (1.0 + below + above + below * carried)
        ratio = -above * inverse
        ratio_ref[l] = ratio
        inv_ref[l] = inverse
        carried = ratio

    for k in reversed(range(steps)):
        first = k == steps - 1
        last = k == 0
        if first:
            loads[k].wait()
            for s in range(species):

                def assemble(l, carry, s=s, k=k):
                    c = s * levels + l
                    state_ref[s, l, :, :tc] = tall_buf[k, c]
                    state_ref[s, l, :, tc:] = yh_buf[k * planes + c]
                    state_ref[s, l] = jnp.where(inside, state_ref[s, l], 0.0)
                    return carry

                lax.fori_loop(0, levels, assemble, 0, unroll=4)
        if not last:
            loads[k - 1].wait()

        wx = se_ref[k]
        wy = se_ref[steps + k]
        east = jnp.maximum(wx, 0.0)
        west = jnp.maximum(-wx, 0.0)
        north = jnp.maximum(wy, 0.0)
        south = jnp.maximum(-wy, 0.0)
        remain = 1.0 - (east + west + north + south)
        if last:
            _last_step(species, levels, tr, tc, state_ref, east, west, north, south, remain,
                       se_ref, d0, inv_ref, ratio_ref, red_ref, adj_ref, ss_ref, prior_ref)
            continue

        for s in range(species):

            def forward(l, reduced, s=s):
                f = state_ref[s, l]
                from_east = pltpu.roll(east * f, rows - 1, 0)
                from_west = pltpu.roll(west * f, 1, 0)
                from_north = pltpu.roll(north * f, lanes - 1, 1)
                from_south = pltpu.roll(south * f, 1, 1)
                moved = f * remain
                moved = moved + from_east + from_west
                moved = moved + from_north + from_south
                below = jnp.where(l > 0, se_ref[d0 + jnp.maximum(l - 1, 0)], zero)
                reduced = (moved + below * reduced) * inv_ref[l]
                red_ref[l] = reduced
                return reduced

            lax.fori_loop(0, levels, forward, zero, unroll=4)

            def backward(i, result, s=s, k=k):
                l = levels - 1 - i
                c = s * levels + l
                result = red_ref[l] - ratio_ref[l] * result
                state_ref[s, l, :, :tc] = jnp.where(
                    inside[:, :tc], result[:, :tc] + tall_buf[k - 1, c], 0.0)
                state_ref[s, l, :, tc:] = jnp.where(
                    inside[:, tc:], result[:, tc:] + yh_buf[(k - 1) * planes + c], 0.0)
                return result

            surface = lax.fori_loop(0, levels, backward, zero, unroll=4)
            if first:
                ss_ref[s] = prior_ref[s] * surface[:tr, :tc]
            else:
                ss_ref[s] = ss_ref[s] + prior_ref[s] * surface[:tr, :tc]


def _last_step(species, levels, tr, tc, forced_ref, east, west, north, south, remain, se_ref,
               d0, inv_ref, ratio_ref, red_ref, out_ref, ss_ref, prior_ref):
    row = lax.broadcasted_iota(jnp.int32, (tr, tc), 0)
    lane = lax.broadcasted_iota(jnp.int32, (tr, tc), 1)
    last_row = row == tr - 1
    first_row = row == 0
    last_lane = lane == tc - 1
    first_lane = lane == 0
    e_a, e_b = east[:tr, :tc], east[tr:, :tc]
    w_a, w_b = west[:tr, :tc], west[tr:, :tc]
    n_a, n_c = north[:tr, :tc], north[:tr, tc:]
    s_a, s_c = south[:tr, :tc], south[:tr, tc:]
    rem = remain[:tr, :tc]
    zero = jnp.zeros((tr, tc), jnp.float32)
    for s in range(species):

        def forward(l, reduced, s=s):
            f_a = forced_ref[s, l, :tr, :tc]
            f_b = forced_ref[s, l, tr:, :tc]
            f_c = forced_ref[s, l, :tr, tc:]
            from_east = jnp.where(last_row, pltpu.roll(e_b * f_b, tr - 1, 0),
                                  pltpu.roll(e_a * f_a, tr - 1, 0))
            from_west = jnp.where(first_row, pltpu.roll(w_b * f_b, 1, 0),
                                  pltpu.roll(w_a * f_a, 1, 0))
            from_north = jnp.where(last_lane, pltpu.roll(n_c * f_c, tc - 1, 1),
                                   pltpu.roll(n_a * f_a, tc - 1, 1))
            from_south = jnp.where(first_lane, pltpu.roll(s_c * f_c, 1, 1),
                                   pltpu.roll(s_a * f_a, 1, 1))
            moved = f_a * rem
            moved = moved + from_east + from_west
            moved = moved + from_north + from_south
            below = jnp.where(l > 0, se_ref[d0 + jnp.maximum(l - 1, 0), :tr, :tc], zero)
            reduced = (moved + below * reduced) * inv_ref[l, :tr, :tc]
            red_ref[l, :tr, :tc] = reduced
            return reduced

        lax.fori_loop(0, levels, forward, zero, unroll=4)

        def backward(i, result, s=s):
            l = levels - 1 - i
            result = red_ref[l, :tr, :tc] - ratio_ref[l, :tr, :tc] * result
            out_ref[s, l] = result
            return result

        surface = lax.fori_loop(0, levels, backward, zero, unroll=4)
        ss_ref[s] = ss_ref[s] + prior_ref[s] * surface


def steps_call(steps, species, levels, n_statics, right, left, sright, sleft, st_own, st_xh,
               mask, prior, tall):
    _, planes, rows, tc = tall.shape
    tr = rows // 2
    lanes = mask.shape[1]
    vmem = pl.BlockSpec(memory_space=pltpu.VMEM)
    anyspace = pl.BlockSpec(memory_space=pl.ANY)
    return pl.pallas_call(
        functools.partial(_steps_kernel, steps, species, levels, n_statics),
        in_specs=[vmem] * 8 + [anyspace],
        out_specs=[vmem, vmem],
        out_shape=[jax.ShapeDtypeStruct((species, levels, tr, tc), jnp.float32),
                   jax.ShapeDtypeStruct(prior.shape, jnp.float32)],
        scratch_shapes=[
            pltpu.VMEM((steps, planes, rows, tc), jnp.float32),
            pltpu.VMEM((steps * planes, rows, tc), jnp.float32),
            pltpu.VMEM((n_statics, rows, lanes), jnp.float32),
            pltpu.VMEM((species, levels, rows, lanes), jnp.float32),
            pltpu.VMEM((levels, rows, lanes), jnp.float32),
            pltpu.VMEM((levels, rows, lanes), jnp.float32),
            pltpu.VMEM((levels, rows, lanes), jnp.float32),
            pltpu.SemaphoreType.DMA((steps,)),
        ],
        compiler_params=pltpu.CompilerParams(vmem_limit_bytes=48 * 1024 * 1024),
    )(right, left, sright, sleft, st_own, st_xh, mask, prior, tall)


def _pairs(axis):
    n = lax.axis_size(axis)
    return [(i, i + 1) for i in range(n - 1)], [(i + 1, i) for i in range(n - 1)]


def _whole(shapes):
    return [pl.BlockSpec(memory_space=pltpu.VMEM) for _ in shapes]


def _xpack_kernel(chans_ref, lo_ref, hi_ref):
    rows = chans_ref.shape[1]
    half = rows // 2
    row = lax.broadcasted_iota(jnp.int32, chans_ref.shape[1:], 0)

    def body(i, carry):
        a = chans_ref[2 * i]
        b = chans_ref[2 * i + 1]
        lo_ref[i] = jnp.where(row < half, a, pltpu.roll(b, half, 0))
        hi_ref[i] = jnp.where(row < half, pltpu.roll(a, half, 0), b)
        return carry

    lax.fori_loop(0, lo_ref.shape[0], body, 0, unroll=4)


def _ypack_kernel(chans_ref, below_ref, above_ref, xh_ref, right_ref, left_ref):
    rows, cols = chans_ref.shape[1:]
    half = rows // 2
    group = cols // half
    row = lax.broadcasted_iota(jnp.int32, (rows, cols), 0)
    lane = lax.broadcasted_iota(jnp.int32, (rows, cols), 1)
    zero = jnp.zeros((rows, cols), jnp.float32)

    def body(g, carry):
        acc = [zero, zero, zero, zero]
        for q2 in range(group // 2):
            i = g * (group // 2) + q2
            b = below_ref[i]
            a = above_ref[i]
            xh0 = jnp.where(row < half, b, pltpu.roll(a, half, 0))
            xh1 = jnp.where(row < half, pltpu.roll(b, half, 0), a)
            xh_ref[2 * i] = xh0
            xh_ref[2 * i + 1] = xh1
            for off, top, bot in ((0, chans_ref[2 * i], xh0), (1, chans_ref[2 * i + 1], xh1)):
                q = 2 * q2 + off
                sel = (lane >= half * q) & (lane < half * q + half)
                rs = (half * q) % cols
                ls = (half * q + half) % cols
                acc[0] = jnp.where(sel, pltpu.roll(top, rs, 1) if rs else top, acc[0])
                acc[1] = jnp.where(sel, pltpu.roll(bot, rs, 1) if rs else bot, acc[1])
                acc[2] = jnp.where(sel, pltpu.roll(top, ls, 1) if ls else top, acc[2])
                acc[3] = jnp.where(sel, pltpu.roll(bot, ls, 1) if ls else bot, acc[3])
        right_ref[g, :rows] = acc[0]
        right_ref[g, rows:] = acc[1]
        left_ref[g, :rows] = acc[2]
        left_ref[g, rows:] = acc[3]
        return carry

    lax.fori_loop(0, right_ref.shape[0], body, 0)


def extend(chans, first_static, n_statics):
    up_x, down_x = _pairs("gx")
    up_y, down_y = _pairs("gy")
    channels, rows, cols = chans.shape
    halo = rows // 2
    group = cols // halo
    pairs = jax.ShapeDtypeStruct((channels // 2, rows, cols), jnp.float32)
    lo, hi = pl.pallas_call(
        _xpack_kernel, out_shape=[pairs, pairs],
        in_specs=_whole([chans]), out_specs=_whole([0, 0]))(chans)
    below = lax.ppermute(lo, "gx", down_x)
    above = lax.ppermute(hi, "gx", up_x)
    packed = jax.ShapeDtypeStruct((channels // group, 2 * rows, cols), jnp.float32)
    xh, right, left = pl.pallas_call(
        _ypack_kernel,
        out_shape=[jax.ShapeDtypeStruct(chans.shape, jnp.float32), packed, packed],
        in_specs=_whole([0, 0, 0]), out_specs=_whole([0, 0, 0]))(chans, below, above)
    right = lax.ppermute(right, "gy", down_y)
    left = lax.ppermute(left, "gy", up_y)
    return xh, right, left


def local(pixel_adjoint, pixel_owner, pixel_column, pixel_level, wind_x, wind_y,
          diffusivity, prior_emission, region_map):
    gx_n = lax.axis_size("gx")
    gy_n = lax.axis_size("gy")
    devices = gx_n * gy_n
    steps, rows, cols = wind_x.shape
    levels = diffusivity.shape[0] + 1
    species = prior_emission.shape[0]
    kernel = pixel_adjoint.shape[1] // species
    pixels = pixel_adjoint.shape[2]
    capacity = 2 * pixels // devices
    cells = rows * cols
    slots = devices * capacity
    halo = rows // 2
    assert steps <= halo
    lanes = 2 * cols
    ext_rows = 2 * rows

    owners = pixel_owner[:, :, 0]
    matches = (owners[:, :, None] == jnp.arange(devices, dtype=jnp.int32)).astype(jnp.int32)
    rank = jnp.sum(jnp.cumsum(matches, axis=1) * matches, axis=2) - 1
    position = owners * capacity + rank
    rows_out = jnp.concatenate(
        [pixel_adjoint, pixel_column.astype(jnp.float32)[:, None, :],
         pixel_level.astype(jnp.float32)[:, None, :]], axis=1)
    place = (position[:, :, None] == jnp.arange(slots, dtype=jnp.int32)).astype(jnp.float32)
    placed = jnp.einsum("kap,kpq->kaq", rows_out, place, precision=HI)
    received = lax.all_to_all(placed, ("gx", "gy"), 2, 2, tiled=True)

    up_x, down_x = _pairs("gx")
    below = lax.ppermute(received, "gx", down_x)
    above = lax.ppermute(received, "gx", up_x)
    tall, right, left = forcing_call(species, kernel, levels, received, below, above, cols)
    up_y, down_y = _pairs("gy")
    right = lax.ppermute(right, "gy", down_y)
    left = lax.ppermute(left, "gy", up_y)

    n_s = 2 * steps + levels - 1
    group = cols // halo
    n_pad = -(-n_s // group) * group
    statics = jnp.concatenate(
        [wind_x, wind_y, diffusivity, jnp.zeros((n_pad - n_s, rows, cols), jnp.float32)], axis=0)
    st_xh, sright, sleft = extend(statics, 0, n_s)

    gxi = lax.axis_index("gx")
    gyi = lax.axis_index("gy")
    r = jnp.arange(ext_rows, dtype=jnp.int32)[:, None]
    c = jnp.arange(lanes, dtype=jnp.int32)[None, :]
    grow = gxi * rows + jnp.where(r < rows + halo, r, r - ext_rows)
    ccol = jnp.where(c < cols + halo, c, c - lanes)
    gcol = gyi * cols + ccol
    inside = ((grow >= 0) & (grow < gx_n * rows) & (gcol >= 0) & (gcol < gy_n * cols)
              & ((c < cols + halo) | (c >= lanes - halo)))
    mask = inside.astype(jnp.float32)

    adjoint, surface_sum = steps_call(steps, species, levels, n_s, right, left, sright, sleft,
                                      statics, st_xh, mask, prior_emission, tall)

    nreg = REG_DEV * devices
    member = (region_map.reshape(-1)[:, None] == jnp.arange(nreg, dtype=jnp.int32)).astype(jnp.float32)
    partial = jnp.dot(surface_sum.reshape(species, cells), member, precision=HI)
    pieces = lax.all_to_all(partial.reshape(species, devices, nreg // devices), ("gx", "gy"), 1, 1,
                            tiled=True)
    gradient = jnp.sum(pieces, axis=1)
    return adjoint, gradient


def solution(mesh):
    in_specs = (
        P(None, None, ("gx", "gy")),
        P(None, ("gx", "gy"), None),
        P(None, ("gx", "gy")),
        P(None, ("gx", "gy")),
        P(None, "gx", "gy"),
        P(None, "gx", "gy"),
        P(None, "gx", "gy"),
        P(None, "gx", "gy"),
        P("gx", "gy"),
    )
    out_specs = (P(None, None, "gx", "gy"), P(None, ("gx", "gy")))
    return jax.shard_map(local, mesh=mesh, in_specs=in_specs, out_specs=out_specs, check_vma=False)
```

```python
import functools

import jax
import jax.numpy as jnp
from jax import lax
from jax.experimental import pallas as pl
from jax.experimental.pallas import tpu as pltpu
from jax.sharding import PartitionSpec as P

HI = lax.Precision.HIGHEST
REG_DEV = 8


def _full(shape):
    nd = len(shape)
    return pl.BlockSpec(shape, lambda i, _n=nd: (0,) * _n)


def _unpack(r, l, q, cols, half):
    lane = lax.broadcasted_iota(jnp.int32, r.shape, 1)
    rs = (cols - half * q) % cols
    ls = (cols - half - half * q) % cols
    return jnp.where(lane < half, pltpu.roll(r, rs, 1) if rs else r,
                     jnp.where(lane >= cols - half, pltpu.roll(l, ls, 1) if ls else l, 0.0))


def _pack_kernel(capacity, adj_ref, owner_ref, col_ref, lev_ref, out_ref, rows_ref):
    steps, n_pay, pixels = adj_ref.shape
    slots = out_ref.shape[2]
    row = lax.broadcasted_iota(jnp.int32, (pixels, pixels), 0)
    lane = lax.broadcasted_iota(jnp.int32, (pixels, pixels), 1)
    slot = lax.broadcasted_iota(jnp.int32, (pixels, slots), 1).astype(jnp.float32)
    for k in range(steps):
        owner = jnp.broadcast_to(owner_ref[k].astype(jnp.float32), (pixels, pixels))
        same = (owner == jnp.transpose(owner)) & (lane < row)
        rank = jnp.sum(jnp.where(same, 1.0, 0.0), axis=1, keepdims=True)
        position = owner[:, :1] * capacity + rank
        place = jnp.where(position == slot, 1.0, 0.0)
        rows_ref[:n_pay] = adj_ref[k]
        rows_ref[n_pay:n_pay + 1] = col_ref[k:k + 1].astype(jnp.float32)
        rows_ref[n_pay + 1:n_pay + 2] = lev_ref[k:k + 1].astype(jnp.float32)
        out_ref[k] = lax.dot_general(rows_ref[...], place, (((1,), (0,)), ((), ())),
                                     precision=lax.Precision.HIGHEST,
                                     preferred_element_type=jnp.float32)


def pack_call(capacity, slots, pixel_adjoint, pixel_owner, pixel_column, pixel_level):
    steps, n_pay, pixels = pixel_adjoint.shape
    vmem = pl.BlockSpec(memory_space=pltpu.VMEM)
    return pl.pallas_call(
        functools.partial(_pack_kernel, capacity),
        in_specs=[vmem] * 4,
        out_specs=vmem,
        out_shape=jax.ShapeDtypeStruct((steps, n_pay + 2, slots), jnp.float32),
        scratch_shapes=[pltpu.VMEM((n_pay + 2, pixels), jnp.float32)],
    )(pixel_adjoint, pixel_owner, pixel_column, pixel_level)


def _exact_dot(a, b):
    return lax.dot_general(a, b.astype(jnp.float32), (((1,), (1,)), ((), ())),
                           precision=lax.Precision.HIGHEST, preferred_element_type=jnp.float32)


def _forcing_kernel(species, kernel, levels, own_ref, below_ref, above_ref,
                    tall_ref, right_ref, left_ref, lown_ref, lnb_ref):
    steps, _, slots = own_ref.shape
    tr2, tc = tall_ref.shape[2:]
    tr = tr2 // 2
    half = tr // 2
    group = tc // half
    n_pay = species * kernel
    lane_t = lax.broadcasted_iota(jnp.int32, (tc, slots), 0)
    row_i = lax.broadcasted_iota(jnp.int32, (tr, slots), 0)
    lev_i = lax.broadcasted_iota(jnp.int32, (levels, slots), 0)
    lane16 = lax.broadcasted_iota(jnp.int32, (tr2, tc), 1)
    right_ref[...] = jnp.zeros(right_ref.shape, jnp.float32)
    left_ref[...] = jnp.zeros(left_ref.shape, jnp.float32)
    for k in range(steps):
        hts = []
        for src, ref in enumerate((own_ref, below_ref, above_ref)):
            blk = ref[k]
            col = blk[n_pay:n_pay + 1].astype(jnp.int32)
            lev = blk[n_pay + 1:n_pay + 2].astype(jnp.int32)
            row_q = col // tc
            lane_q = col % tc
            if src == 1:
                row_q = jnp.where(row_q < half, row_q, -1)
            elif src == 2:
                row_q = jnp.where(row_q >= half, row_q, -1)
            rmask = row_i == row_q
            hts.append((lane_t == lane_q).astype(jnp.bfloat16))
            offset = lev_i - lev
            dst = lown_ref if src == 0 else lnb_ref
            c0 = 0 if src < 2 else slots
            for s in range(species):
                prof = jnp.zeros((levels, slots), jnp.float32)
                for j in range(kernel):
                    prof = prof + jnp.where(offset == j, blk[s * kernel + j:s * kernel + j + 1], 0.0)
                for l in range(levels):
                    c = s * levels + l
                    dst[c * tr:(c + 1) * tr, c0:c0 + slots] = jnp.where(
                        rmask, jnp.broadcast_to(prof[l:l + 1], (tr, slots)), 0.0)
        own = _exact_dot(lown_ref[...], hts[0])
        xh = _exact_dot(lnb_ref[...], jnp.concatenate([hts[1], hts[2]], axis=1))
        planes = own.shape[0] // tr
        tall_ref[k, :, :tr, :] = own.reshape(planes, tr, tc)
        tall_ref[k, :, tr:, :] = xh.reshape(planes, tr, tc)
        for c in range(planes):
            g, q = divmod(k * planes + c, group)
            plane = tall_ref[k, c]
            sel = (lane16 >= half * q) & (lane16 < half * q + half)
            rs = (half * q) % tc
            ls = (half * q + half) % tc
            right_ref[g] = jnp.where(sel, pltpu.roll(plane, rs, 1) if rs else plane, right_ref[g])
            left_ref[g] = jnp.where(sel, pltpu.roll(plane, ls, 1) if ls else plane, left_ref[g])


def forcing_call(species, kernel, levels, own, below, above, cols):
    steps, _, slots = own.shape
    tr = 8
    planes = species * levels
    group = cols // (tr // 2)
    packed = jax.ShapeDtypeStruct((steps * planes // group, 2 * tr, cols), jnp.float32)
    vmem = pl.BlockSpec(memory_space=pltpu.VMEM)
    return pl.pallas_call(
        functools.partial(_forcing_kernel, species, kernel, levels),
        in_specs=[vmem, vmem, vmem],
        out_specs=[vmem, vmem, vmem],
        out_shape=[jax.ShapeDtypeStruct((steps, planes, 2 * tr, cols), jnp.float32), packed,
                   packed],
        scratch_shapes=[pltpu.VMEM((planes * tr, slots), jnp.float32),
                        pltpu.VMEM((planes * tr, 2 * slots), jnp.float32)],
    )(own, below, above)


def _steps_kernel(steps, species, levels, n_statics,
                  right_ref, left_ref, sright_ref, sleft_ref, st_own, st_xh, mask_ref, prior_ref,
                  tall_hbm, adj_ref, ss_ref,
                  tall_buf, yh_buf, se_ref, state_ref, red_ref, ratio_ref, inv_ref, sems):
    planes = species * levels
    rows, lanes = mask_ref.shape
    tr, tc = adj_ref.shape[2:]
    half = tr // 2
    group = tc // half
    d0 = 2 * steps

    loads = {}
    for k in reversed(range(steps)):
        copy = pltpu.make_async_copy(tall_hbm.at[k], tall_buf.at[k], sems.at[k])
        copy.start()
        loads[k] = copy

    n_fgroups = right_ref.shape[0]

    def unpack_group(g, carry):
        r = right_ref[g]
        l = left_ref[g]
        for q in range(group):
            yh_buf[g * group + q] = _unpack(r, l, q, tc, half)
        return carry

    lax.fori_loop(0, n_fgroups, unpack_group, 0)
    for c in range(n_statics):
        se_ref[c, :, tc:] = _unpack(sright_ref[c // group], sleft_ref[c // group], c % group,
                                    tc, half)

    def assemble_static(c, carry):
        se_ref[c, :tr, :tc] = st_own[c]
        se_ref[c, tr:, :tc] = st_xh[c]
        return carry

    lax.fori_loop(0, n_statics, assemble_static, 0)

    zero = jnp.zeros((rows, lanes), jnp.float32)
    inside = mask_ref[...] > 0.5
    carried = zero
    for l in range(levels):
        below = se_ref[d0 + l - 1] if l > 0 else zero
        above = se_ref[d0 + l] if l < levels - 1 else zero
        inverse = 1.0 / (1.0 + below + above + below * carried)
        ratio = -above * inverse
        ratio_ref[l] = ratio
        inv_ref[l] = inverse
        carried = ratio

    for k in reversed(range(steps)):
        first = k == steps - 1
        last = k == 0
        if first:
            loads[k].wait()
            for s in range(species):

                def assemble(l, carry, s=s, k=k):
                    c = s * levels + l
                    state_ref[s, l, :, :tc] = tall_buf[k, c]
                    state_ref[s, l, :, tc:] = yh_buf[k * planes + c]
                    state_ref[s, l] = jnp.where(inside, state_ref[s, l], 0.0)
                    return carry

                lax.fori_loop(0, levels, assemble, 0, unroll=4)
        if not last:
            loads[k - 1].wait()

        wx = se_ref[k]
        wy = se_ref[steps + k]
        east = jnp.maximum(wx, 0.0)
        west = jnp.maximum(-wx, 0.0)
        north = jnp.maximum(wy, 0.0)
        south = jnp.maximum(-wy, 0.0)
        remain = 1.0 - (east + west + north + south)
        if last:
            _last_step(species, levels, tr, tc, state_ref, east, west, north, south, remain,
                       se_ref, d0, inv_ref, ratio_ref, red_ref, adj_ref, ss_ref, prior_ref)
            continue

        for s in range(species):

            def forward(l, reduced, s=s):
                f = state_ref[s, l]
                from_east = pltpu.roll(east * f, rows - 1, 0)
                from_west = pltpu.roll(west * f, 1, 0)
                from_north = pltpu.roll(north * f, lanes - 1, 1)
                from_south = pltpu.roll(south * f, 1, 1)
                moved = f * remain
                moved = moved + from_east + from_west
                moved = moved + from_north + from_south
                below = jnp.where(l > 0, se_ref[d0 + jnp.maximum(l - 1, 0)], zero)
                reduced = (moved + below * reduced) * inv_ref[l]
                red_ref[l] = reduced
                return reduced

            lax.fori_loop(0, levels, forward, zero, unroll=4)

            def backward(i, result, s=s, k=k):
                l = levels - 1 - i
                c = s * levels + l
                result = red_ref[l] - ratio_ref[l] * result
                state_ref[s, l, :, :tc] = jnp.where(
                    inside[:, :tc], result[:, :tc] + tall_buf[k - 1, c], 0.0)
                state_ref[s, l, :, tc:] = jnp.where(
                    inside[:, tc:], result[:, tc:] + yh_buf[(k - 1) * planes + c], 0.0)
                return result

            surface = lax.fori_loop(0, levels, backward, zero, unroll=4)
            if first:
                ss_ref[s] = prior_ref[s] * surface[:tr, :tc]
            else:
                ss_ref[s] = ss_ref[s] + prior_ref[s] * surface[:tr, :tc]


def _last_step(species, levels, tr, tc, forced_ref, east, west, north, south, remain, se_ref,
               d0, inv_ref, ratio_ref, red_ref, out_ref, ss_ref, prior_ref):
    row = lax.broadcasted_iota(jnp.int32, (tr, tc), 0)
    lane = lax.broadcasted_iota(jnp.int32, (tr, tc), 1)
    last_row = row == tr - 1
    first_row = row == 0
    last_lane = lane == tc - 1
    first_lane = lane == 0
    e_a, e_b = east[:tr, :tc], east[tr:, :tc]
    w_a, w_b = west[:tr, :tc], west[tr:, :tc]
    n_a, n_c = north[:tr, :tc], north[:tr, tc:]
    s_a, s_c = south[:tr, :tc], south[:tr, tc:]
    rem = remain[:tr, :tc]
    zero = jnp.zeros((tr, tc), jnp.float32)
    for s in range(species):

        def forward(l, reduced, s=s):
            f_a = forced_ref[s, l, :tr, :tc]
            f_b = forced_ref[s, l, tr:, :tc]
            f_c = forced_ref[s, l, :tr, tc:]
            from_east = jnp.where(last_row, pltpu.roll(e_b * f_b, tr - 1, 0),
                                  pltpu.roll(e_a * f_a, tr - 1, 0))
            from_west = jnp.where(first_row, pltpu.roll(w_b * f_b, 1, 0),
                                  pltpu.roll(w_a * f_a, 1, 0))
            from_north = jnp.where(last_lane, pltpu.roll(n_c * f_c, tc - 1, 1),
                                   pltpu.roll(n_a * f_a, tc - 1, 1))
            from_south = jnp.where(first_lane, pltpu.roll(s_c * f_c, 1, 1),
                                   pltpu.roll(s_a * f_a, 1, 1))
            moved = f_a * rem
            moved = moved + from_east + from_west
            moved = moved + from_north + from_south
            below = jnp.where(l > 0, se_ref[d0 + jnp.maximum(l - 1, 0), :tr, :tc], zero)
            reduced = (moved + below * reduced) * inv_ref[l, :tr, :tc]
            red_ref[l, :tr, :tc] = reduced
            return reduced

        lax.fori_loop(0, levels, forward, zero, unroll=4)

        def backward(i, result, s=s):
            l = levels - 1 - i
            result = red_ref[l, :tr, :tc] - ratio_ref[l, :tr, :tc] * result
            out_ref[s, l] = result
            return result

        surface = lax.fori_loop(0, levels, backward, zero, unroll=4)
        ss_ref[s] = ss_ref[s] + prior_ref[s] * surface


def steps_call(steps, species, levels, n_statics, right, left, sright, sleft, st_own, st_xh,
               mask, prior, tall):
    _, planes, rows, tc = tall.shape
    tr = rows // 2
    lanes = mask.shape[1]
    vmem = pl.BlockSpec(memory_space=pltpu.VMEM)
    anyspace = pl.BlockSpec(memory_space=pl.ANY)
    return pl.pallas_call(
        functools.partial(_steps_kernel, steps, species, levels, n_statics),
        in_specs=[vmem] * 8 + [anyspace],
        out_specs=[vmem, vmem],
        out_shape=[jax.ShapeDtypeStruct((species, levels, tr, tc), jnp.float32),
                   jax.ShapeDtypeStruct(prior.shape, jnp.float32)],
        scratch_shapes=[
            pltpu.VMEM((steps, planes, rows, tc), jnp.float32),
            pltpu.VMEM((steps * planes, rows, tc), jnp.float32),
            pltpu.VMEM((n_statics, rows, lanes), jnp.float32),
            pltpu.VMEM((species, levels, rows, lanes), jnp.float32),
            pltpu.VMEM((levels, rows, lanes), jnp.float32),
            pltpu.VMEM((levels, rows, lanes), jnp.float32),
            pltpu.VMEM((levels, rows, lanes), jnp.float32),
            pltpu.SemaphoreType.DMA((steps,)),
        ],
        compiler_params=pltpu.CompilerParams(vmem_limit_bytes=48 * 1024 * 1024),
    )(right, left, sright, sleft, st_own, st_xh, mask, prior, tall)


def _pairs(axis):
    n = lax.axis_size(axis)
    return [(i, i + 1) for i in range(n - 1)], [(i + 1, i) for i in range(n - 1)]


def _whole(shapes):
    return [pl.BlockSpec(memory_space=pltpu.VMEM) for _ in shapes]


def _xpack_kernel(chans_ref, lo_ref, hi_ref):
    rows = chans_ref.shape[1]
    half = rows // 2
    row = lax.broadcasted_iota(jnp.int32, chans_ref.shape[1:], 0)

    def body(i, carry):
        a = chans_ref[2 * i]
        b = chans_ref[2 * i + 1]
        lo_ref[i] = jnp.where(row < half, a, pltpu.roll(b, half, 0))
        hi_ref[i] = jnp.where(row < half, pltpu.roll(a, half, 0), b)
        return carry

    lax.fori_loop(0, lo_ref.shape[0], body, 0, unroll=4)


def _ypack_kernel(chans_ref, below_ref, above_ref, xh_ref, right_ref, left_ref):
    rows, cols = chans_ref.shape[1:]
    half = rows // 2
    group = cols // half
    row = lax.broadcasted_iota(jnp.int32, (rows, cols), 0)
    lane = lax.broadcasted_iota(jnp.int32, (rows, cols), 1)
    zero = jnp.zeros((rows, cols), jnp.float32)

    def body(g, carry):
        acc = [zero, zero, zero, zero]
        for q2 in range(group // 2):
            i = g * (group // 2) + q2
            b = below_ref[i]
            a = above_ref[i]
            xh0 = jnp.where(row < half, b, pltpu.roll(a, half, 0))
            xh1 = jnp.where(row < half, pltpu.roll(b, half, 0), a)
            xh_ref[2 * i] = xh0
            xh_ref[2 * i + 1] = xh1
            for off, top, bot in ((0, chans_ref[2 * i], xh0), (1, chans_ref[2 * i + 1], xh1)):
                q = 2 * q2 + off
                sel = (lane >= half * q) & (lane < half * q + half)
                rs = (half * q) % cols
                ls = (half * q + half) % cols
                acc[0] = jnp.where(sel, pltpu.roll(top, rs, 1) if rs else top, acc[0])
                acc[1] = jnp.where(sel, pltpu.roll(bot, rs, 1) if rs else bot, acc[1])
                acc[2] = jnp.where(sel, pltpu.roll(top, ls, 1) if ls else top, acc[2])
                acc[3] = jnp.where(sel, pltpu.roll(bot, ls, 1) if ls else bot, acc[3])
        right_ref[g, :rows] = acc[0]
        right_ref[g, rows:] = acc[1]
        left_ref[g, :rows] = acc[2]
        left_ref[g, rows:] = acc[3]
        return carry

    lax.fori_loop(0, right_ref.shape[0], body, 0)


def extend(chans, first_static, n_statics):
    up_x, down_x = _pairs("gx")
    up_y, down_y = _pairs("gy")
    channels, rows, cols = chans.shape
    halo = rows // 2
    group = cols // halo
    pairs = jax.ShapeDtypeStruct((channels // 2, rows, cols), jnp.float32)
    lo, hi = pl.pallas_call(
        _xpack_kernel, out_shape=[pairs, pairs],
        in_specs=_whole([chans]), out_specs=_whole([0, 0]))(chans)
    below = lax.ppermute(lo, "gx", down_x)
    above = lax.ppermute(hi, "gx", up_x)
    packed = jax.ShapeDtypeStruct((channels // group, 2 * rows, cols), jnp.float32)
    xh, right, left = pl.pallas_call(
        _ypack_kernel,
        out_shape=[jax.ShapeDtypeStruct(chans.shape, jnp.float32), packed, packed],
        in_specs=_whole([0, 0, 0]), out_specs=_whole([0, 0, 0]))(chans, below, above)
    right = lax.ppermute(right, "gy", down_y)
    left = lax.ppermute(left, "gy", up_y)
    return xh, right, left


def local(pixel_adjoint, pixel_owner, pixel_column, pixel_level, wind_x, wind_y,
          diffusivity, prior_emission, region_map):
    gx_n = lax.axis_size("gx")
    gy_n = lax.axis_size("gy")
    devices = gx_n * gy_n
    steps, rows, cols = wind_x.shape
    levels = diffusivity.shape[0] + 1
    species = prior_emission.shape[0]
    kernel = pixel_adjoint.shape[1] // species
    pixels = pixel_adjoint.shape[2]
    capacity = 2 * pixels // devices
    cells = rows * cols
    slots = devices * capacity
    halo = rows // 2
    assert steps <= halo
    lanes = 2 * cols
    ext_rows = 2 * rows

    placed = pack_call(capacity, slots, pixel_adjoint, pixel_owner, pixel_column, pixel_level)
    received = lax.all_to_all(placed, ("gx", "gy"), 2, 2, tiled=True)

    up_x, down_x = _pairs("gx")
    below = lax.ppermute(received, "gx", down_x)
    above = lax.ppermute(received, "gx", up_x)
    tall, right, left = forcing_call(species, kernel, levels, received, below, above, cols)
    up_y, down_y = _pairs("gy")
    right = lax.ppermute(right, "gy", down_y)
    left = lax.ppermute(left, "gy", up_y)

    n_s = 2 * steps + levels - 1
    group = cols // halo
    n_pad = -(-n_s // group) * group
    statics = jnp.concatenate(
        [wind_x, wind_y, diffusivity, jnp.zeros((n_pad - n_s, rows, cols), jnp.float32)], axis=0)
    st_xh, sright, sleft = extend(statics, 0, n_s)

    gxi = lax.axis_index("gx")
    gyi = lax.axis_index("gy")
    r = jnp.arange(ext_rows, dtype=jnp.int32)[:, None]
    c = jnp.arange(lanes, dtype=jnp.int32)[None, :]
    grow = gxi * rows + jnp.where(r < rows + halo, r, r - ext_rows)
    ccol = jnp.where(c < cols + halo, c, c - lanes)
    gcol = gyi * cols + ccol
    inside = ((grow >= 0) & (grow < gx_n * rows) & (gcol >= 0) & (gcol < gy_n * cols)
              & ((c < cols + halo) | (c >= lanes - halo)))
    mask = inside.astype(jnp.float32)

    adjoint, surface_sum = steps_call(steps, species, levels, n_s, right, left, sright, sleft,
                                      statics, st_xh, mask, prior_emission, tall)

    nreg = REG_DEV * devices
    member = (region_map.reshape(-1)[:, None] == jnp.arange(nreg, dtype=jnp.int32)).astype(jnp.float32)
    partial = jnp.dot(surface_sum.reshape(species, cells), member, precision=HI)
    pieces = lax.all_to_all(partial.reshape(species, devices, nreg // devices), ("gx", "gy"), 1, 1,
                            tiled=True)
    gradient = jnp.sum(pieces, axis=1)
    return adjoint, gradient


def solution(mesh):
    in_specs = (
        P(None, None, ("gx", "gy")),
        P(None, ("gx", "gy"), None),
        P(None, ("gx", "gy")),
        P(None, ("gx", "gy")),
        P(None, "gx", "gy"),
        P(None, "gx", "gy"),
        P(None, "gx", "gy"),
        P(None, "gx", "gy"),
        P("gx", "gy"),
    )
    out_specs = (P(None, None, "gx", "gy"), P(None, ("gx", "gy")))
    return jax.shard_map(local, mesh=mesh, in_specs=in_specs, out_specs=out_specs, check_vma=False)
```

```python
import functools

import jax
import jax.numpy as jnp
from jax import lax
from jax.experimental import pallas as pl
from jax.experimental.pallas import tpu as pltpu
from jax.sharding import PartitionSpec as P

HI = lax.Precision.HIGHEST
REG_DEV = 8


def _full(shape):
    nd = len(shape)
    return pl.BlockSpec(shape, lambda i, _n=nd: (0,) * _n)


def _unpack(r, l, q, cols, half):
    lane = lax.broadcasted_iota(jnp.int32, r.shape, 1)
    rs = (cols - half * q) % cols
    ls = (cols - half - half * q) % cols
    return jnp.where(lane < half, pltpu.roll(r, rs, 1) if rs else r,
                     jnp.where(lane >= cols - half, pltpu.roll(l, ls, 1) if ls else l, 0.0))


def _pack_kernel(capacity, adj_ref, owner_ref, col_ref, lev_ref, out_ref, rows_ref):
    steps, n_pay, pixels = adj_ref.shape
    slots = out_ref.shape[2]
    row = lax.broadcasted_iota(jnp.int32, (pixels, pixels), 0)
    lane = lax.broadcasted_iota(jnp.int32, (pixels, pixels), 1)
    slot = lax.broadcasted_iota(jnp.int32, (pixels, slots), 1).astype(jnp.float32)
    for k in range(steps):
        owner = jnp.broadcast_to(owner_ref[k].astype(jnp.float32), (pixels, pixels))
        same = (owner == jnp.transpose(owner)) & (lane < row)
        rank = jnp.sum(jnp.where(same, 1.0, 0.0), axis=1, keepdims=True)
        position = owner[:, :1] * capacity + rank
        place = jnp.where(position == slot, 1.0, 0.0)
        rows_ref[:n_pay] = adj_ref[k]
        rows_ref[n_pay:n_pay + 1] = col_ref[k:k + 1].astype(jnp.float32)
        rows_ref[n_pay + 1:n_pay + 2] = lev_ref[k:k + 1].astype(jnp.float32)
        out_ref[k] = lax.dot_general(rows_ref[...], place, (((1,), (0,)), ((), ())),
                                     precision=lax.Precision.HIGHEST,
                                     preferred_element_type=jnp.float32)


def pack_call(capacity, slots, pixel_adjoint, pixel_owner, pixel_column, pixel_level):
    steps, n_pay, pixels = pixel_adjoint.shape
    vmem = pl.BlockSpec(memory_space=pltpu.VMEM)
    return pl.pallas_call(
        functools.partial(_pack_kernel, capacity),
        in_specs=[vmem] * 4,
        out_specs=vmem,
        out_shape=jax.ShapeDtypeStruct((steps, n_pay + 2, slots), jnp.float32),
        scratch_shapes=[pltpu.VMEM((n_pay + 2, pixels), jnp.float32)],
    )(pixel_adjoint, pixel_owner, pixel_column, pixel_level)


def _exact_dot(a, b):
    dims = (((1,), (1,)), ((), ()))
    hi = a.astype(jnp.bfloat16)
    rest = a - hi.astype(jnp.float32)
    mid = rest.astype(jnp.bfloat16)
    lo = (rest - mid.astype(jnp.float32)).astype(jnp.bfloat16)
    out = lax.dot_general(hi, b, dims, preferred_element_type=jnp.float32)
    out = out + lax.dot_general(mid, b, dims, preferred_element_type=jnp.float32)
    return out + lax.dot_general(lo, b, dims, preferred_element_type=jnp.float32)


def _forcing_kernel(species, kernel, levels, own_ref, below_ref, above_ref,
                    tall_ref, right_ref, left_ref, lown_ref, lnb_ref):
    steps, _, slots = own_ref.shape
    tr2, tc = tall_ref.shape[2:]
    tr = tr2 // 2
    half = tr // 2
    group = tc // half
    n_pay = species * kernel
    lane_t = lax.broadcasted_iota(jnp.int32, (tc, slots), 0)
    row_i = lax.broadcasted_iota(jnp.int32, (tr, slots), 0)
    lev_i = lax.broadcasted_iota(jnp.int32, (levels, slots), 0)
    lane16 = lax.broadcasted_iota(jnp.int32, (tr2, tc), 1)
    right_ref[...] = jnp.zeros(right_ref.shape, jnp.float32)
    left_ref[...] = jnp.zeros(left_ref.shape, jnp.float32)
    for k in range(steps):
        hts = []
        for src, ref in enumerate((own_ref, below_ref, above_ref)):
            blk = ref[k]
            col = blk[n_pay:n_pay + 1].astype(jnp.int32)
            lev = blk[n_pay + 1:n_pay + 2].astype(jnp.int32)
            row_q = col // tc
            lane_q = col % tc
            if src == 1:
                row_q = jnp.where(row_q < half, row_q, -1)
            elif src == 2:
                row_q = jnp.where(row_q >= half, row_q, -1)
            rmask = row_i == row_q
            hts.append((lane_t == lane_q).astype(jnp.bfloat16))
            offset = lev_i - lev
            dst = lown_ref if src == 0 else lnb_ref
            c0 = 0 if src < 2 else slots
            for s in range(species):
                prof = jnp.zeros((levels, slots), jnp.float32)
                for j in range(kernel):
                    prof = prof + jnp.where(offset == j, blk[s * kernel + j:s * kernel + j + 1], 0.0)
                for l in range(levels):
                    c = s * levels + l
                    dst[c * tr:(c + 1) * tr, c0:c0 + slots] = jnp.where(
                        rmask, jnp.broadcast_to(prof[l:l + 1], (tr, slots)), 0.0)
        own = _exact_dot(lown_ref[...], hts[0])
        xh = _exact_dot(lnb_ref[...], jnp.concatenate([hts[1], hts[2]], axis=1))
        planes = own.shape[0] // tr
        tall_ref[k, :, :tr, :] = own.reshape(planes, tr, tc)
        tall_ref[k, :, tr:, :] = xh.reshape(planes, tr, tc)
        for c in range(planes):
            g, q = divmod(k * planes + c, group)
            plane = tall_ref[k, c]
            sel = (lane16 >= half * q) & (lane16 < half * q + half)
            rs = (half * q) % tc
            ls = (half * q + half) % tc
            right_ref[g] = jnp.where(sel, pltpu.roll(plane, rs, 1) if rs else plane, right_ref[g])
            left_ref[g] = jnp.where(sel, pltpu.roll(plane, ls, 1) if ls else plane, left_ref[g])


def forcing_call(species, kernel, levels, own, below, above, cols):
    steps, _, slots = own.shape
    tr = 8
    planes = species * levels
    group = cols // (tr // 2)
    packed = jax.ShapeDtypeStruct((steps * planes // group, 2 * tr, cols), jnp.float32)
    vmem = pl.BlockSpec(memory_space=pltpu.VMEM)
    return pl.pallas_call(
        functools.partial(_forcing_kernel, species, kernel, levels),
        in_specs=[vmem, vmem, vmem],
        out_specs=[vmem, vmem, vmem],
        out_shape=[jax.ShapeDtypeStruct((steps, planes, 2 * tr, cols), jnp.float32), packed,
                   packed],
        scratch_shapes=[pltpu.VMEM((planes * tr, slots), jnp.float32),
                        pltpu.VMEM((planes * tr, 2 * slots), jnp.float32)],
    )(own, below, above)


def _steps_kernel(steps, species, levels, n_statics,
                  right_ref, left_ref, sright_ref, sleft_ref, st_own, st_xh, mask_ref, prior_ref,
                  tall_hbm, adj_ref, ss_ref,
                  tall_buf, yh_buf, se_ref, state_ref, red_ref, ratio_ref, inv_ref, sems):
    planes = species * levels
    rows, lanes = mask_ref.shape
    tr, tc = adj_ref.shape[2:]
    half = tr // 2
    group = tc // half
    d0 = 2 * steps

    loads = {}
    for k in reversed(range(steps)):
        copy = pltpu.make_async_copy(tall_hbm.at[k], tall_buf.at[k], sems.at[k])
        copy.start()
        loads[k] = copy

    n_fgroups = right_ref.shape[0]

    def unpack_group(g, carry):
        r = right_ref[g]
        l = left_ref[g]
        for q in range(group):
            yh_buf[g * group + q] = _unpack(r, l, q, tc, half)
        return carry

    lax.fori_loop(0, n_fgroups, unpack_group, 0)
    for c in range(n_statics):
        se_ref[c, :, tc:] = _unpack(sright_ref[c // group], sleft_ref[c // group], c % group,
                                    tc, half)

    def assemble_static(c, carry):
        se_ref[c, :tr, :tc] = st_own[c]
        se_ref[c, tr:, :tc] = st_xh[c]
        return carry

    lax.fori_loop(0, n_statics, assemble_static, 0)

    zero = jnp.zeros((rows, lanes), jnp.float32)
    inside = mask_ref[...] > 0.5
    carried = zero
    for l in range(levels):
        below = se_ref[d0 + l - 1] if l > 0 else zero
        above = se_ref[d0 + l] if l < levels - 1 else zero
        inverse = 1.0 / (1.0 + below + above + below * carried)
        ratio = -above * inverse
        ratio_ref[l] = ratio
        inv_ref[l] = inverse
        carried = ratio

    for k in reversed(range(steps)):
        first = k == steps - 1
        last = k == 0
        if first:
            loads[k].wait()
            for s in range(species):

                def assemble(l, carry, s=s, k=k):
                    c = s * levels + l
                    state_ref[s, l, :, :tc] = tall_buf[k, c]
                    state_ref[s, l, :, tc:] = yh_buf[k * planes + c]
                    state_ref[s, l] = jnp.where(inside, state_ref[s, l], 0.0)
                    return carry

                lax.fori_loop(0, levels, assemble, 0, unroll=4)
        if not last:
            loads[k - 1].wait()

        wx = se_ref[k]
        wy = se_ref[steps + k]
        east = jnp.maximum(wx, 0.0)
        west = jnp.maximum(-wx, 0.0)
        north = jnp.maximum(wy, 0.0)
        south = jnp.maximum(-wy, 0.0)
        remain = 1.0 - (east + west + north + south)
        if last:
            _last_step(species, levels, tr, tc, state_ref, east, west, north, south, remain,
                       se_ref, d0, inv_ref, ratio_ref, red_ref, adj_ref, ss_ref, prior_ref)
            continue

        def forward(l, reduced):
            below = jnp.where(l > 0, se_ref[d0 + jnp.maximum(l - 1, 0)], zero)
            inverse = inv_ref[l]
            out = []
            for s in range(species):
                f = state_ref[s, l]
                from_east = pltpu.roll(east * f, rows - 1, 0)
                from_west = pltpu.roll(west * f, 1, 0)
                from_north = pltpu.roll(north * f, lanes - 1, 1)
                from_south = pltpu.roll(south * f, 1, 1)
                moved = f * remain
                moved = moved + from_east + from_west
                moved = moved + from_north + from_south
                r = (moved + below * reduced[s]) * inverse
                red_ref[s, l] = r
                out.append(r)
            return tuple(out)

        lax.fori_loop(0, levels, forward, (zero,) * species, unroll=4)

        def backward(i, result, k=k):
            l = levels - 1 - i
            ratio = ratio_ref[l]
            out = []
            for s in range(species):
                c = s * levels + l
                r = red_ref[s, l] - ratio * result[s]
                state_ref[s, l, :, :tc] = jnp.where(
                    inside[:, :tc], r[:, :tc] + tall_buf[k - 1, c], 0.0)
                state_ref[s, l, :, tc:] = jnp.where(
                    inside[:, tc:], r[:, tc:] + yh_buf[(k - 1) * planes + c], 0.0)
                out.append(r)
            return tuple(out)

        surface = lax.fori_loop(0, levels, backward, (zero,) * species, unroll=4)
        for s in range(species):
            if first:
                ss_ref[s] = prior_ref[s] * surface[s][:tr, :tc]
            else:
                ss_ref[s] = ss_ref[s] + prior_ref[s] * surface[s][:tr, :tc]


def _last_step(species, levels, tr, tc, forced_ref, east, west, north, south, remain, se_ref,
               d0, inv_ref, ratio_ref, red_ref, out_ref, ss_ref, prior_ref):
    row = lax.broadcasted_iota(jnp.int32, (tr, tc), 0)
    lane = lax.broadcasted_iota(jnp.int32, (tr, tc), 1)
    last_row = row == tr - 1
    first_row = row == 0
    last_lane = lane == tc - 1
    first_lane = lane == 0
    e_a, e_b = east[:tr, :tc], east[tr:, :tc]
    w_a, w_b = west[:tr, :tc], west[tr:, :tc]
    n_a, n_c = north[:tr, :tc], north[:tr, tc:]
    s_a, s_c = south[:tr, :tc], south[:tr, tc:]
    rem = remain[:tr, :tc]
    zero = jnp.zeros((tr, tc), jnp.float32)
    def forward(l, reduced):
        below = jnp.where(l > 0, se_ref[d0 + jnp.maximum(l - 1, 0), :tr, :tc], zero)
        inverse = inv_ref[l, :tr, :tc]
        out = []
        for s in range(species):
            f_a = forced_ref[s, l, :tr, :tc]
            f_b = forced_ref[s, l, tr:, :tc]
            f_c = forced_ref[s, l, :tr, tc:]
            from_east = jnp.where(last_row, pltpu.roll(e_b * f_b, tr - 1, 0),
                                  pltpu.roll(e_a * f_a, tr - 1, 0))
            from_west = jnp.where(first_row, pltpu.roll(w_b * f_b, 1, 0),
                                  pltpu.roll(w_a * f_a, 1, 0))
            from_north = jnp.where(last_lane, pltpu.roll(n_c * f_c, tc - 1, 1),
                                   pltpu.roll(n_a * f_a, tc - 1, 1))
            from_south = jnp.where(first_lane, pltpu.roll(s_c * f_c, 1, 1),
                                   pltpu.roll(s_a * f_a, 1, 1))
            moved = f_a * rem
            moved = moved + from_east + from_west
            moved = moved + from_north + from_south
            r = (moved + below * reduced[s]) * inverse
            red_ref[s, l, :tr, :tc] = r
            out.append(r)
        return tuple(out)

    lax.fori_loop(0, levels, forward, (zero,) * species, unroll=4)

    def backward(i, result):
        l = levels - 1 - i
        ratio = ratio_ref[l, :tr, :tc]
        out = []
        for s in range(species):
            r = red_ref[s, l, :tr, :tc] - ratio * result[s]
            out_ref[s, l] = r
            out.append(r)
        return tuple(out)

    surface = lax.fori_loop(0, levels, backward, (zero,) * species, unroll=4)
    for s in range(species):
        ss_ref[s] = ss_ref[s] + prior_ref[s] * surface[s]


def steps_call(steps, species, levels, n_statics, right, left, sright, sleft, st_own, st_xh,
               mask, prior, tall):
    _, planes, rows, tc = tall.shape
    tr = rows // 2
    lanes = mask.shape[1]
    vmem = pl.BlockSpec(memory_space=pltpu.VMEM)
    anyspace = pl.BlockSpec(memory_space=pl.ANY)
    return pl.pallas_call(
        functools.partial(_steps_kernel, steps, species, levels, n_statics),
        in_specs=[vmem] * 8 + [anyspace],
        out_specs=[vmem, vmem],
        out_shape=[jax.ShapeDtypeStruct((species, levels, tr, tc), jnp.float32),
                   jax.ShapeDtypeStruct(prior.shape, jnp.float32)],
        scratch_shapes=[
            pltpu.VMEM((steps, planes, rows, tc), jnp.float32),
            pltpu.VMEM((steps * planes, rows, tc), jnp.float32),
            pltpu.VMEM((n_statics, rows, lanes), jnp.float32),
            pltpu.VMEM((species, levels, rows, lanes), jnp.float32),
            pltpu.VMEM((species, levels, rows, lanes), jnp.float32),
            pltpu.VMEM((levels, rows, lanes), jnp.float32),
            pltpu.VMEM((levels, rows, lanes), jnp.float32),
            pltpu.SemaphoreType.DMA((steps,)),
        ],
        compiler_params=pltpu.CompilerParams(vmem_limit_bytes=48 * 1024 * 1024),
    )(right, left, sright, sleft, st_own, st_xh, mask, prior, tall)


def _pairs(axis):
    n = lax.axis_size(axis)
    return [(i, i + 1) for i in range(n - 1)], [(i + 1, i) for i in range(n - 1)]


def _whole(shapes):
    return [pl.BlockSpec(memory_space=pltpu.VMEM) for _ in shapes]


def _xpack_kernel(chans_ref, lo_ref, hi_ref):
    rows = chans_ref.shape[1]
    half = rows // 2
    row = lax.broadcasted_iota(jnp.int32, chans_ref.shape[1:], 0)

    def body(i, carry):
        a = chans_ref[2 * i]
        b = chans_ref[2 * i + 1]
        lo_ref[i] = jnp.where(row < half, a, pltpu.roll(b, half, 0))
        hi_ref[i] = jnp.where(row < half, pltpu.roll(a, half, 0), b)
        return carry

    lax.fori_loop(0, lo_ref.shape[0], body, 0, unroll=4)


def _ypack_kernel(chans_ref, below_ref, above_ref, xh_ref, right_ref, left_ref):
    rows, cols = chans_ref.shape[1:]
    half = rows // 2
    group = cols // half
    row = lax.broadcasted_iota(jnp.int32, (rows, cols), 0)
    lane = lax.broadcasted_iota(jnp.int32, (rows, cols), 1)
    zero = jnp.zeros((rows, cols), jnp.float32)

    def body(g, carry):
        acc = [zero, zero, zero, zero]
        for q2 in range(group // 2):
            i = g * (group // 2) + q2
            b = below_ref[i]
            a = above_ref[i]
            xh0 = jnp.where(row < half, b, pltpu.roll(a, half, 0))
            xh1 = jnp.where(row < half, pltpu.roll(b, half, 0), a)
            xh_ref[2 * i] = xh0
            xh_ref[2 * i + 1] = xh1
            for off, top, bot in ((0, chans_ref[2 * i], xh0), (1, chans_ref[2 * i + 1], xh1)):
                q = 2 * q2 + off
                sel = (lane >= half * q) & (lane < half * q + half)
                rs = (half * q) % cols
                ls = (half * q + half) % cols
                acc[0] = jnp.where(sel, pltpu.roll(top, rs, 1) if rs else top, acc[0])
                acc[1] = jnp.where(sel, pltpu.roll(bot, rs, 1) if rs else bot, acc[1])
                acc[2] = jnp.where(sel, pltpu.roll(top, ls, 1) if ls else top, acc[2])
                acc[3] = jnp.where(sel, pltpu.roll(bot, ls, 1) if ls else bot, acc[3])
        right_ref[g, :rows] = acc[0]
        right_ref[g, rows:] = acc[1]
        left_ref[g, :rows] = acc[2]
        left_ref[g, rows:] = acc[3]
        return carry

    lax.fori_loop(0, right_ref.shape[0], body, 0)


def extend(chans, first_static, n_statics):
    up_x, down_x = _pairs("gx")
    up_y, down_y = _pairs("gy")
    channels, rows, cols = chans.shape
    halo = rows // 2
    group = cols // halo
    pairs = jax.ShapeDtypeStruct((channels // 2, rows, cols), jnp.float32)
    lo, hi = pl.pallas_call(
        _xpack_kernel, out_shape=[pairs, pairs],
        in_specs=_whole([chans]), out_specs=_whole([0, 0]))(chans)
    below = lax.ppermute(lo, "gx", down_x)
    above = lax.ppermute(hi, "gx", up_x)
    packed = jax.ShapeDtypeStruct((channels // group, 2 * rows, cols), jnp.float32)
    xh, right, left = pl.pallas_call(
        _ypack_kernel,
        out_shape=[jax.ShapeDtypeStruct(chans.shape, jnp.float32), packed, packed],
        in_specs=_whole([0, 0, 0]), out_specs=_whole([0, 0, 0]))(chans, below, above)
    right = lax.ppermute(right, "gy", down_y)
    left = lax.ppermute(left, "gy", up_y)
    return xh, right, left


def local(pixel_adjoint, pixel_owner, pixel_column, pixel_level, wind_x, wind_y,
          diffusivity, prior_emission, region_map):
    gx_n = lax.axis_size("gx")
    gy_n = lax.axis_size("gy")
    devices = gx_n * gy_n
    steps, rows, cols = wind_x.shape
    levels = diffusivity.shape[0] + 1
    species = prior_emission.shape[0]
    kernel = pixel_adjoint.shape[1] // species
    pixels = pixel_adjoint.shape[2]
    capacity = 2 * pixels // devices
    cells = rows * cols
    slots = devices * capacity
    halo = rows // 2
    assert steps <= halo
    lanes = 2 * cols
    ext_rows = 2 * rows

    placed = pack_call(capacity, slots, pixel_adjoint, pixel_owner, pixel_column, pixel_level)
    received = lax.all_to_all(placed, ("gx", "gy"), 2, 2, tiled=True)

    up_x, down_x = _pairs("gx")
    below = lax.ppermute(received, "gx", down_x)
    above = lax.ppermute(received, "gx", up_x)
    tall, right, left = forcing_call(species, kernel, levels, received, below, above, cols)
    up_y, down_y = _pairs("gy")
    right = lax.ppermute(right, "gy", down_y)
    left = lax.ppermute(left, "gy", up_y)

    n_s = 2 * steps + levels - 1
    group = cols // halo
    n_pad = -(-n_s // group) * group
    statics = jnp.concatenate(
        [wind_x, wind_y, diffusivity, jnp.zeros((n_pad - n_s, rows, cols), jnp.float32)], axis=0)
    st_xh, sright, sleft = extend(statics, 0, n_s)

    gxi = lax.axis_index("gx")
    gyi = lax.axis_index("gy")
    r = jnp.arange(ext_rows, dtype=jnp.int32)[:, None]
    c = jnp.arange(lanes, dtype=jnp.int32)[None, :]
    grow = gxi * rows + jnp.where(r < rows + halo, r, r - ext_rows)
    ccol = jnp.where(c < cols + halo, c, c - lanes)
    gcol = gyi * cols + ccol
    inside = ((grow >= 0) & (grow < gx_n * rows) & (gcol >= 0) & (gcol < gy_n * cols)
              & ((c < cols + halo) | (c >= lanes - halo)))
    mask = inside.astype(jnp.float32)

    adjoint, surface_sum = steps_call(steps, species, levels, n_s, right, left, sright, sleft,
                                      statics, st_xh, mask, prior_emission, tall)

    nreg = REG_DEV * devices
    member = (region_map.reshape(-1)[:, None] == jnp.arange(nreg, dtype=jnp.int32)).astype(jnp.float32)
    partial = jnp.dot(surface_sum.reshape(species, cells), member, precision=HI)
    pieces = lax.all_to_all(partial.reshape(species, devices, nreg // devices), ("gx", "gy"), 1, 1,
                            tiled=True)
    gradient = jnp.sum(pieces, axis=1)
    return adjoint, gradient


def solution(mesh):
    in_specs = (
        P(None, None, ("gx", "gy")),
        P(None, ("gx", "gy"), None),
        P(None, ("gx", "gy")),
        P(None, ("gx", "gy")),
        P(None, "gx", "gy"),
        P(None, "gx", "gy"),
        P(None, "gx", "gy"),
        P(None, "gx", "gy"),
        P("gx", "gy"),
    )
    out_specs = (P(None, None, "gx", "gy"), P(None, ("gx", "gy")))
    return jax.shard_map(local, mesh=mesh, in_specs=in_specs, out_specs=out_specs, check_vma=False)
```

```python
import functools

import jax
import jax.numpy as jnp
from jax import lax
from jax.experimental import pallas as pl
from jax.experimental.pallas import tpu as pltpu
from jax.sharding import PartitionSpec as P

HI = lax.Precision.HIGHEST
REG_DEV = 8


def _full(shape):
    nd = len(shape)
    return pl.BlockSpec(shape, lambda i, _n=nd: (0,) * _n)


def _unpack(r, l, q, cols, half):
    lane = lax.broadcasted_iota(jnp.int32, r.shape, 1)
    rs = (cols - half * q) % cols
    ls = (cols - half - half * q) % cols
    return jnp.where(lane < half, pltpu.roll(r, rs, 1) if rs else r,
                     jnp.where(lane >= cols - half, pltpu.roll(l, ls, 1) if ls else l, 0.0))


def _static_plane(c, refs):
    for ref in refs:
        if c < ref.shape[0]:
            return ref[c]
        c -= ref.shape[0]
    return jnp.zeros(refs[0].shape[1:], jnp.float32)


def _pack_kernel(capacity, adj_ref, owner_ref, col_ref, lev_ref, wx_ref, wy_ref, diff_ref,
                 out_ref, lo_ref, hi_ref, rows_ref):
    steps, n_pay, pixels = adj_ref.shape
    slots = out_ref.shape[2]
    row = lax.broadcasted_iota(jnp.int32, (pixels, pixels), 0)
    lane = lax.broadcasted_iota(jnp.int32, (pixels, pixels), 1)
    slot = lax.broadcasted_iota(jnp.int32, (pixels, slots), 1).astype(jnp.float32)
    for k in range(steps):
        owner = jnp.broadcast_to(owner_ref[k].astype(jnp.float32), (pixels, pixels))
        same = (owner == jnp.transpose(owner)) & (lane < row)
        rank = jnp.sum(jnp.where(same, 1.0, 0.0), axis=1, keepdims=True)
        position = owner[:, :1] * capacity + rank
        place = jnp.where(position == slot, 1.0, 0.0)
        rows_ref[:n_pay] = adj_ref[k]
        rows_ref[n_pay:n_pay + 1] = col_ref[k:k + 1].astype(jnp.float32)
        rows_ref[n_pay + 1:n_pay + 2] = lev_ref[k:k + 1].astype(jnp.float32)
        out_ref[k] = lax.dot_general(rows_ref[...], place, (((1,), (0,)), ((), ())),
                                     precision=lax.Precision.HIGHEST,
                                     preferred_element_type=jnp.float32)
    statics = (wx_ref, wy_ref, diff_ref)
    tr = wx_ref.shape[1]
    half = tr // 2
    trow = lax.broadcasted_iota(jnp.int32, wx_ref.shape[1:], 0)
    for i in range(lo_ref.shape[0]):
        a = _static_plane(2 * i, statics)
        b = _static_plane(2 * i + 1, statics)
        lo_ref[i] = jnp.where(trow < half, a, pltpu.roll(b, half, 0))
        hi_ref[i] = jnp.where(trow < half, pltpu.roll(a, half, 0), b)


def pack_call(capacity, slots, n_pad, pixel_adjoint, pixel_owner, pixel_column, pixel_level,
              wind_x, wind_y, diffusivity):
    steps, n_pay, pixels = pixel_adjoint.shape
    rows, cols = wind_x.shape[1:]
    pairs = jax.ShapeDtypeStruct((n_pad // 2, rows, cols), jnp.float32)
    vmem = pl.BlockSpec(memory_space=pltpu.VMEM)
    return pl.pallas_call(
        functools.partial(_pack_kernel, capacity),
        in_specs=[vmem] * 7,
        out_specs=[vmem] * 3,
        out_shape=[jax.ShapeDtypeStruct((steps, n_pay + 2, slots), jnp.float32), pairs, pairs],
        scratch_shapes=[pltpu.VMEM((n_pay + 2, pixels), jnp.float32)],
    )(pixel_adjoint, pixel_owner, pixel_column, pixel_level, wind_x, wind_y, diffusivity)


def _exact_dot(a, b):
    dims = (((1,), (1,)), ((), ()))
    hi = a.astype(jnp.bfloat16)
    rest = a - hi.astype(jnp.float32)
    mid = rest.astype(jnp.bfloat16)
    lo = (rest - mid.astype(jnp.float32)).astype(jnp.bfloat16)
    out = lax.dot_general(hi, b, dims, preferred_element_type=jnp.float32)
    out = out + lax.dot_general(mid, b, dims, preferred_element_type=jnp.float32)
    return out + lax.dot_general(lo, b, dims, preferred_element_type=jnp.float32)


def _forcing_kernel(species, kernel, levels, n_statics, own_ref, below_ref, above_ref, wx_ref,
                    wy_ref, diff_ref, sb_ref, sa_ref,
                    tall_ref, right_ref, left_ref, st_xh_ref, lown_ref, lnb_ref):
    steps, _, slots = own_ref.shape
    tr2, tc = tall_ref.shape[2:]
    tr = tr2 // 2
    half = tr // 2
    group = tc // half
    n_pay = species * kernel
    lane_t = lax.broadcasted_iota(jnp.int32, (tc, slots), 0)
    row_i = lax.broadcasted_iota(jnp.int32, (tr, slots), 0)
    lev_i = lax.broadcasted_iota(jnp.int32, (levels, slots), 0)
    lane16 = lax.broadcasted_iota(jnp.int32, (tr2, tc), 1)
    right_ref[...] = jnp.zeros(right_ref.shape, jnp.float32)
    left_ref[...] = jnp.zeros(left_ref.shape, jnp.float32)
    for k in range(steps):
        hts = []
        for src, ref in enumerate((own_ref, below_ref, above_ref)):
            blk = ref[k]
            col = blk[n_pay:n_pay + 1].astype(jnp.int32)
            lev = blk[n_pay + 1:n_pay + 2].astype(jnp.int32)
            row_q = col // tc
            lane_q = col % tc
            if src == 1:
                row_q = jnp.where(row_q < half, row_q, -1)
            elif src == 2:
                row_q = jnp.where(row_q >= half, row_q, -1)
            rmask = row_i == row_q
            hts.append((lane_t == lane_q).astype(jnp.bfloat16))
            offset = lev_i - lev
            dst = lown_ref if src == 0 else lnb_ref
            c0 = 0 if src < 2 else slots
            for s in range(species):
                prof = jnp.zeros((levels, slots), jnp.float32)
                for j in range(kernel):
                    prof = prof + jnp.where(offset == j, blk[s * kernel + j:s * kernel + j + 1], 0.0)
                for l in range(levels):
                    c = s * levels + l
                    dst[c * tr:(c + 1) * tr, c0:c0 + slots] = jnp.where(
                        rmask, jnp.broadcast_to(prof[l:l + 1], (tr, slots)), 0.0)
        own = _exact_dot(lown_ref[...], hts[0])
        xh = _exact_dot(lnb_ref[...], jnp.concatenate([hts[1], hts[2]], axis=1))
        planes = own.shape[0] // tr
        tall_ref[k, :, :tr, :] = own.reshape(planes, tr, tc)
        tall_ref[k, :, tr:, :] = xh.reshape(planes, tr, tc)
        for c in range(planes):
            g, q = divmod(k * planes + c, group)
            plane = tall_ref[k, c]
            sel = (lane16 >= half * q) & (lane16 < half * q + half)
            rs = (half * q) % tc
            ls = (half * q + half) % tc
            right_ref[g] = jnp.where(sel, pltpu.roll(plane, rs, 1) if rs else plane, right_ref[g])
            left_ref[g] = jnp.where(sel, pltpu.roll(plane, ls, 1) if ls else plane, left_ref[g])
    statics = (wx_ref, wy_ref, diff_ref)
    trow = lax.broadcasted_iota(jnp.int32, (tr, tc), 0)
    base = steps * species * levels
    for i in range(sb_ref.shape[0]):
        b = sb_ref[i]
        a = sa_ref[i]
        xhs = (jnp.where(trow < half, b, pltpu.roll(a, half, 0)),
               jnp.where(trow < half, pltpu.roll(b, half, 0), a))
        for off in range(2):
            c = 2 * i + off
            st_xh_ref[c] = xhs[off]
            if c >= n_statics:
                continue
            g, q = divmod(base + c, group)
            sel = (lane16 >= half * q) & (lane16 < half * q + half)
            rs = (half * q) % tc
            ls = (half * q + half) % tc
            for part, plane in ((slice(0, tr), _static_plane(c, statics)),
                                (slice(tr, tr2), xhs[off])):
                selp = sel[part]
                right_ref[g, part] = jnp.where(
                    selp, pltpu.roll(plane, rs, 1) if rs else plane, right_ref[g, part])
                left_ref[g, part] = jnp.where(
                    selp, pltpu.roll(plane, ls, 1) if ls else plane, left_ref[g, part])


def forcing_call(species, kernel, levels, n_statics, own, below, above, wind_x, wind_y,
                 diffusivity, st_below, st_above):
    steps, _, slots = own.shape
    tr, cols = wind_x.shape[1:]
    planes = species * levels
    group = cols // (tr // 2)
    n_groups = -(-(steps * planes + n_statics) // group)
    packed = jax.ShapeDtypeStruct((n_groups, 2 * tr, cols), jnp.float32)
    vmem = pl.BlockSpec(memory_space=pltpu.VMEM)
    return pl.pallas_call(
        functools.partial(_forcing_kernel, species, kernel, levels, n_statics),
        in_specs=[vmem] * 8,
        out_specs=[vmem] * 4,
        out_shape=[jax.ShapeDtypeStruct((steps, planes, 2 * tr, cols), jnp.float32), packed,
                   packed, jax.ShapeDtypeStruct((2 * st_below.shape[0], tr, cols), jnp.float32)],
        scratch_shapes=[pltpu.VMEM((planes * tr, slots), jnp.float32),
                        pltpu.VMEM((planes * tr, 2 * slots), jnp.float32)],
    )(own, below, above, wind_x, wind_y, diffusivity, st_below, st_above)


def _steps_kernel(steps, species, levels, n_statics,
                  right_ref, left_ref, wx_ref, wy_ref, diff_ref, st_xh, mask_ref, prior_ref,
                  tall_hbm, adj_ref, ss_ref,
                  tall_buf, yh_buf, se_ref, state_ref, red_ref, ratio_ref, inv_ref, sems):
    planes = species * levels
    rows, lanes = mask_ref.shape
    tr, tc = adj_ref.shape[2:]
    half = tr // 2
    group = tc // half
    d0 = 2 * steps

    loads = {}
    for k in reversed(range(steps)):
        copy = pltpu.make_async_copy(tall_hbm.at[k], tall_buf.at[k], sems.at[k])
        copy.start()
        loads[k] = copy

    n_fgroups = steps * planes // group

    def unpack_group(g, carry):
        r = right_ref[g]
        l = left_ref[g]
        for q in range(group):
            yh_buf[g * group + q] = _unpack(r, l, q, tc, half)
        return carry

    lax.fori_loop(0, n_fgroups, unpack_group, 0)
    for c in range(n_statics):
        g, q = divmod(n_fgroups * group + c, group)
        se_ref[c, :, tc:] = _unpack(right_ref[g], left_ref[g], q, tc, half)

    for c in range(n_statics):
        se_ref[c, :tr, :tc] = _static_plane(c, (wx_ref, wy_ref, diff_ref))
        se_ref[c, tr:, :tc] = st_xh[c]

    zero = jnp.zeros((rows, lanes), jnp.float32)
    inside = mask_ref[...] > 0.5
    carried = zero
    for l in range(levels):
        below = se_ref[d0 + l - 1] if l > 0 else zero
        above = se_ref[d0 + l] if l < levels - 1 else zero
        inverse = 1.0 / (1.0 + below + above + below * carried)
        ratio = -above * inverse
        ratio_ref[l] = ratio
        inv_ref[l] = inverse
        carried = ratio

    for k in reversed(range(steps)):
        first = k == steps - 1
        last = k == 0
        if first:
            loads[k].wait()
            for s in range(species):

                def assemble(l, carry, s=s, k=k):
                    c = s * levels + l
                    state_ref[s, l, :, :tc] = tall_buf[k, c]
                    state_ref[s, l, :, tc:] = yh_buf[k * planes + c]
                    state_ref[s, l] = jnp.where(inside, state_ref[s, l], 0.0)
                    return carry

                lax.fori_loop(0, levels, assemble, 0, unroll=4)
        if not last:
            loads[k - 1].wait()

        wx = se_ref[k]
        wy = se_ref[steps + k]
        east = jnp.maximum(wx, 0.0)
        west = jnp.maximum(-wx, 0.0)
        north = jnp.maximum(wy, 0.0)
        south = jnp.maximum(-wy, 0.0)
        remain = 1.0 - (east + west + north + south)
        if last:
            _last_step(species, levels, tr, tc, state_ref, east, west, north, south, remain,
                       se_ref, d0, inv_ref, ratio_ref, red_ref, adj_ref, ss_ref, prior_ref)
            continue

        def forward(l, reduced):
            below = jnp.where(l > 0, se_ref[d0 + jnp.maximum(l - 1, 0)], zero)
            inverse = inv_ref[l]
            out = []
            for s in range(species):
                f = state_ref[s, l]
                from_east = pltpu.roll(east * f, rows - 1, 0)
                from_west = pltpu.roll(west * f, 1, 0)
                from_north = pltpu.roll(north * f, lanes - 1, 1)
                from_south = pltpu.roll(south * f, 1, 1)
                moved = f * remain
                moved = moved + from_east + from_west
                moved = moved + from_north + from_south
                r = (moved + below * reduced[s]) * inverse
                red_ref[s, l] = r
                out.append(r)
            return tuple(out)

        lax.fori_loop(0, levels, forward, (zero,) * species, unroll=4)

        def backward(i, result, k=k):
            l = levels - 1 - i
            ratio = ratio_ref[l]
            out = []
            for s in range(species):
                c = s * levels + l
                r = red_ref[s, l] - ratio * result[s]
                state_ref[s, l, :, :tc] = jnp.where(
                    inside[:, :tc], r[:, :tc] + tall_buf[k - 1, c], 0.0)
                state_ref[s, l, :, tc:] = jnp.where(
                    inside[:, tc:], r[:, tc:] + yh_buf[(k - 1) * planes + c], 0.0)
                out.append(r)
            return tuple(out)

        surface = lax.fori_loop(0, levels, backward, (zero,) * species, unroll=4)
        for s in range(species):
            if first:
                ss_ref[s] = prior_ref[s] * surface[s][:tr, :tc]
            else:
                ss_ref[s] = ss_ref[s] + prior_ref[s] * surface[s][:tr, :tc]


def _last_step(species, levels, tr, tc, forced_ref, east, west, north, south, remain, se_ref,
               d0, inv_ref, ratio_ref, red_ref, out_ref, ss_ref, prior_ref):
    row = lax.broadcasted_iota(jnp.int32, (tr, tc), 0)
    lane = lax.broadcasted_iota(jnp.int32, (tr, tc), 1)
    last_row = row == tr - 1
    first_row = row == 0
    last_lane = lane == tc - 1
    first_lane = lane == 0
    e_a, e_b = east[:tr, :tc], east[tr:, :tc]
    w_a, w_b = west[:tr, :tc], west[tr:, :tc]
    n_a, n_c = north[:tr, :tc], north[:tr, tc:]
    s_a, s_c = south[:tr, :tc], south[:tr, tc:]
    rem = remain[:tr, :tc]
    zero = jnp.zeros((tr, tc), jnp.float32)
    def forward(l, reduced):
        below = jnp.where(l > 0, se_ref[d0 + jnp.maximum(l - 1, 0), :tr, :tc], zero)
        inverse = inv_ref[l, :tr, :tc]
        out = []
        for s in range(species):
            f_a = forced_ref[s, l, :tr, :tc]
            f_b = forced_ref[s, l, tr:, :tc]
            f_c = forced_ref[s, l, :tr, tc:]
            from_east = jnp.where(last_row, pltpu.roll(e_b * f_b, tr - 1, 0),
                                  pltpu.roll(e_a * f_a, tr - 1, 0))
            from_west = jnp.where(first_row, pltpu.roll(w_b * f_b, 1, 0),
                                  pltpu.roll(w_a * f_a, 1, 0))
            from_north = jnp.where(last_lane, pltpu.roll(n_c * f_c, tc - 1, 1),
                                   pltpu.roll(n_a * f_a, tc - 1, 1))
            from_south = jnp.where(first_lane, pltpu.roll(s_c * f_c, 1, 1),
                                   pltpu.roll(s_a * f_a, 1, 1))
            moved = f_a * rem
            moved = moved + from_east + from_west
            moved = moved + from_north + from_south
            r = (moved + below * reduced[s]) * inverse
            red_ref[s, l, :tr, :tc] = r
            out.append(r)
        return tuple(out)

    lax.fori_loop(0, levels, forward, (zero,) * species, unroll=4)

    def backward(i, result):
        l = levels - 1 - i
        ratio = ratio_ref[l, :tr, :tc]
        out = []
        for s in range(species):
            r = red_ref[s, l, :tr, :tc] - ratio * result[s]
            out_ref[s, l] = r
            out.append(r)
        return tuple(out)

    surface = lax.fori_loop(0, levels, backward, (zero,) * species, unroll=4)
    for s in range(species):
        ss_ref[s] = ss_ref[s] + prior_ref[s] * surface[s]


def steps_call(steps, species, levels, n_statics, right, left, wind_x, wind_y, diffusivity,
               st_xh, mask, prior, tall):
    _, planes, rows, tc = tall.shape
    tr = rows // 2
    lanes = mask.shape[1]
    vmem = pl.BlockSpec(memory_space=pltpu.VMEM)
    anyspace = pl.BlockSpec(memory_space=pl.ANY)
    return pl.pallas_call(
        functools.partial(_steps_kernel, steps, species, levels, n_statics),
        in_specs=[vmem] * 8 + [anyspace],
        out_specs=[vmem, vmem],
        out_shape=[jax.ShapeDtypeStruct((species, levels, tr, tc), jnp.float32),
                   jax.ShapeDtypeStruct(prior.shape, jnp.float32)],
        scratch_shapes=[
            pltpu.VMEM((steps, planes, rows, tc), jnp.float32),
            pltpu.VMEM((steps * planes, rows, tc), jnp.float32),
            pltpu.VMEM((n_statics, rows, lanes), jnp.float32),
            pltpu.VMEM((species, levels, rows, lanes), jnp.float32),
            pltpu.VMEM((species, levels, rows, lanes), jnp.float32),
            pltpu.VMEM((levels, rows, lanes), jnp.float32),
            pltpu.VMEM((levels, rows, lanes), jnp.float32),
            pltpu.SemaphoreType.DMA((steps,)),
        ],
        compiler_params=pltpu.CompilerParams(vmem_limit_bytes=48 * 1024 * 1024),
    )(right, left, wind_x, wind_y, diffusivity, st_xh, mask, prior, tall)


def _pairs(axis):
    n = lax.axis_size(axis)
    return [(i, i + 1) for i in range(n - 1)], [(i + 1, i) for i in range(n - 1)]


def local(pixel_adjoint, pixel_owner, pixel_column, pixel_level, wind_x, wind_y,
          diffusivity, prior_emission, region_map):
    gx_n = lax.axis_size("gx")
    gy_n = lax.axis_size("gy")
    devices = gx_n * gy_n
    steps, rows, cols = wind_x.shape
    levels = diffusivity.shape[0] + 1
    species = prior_emission.shape[0]
    kernel = pixel_adjoint.shape[1] // species
    pixels = pixel_adjoint.shape[2]
    capacity = 2 * pixels // devices
    cells = rows * cols
    slots = devices * capacity
    halo = rows // 2
    assert steps <= halo
    lanes = 2 * cols
    ext_rows = 2 * rows

    n_s = 2 * steps + levels - 1
    group = cols // halo
    n_pad = -(-n_s // group) * group
    placed, st_lo, st_hi = pack_call(capacity, slots, n_pad, pixel_adjoint, pixel_owner,
                                     pixel_column, pixel_level, wind_x, wind_y, diffusivity)
    up_x, down_x = _pairs("gx")
    up_y, down_y = _pairs("gy")
    st_below = lax.ppermute(st_lo, "gx", down_x)
    st_above = lax.ppermute(st_hi, "gx", up_x)
    received = lax.all_to_all(placed, ("gx", "gy"), 2, 2, tiled=True)

    below = lax.ppermute(received, "gx", down_x)
    above = lax.ppermute(received, "gx", up_x)
    tall, right, left, st_xh = forcing_call(species, kernel, levels, n_s, received, below, above,
                                            wind_x, wind_y, diffusivity, st_below, st_above)
    right = lax.ppermute(right, "gy", down_y)
    left = lax.ppermute(left, "gy", up_y)

    gxi = lax.axis_index("gx")
    gyi = lax.axis_index("gy")
    r = jnp.arange(ext_rows, dtype=jnp.int32)[:, None]
    c = jnp.arange(lanes, dtype=jnp.int32)[None, :]
    grow = gxi * rows + jnp.where(r < rows + halo, r, r - ext_rows)
    ccol = jnp.where(c < cols + halo, c, c - lanes)
    gcol = gyi * cols + ccol
    inside = ((grow >= 0) & (grow < gx_n * rows) & (gcol >= 0) & (gcol < gy_n * cols)
              & ((c < cols + halo) | (c >= lanes - halo)))
    mask = inside.astype(jnp.float32)

    adjoint, surface_sum = steps_call(steps, species, levels, n_s, right, left, wind_x, wind_y,
                                      diffusivity, st_xh, mask, prior_emission, tall)

    nreg = REG_DEV * devices
    member = (region_map.reshape(-1)[:, None] == jnp.arange(nreg, dtype=jnp.int32)).astype(jnp.float32)
    partial = jnp.dot(surface_sum.reshape(species, cells), member, precision=HI)
    pieces = lax.all_to_all(partial.reshape(species, devices, nreg // devices), ("gx", "gy"), 1, 1,
                            tiled=True)
    gradient = jnp.sum(pieces, axis=1)
    return adjoint, gradient


def solution(mesh):
    in_specs = (
        P(None, None, ("gx", "gy")),
        P(None, ("gx", "gy"), None),
        P(None, ("gx", "gy")),
        P(None, ("gx", "gy")),
        P(None, "gx", "gy"),
        P(None, "gx", "gy"),
        P(None, "gx", "gy"),
        P(None, "gx", "gy"),
        P("gx", "gy"),
    )
    out_specs = (P(None, None, "gx", "gy"), P(None, ("gx", "gy")))
    return jax.shard_map(local, mesh=mesh, in_specs=in_specs, out_specs=out_specs, check_vma=False)
```

```python
import functools

import jax
import jax.numpy as jnp
from jax import lax
from jax.experimental import pallas as pl
from jax.experimental.pallas import tpu as pltpu
from jax.sharding import PartitionSpec as P

HI = lax.Precision.HIGHEST
REG_DEV = 8


def _full(shape):
    nd = len(shape)
    return pl.BlockSpec(shape, lambda i, _n=nd: (0,) * _n)


def _unpack(r, l, q, cols, half):
    lane = lax.broadcasted_iota(jnp.int32, r.shape, 1)
    rs = (cols - half * q) % cols
    ls = (cols - half - half * q) % cols
    return jnp.where(lane < half, pltpu.roll(r, rs, 1) if rs else r,
                     jnp.where(lane >= cols - half, pltpu.roll(l, ls, 1) if ls else l, 0.0))


def _static_plane(c, refs):
    for ref in refs:
        if c < ref.shape[0]:
            return ref[c]
        c -= ref.shape[0]
    return jnp.zeros(refs[0].shape[1:], jnp.float32)


def _pack_kernel(capacity, adj_ref, owner_ref, col_ref, lev_ref, wx_ref, wy_ref, diff_ref,
                 out_ref, lo_ref, hi_ref, rows_ref, tbuf_ref):
    steps, n_pay, pixels = adj_ref.shape
    devices, width = out_ref.shape
    block = width // (steps * capacity)
    row = lax.broadcasted_iota(jnp.int32, (pixels, pixels), 0)
    lane = lax.broadcasted_iota(jnp.int32, (pixels, pixels), 1)
    dest = lax.broadcasted_iota(jnp.int32, (pixels, devices), 1).astype(jnp.float32)
    tbuf_ref[...] = jnp.zeros(tbuf_ref.shape, jnp.float32)
    for k in range(steps):
        across = jnp.broadcast_to(owner_ref[k:k + 1].astype(jnp.float32), (pixels, pixels))
        down = jnp.transpose(across)
        same = (down == across) & (lane < row)
        rank = jnp.sum(jnp.where(same, 1.0, 0.0), axis=1, keepdims=True)
        owner = down[:, :devices]
        rows_ref[:n_pay] = adj_ref[k]
        rows_ref[n_pay:n_pay + 1] = col_ref[k:k + 1].astype(jnp.float32)
        rows_ref[n_pay + 1:n_pay + 2] = lev_ref[k:k + 1].astype(jnp.float32)
        for j in range(capacity):
            pick = jnp.where((owner == dest) & (rank[:, :1] == j), 1.0, 0.0)
            at = (k * capacity + j) * block
            tbuf_ref[at:at + n_pay + 2] = lax.dot_general(
                rows_ref[...], pick, (((1,), (0,)), ((), ())),
                precision=lax.Precision.HIGHEST, preferred_element_type=jnp.float32)
    out_ref[...] = jnp.transpose(tbuf_ref[...])
    statics = (wx_ref, wy_ref, diff_ref)
    tr = wx_ref.shape[1]
    half = tr // 2
    trow = lax.broadcasted_iota(jnp.int32, wx_ref.shape[1:], 0)
    for i in range(lo_ref.shape[0]):
        a = _static_plane(2 * i, statics)
        b = _static_plane(2 * i + 1, statics)
        lo_ref[i] = jnp.where(trow < half, a, pltpu.roll(b, half, 0))
        hi_ref[i] = jnp.where(trow < half, pltpu.roll(a, half, 0), b)


def pack_call(capacity, devices, n_pad, pixel_adjoint, pixel_owner, pixel_column, pixel_level,
              wind_x, wind_y, diffusivity):
    steps, n_pay, pixels = pixel_adjoint.shape
    rows, cols = wind_x.shape[1:]
    block = -(-(n_pay + 2) // 16) * 16
    width = steps * capacity * block
    pairs = jax.ShapeDtypeStruct((n_pad // 2, rows, cols), jnp.float32)
    vmem = pl.BlockSpec(memory_space=pltpu.VMEM)
    return pl.pallas_call(
        functools.partial(_pack_kernel, capacity),
        in_specs=[vmem] * 7,
        out_specs=[vmem] * 3,
        out_shape=[jax.ShapeDtypeStruct((devices, width), jnp.float32), pairs, pairs],
        scratch_shapes=[pltpu.VMEM((n_pay + 2, pixels), jnp.float32),
                        pltpu.VMEM((width, devices), jnp.float32)],
    )(pixel_adjoint, pixel_owner.reshape(steps, pixels), pixel_column, pixel_level, wind_x,
      wind_y, diffusivity)


def _exact_dot(a, b):
    dims = (((1,), (1,)), ((), ()))
    hi = a.astype(jnp.bfloat16)
    rest = a - hi.astype(jnp.float32)
    mid = rest.astype(jnp.bfloat16)
    lo = (rest - mid.astype(jnp.float32)).astype(jnp.bfloat16)
    out = lax.dot_general(hi, b, dims, preferred_element_type=jnp.float32)
    out = out + lax.dot_general(mid, b, dims, preferred_element_type=jnp.float32)
    return out + lax.dot_general(lo, b, dims, preferred_element_type=jnp.float32)


def _forcing_kernel(species, kernel, levels, n_statics, own_ref, below_ref, above_ref, wx_ref,
                    wy_ref, diff_ref, sb_ref, sa_ref,
                    tall_ref, right_ref, left_ref, st_xh_ref, lown_ref, lnb_ref, *trans):
    steps = tall_ref.shape[0]
    devices, width = own_ref.shape
    capacity = 2
    block = width // (steps * capacity)
    slots = devices * capacity
    tr2, tc = tall_ref.shape[2:]
    tr = tr2 // 2
    half = tr // 2
    group = tc // half
    n_pay = species * kernel
    lane_t = lax.broadcasted_iota(jnp.int32, (tc, slots), 0)
    row_i = lax.broadcasted_iota(jnp.int32, (tr, slots), 0)
    lev_i = lax.broadcasted_iota(jnp.int32, (levels, slots), 0)
    lane16 = lax.broadcasted_iota(jnp.int32, (tr2, tc), 1)
    right_ref[...] = jnp.zeros(right_ref.shape, jnp.float32)
    left_ref[...] = jnp.zeros(left_ref.shape, jnp.float32)
    for tref, ref in zip(trans, (own_ref, below_ref, above_ref)):
        tref[...] = jnp.transpose(ref[...])
    for k in range(steps):
        hts = []
        for src, tref in enumerate(trans):
            at = k * capacity * block
            blk = jnp.concatenate(
                [tref[at + j * block:at + j * block + n_pay + 2] for j in range(capacity)], axis=1)
            col = blk[n_pay:n_pay + 1].astype(jnp.int32)
            lev = blk[n_pay + 1:n_pay + 2].astype(jnp.int32)
            row_q = col // tc
            lane_q = col % tc
            if src == 1:
                row_q = jnp.where(row_q < half, row_q, -1)
            elif src == 2:
                row_q = jnp.where(row_q >= half, row_q, -1)
            rmask = row_i == row_q
            hts.append((lane_t == lane_q).astype(jnp.bfloat16))
            offset = lev_i - lev
            dst = lown_ref if src == 0 else lnb_ref
            c0 = 0 if src < 2 else slots
            for s in range(species):
                prof = jnp.zeros((levels, slots), jnp.float32)
                for j in range(kernel):
                    prof = prof + jnp.where(offset == j, blk[s * kernel + j:s * kernel + j + 1], 0.0)
                for l in range(levels):
                    c = s * levels + l
                    dst[c * tr:(c + 1) * tr, c0:c0 + slots] = jnp.where(
                        rmask, jnp.broadcast_to(prof[l:l + 1], (tr, slots)), 0.0)
        own = _exact_dot(lown_ref[...], hts[0])
        xh = _exact_dot(lnb_ref[...], jnp.concatenate([hts[1], hts[2]], axis=1))
        planes = own.shape[0] // tr
        tall_ref[k, :, :tr, :] = own.reshape(planes, tr, tc)
        tall_ref[k, :, tr:, :] = xh.reshape(planes, tr, tc)
        for c in range(planes):
            g, q = divmod(k * planes + c, group)
            plane = tall_ref[k, c]
            sel = (lane16 >= half * q) & (lane16 < half * q + half)
            rs = (half * q) % tc
            ls = (half * q + half) % tc
            right_ref[g] = jnp.where(sel, pltpu.roll(plane, rs, 1) if rs else plane, right_ref[g])
            left_ref[g] = jnp.where(sel, pltpu.roll(plane, ls, 1) if ls else plane, left_ref[g])
    statics = (wx_ref, wy_ref, diff_ref)
    trow = lax.broadcasted_iota(jnp.int32, (tr, tc), 0)
    base = steps * species * levels
    for i in range(sb_ref.shape[0]):
        b = sb_ref[i]
        a = sa_ref[i]
        xhs = (jnp.where(trow < half, b, pltpu.roll(a, half, 0)),
               jnp.where(trow < half, pltpu.roll(b, half, 0), a))
        for off in range(2):
            c = 2 * i + off
            st_xh_ref[c] = xhs[off]
            if c >= n_statics:
                continue
            g, q = divmod(base + c, group)
            sel = (lane16 >= half * q) & (lane16 < half * q + half)
            rs = (half * q) % tc
            ls = (half * q + half) % tc
            for part, plane in ((slice(0, tr), _static_plane(c, statics)),
                                (slice(tr, tr2), xhs[off])):
                selp = sel[part]
                right_ref[g, part] = jnp.where(
                    selp, pltpu.roll(plane, rs, 1) if rs else plane, right_ref[g, part])
                left_ref[g, part] = jnp.where(
                    selp, pltpu.roll(plane, ls, 1) if ls else plane, left_ref[g, part])


def forcing_call(species, kernel, levels, n_statics, own, below, above, wind_x, wind_y,
                 diffusivity, st_below, st_above):
    steps = wind_x.shape[0]
    devices, width = own.shape
    slots = 2 * devices
    tr, cols = wind_x.shape[1:]
    planes = species * levels
    group = cols // (tr // 2)
    n_groups = -(-(steps * planes + n_statics) // group)
    packed = jax.ShapeDtypeStruct((n_groups, 2 * tr, cols), jnp.float32)
    vmem = pl.BlockSpec(memory_space=pltpu.VMEM)
    return pl.pallas_call(
        functools.partial(_forcing_kernel, species, kernel, levels, n_statics),
        in_specs=[vmem] * 8,
        out_specs=[vmem] * 4,
        out_shape=[jax.ShapeDtypeStruct((steps, planes, 2 * tr, cols), jnp.float32), packed,
                   packed, jax.ShapeDtypeStruct((2 * st_below.shape[0], tr, cols), jnp.float32)],
        scratch_shapes=[pltpu.VMEM((planes * tr, slots), jnp.float32),
                        pltpu.VMEM((planes * tr, 2 * slots), jnp.float32)]
        + [pltpu.VMEM((width, devices), jnp.float32)] * 3,
    )(own, below, above, wind_x, wind_y, diffusivity, st_below, st_above)


def _steps_kernel(steps, species, levels, n_statics,
                  right_ref, left_ref, wx_ref, wy_ref, diff_ref, st_xh, mask_ref, prior_ref,
                  tall_hbm, adj_ref, ss_ref,
                  tall_buf, yh_buf, se_ref, state_ref, red_ref, ratio_ref, inv_ref, sems):
    planes = species * levels
    rows, lanes = mask_ref.shape
    tr, tc = adj_ref.shape[2:]
    half = tr // 2
    group = tc // half
    d0 = 2 * steps

    loads = {}
    for k in reversed(range(steps)):
        copy = pltpu.make_async_copy(tall_hbm.at[k], tall_buf.at[k], sems.at[k])
        copy.start()
        loads[k] = copy

    n_fgroups = steps * planes // group

    def unpack_group(g, carry):
        r = right_ref[g]
        l = left_ref[g]
        for q in range(group):
            yh_buf[g * group + q] = _unpack(r, l, q, tc, half)
        return carry

    lax.fori_loop(0, n_fgroups, unpack_group, 0)
    for c in range(n_statics):
        g, q = divmod(n_fgroups * group + c, group)
        se_ref[c, :, tc:] = _unpack(right_ref[g], left_ref[g], q, tc, half)

    for c in range(n_statics):
        se_ref[c, :tr, :tc] = _static_plane(c, (wx_ref, wy_ref, diff_ref))
        se_ref[c, tr:, :tc] = st_xh[c]

    zero = jnp.zeros((rows, lanes), jnp.float32)
    inside = mask_ref[...] > 0.5
    carried = zero
    for l in range(levels):
        below = se_ref[d0 + l - 1] if l > 0 else zero
        above = se_ref[d0 + l] if l < levels - 1 else zero
        inverse = 1.0 / (1.0 + below + above + below * carried)
        ratio = -above * inverse
        ratio_ref[l] = ratio
        inv_ref[l] = inverse
        carried = ratio

    for k in reversed(range(steps)):
        first = k == steps - 1
        last = k == 0
        if first:
            loads[k].wait()
            for s in range(species):

                def assemble(l, carry, s=s, k=k):
                    c = s * levels + l
                    state_ref[s, l, :, :tc] = tall_buf[k, c]
                    state_ref[s, l, :, tc:] = yh_buf[k * planes + c]
                    state_ref[s, l] = jnp.where(inside, state_ref[s, l], 0.0)
                    return carry

                lax.fori_loop(0, levels, assemble, 0, unroll=4)
        if not last:
            loads[k - 1].wait()

        wx = se_ref[k]
        wy = se_ref[steps + k]
        east = jnp.maximum(wx, 0.0)
        west = jnp.maximum(-wx, 0.0)
        north = jnp.maximum(wy, 0.0)
        south = jnp.maximum(-wy, 0.0)
        remain = 1.0 - (east + west + north + south)
        if last:
            _last_step(species, levels, tr, tc, state_ref, east, west, north, south, remain,
                       se_ref, d0, inv_ref, ratio_ref, red_ref, adj_ref, ss_ref, prior_ref)
            continue

        def forward(l, reduced):
            below = jnp.where(l > 0, se_ref[d0 + jnp.maximum(l - 1, 0)], zero)
            inverse = inv_ref[l]
            out = []
            for s in range(species):
                f = state_ref[s, l]
                from_east = pltpu.roll(east * f, rows - 1, 0)
                from_west = pltpu.roll(west * f, 1, 0)
                from_north = pltpu.roll(north * f, lanes - 1, 1)
                from_south = pltpu.roll(south * f, 1, 1)
                moved = f * remain
                moved = moved + from_east + from_west
                moved = moved + from_north + from_south
                r = (moved + below * reduced[s]) * inverse
                red_ref[s, l] = r
                out.append(r)
            return tuple(out)

        lax.fori_loop(0, levels, forward, (zero,) * species, unroll=4)

        def backward(i, result, k=k):
            l = levels - 1 - i
            ratio = ratio_ref[l]
            out = []
            for s in range(species):
                c = s * levels + l
                r = red_ref[s, l] - ratio * result[s]
                state_ref[s, l, :, :tc] = jnp.where(
                    inside[:, :tc], r[:, :tc] + tall_buf[k - 1, c], 0.0)
                state_ref[s, l, :, tc:] = jnp.where(
                    inside[:, tc:], r[:, tc:] + yh_buf[(k - 1) * planes + c], 0.0)
                out.append(r)
            return tuple(out)

        surface = lax.fori_loop(0, levels, backward, (zero,) * species, unroll=4)
        for s in range(species):
            if first:
                ss_ref[s] = prior_ref[s] * surface[s][:tr, :tc]
            else:
                ss_ref[s] = ss_ref[s] + prior_ref[s] * surface[s][:tr, :tc]


def _last_step(species, levels, tr, tc, forced_ref, east, west, north, south, remain, se_ref,
               d0, inv_ref, ratio_ref, red_ref, out_ref, ss_ref, prior_ref):
    row = lax.broadcasted_iota(jnp.int32, (tr, tc), 0)
    lane = lax.broadcasted_iota(jnp.int32, (tr, tc), 1)
    last_row = row == tr - 1
    first_row = row == 0
    last_lane = lane == tc - 1
    first_lane = lane == 0
    e_a, e_b = east[:tr, :tc], east[tr:, :tc]
    w_a, w_b = west[:tr, :tc], west[tr:, :tc]
    n_a, n_c = north[:tr, :tc], north[:tr, tc:]
    s_a, s_c = south[:tr, :tc], south[:tr, tc:]
    rem = remain[:tr, :tc]
    zero = jnp.zeros((tr, tc), jnp.float32)
    def forward(l, reduced):
        below = jnp.where(l > 0, se_ref[d0 + jnp.maximum(l - 1, 0), :tr, :tc], zero)
        inverse = inv_ref[l, :tr, :tc]
        out = []
        for s in range(species):
            f_a = forced_ref[s, l, :tr, :tc]
            f_b = forced_ref[s, l, tr:, :tc]
            f_c = forced_ref[s, l, :tr, tc:]
            from_east = jnp.where(last_row, pltpu.roll(e_b * f_b, tr - 1, 0),
                                  pltpu.roll(e_a * f_a, tr - 1, 0))
            from_west = jnp.where(first_row, pltpu.roll(w_b * f_b, 1, 0),
                                  pltpu.roll(w_a * f_a, 1, 0))
            from_north = jnp.where(last_lane, pltpu.roll(n_c * f_c, tc - 1, 1),
                                   pltpu.roll(n_a * f_a, tc - 1, 1))
            from_south = jnp.where(first_lane, pltpu.roll(s_c * f_c, 1, 1),
                                   pltpu.roll(s_a * f_a, 1, 1))
            moved = f_a * rem
            moved = moved + from_east + from_west
            moved = moved + from_north + from_south
            r = (moved + below * reduced[s]) * inverse
            red_ref[s, l, :tr, :tc] = r
            out.append(r)
        return tuple(out)

    lax.fori_loop(0, levels, forward, (zero,) * species, unroll=4)

    def backward(i, result):
        l = levels - 1 - i
        ratio = ratio_ref[l, :tr, :tc]
        out = []
        for s in range(species):
            r = red_ref[s, l, :tr, :tc] - ratio * result[s]
            out_ref[s, l] = r
            out.append(r)
        return tuple(out)

    surface = lax.fori_loop(0, levels, backward, (zero,) * species, unroll=4)
    for s in range(species):
        ss_ref[s] = ss_ref[s] + prior_ref[s] * surface[s]


def steps_call(steps, species, levels, n_statics, right, left, wind_x, wind_y, diffusivity,
               st_xh, mask, prior, tall):
    _, planes, rows, tc = tall.shape
    tr = rows // 2
    lanes = mask.shape[1]
    vmem = pl.BlockSpec(memory_space=pltpu.VMEM)
    anyspace = pl.BlockSpec(memory_space=pl.ANY)
    return pl.pallas_call(
        functools.partial(_steps_kernel, steps, species, levels, n_statics),
        in_specs=[vmem] * 8 + [anyspace],
        out_specs=[vmem, vmem],
        out_shape=[jax.ShapeDtypeStruct((species, levels, tr, tc), jnp.float32),
                   jax.ShapeDtypeStruct(prior.shape, jnp.float32)],
        scratch_shapes=[
            pltpu.VMEM((steps, planes, rows, tc), jnp.float32),
            pltpu.VMEM((steps * planes, rows, tc), jnp.float32),
            pltpu.VMEM((n_statics, rows, lanes), jnp.float32),
            pltpu.VMEM((species, levels, rows, lanes), jnp.float32),
            pltpu.VMEM((species, levels, rows, lanes), jnp.float32),
            pltpu.VMEM((levels, rows, lanes), jnp.float32),
            pltpu.VMEM((levels, rows, lanes), jnp.float32),
            pltpu.SemaphoreType.DMA((steps,)),
        ],
        compiler_params=pltpu.CompilerParams(vmem_limit_bytes=48 * 1024 * 1024),
    )(right, left, wind_x, wind_y, diffusivity, st_xh, mask, prior, tall)


def _pairs(axis):
    n = lax.axis_size(axis)
    return [(i, i + 1) for i in range(n - 1)], [(i + 1, i) for i in range(n - 1)]


def local(pixel_adjoint, pixel_owner, pixel_column, pixel_level, wind_x, wind_y,
          diffusivity, prior_emission, region_map):
    gx_n = lax.axis_size("gx")
    gy_n = lax.axis_size("gy")
    devices = gx_n * gy_n
    steps, rows, cols = wind_x.shape
    levels = diffusivity.shape[0] + 1
    species = prior_emission.shape[0]
    kernel = pixel_adjoint.shape[1] // species
    pixels = pixel_adjoint.shape[2]
    capacity = 2 * pixels // devices
    cells = rows * cols
    slots = devices * capacity
    halo = rows // 2
    assert steps <= halo
    lanes = 2 * cols
    ext_rows = 2 * rows

    n_s = 2 * steps + levels - 1
    group = cols // halo
    n_pad = -(-n_s // group) * group
    placed, st_lo, st_hi = pack_call(capacity, devices, n_pad, pixel_adjoint, pixel_owner,
                                     pixel_column, pixel_level, wind_x, wind_y, diffusivity)
    up_x, down_x = _pairs("gx")
    up_y, down_y = _pairs("gy")
    st_below = lax.ppermute(st_lo, "gx", down_x)
    st_above = lax.ppermute(st_hi, "gx", up_x)
    received = lax.all_to_all(placed, ("gx", "gy"), 0, 0, tiled=True)

    below = lax.ppermute(received, "gx", down_x)
    above = lax.ppermute(received, "gx", up_x)
    tall, right, left, st_xh = forcing_call(species, kernel, levels, n_s, received, below, above,
                                            wind_x, wind_y, diffusivity, st_below, st_above)
    right = lax.ppermute(right, "gy", down_y)
    left = lax.ppermute(left, "gy", up_y)

    gxi = lax.axis_index("gx")
    gyi = lax.axis_index("gy")
    r = jnp.arange(ext_rows, dtype=jnp.int32)[:, None]
    c = jnp.arange(lanes, dtype=jnp.int32)[None, :]
    grow = gxi * rows + jnp.where(r < rows + halo, r, r - ext_rows)
    ccol = jnp.where(c < cols + halo, c, c - lanes)
    gcol = gyi * cols + ccol
    inside = ((grow >= 0) & (grow < gx_n * rows) & (gcol >= 0) & (gcol < gy_n * cols)
              & ((c < cols + halo) | (c >= lanes - halo)))
    mask = inside.astype(jnp.float32)

    adjoint, surface_sum = steps_call(steps, species, levels, n_s, right, left, wind_x, wind_y,
                                      diffusivity, st_xh, mask, prior_emission, tall)

    nreg = REG_DEV * devices
    member = (region_map.reshape(-1)[:, None] == jnp.arange(nreg, dtype=jnp.int32)).astype(jnp.float32)
    partial = jnp.dot(surface_sum.reshape(species, cells), member, precision=HI)
    pieces = lax.all_to_all(partial.reshape(species, devices, nreg // devices), ("gx", "gy"), 1, 1,
                            tiled=True)
    gradient = jnp.sum(pieces, axis=1)
    return adjoint, gradient


def solution(mesh):
    in_specs = (
        P(None, None, ("gx", "gy")),
        P(None, ("gx", "gy"), None),
        P(None, ("gx", "gy")),
        P(None, ("gx", "gy")),
        P(None, "gx", "gy"),
        P(None, "gx", "gy"),
        P(None, "gx", "gy"),
        P(None, "gx", "gy"),
        P("gx", "gy"),
    )
    out_specs = (P(None, None, "gx", "gy"), P(None, ("gx", "gy")))
    return jax.shard_map(local, mesh=mesh, in_specs=in_specs, out_specs=out_specs, check_vma=False)
```

```python
import functools

import jax
import jax.numpy as jnp
from jax import lax
from jax.experimental import pallas as pl
from jax.experimental.pallas import tpu as pltpu
from jax.sharding import PartitionSpec as P

HI = lax.Precision.HIGHEST
REG_DEV = 8


def _full(shape):
    nd = len(shape)
    return pl.BlockSpec(shape, lambda i, _n=nd: (0,) * _n)


def _unpack(r, l, q, cols, half):
    lane = lax.broadcasted_iota(jnp.int32, r.shape, 1)
    rs = (cols - half * q) % cols
    ls = (cols - half - half * q) % cols
    return jnp.where(lane < half, pltpu.roll(r, rs, 1) if rs else r,
                     jnp.where(lane >= cols - half, pltpu.roll(l, ls, 1) if ls else l, 0.0))


def _static_plane(c, refs):
    for ref in refs:
        if c < ref.shape[0]:
            return ref[c]
        c -= ref.shape[0]
    return jnp.zeros(refs[0].shape[1:], jnp.float32)


def _pack_kernel(capacity, adj_ref, owner_ref, col_ref, lev_ref, wx_ref, wy_ref, diff_ref,
                 out_ref, lo_ref, hi_ref, rows_ref, tbuf_ref):
    steps, n_pay, pixels = adj_ref.shape
    devices, width = out_ref.shape
    block = width // (steps * capacity)
    row = lax.broadcasted_iota(jnp.int32, (pixels, pixels), 0)
    lane = lax.broadcasted_iota(jnp.int32, (pixels, pixels), 1)
    dest = lax.broadcasted_iota(jnp.int32, (pixels, devices), 1).astype(jnp.float32)
    tbuf_ref[...] = jnp.zeros(tbuf_ref.shape, jnp.float32)
    for k in range(steps):
        across = jnp.broadcast_to(owner_ref[k:k + 1].astype(jnp.float32), (pixels, pixels))
        down = jnp.transpose(across)
        same = (down == across) & (lane < row)
        rank = jnp.sum(jnp.where(same, 1.0, 0.0), axis=1, keepdims=True)
        owner = down[:, :devices]
        rows_ref[:n_pay] = adj_ref[k]
        rows_ref[n_pay:n_pay + 1] = col_ref[k:k + 1].astype(jnp.float32)
        rows_ref[n_pay + 1:n_pay + 2] = lev_ref[k:k + 1].astype(jnp.float32)
        for j in range(capacity):
            pick = jnp.where((owner == dest) & (rank[:, :1] == j), 1.0, 0.0)
            at = (k * capacity + j) * block
            tbuf_ref[at:at + n_pay + 2] = lax.dot_general(
                rows_ref[...], pick, (((1,), (0,)), ((), ())),
                precision=lax.Precision.HIGHEST, preferred_element_type=jnp.float32)
    out_ref[...] = jnp.transpose(tbuf_ref[...])
    statics = (wx_ref, wy_ref, diff_ref)
    tr = wx_ref.shape[1]
    half = tr // 2
    trow = lax.broadcasted_iota(jnp.int32, wx_ref.shape[1:], 0)
    for i in range(lo_ref.shape[0]):
        a = _static_plane(2 * i, statics)
        b = _static_plane(2 * i + 1, statics)
        lo_ref[i] = jnp.where(trow < half, a, pltpu.roll(b, half, 0))
        hi_ref[i] = jnp.where(trow < half, pltpu.roll(a, half, 0), b)


def pack_call(capacity, devices, n_pad, pixel_adjoint, pixel_owner, pixel_column, pixel_level,
              wind_x, wind_y, diffusivity):
    steps, n_pay, pixels = pixel_adjoint.shape
    rows, cols = wind_x.shape[1:]
    block = -(-(n_pay + 2) // 16) * 16
    width = steps * capacity * block
    pairs = jax.ShapeDtypeStruct((n_pad // 2, rows, cols), jnp.float32)
    vmem = pl.BlockSpec(memory_space=pltpu.VMEM)
    return pl.pallas_call(
        functools.partial(_pack_kernel, capacity),
        in_specs=[vmem] * 7,
        out_specs=[vmem] * 3,
        out_shape=[jax.ShapeDtypeStruct((devices, width), jnp.float32), pairs, pairs],
        scratch_shapes=[pltpu.VMEM((n_pay + 2, pixels), jnp.float32),
                        pltpu.VMEM((width, devices), jnp.float32)],
    )(pixel_adjoint, pixel_owner.reshape(steps, pixels), pixel_column, pixel_level, wind_x,
      wind_y, diffusivity)


def _exact_dot(a, b):
    dims = (((1,), (1,)), ((), ()))
    hi = a.astype(jnp.bfloat16)
    rest = a - hi.astype(jnp.float32)
    mid = rest.astype(jnp.bfloat16)
    lo = (rest - mid.astype(jnp.float32)).astype(jnp.bfloat16)
    out = lax.dot_general(hi, b, dims, preferred_element_type=jnp.float32)
    out = out + lax.dot_general(mid, b, dims, preferred_element_type=jnp.float32)
    return out + lax.dot_general(lo, b, dims, preferred_element_type=jnp.float32)


def _forcing_kernel(species, kernel, levels, n_statics, own_ref, below_ref, above_ref, wx_ref,
                    wy_ref, diff_ref, sb_ref, sa_ref,
                    tall_ref, right_ref, left_ref, st_xh_ref, lown_ref, lnb_ref, *trans):
    steps = tall_ref.shape[0]
    devices, width = own_ref.shape
    capacity = 2
    block = width // (steps * capacity)
    slots = devices * capacity
    tr2, tc = tall_ref.shape[2:]
    tr = tr2 // 2
    half = tr // 2
    group = tc // half
    n_pay = species * kernel
    lane_t = lax.broadcasted_iota(jnp.int32, (tc, slots), 0)
    row_i = lax.broadcasted_iota(jnp.int32, (tr, slots), 0)
    lev_i = lax.broadcasted_iota(jnp.int32, (levels, slots), 0)
    lane16 = lax.broadcasted_iota(jnp.int32, (tr2, tc), 1)
    right_ref[...] = jnp.zeros(right_ref.shape, jnp.float32)
    left_ref[...] = jnp.zeros(left_ref.shape, jnp.float32)
    for tref, ref in zip(trans, (own_ref, below_ref, above_ref)):
        tref[...] = jnp.transpose(ref[...])
    for k in range(steps):
        hts = []
        for src, tref in enumerate(trans):
            at = k * capacity * block
            blk = jnp.concatenate(
                [tref[at + j * block:at + j * block + n_pay + 2] for j in range(capacity)], axis=1)
            col = blk[n_pay:n_pay + 1].astype(jnp.int32)
            lev = blk[n_pay + 1:n_pay + 2].astype(jnp.int32)
            row_q = col // tc
            lane_q = col % tc
            if src == 1:
                row_q = jnp.where(row_q < half, row_q, -1)
            elif src == 2:
                row_q = jnp.where(row_q >= half, row_q, -1)
            rmask = row_i == row_q
            hts.append((lane_t == lane_q).astype(jnp.bfloat16))
            offset = lev_i - lev
            dst = lown_ref if src == 0 else lnb_ref
            c0 = 0 if src < 2 else slots
            for s in range(species):
                prof = jnp.zeros((levels, slots), jnp.float32)
                for j in range(kernel):
                    prof = prof + jnp.where(offset == j, blk[s * kernel + j:s * kernel + j + 1], 0.0)
                for l in range(levels):
                    c = s * levels + l
                    dst[c * tr:(c + 1) * tr, c0:c0 + slots] = jnp.where(
                        rmask, jnp.broadcast_to(prof[l:l + 1], (tr, slots)), 0.0)
        own = _exact_dot(lown_ref[...], hts[0])
        xh = _exact_dot(lnb_ref[...], jnp.concatenate([hts[1], hts[2]], axis=1))
        planes = own.shape[0] // tr
        tall_ref[k, :, :tr, :] = own.reshape(planes, tr, tc)
        tall_ref[k, :, tr:, :] = xh.reshape(planes, tr, tc)
        for c in range(planes):
            g, q = divmod(k * planes + c, group)
            plane = tall_ref[k, c]
            sel = (lane16 >= half * q) & (lane16 < half * q + half)
            rs = (half * q) % tc
            ls = (half * q + half) % tc
            right_ref[g] = jnp.where(sel, pltpu.roll(plane, rs, 1) if rs else plane, right_ref[g])
            left_ref[g] = jnp.where(sel, pltpu.roll(plane, ls, 1) if ls else plane, left_ref[g])
    statics = (wx_ref, wy_ref, diff_ref)
    trow = lax.broadcasted_iota(jnp.int32, (tr, tc), 0)
    base = steps * species * levels
    for i in range(sb_ref.shape[0]):
        b = sb_ref[i]
        a = sa_ref[i]
        xhs = (jnp.where(trow < half, b, pltpu.roll(a, half, 0)),
               jnp.where(trow < half, pltpu.roll(b, half, 0), a))
        for off in range(2):
            c = 2 * i + off
            st_xh_ref[c] = xhs[off]
            if c >= n_statics:
                continue
            g, q = divmod(base + c, group)
            sel = (lane16 >= half * q) & (lane16 < half * q + half)
            rs = (half * q) % tc
            ls = (half * q + half) % tc
            for part, plane in ((slice(0, tr), _static_plane(c, statics)),
                                (slice(tr, tr2), xhs[off])):
                selp = sel[part]
                right_ref[g, part] = jnp.where(
                    selp, pltpu.roll(plane, rs, 1) if rs else plane, right_ref[g, part])
                left_ref[g, part] = jnp.where(
                    selp, pltpu.roll(plane, ls, 1) if ls else plane, left_ref[g, part])


def forcing_call(species, kernel, levels, n_statics, own, below, above, wind_x, wind_y,
                 diffusivity, st_below, st_above):
    steps = wind_x.shape[0]
    devices, width = own.shape
    slots = 2 * devices
    tr, cols = wind_x.shape[1:]
    planes = species * levels
    group = cols // (tr // 2)
    n_groups = -(-(steps * planes + n_statics) // group)
    packed = jax.ShapeDtypeStruct((n_groups, 2 * tr, cols), jnp.float32)
    vmem = pl.BlockSpec(memory_space=pltpu.VMEM)
    return pl.pallas_call(
        functools.partial(_forcing_kernel, species, kernel, levels, n_statics),
        in_specs=[vmem] * 8,
        out_specs=[vmem] * 4,
        out_shape=[jax.ShapeDtypeStruct((steps, planes, 2 * tr, cols), jnp.float32), packed,
                   packed, jax.ShapeDtypeStruct((2 * st_below.shape[0], tr, cols), jnp.float32)],
        scratch_shapes=[pltpu.VMEM((planes * tr, slots), jnp.float32),
                        pltpu.VMEM((planes * tr, 2 * slots), jnp.float32)]
        + [pltpu.VMEM((width, devices), jnp.float32)] * 3,
    )(own, below, above, wind_x, wind_y, diffusivity, st_below, st_above)


def _steps_kernel(steps, species, levels, n_statics, *refs):
    n_in = 8
    hbm = refs[:n_in]
    tall_hbm, adj_ref, ss_ref = refs[n_in:n_in + 3]
    (tall_buf, yh_buf, se_ref, state_ref, red_ref, ratio_ref, inv_ref,
     sems) = refs[n_in + 3:n_in + 11]
    vbufs = refs[n_in + 11:n_in + 11 + n_in]
    in_sems = refs[n_in + 11 + n_in]
    fetch = []
    for i in range(n_in):
        copy = pltpu.make_async_copy(hbm[i], vbufs[i], in_sems.at[i])
        copy.start()
        fetch.append(copy)
    right_ref, left_ref, wx_ref, wy_ref, diff_ref, st_xh, mask_ref, prior_ref = vbufs
    planes = species * levels
    rows, lanes = mask_ref.shape
    tr, tc = adj_ref.shape[2:]
    half = tr // 2
    group = tc // half
    d0 = 2 * steps

    loads = {}
    for k in reversed(range(steps)):
        copy = pltpu.make_async_copy(tall_hbm.at[k], tall_buf.at[k], sems.at[k])
        copy.start()
        loads[k] = copy

    n_fgroups = steps * planes // group

    def unpack_group(g, carry):
        r = right_ref[g]
        l = left_ref[g]
        for q in range(group):
            yh_buf[g * group + q] = _unpack(r, l, q, tc, half)
        return carry

    fetch[0].wait()
    fetch[1].wait()
    lax.fori_loop(0, n_fgroups, unpack_group, 0)
    for c in range(n_statics):
        g, q = divmod(n_fgroups * group + c, group)
        se_ref[c, :, tc:] = _unpack(right_ref[g], left_ref[g], q, tc, half)

    for i in range(2, 6):
        fetch[i].wait()
    for c in range(n_statics):
        se_ref[c, :tr, :tc] = _static_plane(c, (wx_ref, wy_ref, diff_ref))
        se_ref[c, tr:, :tc] = st_xh[c]

    fetch[6].wait()
    fetch[7].wait()
    zero = jnp.zeros((rows, lanes), jnp.float32)
    inside = mask_ref[...] > 0.5
    carried = zero
    for l in range(levels):
        below = se_ref[d0 + l - 1] if l > 0 else zero
        above = se_ref[d0 + l] if l < levels - 1 else zero
        inverse = 1.0 / (1.0 + below + above + below * carried)
        ratio = -above * inverse
        ratio_ref[l] = ratio
        inv_ref[l] = inverse
        carried = ratio

    for k in reversed(range(steps)):
        first = k == steps - 1
        last = k == 0
        if first:
            loads[k].wait()
            for s in range(species):

                def assemble(l, carry, s=s, k=k):
                    c = s * levels + l
                    state_ref[s, l, :, :tc] = tall_buf[k, c]
                    state_ref[s, l, :, tc:] = yh_buf[k * planes + c]
                    state_ref[s, l] = jnp.where(inside, state_ref[s, l], 0.0)
                    return carry

                lax.fori_loop(0, levels, assemble, 0, unroll=4)
        if not last:
            loads[k - 1].wait()

        wx = se_ref[k]
        wy = se_ref[steps + k]
        east = jnp.maximum(wx, 0.0)
        west = jnp.maximum(-wx, 0.0)
        north = jnp.maximum(wy, 0.0)
        south = jnp.maximum(-wy, 0.0)
        remain = 1.0 - (east + west + north + south)
        if last:
            _last_step(species, levels, tr, tc, state_ref, east, west, north, south, remain,
                       se_ref, d0, inv_ref, ratio_ref, red_ref, adj_ref, ss_ref, prior_ref)
            continue

        def forward(l, reduced):
            below = jnp.where(l > 0, se_ref[d0 + jnp.maximum(l - 1, 0)], zero)
            inverse = inv_ref[l]
            out = []
            for s in range(species):
                f = state_ref[s, l]
                from_east = pltpu.roll(east * f, rows - 1, 0)
                from_west = pltpu.roll(west * f, 1, 0)
                from_north = pltpu.roll(north * f, lanes - 1, 1)
                from_south = pltpu.roll(south * f, 1, 1)
                moved = f * remain
                moved = moved + from_east + from_west
                moved = moved + from_north + from_south
                r = (moved + below * reduced[s]) * inverse
                red_ref[s, l] = r
                out.append(r)
            return tuple(out)

        lax.fori_loop(0, levels, forward, (zero,) * species, unroll=4)

        def backward(i, result, k=k):
            l = levels - 1 - i
            ratio = ratio_ref[l]
            out = []
            for s in range(species):
                c = s * levels + l
                r = red_ref[s, l] - ratio * result[s]
                state_ref[s, l, :, :tc] = jnp.where(
                    inside[:, :tc], r[:, :tc] + tall_buf[k - 1, c], 0.0)
                state_ref[s, l, :, tc:] = jnp.where(
                    inside[:, tc:], r[:, tc:] + yh_buf[(k - 1) * planes + c], 0.0)
                out.append(r)
            return tuple(out)

        surface = lax.fori_loop(0, levels, backward, (zero,) * species, unroll=4)
        for s in range(species):
            if first:
                ss_ref[s] = prior_ref[s] * surface[s][:tr, :tc]
            else:
                ss_ref[s] = ss_ref[s] + prior_ref[s] * surface[s][:tr, :tc]


def _last_step(species, levels, tr, tc, forced_ref, east, west, north, south, remain, se_ref,
               d0, inv_ref, ratio_ref, red_ref, out_ref, ss_ref, prior_ref):
    row = lax.broadcasted_iota(jnp.int32, (tr, tc), 0)
    lane = lax.broadcasted_iota(jnp.int32, (tr, tc), 1)
    last_row = row == tr - 1
    first_row = row == 0
    last_lane = lane == tc - 1
    first_lane = lane == 0
    e_a, e_b = east[:tr, :tc], east[tr:, :tc]
    w_a, w_b = west[:tr, :tc], west[tr:, :tc]
    n_a, n_c = north[:tr, :tc], north[:tr, tc:]
    s_a, s_c = south[:tr, :tc], south[:tr, tc:]
    rem = remain[:tr, :tc]
    zero = jnp.zeros((tr, tc), jnp.float32)
    def forward(l, reduced):
        below = jnp.where(l > 0, se_ref[d0 + jnp.maximum(l - 1, 0), :tr, :tc], zero)
        inverse = inv_ref[l, :tr, :tc]
        out = []
        for s in range(species):
            f_a = forced_ref[s, l, :tr, :tc]
            f_b = forced_ref[s, l, tr:, :tc]
            f_c = forced_ref[s, l, :tr, tc:]
            from_east = jnp.where(last_row, pltpu.roll(e_b * f_b, tr - 1, 0),
                                  pltpu.roll(e_a * f_a, tr - 1, 0))
            from_west = jnp.where(first_row, pltpu.roll(w_b * f_b, 1, 0),
                                  pltpu.roll(w_a * f_a, 1, 0))
            from_north = jnp.where(last_lane, pltpu.roll(n_c * f_c, tc - 1, 1),
                                   pltpu.roll(n_a * f_a, tc - 1, 1))
            from_south = jnp.where(first_lane, pltpu.roll(s_c * f_c, 1, 1),
                                   pltpu.roll(s_a * f_a, 1, 1))
            moved = f_a * rem
            moved = moved + from_east + from_west
            moved = moved + from_north + from_south
            r = (moved + below * reduced[s]) * inverse
            red_ref[s, l, :tr, :tc] = r
            out.append(r)
        return tuple(out)

    lax.fori_loop(0, levels, forward, (zero,) * species, unroll=4)

    def backward(i, result):
        l = levels - 1 - i
        ratio = ratio_ref[l, :tr, :tc]
        out = []
        for s in range(species):
            r = red_ref[s, l, :tr, :tc] - ratio * result[s]
            out_ref[s, l] = r
            out.append(r)
        return tuple(out)

    surface = lax.fori_loop(0, levels, backward, (zero,) * species, unroll=4)
    for s in range(species):
        ss_ref[s] = ss_ref[s] + prior_ref[s] * surface[s]


def steps_call(steps, species, levels, n_statics, right, left, wind_x, wind_y, diffusivity,
               st_xh, mask, prior, tall):
    _, planes, rows, tc = tall.shape
    tr = rows // 2
    lanes = mask.shape[1]
    vmem = pl.BlockSpec(memory_space=pltpu.VMEM)
    anyspace = pl.BlockSpec(memory_space=pl.ANY)
    ins = (right, left, wind_x, wind_y, diffusivity, st_xh, mask, prior)
    return pl.pallas_call(
        functools.partial(_steps_kernel, steps, species, levels, n_statics),
        in_specs=[anyspace] * (len(ins) + 1),
        out_specs=[vmem, vmem],
        out_shape=[jax.ShapeDtypeStruct((species, levels, tr, tc), jnp.float32),
                   jax.ShapeDtypeStruct(prior.shape, jnp.float32)],
        scratch_shapes=[
            pltpu.VMEM((steps, planes, rows, tc), jnp.float32),
            pltpu.VMEM((steps * planes, rows, tc), jnp.float32),
            pltpu.VMEM((n_statics, rows, lanes), jnp.float32),
            pltpu.VMEM((species, levels, rows, lanes), jnp.float32),
            pltpu.VMEM((species, levels, rows, lanes), jnp.float32),
            pltpu.VMEM((levels, rows, lanes), jnp.float32),
            pltpu.VMEM((levels, rows, lanes), jnp.float32),
            pltpu.SemaphoreType.DMA((steps,)),
        ] + [pltpu.VMEM(a.shape, a.dtype) for a in ins] + [
            pltpu.SemaphoreType.DMA((len(ins),)),
        ],
        compiler_params=pltpu.CompilerParams(vmem_limit_bytes=48 * 1024 * 1024),
    )(*ins, tall)


def _pairs(axis):
    n = lax.axis_size(axis)
    return [(i, i + 1) for i in range(n - 1)], [(i + 1, i) for i in range(n - 1)]


def local(pixel_adjoint, pixel_owner, pixel_column, pixel_level, wind_x, wind_y,
          diffusivity, prior_emission, region_map):
    gx_n = lax.axis_size("gx")
    gy_n = lax.axis_size("gy")
    devices = gx_n * gy_n
    steps, rows, cols = wind_x.shape
    levels = diffusivity.shape[0] + 1
    species = prior_emission.shape[0]
    kernel = pixel_adjoint.shape[1] // species
    pixels = pixel_adjoint.shape[2]
    capacity = 2 * pixels // devices
    cells = rows * cols
    slots = devices * capacity
    halo = rows // 2
    assert steps <= halo
    lanes = 2 * cols
    ext_rows = 2 * rows

    n_s = 2 * steps + levels - 1
    group = cols // halo
    n_pad = -(-n_s // group) * group
    placed, st_lo, st_hi = pack_call(capacity, devices, n_pad, pixel_adjoint, pixel_owner,
                                     pixel_column, pixel_level, wind_x, wind_y, diffusivity)
    up_x, down_x = _pairs("gx")
    up_y, down_y = _pairs("gy")
    st_below = lax.ppermute(st_lo, "gx", down_x)
    st_above = lax.ppermute(st_hi, "gx", up_x)
    received = lax.all_to_all(placed, ("gx", "gy"), 0, 0, tiled=True)

    below = lax.ppermute(received, "gx", down_x)
    above = lax.ppermute(received, "gx", up_x)
    tall, right, left, st_xh = forcing_call(species, kernel, levels, n_s, received, below, above,
                                            wind_x, wind_y, diffusivity, st_below, st_above)
    right = lax.ppermute(right, "gy", down_y)
    left = lax.ppermute(left, "gy", up_y)

    gxi = lax.axis_index("gx")
    gyi = lax.axis_index("gy")
    r = jnp.arange(ext_rows, dtype=jnp.int32)[:, None]
    c = jnp.arange(lanes, dtype=jnp.int32)[None, :]
    grow = gxi * rows + jnp.where(r < rows + halo, r, r - ext_rows)
    ccol = jnp.where(c < cols + halo, c, c - lanes)
    gcol = gyi * cols + ccol
    inside = ((grow >= 0) & (grow < gx_n * rows) & (gcol >= 0) & (gcol < gy_n * cols)
              & ((c < cols + halo) | (c >= lanes - halo)))
    mask = inside.astype(jnp.float32)

    adjoint, surface_sum = steps_call(steps, species, levels, n_s, right, left, wind_x, wind_y,
                                      diffusivity, st_xh, mask, prior_emission, tall)

    nreg = REG_DEV * devices
    member = (region_map.reshape(-1)[:, None] == jnp.arange(nreg, dtype=jnp.int32)).astype(jnp.float32)
    partial = jnp.dot(surface_sum.reshape(species, cells), member, precision=HI)
    pieces = lax.all_to_all(partial.reshape(species, devices, nreg // devices), ("gx", "gy"), 1, 1,
                            tiled=True)
    gradient = jnp.sum(pieces, axis=1)
    return adjoint, gradient


def solution(mesh):
    in_specs = (
        P(None, None, ("gx", "gy")),
        P(None, ("gx", "gy"), None),
        P(None, ("gx", "gy")),
        P(None, ("gx", "gy")),
        P(None, "gx", "gy"),
        P(None, "gx", "gy"),
        P(None, "gx", "gy"),
        P(None, "gx", "gy"),
        P("gx", "gy"),
    )
    out_specs = (P(None, None, "gx", "gy"), P(None, ("gx", "gy")))
    return jax.shard_map(local, mesh=mesh, in_specs=in_specs, out_specs=out_specs, check_vma=False)
```

```python
import functools

import jax
import jax.numpy as jnp
from jax import lax
from jax.experimental import pallas as pl
from jax.experimental.pallas import tpu as pltpu
from jax.sharding import PartitionSpec as P

HI = lax.Precision.HIGHEST
REG_DEV = 8


def _full(shape):
    nd = len(shape)
    return pl.BlockSpec(shape, lambda i, _n=nd: (0,) * _n)


def _unpack(r, l, q, cols, half):
    lane = lax.broadcasted_iota(jnp.int32, r.shape, 1)
    rs = (cols - half * q) % cols
    ls = (cols - half - half * q) % cols
    return jnp.where(lane < half, pltpu.roll(r, rs, 1) if rs else r,
                     jnp.where(lane >= cols - half, pltpu.roll(l, ls, 1) if ls else l, 0.0))


def _static_plane(c, refs):
    for ref in refs:
        if c < ref.shape[0]:
            return ref[c]
        c -= ref.shape[0]
    return jnp.zeros(refs[0].shape[1:], jnp.float32)


def _pack_kernel(capacity, adj_ref, owner_ref, col_ref, lev_ref, wx_ref, wy_ref, diff_ref,
                 out_ref, lo_ref, hi_ref, rows_ref, tbuf_ref):
    steps, n_pay, pixels = adj_ref.shape
    devices, width = out_ref.shape
    block = width // (steps * capacity)
    row = lax.broadcasted_iota(jnp.int32, (pixels, pixels), 0)
    lane = lax.broadcasted_iota(jnp.int32, (pixels, pixels), 1)
    dest = lax.broadcasted_iota(jnp.int32, (pixels, devices), 1).astype(jnp.float32)
    tbuf_ref[...] = jnp.zeros(tbuf_ref.shape, jnp.float32)
    for k in range(steps):
        across = jnp.broadcast_to(owner_ref[k:k + 1].astype(jnp.float32), (pixels, pixels))
        down = jnp.transpose(across)
        same = (down == across) & (lane < row)
        rank = jnp.sum(jnp.where(same, 1.0, 0.0), axis=1, keepdims=True)
        owner = down[:, :devices]
        rows_ref[:n_pay] = adj_ref[k]
        rows_ref[n_pay:n_pay + 1] = col_ref[k:k + 1].astype(jnp.float32)
        rows_ref[n_pay + 1:n_pay + 2] = lev_ref[k:k + 1].astype(jnp.float32)
        for j in range(capacity):
            pick = jnp.where((owner == dest) & (rank[:, :1] == j), 1.0, 0.0)
            at = (k * capacity + j) * block
            tbuf_ref[at:at + n_pay + 2] = lax.dot_general(
                rows_ref[...], pick, (((1,), (0,)), ((), ())),
                precision=lax.Precision.HIGHEST, preferred_element_type=jnp.float32)
    out_ref[...] = jnp.transpose(tbuf_ref[...])
    statics = (wx_ref, wy_ref, diff_ref)
    tr = wx_ref.shape[1]
    half = tr // 2
    trow = lax.broadcasted_iota(jnp.int32, wx_ref.shape[1:], 0)
    for i in range(lo_ref.shape[0]):
        a = _static_plane(2 * i, statics)
        b = _static_plane(2 * i + 1, statics)
        lo_ref[i] = jnp.where(trow < half, a, pltpu.roll(b, half, 0))
        hi_ref[i] = jnp.where(trow < half, pltpu.roll(a, half, 0), b)


def pack_call(capacity, devices, n_pad, pixel_adjoint, pixel_owner, pixel_column, pixel_level,
              wind_x, wind_y, diffusivity):
    steps, n_pay, pixels = pixel_adjoint.shape
    rows, cols = wind_x.shape[1:]
    block = -(-(n_pay + 2) // 16) * 16
    width = steps * capacity * block
    pairs = jax.ShapeDtypeStruct((n_pad // 2, rows, cols), jnp.float32)
    vmem = pl.BlockSpec(memory_space=pltpu.VMEM)
    return pl.pallas_call(
        functools.partial(_pack_kernel, capacity),
        in_specs=[vmem] * 7,
        out_specs=[vmem] * 3,
        out_shape=[jax.ShapeDtypeStruct((devices, width), jnp.float32), pairs, pairs],
        scratch_shapes=[pltpu.VMEM((n_pay + 2, pixels), jnp.float32),
                        pltpu.VMEM((width, devices), jnp.float32)],
    )(pixel_adjoint, pixel_owner.reshape(steps, pixels), pixel_column, pixel_level, wind_x,
      wind_y, diffusivity)


def _exact_dot(a, b):
    dims = (((1,), (1,)), ((), ()))
    hi = a.astype(jnp.bfloat16)
    rest = a - hi.astype(jnp.float32)
    mid = rest.astype(jnp.bfloat16)
    lo = (rest - mid.astype(jnp.float32)).astype(jnp.bfloat16)
    out = lax.dot_general(hi, b, dims, preferred_element_type=jnp.float32)
    out = out + lax.dot_general(mid, b, dims, preferred_element_type=jnp.float32)
    return out + lax.dot_general(lo, b, dims, preferred_element_type=jnp.float32)


def _forcing_kernel(species, kernel, levels, n_statics, own_ref, below_ref, above_ref, wx_ref,
                    wy_ref, diff_ref, sb_ref, sa_ref, prior_ref,
                    tall_hbm, right_ref, left_ref, comb_hbm, lown_ref, lnb_ref, tall_ref, comb_ref,
                    sems, *trans):
    steps = tall_ref.shape[0]
    devices, width = own_ref.shape
    capacity = 2
    block = width // (steps * capacity)
    slots = devices * capacity
    tr2, tc = tall_ref.shape[2:]
    tr = tr2 // 2
    half = tr // 2
    group = tc // half
    n_pay = species * kernel
    lane_t = lax.broadcasted_iota(jnp.int32, (tc, slots), 0)
    row_i = lax.broadcasted_iota(jnp.int32, (tr, slots), 0)
    lev_i = lax.broadcasted_iota(jnp.int32, (levels, slots), 0)
    lane16 = lax.broadcasted_iota(jnp.int32, (tr2, tc), 1)
    right_ref[...] = jnp.zeros(right_ref.shape, jnp.float32)
    left_ref[...] = jnp.zeros(left_ref.shape, jnp.float32)
    out_copies = []
    for tref, ref in zip(trans, (own_ref, below_ref, above_ref)):
        tref[...] = jnp.transpose(ref[...])
    for k in range(steps):
        hts = []
        for src, tref in enumerate(trans):
            at = k * capacity * block
            blk = jnp.concatenate(
                [tref[at + j * block:at + j * block + n_pay + 2] for j in range(capacity)], axis=1)
            col = blk[n_pay:n_pay + 1].astype(jnp.int32)
            lev = blk[n_pay + 1:n_pay + 2].astype(jnp.int32)
            row_q = col // tc
            lane_q = col % tc
            if src == 1:
                row_q = jnp.where(row_q < half, row_q, -1)
            elif src == 2:
                row_q = jnp.where(row_q >= half, row_q, -1)
            rmask = row_i == row_q
            hts.append((lane_t == lane_q).astype(jnp.bfloat16))
            offset = lev_i - lev
            dst = lown_ref if src == 0 else lnb_ref
            c0 = 0 if src < 2 else slots
            for s in range(species):
                prof = jnp.zeros((levels, slots), jnp.float32)
                for j in range(kernel):
                    prof = prof + jnp.where(offset == j, blk[s * kernel + j:s * kernel + j + 1], 0.0)
                for l in range(levels):
                    c = s * levels + l
                    dst[c * tr:(c + 1) * tr, c0:c0 + slots] = jnp.where(
                        rmask, jnp.broadcast_to(prof[l:l + 1], (tr, slots)), 0.0)
        own = _exact_dot(lown_ref[...], hts[0])
        xh = _exact_dot(lnb_ref[...], jnp.concatenate([hts[1], hts[2]], axis=1))
        planes = own.shape[0] // tr
        tall_ref[k, :, :tr, :] = own.reshape(planes, tr, tc)
        tall_ref[k, :, tr:, :] = xh.reshape(planes, tr, tc)
        out_copy = pltpu.make_async_copy(tall_ref.at[k], tall_hbm.at[k], sems.at[k])
        out_copy.start()
        out_copies.append(out_copy)
        for c in range(planes):
            g, q = divmod(k * planes + c, group)
            plane = tall_ref[k, c]
            sel = (lane16 >= half * q) & (lane16 < half * q + half)
            rs = (half * q) % tc
            ls = (half * q + half) % tc
            right_ref[g] = jnp.where(sel, pltpu.roll(plane, rs, 1) if rs else plane, right_ref[g])
            left_ref[g] = jnp.where(sel, pltpu.roll(plane, ls, 1) if ls else plane, left_ref[g])
    statics = (wx_ref, wy_ref, diff_ref)
    trow = lax.broadcasted_iota(jnp.int32, (tr, tc), 0)
    base = steps * species * levels
    for i in range(sb_ref.shape[0]):
        b = sb_ref[i]
        a = sa_ref[i]
        xhs = (jnp.where(trow < half, b, pltpu.roll(a, half, 0)),
               jnp.where(trow < half, pltpu.roll(b, half, 0), a))
        for off in range(2):
            c = 2 * i + off
            if c >= n_statics:
                continue
            comb_ref[c, :tr] = _static_plane(c, statics)
            comb_ref[c, tr:] = xhs[off]
            g, q = divmod(base + c, group)
            sel = (lane16 >= half * q) & (lane16 < half * q + half)
            rs = (half * q) % tc
            ls = (half * q + half) % tc
            for part, plane in ((slice(0, tr), _static_plane(c, statics)),
                                (slice(tr, tr2), xhs[off])):
                selp = sel[part]
                right_ref[g, part] = jnp.where(
                    selp, pltpu.roll(plane, rs, 1) if rs else plane, right_ref[g, part])
                left_ref[g, part] = jnp.where(
                    selp, pltpu.roll(plane, ls, 1) if ls else plane, left_ref[g, part])
    for s in range(prior_ref.shape[0]):
        comb_ref[n_statics + s, :tr] = prior_ref[s]
        comb_ref[n_statics + s, tr:] = jnp.zeros((tr, tc), jnp.float32)
    comb_copy = pltpu.make_async_copy(comb_ref, comb_hbm, sems.at[steps])
    comb_copy.start()
    comb_copy.wait()
    for out_copy in out_copies:
        out_copy.wait()


def forcing_call(species, kernel, levels, n_statics, own, below, above, wind_x, wind_y,
                 diffusivity, st_below, st_above, prior):
    steps = wind_x.shape[0]
    devices, width = own.shape
    slots = 2 * devices
    tr, cols = wind_x.shape[1:]
    planes = species * levels
    group = cols // (tr // 2)
    n_groups = -(-(steps * planes + n_statics) // group)
    packed = jax.ShapeDtypeStruct((n_groups, 2 * tr, cols), jnp.float32)
    tall = jax.ShapeDtypeStruct((steps, planes, 2 * tr, cols), jnp.float32)
    comb = jax.ShapeDtypeStruct((n_statics + prior.shape[0], 2 * tr, cols), jnp.float32)
    vmem = pl.BlockSpec(memory_space=pltpu.VMEM)
    anyspace = pl.BlockSpec(memory_space=pl.ANY)
    return pl.pallas_call(
        functools.partial(_forcing_kernel, species, kernel, levels, n_statics),
        in_specs=[vmem] * 9,
        out_specs=[anyspace, vmem, vmem, anyspace],
        out_shape=[tall, packed, packed, comb],
        scratch_shapes=[pltpu.VMEM((planes * tr, slots), jnp.float32),
                        pltpu.VMEM((planes * tr, 2 * slots), jnp.float32),
                        pltpu.VMEM(tall.shape, jnp.float32),
                        pltpu.VMEM(comb.shape, jnp.float32),
                        pltpu.SemaphoreType.DMA((steps + 1,))]
        + [pltpu.VMEM((width, devices), jnp.float32)] * 3,
    )(own, below, above, wind_x, wind_y, diffusivity, st_below, st_above, prior)


def _steps_kernel(steps, species, levels, n_statics, grid_rows, grid_cols, *refs):
    n_in = 3
    hbm = refs[:n_in]
    tall_hbm, adj_ref, ss_ref = refs[n_in:n_in + 3]
    (tall_buf, yh_buf, se_ref, state_ref, red_ref, ratio_ref, inv_ref,
     sems) = refs[n_in + 3:n_in + 11]
    vbufs = refs[n_in + 11:n_in + 11 + n_in]
    in_sems = refs[n_in + 11 + n_in]
    fetch = []
    for i in range(n_in):
        copy = pltpu.make_async_copy(hbm[i], vbufs[i], in_sems.at[i])
        copy.start()
        fetch.append(copy)
    right_ref, left_ref, comb_ref = vbufs
    planes = species * levels
    tr, tc = adj_ref.shape[2:]
    rows, lanes = 2 * tr, 2 * tc
    half = tr // 2
    group = tc // half
    d0 = 2 * steps

    loads = {}
    for k in reversed(range(steps)):
        copy = pltpu.make_async_copy(tall_hbm.at[k], tall_buf.at[k], sems.at[k])
        copy.start()
        loads[k] = copy

    n_fgroups = steps * planes // group

    def unpack_group(g, carry):
        r = right_ref[g]
        l = left_ref[g]
        for q in range(group):
            yh_buf[g * group + q] = _unpack(r, l, q, tc, half)
        return carry

    fetch[0].wait()
    fetch[1].wait()
    lax.fori_loop(0, n_fgroups, unpack_group, 0)
    for c in range(n_statics):
        g, q = divmod(n_fgroups * group + c, group)
        se_ref[c, :, tc:] = _unpack(right_ref[g], left_ref[g], q, tc, half)

    fetch[2].wait()

    def assemble_static(c, carry):
        se_ref[c, :, :tc] = comb_ref[c]
        return carry

    lax.fori_loop(0, n_statics, assemble_static, 0)
    prior_ref = comb_ref.at[pl.ds(n_statics, species), pl.ds(0, tr)]

    zero = jnp.zeros((rows, lanes), jnp.float32)
    half_rows = tr // 2
    r = lax.broadcasted_iota(jnp.int32, (rows, lanes), 0)
    c = lax.broadcasted_iota(jnp.int32, (rows, lanes), 1)
    grow = lax.axis_index("gx") * tr + jnp.where(r < tr + half_rows, r, r - rows)
    gcol = lax.axis_index("gy") * tc + jnp.where(c < tc + half_rows, c, c - lanes)
    inside = ((grow >= 0) & (grow < grid_rows) & (gcol >= 0) & (gcol < grid_cols)
              & ((c < tc + half_rows) | (c >= lanes - half_rows)))
    carried = zero
    for l in range(levels):
        below = se_ref[d0 + l - 1] if l > 0 else zero
        above = se_ref[d0 + l] if l < levels - 1 else zero
        inverse = 1.0 / (1.0 + below + above + below * carried)
        ratio = -above * inverse
        ratio_ref[l] = ratio
        inv_ref[l] = inverse
        carried = ratio

    for k in reversed(range(steps)):
        first = k == steps - 1
        last = k == 0
        if first:
            loads[k].wait()
            for s in range(species):

                def assemble(l, carry, s=s, k=k):
                    c = s * levels + l
                    state_ref[s, l, :, :tc] = tall_buf[k, c]
                    state_ref[s, l, :, tc:] = yh_buf[k * planes + c]
                    state_ref[s, l] = jnp.where(inside, state_ref[s, l], 0.0)
                    return carry

                lax.fori_loop(0, levels, assemble, 0, unroll=4)
        if not last:
            loads[k - 1].wait()

        wx = se_ref[k]
        wy = se_ref[steps + k]
        east = jnp.maximum(wx, 0.0)
        west = jnp.maximum(-wx, 0.0)
        north = jnp.maximum(wy, 0.0)
        south = jnp.maximum(-wy, 0.0)
        remain = 1.0 - (east + west + north + south)
        if last:
            _last_step(species, levels, tr, tc, state_ref, east, west, north, south, remain,
                       se_ref, d0, inv_ref, ratio_ref, red_ref, adj_ref, ss_ref, prior_ref)
            continue

        def forward(l, reduced):
            below = jnp.where(l > 0, se_ref[d0 + jnp.maximum(l - 1, 0)], zero)
            inverse = inv_ref[l]
            out = []
            for s in range(species):
                f = state_ref[s, l]
                from_east = pltpu.roll(east * f, rows - 1, 0)
                from_west = pltpu.roll(west * f, 1, 0)
                from_north = pltpu.roll(north * f, lanes - 1, 1)
                from_south = pltpu.roll(south * f, 1, 1)
                moved = f * remain
                moved = moved + from_east + from_west
                moved = moved + from_north + from_south
                r = (moved + below * reduced[s]) * inverse
                red_ref[s, l] = r
                out.append(r)
            return tuple(out)

        lax.fori_loop(0, levels, forward, (zero,) * species, unroll=4)

        def backward(i, result, k=k):
            l = levels - 1 - i
            ratio = ratio_ref[l]
            out = []
            for s in range(species):
                c = s * levels + l
                r = red_ref[s, l] - ratio * result[s]
                state_ref[s, l, :, :tc] = jnp.where(
                    inside[:, :tc], r[:, :tc] + tall_buf[k - 1, c], 0.0)
                state_ref[s, l, :, tc:] = jnp.where(
                    inside[:, tc:], r[:, tc:] + yh_buf[(k - 1) * planes + c], 0.0)
                out.append(r)
            return tuple(out)

        surface = lax.fori_loop(0, levels, backward, (zero,) * species, unroll=4)
        for s in range(species):
            if first:
                ss_ref[s] = prior_ref[s] * surface[s][:tr, :tc]
            else:
                ss_ref[s] = ss_ref[s] + prior_ref[s] * surface[s][:tr, :tc]


def _last_step(species, levels, tr, tc, forced_ref, east, west, north, south, remain, se_ref,
               d0, inv_ref, ratio_ref, red_ref, out_ref, ss_ref, prior_ref):
    row = lax.broadcasted_iota(jnp.int32, (tr, tc), 0)
    lane = lax.broadcasted_iota(jnp.int32, (tr, tc), 1)
    last_row = row == tr - 1
    first_row = row == 0
    last_lane = lane == tc - 1
    first_lane = lane == 0
    e_a, e_b = east[:tr, :tc], east[tr:, :tc]
    w_a, w_b = west[:tr, :tc], west[tr:, :tc]
    n_a, n_c = north[:tr, :tc], north[:tr, tc:]
    s_a, s_c = south[:tr, :tc], south[:tr, tc:]
    rem = remain[:tr, :tc]
    zero = jnp.zeros((tr, tc), jnp.float32)
    def forward(l, reduced):
        below = jnp.where(l > 0, se_ref[d0 + jnp.maximum(l - 1, 0), :tr, :tc], zero)
        inverse = inv_ref[l, :tr, :tc]
        out = []
        for s in range(species):
            f_a = forced_ref[s, l, :tr, :tc]
            f_b = forced_ref[s, l, tr:, :tc]
            f_c = forced_ref[s, l, :tr, tc:]
            from_east = jnp.where(last_row, pltpu.roll(e_b * f_b, tr - 1, 0),
                                  pltpu.roll(e_a * f_a, tr - 1, 0))
            from_west = jnp.where(first_row, pltpu.roll(w_b * f_b, 1, 0),
                                  pltpu.roll(w_a * f_a, 1, 0))
            from_north = jnp.where(last_lane, pltpu.roll(n_c * f_c, tc - 1, 1),
                                   pltpu.roll(n_a * f_a, tc - 1, 1))
            from_south = jnp.where(first_lane, pltpu.roll(s_c * f_c, 1, 1),
                                   pltpu.roll(s_a * f_a, 1, 1))
            moved = f_a * rem
            moved = moved + from_east + from_west
            moved = moved + from_north + from_south
            r = (moved + below * reduced[s]) * inverse
            red_ref[s, l, :tr, :tc] = r
            out.append(r)
        return tuple(out)

    lax.fori_loop(0, levels, forward, (zero,) * species, unroll=4)

    def backward(i, result):
        l = levels - 1 - i
        ratio = ratio_ref[l, :tr, :tc]
        out = []
        for s in range(species):
            r = red_ref[s, l, :tr, :tc] - ratio * result[s]
            out_ref[s, l] = r
            out.append(r)
        return tuple(out)

    surface = lax.fori_loop(0, levels, backward, (zero,) * species, unroll=4)
    for s in range(species):
        ss_ref[s] = ss_ref[s] + prior_ref[s] * surface[s]


def steps_call(steps, species, levels, n_statics, grid_rows, grid_cols, right, left, comb,
               tall):
    _, planes, rows, tc = tall.shape
    tr = rows // 2
    lanes = 2 * tc
    vmem = pl.BlockSpec(memory_space=pltpu.VMEM)
    anyspace = pl.BlockSpec(memory_space=pl.ANY)
    ins = (right, left, comb)
    return pl.pallas_call(
        functools.partial(_steps_kernel, steps, species, levels, n_statics, grid_rows, grid_cols),
        in_specs=[anyspace] * (len(ins) + 1),
        out_specs=[vmem, vmem],
        out_shape=[jax.ShapeDtypeStruct((species, levels, tr, tc), jnp.float32),
                   jax.ShapeDtypeStruct((species, tr, tc), jnp.float32)],
        scratch_shapes=[
            pltpu.VMEM((steps, planes, rows, tc), jnp.float32),
            pltpu.VMEM((steps * planes, rows, tc), jnp.float32),
            pltpu.VMEM((n_statics, rows, lanes), jnp.float32),
            pltpu.VMEM((species, levels, rows, lanes), jnp.float32),
            pltpu.VMEM((species, levels, rows, lanes), jnp.float32),
            pltpu.VMEM((levels, rows, lanes), jnp.float32),
            pltpu.VMEM((levels, rows, lanes), jnp.float32),
            pltpu.SemaphoreType.DMA((steps,)),
        ] + [pltpu.VMEM(a.shape, a.dtype) for a in ins] + [
            pltpu.SemaphoreType.DMA((len(ins),)),
        ],
        compiler_params=pltpu.CompilerParams(vmem_limit_bytes=48 * 1024 * 1024),
    )(*ins, tall)


def _pairs(axis):
    n = lax.axis_size(axis)
    return [(i, i + 1) for i in range(n - 1)], [(i + 1, i) for i in range(n - 1)]


def local(pixel_adjoint, pixel_owner, pixel_column, pixel_level, wind_x, wind_y,
          diffusivity, prior_emission, region_map):
    gx_n = lax.axis_size("gx")
    gy_n = lax.axis_size("gy")
    devices = gx_n * gy_n
    steps, rows, cols = wind_x.shape
    levels = diffusivity.shape[0] + 1
    species = prior_emission.shape[0]
    kernel = pixel_adjoint.shape[1] // species
    pixels = pixel_adjoint.shape[2]
    capacity = 2 * pixels // devices
    cells = rows * cols
    slots = devices * capacity
    halo = rows // 2
    assert steps <= halo
    lanes = 2 * cols
    ext_rows = 2 * rows

    n_s = 2 * steps + levels - 1
    group = cols // halo
    n_pad = -(-n_s // group) * group
    placed, st_lo, st_hi = pack_call(capacity, devices, n_pad, pixel_adjoint, pixel_owner,
                                     pixel_column, pixel_level, wind_x, wind_y, diffusivity)
    up_x, down_x = _pairs("gx")
    up_y, down_y = _pairs("gy")
    st_below = lax.ppermute(st_lo, "gx", down_x)
    st_above = lax.ppermute(st_hi, "gx", up_x)
    received = lax.all_to_all(placed, ("gx", "gy"), 0, 0, tiled=True)

    below = lax.ppermute(received, "gx", down_x)
    above = lax.ppermute(received, "gx", up_x)
    tall, right, left, comb = forcing_call(species, kernel, levels, n_s, received, below, above,
                                           wind_x, wind_y, diffusivity, st_below, st_above,
                                           prior_emission)
    right = lax.ppermute(right, "gy", down_y)
    left = lax.ppermute(left, "gy", up_y)

    adjoint, surface_sum = steps_call(steps, species, levels, n_s, gx_n * rows, gy_n * cols,
                                      right, left, comb, tall)

    nreg = REG_DEV * devices
    member = (region_map.reshape(-1)[:, None] == jnp.arange(nreg, dtype=jnp.int32)).astype(jnp.float32)
    partial = jnp.dot(surface_sum.reshape(species, cells), member, precision=HI)
    pieces = lax.all_to_all(partial.reshape(species, devices, nreg // devices), ("gx", "gy"), 1, 1,
                            tiled=True)
    gradient = jnp.sum(pieces, axis=1)
    return adjoint, gradient


def solution(mesh):
    in_specs = (
        P(None, None, ("gx", "gy")),
        P(None, ("gx", "gy"), None),
        P(None, ("gx", "gy")),
        P(None, ("gx", "gy")),
        P(None, "gx", "gy"),
        P(None, "gx", "gy"),
        P(None, "gx", "gy"),
        P(None, "gx", "gy"),
        P("gx", "gy"),
    )
    out_specs = (P(None, None, "gx", "gy"), P(None, ("gx", "gy")))
    return jax.shard_map(local, mesh=mesh, in_specs=in_specs, out_specs=out_specs, check_vma=False)
```

```python
import functools

import jax
import jax.numpy as jnp
from jax import lax
from jax.experimental import pallas as pl
from jax.experimental.pallas import tpu as pltpu
from jax.sharding import PartitionSpec as P

HI = lax.Precision.HIGHEST
REG_DEV = 8


def _full(shape):
    nd = len(shape)
    return pl.BlockSpec(shape, lambda i, _n=nd: (0,) * _n)


def _unpack(r, l, q, cols, half):
    lane = lax.broadcasted_iota(jnp.int32, r.shape, 1)
    rs = (cols - half * q) % cols
    ls = (cols - half - half * q) % cols
    return jnp.where(lane < half, pltpu.roll(r, rs, 1) if rs else r,
                     jnp.where(lane >= cols - half, pltpu.roll(l, ls, 1) if ls else l, 0.0))


def _static_plane(c, refs):
    for ref in refs:
        if c < ref.shape[0]:
            return ref[c]
        c -= ref.shape[0]
    return jnp.zeros(refs[0].shape[1:], jnp.float32)


def _pack_kernel(capacity, adj_ref, owner_ref, col_ref, lev_ref, wx_ref, wy_ref, diff_ref,
                 out_ref, lo_ref, hi_ref, rows_ref, tbuf_ref):
    steps, n_pay, pixels = adj_ref.shape
    devices, width = out_ref.shape
    block = width // (steps * capacity)
    row = lax.broadcasted_iota(jnp.int32, (pixels, pixels), 0)
    lane = lax.broadcasted_iota(jnp.int32, (pixels, pixels), 1)
    dest = lax.broadcasted_iota(jnp.int32, (pixels, devices), 1).astype(jnp.float32)
    tbuf_ref[...] = jnp.zeros(tbuf_ref.shape, jnp.float32)
    for k in range(steps):
        across = jnp.broadcast_to(owner_ref[k:k + 1].astype(jnp.float32), (pixels, pixels))
        down = jnp.transpose(across)
        same = (down == across) & (lane < row)
        rank = jnp.sum(jnp.where(same, 1.0, 0.0), axis=1, keepdims=True)
        owner = down[:, :devices]
        rows_ref[:n_pay] = adj_ref[k]
        rows_ref[n_pay:n_pay + 1] = col_ref[k:k + 1].astype(jnp.float32)
        rows_ref[n_pay + 1:n_pay + 2] = lev_ref[k:k + 1].astype(jnp.float32)
        for j in range(capacity):
            pick = jnp.where((owner == dest) & (rank[:, :1] == j), 1.0, 0.0)
            at = (k * capacity + j) * block
            tbuf_ref[at:at + n_pay + 2] = lax.dot_general(
                rows_ref[...], pick, (((1,), (0,)), ((), ())),
                precision=lax.Precision.HIGHEST, preferred_element_type=jnp.float32)
    out_ref[...] = jnp.transpose(tbuf_ref[...])
    statics = (wx_ref, wy_ref, diff_ref)
    tr = wx_ref.shape[1]
    half = tr // 2
    trow = lax.broadcasted_iota(jnp.int32, wx_ref.shape[1:], 0)
    for i in range(lo_ref.shape[0]):
        a = _static_plane(2 * i, statics)
        b = _static_plane(2 * i + 1, statics)
        lo_ref[i] = jnp.where(trow < half, a, pltpu.roll(b, half, 0))
        hi_ref[i] = jnp.where(trow < half, pltpu.roll(a, half, 0), b)


def pack_call(capacity, devices, n_pad, pixel_adjoint, pixel_owner, pixel_column, pixel_level,
              wind_x, wind_y, diffusivity):
    steps, n_pay, pixels = pixel_adjoint.shape
    rows, cols = wind_x.shape[1:]
    block = -(-(n_pay + 2) // 16) * 16
    width = steps * capacity * block
    pairs = jax.ShapeDtypeStruct((n_pad // 2, rows, cols), jnp.float32)
    vmem = pl.BlockSpec(memory_space=pltpu.VMEM)
    return pl.pallas_call(
        functools.partial(_pack_kernel, capacity),
        in_specs=[vmem] * 7,
        out_specs=[vmem] * 3,
        out_shape=[jax.ShapeDtypeStruct((devices, width), jnp.float32), pairs, pairs],
        scratch_shapes=[pltpu.VMEM((n_pay + 2, pixels), jnp.float32),
                        pltpu.VMEM((width, devices), jnp.float32)],
    )(pixel_adjoint, pixel_owner.reshape(steps, pixels), pixel_column, pixel_level, wind_x,
      wind_y, diffusivity)


def _exact_dot(a, b):
    dims = (((1,), (1,)), ((), ()))
    hi = a.astype(jnp.bfloat16)
    rest = a - hi.astype(jnp.float32)
    mid = rest.astype(jnp.bfloat16)
    lo = (rest - mid.astype(jnp.float32)).astype(jnp.bfloat16)
    out = lax.dot_general(hi, b, dims, preferred_element_type=jnp.float32)
    out = out + lax.dot_general(mid, b, dims, preferred_element_type=jnp.float32)
    return out + lax.dot_general(lo, b, dims, preferred_element_type=jnp.float32)


def _forcing_kernel(species, kernel, levels, n_statics, own_ref, below_ref, above_ref, wx_ref,
                    wy_ref, diff_ref, sb_ref, sa_ref,
                    tall_ref, right_ref, left_ref, st_xh_ref, lown_ref, lnb_ref, *trans):
    steps = tall_ref.shape[0]
    devices, width = own_ref.shape
    capacity = 2
    block = width // (steps * capacity)
    slots = devices * capacity
    tr2, tc = tall_ref.shape[2:]
    tr = tr2 // 2
    half = tr // 2
    group = tc // half
    n_pay = species * kernel
    lane_t = lax.broadcasted_iota(jnp.int32, (tc, slots), 0)
    row_i = lax.broadcasted_iota(jnp.int32, (tr, slots), 0)
    lev_i = lax.broadcasted_iota(jnp.int32, (levels, slots), 0)
    lane16 = lax.broadcasted_iota(jnp.int32, (tr2, tc), 1)
    right_ref[...] = jnp.zeros(right_ref.shape, jnp.float32)
    left_ref[...] = jnp.zeros(left_ref.shape, jnp.float32)
    for tref, ref in zip(trans, (own_ref, below_ref, above_ref)):
        tref[...] = jnp.transpose(ref[...])
    for k in range(steps):
        hts = []
        for src, tref in enumerate(trans):
            at = k * capacity * block
            blk = jnp.concatenate(
                [tref[at + j * block:at + j * block + n_pay + 2] for j in range(capacity)], axis=1)
            col = blk[n_pay:n_pay + 1].astype(jnp.int32)
            lev = blk[n_pay + 1:n_pay + 2].astype(jnp.int32)
            row_q = col // tc
            lane_q = col % tc
            if src == 1:
                row_q = jnp.where(row_q < half, row_q, -1)
            elif src == 2:
                row_q = jnp.where(row_q >= half, row_q, -1)
            rmask = row_i == row_q
            hts.append((lane_t == lane_q).astype(jnp.bfloat16))
            offset = lev_i - lev
            dst = lown_ref if src == 0 else lnb_ref
            c0 = 0 if src < 2 else slots
            for s in range(species):
                prof = jnp.zeros((levels, slots), jnp.float32)
                for j in range(kernel):
                    prof = prof + jnp.where(offset == j, blk[s * kernel + j:s * kernel + j + 1], 0.0)
                for l in range(levels):
                    c = s * levels + l
                    dst[c * tr:(c + 1) * tr, c0:c0 + slots] = jnp.where(
                        rmask, jnp.broadcast_to(prof[l:l + 1], (tr, slots)), 0.0)
        own = _exact_dot(lown_ref[...], hts[0])
        xh = _exact_dot(lnb_ref[...], jnp.concatenate([hts[1], hts[2]], axis=1))
        planes = own.shape[0] // tr
        tall_ref[k, :, :tr, :] = own.reshape(planes, tr, tc)
        tall_ref[k, :, tr:, :] = xh.reshape(planes, tr, tc)
        for c in range(planes):
            g, q = divmod(k * planes + c, group)
            plane = tall_ref[k, c]
            sel = (lane16 >= half * q) & (lane16 < half * q + half)
            rs = (half * q) % tc
            ls = (half * q + half) % tc
            right_ref[g] = jnp.where(sel, pltpu.roll(plane, rs, 1) if rs else plane, right_ref[g])
            left_ref[g] = jnp.where(sel, pltpu.roll(plane, ls, 1) if ls else plane, left_ref[g])
    statics = (wx_ref, wy_ref, diff_ref)
    trow = lax.broadcasted_iota(jnp.int32, (tr, tc), 0)
    base = steps * species * levels
    for i in range(sb_ref.shape[0]):
        b = sb_ref[i]
        a = sa_ref[i]
        xhs = (jnp.where(trow < half, b, pltpu.roll(a, half, 0)),
               jnp.where(trow < half, pltpu.roll(b, half, 0), a))
        for off in range(2):
            c = 2 * i + off
            st_xh_ref[c] = xhs[off]
            if c >= n_statics:
                continue
            g, q = divmod(base + c, group)
            sel = (lane16 >= half * q) & (lane16 < half * q + half)
            rs = (half * q) % tc
            ls = (half * q + half) % tc
            for part, plane in ((slice(0, tr), _static_plane(c, statics)),
                                (slice(tr, tr2), xhs[off])):
                selp = sel[part]
                right_ref[g, part] = jnp.where(
                    selp, pltpu.roll(plane, rs, 1) if rs else plane, right_ref[g, part])
                left_ref[g, part] = jnp.where(
                    selp, pltpu.roll(plane, ls, 1) if ls else plane, left_ref[g, part])


def forcing_call(species, kernel, levels, n_statics, own, below, above, wind_x, wind_y,
                 diffusivity, st_below, st_above):
    steps = wind_x.shape[0]
    devices, width = own.shape
    slots = 2 * devices
    tr, cols = wind_x.shape[1:]
    planes = species * levels
    group = cols // (tr // 2)
    n_groups = -(-(steps * planes + n_statics) // group)
    packed = jax.ShapeDtypeStruct((n_groups, 2 * tr, cols), jnp.float32)
    vmem = pl.BlockSpec(memory_space=pltpu.VMEM)
    return pl.pallas_call(
        functools.partial(_forcing_kernel, species, kernel, levels, n_statics),
        in_specs=[vmem] * 8,
        out_specs=[vmem] * 4,
        out_shape=[jax.ShapeDtypeStruct((steps, planes, 2 * tr, cols), jnp.float32), packed,
                   packed, jax.ShapeDtypeStruct((2 * st_below.shape[0], tr, cols), jnp.float32)],
        scratch_shapes=[pltpu.VMEM((planes * tr, slots), jnp.float32),
                        pltpu.VMEM((planes * tr, 2 * slots), jnp.float32)]
        + [pltpu.VMEM((width, devices), jnp.float32)] * 3,
    )(own, below, above, wind_x, wind_y, diffusivity, st_below, st_above)


def _steps_kernel(steps, species, levels, n_statics,
                  right_ref, left_ref, wx_ref, wy_ref, diff_ref, st_xh, mask_ref, prior_ref,
                  tall_hbm, adj_ref, ss_ref,
                  tall_buf, yh_buf, se_ref, state_ref, red_ref, ratio_ref, inv_ref, sems):
    planes = species * levels
    rows, lanes = mask_ref.shape
    tr, tc = adj_ref.shape[2:]
    half = tr // 2
    group = tc // half
    d0 = 2 * steps

    loads = {}
    for k in reversed(range(steps)):
        copy = pltpu.make_async_copy(tall_hbm.at[k], tall_buf.at[k], sems.at[k])
        copy.start()
        loads[k] = copy

    n_fgroups = steps * planes // group

    def unpack_group(g, carry):
        r = right_ref[g]
        l = left_ref[g]
        for q in range(group):
            yh_buf[g * group + q] = _unpack(r, l, q, tc, half)
        return carry

    lax.fori_loop(0, n_fgroups, unpack_group, 0)
    for c in range(n_statics):
        g, q = divmod(n_fgroups * group + c, group)
        se_ref[c, :, tc:] = _unpack(right_ref[g], left_ref[g], q, tc, half)

    for c in range(n_statics):
        se_ref[c, :tr, :tc] = _static_plane(c, (wx_ref, wy_ref, diff_ref))
        se_ref[c, tr:, :tc] = st_xh[c]

    zero = jnp.zeros((rows, lanes), jnp.float32)
    inside = mask_ref[...] > 0.5
    carried = zero
    for l in range(levels):
        below = se_ref[d0 + l - 1] if l > 0 else zero
        above = se_ref[d0 + l] if l < levels - 1 else zero
        inverse = 1.0 / (1.0 + below + above + below * carried)
        ratio = -above * inverse
        ratio_ref[l] = ratio
        inv_ref[l] = inverse
        carried = ratio

    for k in reversed(range(steps)):
        first = k == steps - 1
        last = k == 0
        if first:
            loads[k].wait()
            for s in range(species):

                def assemble(l, carry, s=s, k=k):
                    c = s * levels + l
                    state_ref[s, l, :, :tc] = tall_buf[k, c]
                    state_ref[s, l, :, tc:] = yh_buf[k * planes + c]
                    state_ref[s, l] = jnp.where(inside, state_ref[s, l], 0.0)
                    return carry

                lax.fori_loop(0, levels, assemble, 0, unroll=4)
        if not last:
            loads[k - 1].wait()

        wx = se_ref[k]
        wy = se_ref[steps + k]
        east = jnp.maximum(wx, 0.0)
        west = jnp.maximum(-wx, 0.0)
        north = jnp.maximum(wy, 0.0)
        south = jnp.maximum(-wy, 0.0)
        remain = 1.0 - (east + west + north + south)
        if last:
            _last_step(species, levels, tr, tc, state_ref, east, west, north, south, remain,
                       se_ref, d0, inv_ref, ratio_ref, red_ref, adj_ref, ss_ref, prior_ref)
            continue

        def forward(l, reduced):
            below = jnp.where(l > 0, se_ref[d0 + jnp.maximum(l - 1, 0)], zero)
            inverse = inv_ref[l]
            out = []
            for s in range(species):
                f = state_ref[s, l]
                from_east = pltpu.roll(east * f, rows - 1, 0)
                from_west = pltpu.roll(west * f, 1, 0)
                from_north = pltpu.roll(north * f, lanes - 1, 1)
                from_south = pltpu.roll(south * f, 1, 1)
                moved = f * remain
                moved = moved + from_east + from_west
                moved = moved + from_north + from_south
                r = (moved + below * reduced[s]) * inverse
                red_ref[s, l] = r
                out.append(r)
            return tuple(out)

        lax.fori_loop(0, levels, forward, (zero,) * species, unroll=8)

        def backward(i, result, k=k):
            l = levels - 1 - i
            ratio = ratio_ref[l]
            out = []
            for s in range(species):
                c = s * levels + l
                r = red_ref[s, l] - ratio * result[s]
                state_ref[s, l, :, :tc] = jnp.where(
                    inside[:, :tc], r[:, :tc] + tall_buf[k - 1, c], 0.0)
                state_ref[s, l, :, tc:] = jnp.where(
                    inside[:, tc:], r[:, tc:] + yh_buf[(k - 1) * planes + c], 0.0)
                out.append(r)
            return tuple(out)

        surface = lax.fori_loop(0, levels, backward, (zero,) * species, unroll=8)
        for s in range(species):
            if first:
                ss_ref[s] = prior_ref[s] * surface[s][:tr, :tc]
            else:
                ss_ref[s] = ss_ref[s] + prior_ref[s] * surface[s][:tr, :tc]


def _last_step(species, levels, tr, tc, forced_ref, east, west, north, south, remain, se_ref,
               d0, inv_ref, ratio_ref, red_ref, out_ref, ss_ref, prior_ref):
    row = lax.broadcasted_iota(jnp.int32, (tr, tc), 0)
    lane = lax.broadcasted_iota(jnp.int32, (tr, tc), 1)
    last_row = row == tr - 1
    first_row = row == 0
    last_lane = lane == tc - 1
    first_lane = lane == 0
    e_a, e_b = east[:tr, :tc], east[tr:, :tc]
    w_a, w_b = west[:tr, :tc], west[tr:, :tc]
    n_a, n_c = north[:tr, :tc], north[:tr, tc:]
    s_a, s_c = south[:tr, :tc], south[:tr, tc:]
    rem = remain[:tr, :tc]
    zero = jnp.zeros((tr, tc), jnp.float32)
    def forward(l, reduced):
        below = jnp.where(l > 0, se_ref[d0 + jnp.maximum(l - 1, 0), :tr, :tc], zero)
        inverse = inv_ref[l, :tr, :tc]
        out = []
        for s in range(species):
            f_a = forced_ref[s, l, :tr, :tc]
            f_b = forced_ref[s, l, tr:, :tc]
            f_c = forced_ref[s, l, :tr, tc:]
            from_east = jnp.where(last_row, pltpu.roll(e_b * f_b, tr - 1, 0),
                                  pltpu.roll(e_a * f_a, tr - 1, 0))
            from_west = jnp.where(first_row, pltpu.roll(w_b * f_b, 1, 0),
                                  pltpu.roll(w_a * f_a, 1, 0))
            from_north = jnp.where(last_lane, pltpu.roll(n_c * f_c, tc - 1, 1),
                                   pltpu.roll(n_a * f_a, tc - 1, 1))
            from_south = jnp.where(first_lane, pltpu.roll(s_c * f_c, 1, 1),
                                   pltpu.roll(s_a * f_a, 1, 1))
            moved = f_a * rem
            moved = moved + from_east + from_west
            moved = moved + from_north + from_south
            r = (moved + below * reduced[s]) * inverse
            red_ref[s, l, :tr, :tc] = r
            out.append(r)
        return tuple(out)

    lax.fori_loop(0, levels, forward, (zero,) * species, unroll=4)

    def backward(i, result):
        l = levels - 1 - i
        ratio = ratio_ref[l, :tr, :tc]
        out = []
        for s in range(species):
            r = red_ref[s, l, :tr, :tc] - ratio * result[s]
            out_ref[s, l] = r
            out.append(r)
        return tuple(out)

    surface = lax.fori_loop(0, levels, backward, (zero,) * species, unroll=4)
    for s in range(species):
        ss_ref[s] = ss_ref[s] + prior_ref[s] * surface[s]


def steps_call(steps, species, levels, n_statics, right, left, wind_x, wind_y, diffusivity,
               st_xh, mask, prior, tall):
    _, planes, rows, tc = tall.shape
    tr = rows // 2
    lanes = mask.shape[1]
    vmem = pl.BlockSpec(memory_space=pltpu.VMEM)
    anyspace = pl.BlockSpec(memory_space=pl.ANY)
    return pl.pallas_call(
        functools.partial(_steps_kernel, steps, species, levels, n_statics),
        in_specs=[vmem] * 8 + [anyspace],
        out_specs=[vmem, vmem],
        out_shape=[jax.ShapeDtypeStruct((species, levels, tr, tc), jnp.float32),
                   jax.ShapeDtypeStruct(prior.shape, jnp.float32)],
        scratch_shapes=[
            pltpu.VMEM((steps, planes, rows, tc), jnp.float32),
            pltpu.VMEM((steps * planes, rows, tc), jnp.float32),
            pltpu.VMEM((n_statics, rows, lanes), jnp.float32),
            pltpu.VMEM((species, levels, rows, lanes), jnp.float32),
            pltpu.VMEM((species, levels, rows, lanes), jnp.float32),
            pltpu.VMEM((levels, rows, lanes), jnp.float32),
            pltpu.VMEM((levels, rows, lanes), jnp.float32),
            pltpu.SemaphoreType.DMA((steps,)),
        ],
        compiler_params=pltpu.CompilerParams(vmem_limit_bytes=48 * 1024 * 1024),
    )(right, left, wind_x, wind_y, diffusivity, st_xh, mask, prior, tall)


def _pairs(axis):
    n = lax.axis_size(axis)
    return [(i, i + 1) for i in range(n - 1)], [(i + 1, i) for i in range(n - 1)]


def local(pixel_adjoint, pixel_owner, pixel_column, pixel_level, wind_x, wind_y,
          diffusivity, prior_emission, region_map):
    gx_n = lax.axis_size("gx")
    gy_n = lax.axis_size("gy")
    devices = gx_n * gy_n
    steps, rows, cols = wind_x.shape
    levels = diffusivity.shape[0] + 1
    species = prior_emission.shape[0]
    kernel = pixel_adjoint.shape[1] // species
    pixels = pixel_adjoint.shape[2]
    capacity = 2 * pixels // devices
    cells = rows * cols
    slots = devices * capacity
    halo = rows // 2
    assert steps <= halo
    lanes = 2 * cols
    ext_rows = 2 * rows

    n_s = 2 * steps + levels - 1
    group = cols // halo
    n_pad = -(-n_s // group) * group
    placed, st_lo, st_hi = pack_call(capacity, devices, n_pad, pixel_adjoint, pixel_owner,
                                     pixel_column, pixel_level, wind_x, wind_y, diffusivity)
    up_x, down_x = _pairs("gx")
    up_y, down_y = _pairs("gy")
    st_below = lax.ppermute(st_lo, "gx", down_x)
    st_above = lax.ppermute(st_hi, "gx", up_x)
    received = lax.all_to_all(placed, ("gx", "gy"), 0, 0, tiled=True)

    below = lax.ppermute(received, "gx", down_x)
    above = lax.ppermute(received, "gx", up_x)
    tall, right, left, st_xh = forcing_call(species, kernel, levels, n_s, received, below, above,
                                            wind_x, wind_y, diffusivity, st_below, st_above)
    right = lax.ppermute(right, "gy", down_y)
    left = lax.ppermute(left, "gy", up_y)

    gxi = lax.axis_index("gx")
    gyi = lax.axis_index("gy")
    r = jnp.arange(ext_rows, dtype=jnp.int32)[:, None]
    c = jnp.arange(lanes, dtype=jnp.int32)[None, :]
    grow = gxi * rows + jnp.where(r < rows + halo, r, r - ext_rows)
    ccol = jnp.where(c < cols + halo, c, c - lanes)
    gcol = gyi * cols + ccol
    inside = ((grow >= 0) & (grow < gx_n * rows) & (gcol >= 0) & (gcol < gy_n * cols)
              & ((c < cols + halo) | (c >= lanes - halo)))
    mask = inside.astype(jnp.float32)

    adjoint, surface_sum = steps_call(steps, species, levels, n_s, right, left, wind_x, wind_y,
                                      diffusivity, st_xh, mask, prior_emission, tall)

    nreg = REG_DEV * devices
    member = (region_map.reshape(-1)[:, None] == jnp.arange(nreg, dtype=jnp.int32)).astype(jnp.float32)
    partial = jnp.dot(surface_sum.reshape(species, cells), member, precision=HI)
    pieces = lax.all_to_all(partial.reshape(species, devices, nreg // devices), ("gx", "gy"), 1, 1,
                            tiled=True)
    gradient = jnp.sum(pieces, axis=1)
    return adjoint, gradient


def solution(mesh):
    in_specs = (
        P(None, None, ("gx", "gy")),
        P(None, ("gx", "gy"), None),
        P(None, ("gx", "gy")),
        P(None, ("gx", "gy")),
        P(None, "gx", "gy"),
        P(None, "gx", "gy"),
        P(None, "gx", "gy"),
        P(None, "gx", "gy"),
        P("gx", "gy"),
    )
    out_specs = (P(None, None, "gx", "gy"), P(None, ("gx", "gy")))
    return jax.shard_map(local, mesh=mesh, in_specs=in_specs, out_specs=out_specs, check_vma=False)
```

```python
import functools

import jax
import jax.numpy as jnp
from jax import lax
from jax.experimental import pallas as pl
from jax.experimental.pallas import tpu as pltpu
from jax.sharding import PartitionSpec as P

HI = lax.Precision.HIGHEST
REG_DEV = 8


def _full(shape):
    nd = len(shape)
    return pl.BlockSpec(shape, lambda i, _n=nd: (0,) * _n)


def _unpack(r, l, q, cols, half):
    lane = lax.broadcasted_iota(jnp.int32, r.shape, 1)
    rs = (cols - half * q) % cols
    ls = (cols - half - half * q) % cols
    return jnp.where(lane < half, pltpu.roll(r, rs, 1) if rs else r,
                     jnp.where(lane >= cols - half, pltpu.roll(l, ls, 1) if ls else l, 0.0))


def _static_plane(c, refs):
    for ref in refs:
        if c < ref.shape[0]:
            return ref[c]
        c -= ref.shape[0]
    return jnp.zeros(refs[0].shape[1:], jnp.float32)


def _pack_kernel(capacity, adj_ref, owner_ref, col_ref, lev_ref, wx_ref, wy_ref, diff_ref,
                 out_ref, lo_ref, hi_ref, rows_ref, tbuf_ref):
    steps, n_pay, pixels = adj_ref.shape
    devices, width = out_ref.shape
    block = width // (steps * capacity)
    row = lax.broadcasted_iota(jnp.int32, (pixels, pixels), 0)
    lane = lax.broadcasted_iota(jnp.int32, (pixels, pixels), 1)
    dest = lax.broadcasted_iota(jnp.int32, (pixels, devices), 1).astype(jnp.float32)
    tbuf_ref[...] = jnp.zeros(tbuf_ref.shape, jnp.float32)
    for k in range(steps):
        across = jnp.broadcast_to(owner_ref[k:k + 1].astype(jnp.float32), (pixels, pixels))
        down = jnp.transpose(across)
        same = (down == across) & (lane < row)
        rank = jnp.sum(jnp.where(same, 1.0, 0.0), axis=1, keepdims=True)
        owner = down[:, :devices]
        rows_ref[:n_pay] = adj_ref[k]
        rows_ref[n_pay:n_pay + 1] = col_ref[k:k + 1].astype(jnp.float32)
        rows_ref[n_pay + 1:n_pay + 2] = lev_ref[k:k + 1].astype(jnp.float32)
        for j in range(capacity):
            pick = jnp.where((owner == dest) & (rank[:, :1] == j), 1.0, 0.0)
            at = (k * capacity + j) * block
            tbuf_ref[at:at + n_pay + 2] = lax.dot_general(
                rows_ref[...], pick, (((1,), (0,)), ((), ())),
                precision=lax.Precision.HIGHEST, preferred_element_type=jnp.float32)
    out_ref[...] = jnp.transpose(tbuf_ref[...])
    statics = (wx_ref, wy_ref, diff_ref)
    tr = wx_ref.shape[1]
    half = tr // 2
    trow = lax.broadcasted_iota(jnp.int32, wx_ref.shape[1:], 0)
    for i in range(lo_ref.shape[0]):
        a = _static_plane(2 * i, statics)
        b = _static_plane(2 * i + 1, statics)
        lo_ref[i] = jnp.where(trow < half, a, pltpu.roll(b, half, 0))
        hi_ref[i] = jnp.where(trow < half, pltpu.roll(a, half, 0), b)


def pack_call(capacity, devices, n_pad, pixel_adjoint, pixel_owner, pixel_column, pixel_level,
              wind_x, wind_y, diffusivity):
    steps, n_pay, pixels = pixel_adjoint.shape
    rows, cols = wind_x.shape[1:]
    block = -(-(n_pay + 2) // 16) * 16
    width = steps * capacity * block
    pairs = jax.ShapeDtypeStruct((n_pad // 2, rows, cols), jnp.float32)
    vmem = pl.BlockSpec(memory_space=pltpu.VMEM)
    return pl.pallas_call(
        functools.partial(_pack_kernel, capacity),
        in_specs=[vmem] * 7,
        out_specs=[vmem] * 3,
        out_shape=[jax.ShapeDtypeStruct((devices, width), jnp.float32), pairs, pairs],
        scratch_shapes=[pltpu.VMEM((n_pay + 2, pixels), jnp.float32),
                        pltpu.VMEM((width, devices), jnp.float32)],
    )(pixel_adjoint, pixel_owner.reshape(steps, pixels), pixel_column, pixel_level, wind_x,
      wind_y, diffusivity)


def _exact_dot(a, b):
    dims = (((1,), (1,)), ((), ()))
    hi = a.astype(jnp.bfloat16)
    rest = a - hi.astype(jnp.float32)
    mid = rest.astype(jnp.bfloat16)
    lo = (rest - mid.astype(jnp.float32)).astype(jnp.bfloat16)
    out = lax.dot_general(hi, b, dims, preferred_element_type=jnp.float32)
    out = out + lax.dot_general(mid, b, dims, preferred_element_type=jnp.float32)
    return out + lax.dot_general(lo, b, dims, preferred_element_type=jnp.float32)


def _forcing_kernel(species, kernel, levels, n_statics, own_ref, below_ref, above_ref, wx_ref,
                    wy_ref, diff_ref, sb_ref, sa_ref,
                    tall_ref, right_ref, left_ref, st_xh_ref, lown_ref, lnb_ref, *trans):
    steps = tall_ref.shape[0]
    devices, width = own_ref.shape
    capacity = 2
    block = width // (steps * capacity)
    slots = devices * capacity
    tr2, tc = tall_ref.shape[2:]
    tr = tr2 // 2
    half = tr // 2
    group = tc // half
    n_pay = species * kernel
    lane_t = lax.broadcasted_iota(jnp.int32, (tc, slots), 0)
    row_i = lax.broadcasted_iota(jnp.int32, (tr, slots), 0)
    lev_i = lax.broadcasted_iota(jnp.int32, (levels, slots), 0)
    lane16 = lax.broadcasted_iota(jnp.int32, (tr2, tc), 1)
    right_ref[...] = jnp.zeros(right_ref.shape, jnp.float32)
    left_ref[...] = jnp.zeros(left_ref.shape, jnp.float32)
    for tref, ref in zip(trans, (own_ref, below_ref, above_ref)):
        tref[...] = jnp.transpose(ref[...])
    for k in range(steps):
        hts = []
        for src, tref in enumerate(trans):
            at = k * capacity * block
            blk = jnp.concatenate(
                [tref[at + j * block:at + j * block + n_pay + 2] for j in range(capacity)], axis=1)
            col = blk[n_pay:n_pay + 1].astype(jnp.int32)
            lev = blk[n_pay + 1:n_pay + 2].astype(jnp.int32)
            row_q = col // tc
            lane_q = col % tc
            if src == 1:
                row_q = jnp.where(row_q < half, row_q, -1)
            elif src == 2:
                row_q = jnp.where(row_q >= half, row_q, -1)
            rmask = row_i == row_q
            hts.append((lane_t == lane_q).astype(jnp.bfloat16))
            offset = lev_i - lev
            dst = lown_ref if src == 0 else lnb_ref
            c0 = 0 if src < 2 else slots
            for s in range(species):
                prof = jnp.zeros((levels, slots), jnp.float32)
                for j in range(kernel):
                    prof = prof + jnp.where(offset == j, blk[s * kernel + j:s * kernel + j + 1], 0.0)
                for l in range(levels):
                    c = s * levels + l
                    dst[c * tr:(c + 1) * tr, c0:c0 + slots] = jnp.where(
                        rmask, jnp.broadcast_to(prof[l:l + 1], (tr, slots)), 0.0)
        own = _exact_dot(lown_ref[...], hts[0])
        xh = _exact_dot(lnb_ref[...], jnp.concatenate([hts[1], hts[2]], axis=1))
        planes = own.shape[0] // tr
        tall_ref[k, :, :tr, :] = own.reshape(planes, tr, tc)
        tall_ref[k, :, tr:, :] = xh.reshape(planes, tr, tc)
        for c in range(planes):
            g, q = divmod(k * planes + c, group)
            plane = tall_ref[k, c]
            sel = (lane16 >= half * q) & (lane16 < half * q + half)
            rs = (half * q) % tc
            ls = (half * q + half) % tc
            right_ref[g] = jnp.where(sel, pltpu.roll(plane, rs, 1) if rs else plane, right_ref[g])
            left_ref[g] = jnp.where(sel, pltpu.roll(plane, ls, 1) if ls else plane, left_ref[g])
    statics = (wx_ref, wy_ref, diff_ref)
    trow = lax.broadcasted_iota(jnp.int32, (tr, tc), 0)
    base = steps * species * levels
    for i in range(sb_ref.shape[0]):
        b = sb_ref[i]
        a = sa_ref[i]
        xhs = (jnp.where(trow < half, b, pltpu.roll(a, half, 0)),
               jnp.where(trow < half, pltpu.roll(b, half, 0), a))
        for off in range(2):
            c = 2 * i + off
            st_xh_ref[c] = xhs[off]
            if c >= n_statics:
                continue
            g, q = divmod(base + c, group)
            sel = (lane16 >= half * q) & (lane16 < half * q + half)
            rs = (half * q) % tc
            ls = (half * q + half) % tc
            for part, plane in ((slice(0, tr), _static_plane(c, statics)),
                                (slice(tr, tr2), xhs[off])):
                selp = sel[part]
                right_ref[g, part] = jnp.where(
                    selp, pltpu.roll(plane, rs, 1) if rs else plane, right_ref[g, part])
                left_ref[g, part] = jnp.where(
                    selp, pltpu.roll(plane, ls, 1) if ls else plane, left_ref[g, part])


def forcing_call(species, kernel, levels, n_statics, own, below, above, wind_x, wind_y,
                 diffusivity, st_below, st_above):
    steps = wind_x.shape[0]
    devices, width = own.shape
    slots = 2 * devices
    tr, cols = wind_x.shape[1:]
    planes = species * levels
    group = cols // (tr // 2)
    n_groups = -(-(steps * planes + n_statics) // group)
    packed = jax.ShapeDtypeStruct((n_groups, 2 * tr, cols), jnp.float32)
    vmem = pl.BlockSpec(memory_space=pltpu.VMEM)
    return pl.pallas_call(
        functools.partial(_forcing_kernel, species, kernel, levels, n_statics),
        in_specs=[vmem] * 8,
        out_specs=[vmem] * 4,
        out_shape=[jax.ShapeDtypeStruct((steps, planes, 2 * tr, cols), jnp.float32), packed,
                   packed, jax.ShapeDtypeStruct((2 * st_below.shape[0], tr, cols), jnp.float32)],
        scratch_shapes=[pltpu.VMEM((planes * tr, slots), jnp.float32),
                        pltpu.VMEM((planes * tr, 2 * slots), jnp.float32)]
        + [pltpu.VMEM((width, devices), jnp.float32)] * 3,
    )(own, below, above, wind_x, wind_y, diffusivity, st_below, st_above)


def _steps_kernel(steps, species, levels, n_statics,
                  right_ref, left_ref, wx_ref, wy_ref, diff_ref, st_xh, mask_ref, prior_ref,
                  tall_hbm, adj_ref, ss_ref,
                  tall_buf, yh_buf, se_ref, state_ref, red_ref, ratio_ref, inv_ref, sems):
    planes = species * levels
    rows, lanes = mask_ref.shape
    tr, tc = adj_ref.shape[2:]
    half = tr // 2
    group = tc // half
    d0 = 2 * steps

    loads = {}
    for k in reversed(range(steps)):
        copy = pltpu.make_async_copy(tall_hbm.at[k], tall_buf.at[k], sems.at[k])
        copy.start()
        loads[k] = copy

    n_fgroups = steps * planes // group

    def unpack_group(g, carry):
        r = right_ref[g]
        l = left_ref[g]
        for q in range(group):
            yh_buf[g * group + q] = _unpack(r, l, q, tc, half)
        return carry

    lax.fori_loop(0, n_fgroups, unpack_group, 0)
    for c in range(n_statics):
        g, q = divmod(n_fgroups * group + c, group)
        se_ref[c, :, tc:] = _unpack(right_ref[g], left_ref[g], q, tc, half)

    for c in range(n_statics):
        se_ref[c, :tr, :tc] = _static_plane(c, (wx_ref, wy_ref, diff_ref))
        se_ref[c, tr:, :tc] = st_xh[c]

    zero = jnp.zeros((rows, lanes), jnp.float32)
    inside = mask_ref[...] > 0.5
    carried = zero
    for l in range(levels):
        below = se_ref[d0 + l - 1] if l > 0 else zero
        above = se_ref[d0 + l] if l < levels - 1 else zero
        inverse = 1.0 / (1.0 + below + above + below * carried)
        ratio = -above * inverse
        ratio_ref[l] = ratio
        inv_ref[l] = inverse
        carried = ratio

    for k in reversed(range(steps)):
        first = k == steps - 1
        last = k == 0
        if first:
            loads[k].wait()
            for s in range(species):

                def assemble(l, carry, s=s, k=k):
                    c = s * levels + l
                    state_ref[s, l, :, :tc] = tall_buf[k, c]
                    state_ref[s, l, :, tc:] = yh_buf[k * planes + c]
                    state_ref[s, l] = jnp.where(inside, state_ref[s, l], 0.0)
                    return carry

                lax.fori_loop(0, levels, assemble, 0, unroll=4)
        if not last:
            loads[k - 1].wait()

        wx = se_ref[k]
        wy = se_ref[steps + k]
        east = jnp.maximum(wx, 0.0)
        west = jnp.maximum(-wx, 0.0)
        north = jnp.maximum(wy, 0.0)
        south = jnp.maximum(-wy, 0.0)
        remain = 1.0 - (east + west + north + south)
        if last:
            _last_step(species, levels, tr, tc, state_ref, east, west, north, south, remain,
                       se_ref, d0, inv_ref, ratio_ref, red_ref, adj_ref, ss_ref, prior_ref)
            continue

        def forward(l, reduced):
            below = jnp.where(l > 0, se_ref[d0 + jnp.maximum(l - 1, 0)], zero)
            inverse = inv_ref[l]
            out = []
            for s in range(species):
                f = state_ref[s, l]
                from_east = pltpu.roll(east * f, rows - 1, 0)
                from_west = pltpu.roll(west * f, 1, 0)
                from_north = pltpu.roll(north * f, lanes - 1, 1)
                from_south = pltpu.roll(south * f, 1, 1)
                moved = f * remain
                moved = moved + from_east + from_west
                moved = moved + from_north + from_south
                r = (moved + below * reduced[s]) * inverse
                red_ref[s, l] = r
                out.append(r)
            return tuple(out)

        lax.fori_loop(0, levels, forward, (zero,) * species, unroll=8)

        def backward(i, result, k=k):
            l = levels - 1 - i
            ratio = ratio_ref[l]
            out = []
            for s in range(species):
                c = s * levels + l
                r = red_ref[s, l] - ratio * result[s]
                state_ref[s, l, :, :tc] = jnp.where(
                    inside[:, :tc], r[:, :tc] + tall_buf[k - 1, c], 0.0)
                state_ref[s, l, :, tc:] = jnp.where(
                    inside[:, tc:], r[:, tc:] + yh_buf[(k - 1) * planes + c], 0.0)
                out.append(r)
            return tuple(out)

        surface = lax.fori_loop(0, levels, backward, (zero,) * species, unroll=8)
        for s in range(species):
            if first:
                ss_ref[s] = prior_ref[s] * surface[s][:tr, :tc]
            else:
                ss_ref[s] = ss_ref[s] + prior_ref[s] * surface[s][:tr, :tc]


def _last_step(species, levels, tr, tc, forced_ref, east, west, north, south, remain, se_ref,
               d0, inv_ref, ratio_ref, red_ref, out_ref, ss_ref, prior_ref):
    row = lax.broadcasted_iota(jnp.int32, (tr, tc), 0)
    lane = lax.broadcasted_iota(jnp.int32, (tr, tc), 1)
    last_row = row == tr - 1
    first_row = row == 0
    last_lane = lane == tc - 1
    first_lane = lane == 0
    e_a, e_b = east[:tr, :tc], east[tr:, :tc]
    w_a, w_b = west[:tr, :tc], west[tr:, :tc]
    n_a, n_c = north[:tr, :tc], north[:tr, tc:]
    s_a, s_c = south[:tr, :tc], south[:tr, tc:]
    rem = remain[:tr, :tc]
    zero = jnp.zeros((tr, tc), jnp.float32)
    def forward(l, reduced):
        below = jnp.where(l > 0, se_ref[d0 + jnp.maximum(l - 1, 0), :tr, :tc], zero)
        inverse = inv_ref[l, :tr, :tc]
        out = []
        for s in range(species):
            f_a = forced_ref[s, l, :tr, :tc]
            f_b = forced_ref[s, l, tr:, :tc]
            f_c = forced_ref[s, l, :tr, tc:]
            from_east = jnp.where(last_row, pltpu.roll(e_b * f_b, tr - 1, 0),
                                  pltpu.roll(e_a * f_a, tr - 1, 0))
            from_west = jnp.where(first_row, pltpu.roll(w_b * f_b, 1, 0),
                                  pltpu.roll(w_a * f_a, 1, 0))
            from_north = jnp.where(last_lane, pltpu.roll(n_c * f_c, tc - 1, 1),
                                   pltpu.roll(n_a * f_a, tc - 1, 1))
            from_south = jnp.where(first_lane, pltpu.roll(s_c * f_c, 1, 1),
                                   pltpu.roll(s_a * f_a, 1, 1))
            moved = f_a * rem
            moved = moved + from_east + from_west
            moved = moved + from_north + from_south
            r = (moved + below * reduced[s]) * inverse
            red_ref[s, l, :tr, :tc] = r
            out.append(r)
        return tuple(out)

    lax.fori_loop(0, levels, forward, (zero,) * species, unroll=4)

    def backward(i, result):
        l = levels - 1 - i
        ratio = ratio_ref[l, :tr, :tc]
        out = []
        for s in range(species):
            r = red_ref[s, l, :tr, :tc] - ratio * result[s]
            out_ref[s, l] = r
            out.append(r)
        return tuple(out)

    surface = lax.fori_loop(0, levels, backward, (zero,) * species, unroll=4)
    for s in range(species):
        ss_ref[s] = ss_ref[s] + prior_ref[s] * surface[s]


def steps_call(steps, species, levels, n_statics, right, left, wind_x, wind_y, diffusivity,
               st_xh, mask, prior, tall):
    _, planes, rows, tc = tall.shape
    tr = rows // 2
    lanes = mask.shape[1]
    vmem = pl.BlockSpec(memory_space=pltpu.VMEM)
    anyspace = pl.BlockSpec(memory_space=pl.ANY)
    return pl.pallas_call(
        functools.partial(_steps_kernel, steps, species, levels, n_statics),
        in_specs=[vmem] * 8 + [anyspace],
        out_specs=[vmem, vmem],
        out_shape=[jax.ShapeDtypeStruct((species, levels, tr, tc), jnp.float32),
                   jax.ShapeDtypeStruct(prior.shape, jnp.float32)],
        scratch_shapes=[
            pltpu.VMEM((steps, planes, rows, tc), jnp.float32),
            pltpu.VMEM((steps * planes, rows, tc), jnp.float32),
            pltpu.VMEM((n_statics, rows, lanes), jnp.float32),
            pltpu.VMEM((species, levels, rows, lanes), jnp.float32),
            pltpu.VMEM((species, levels, rows, lanes), jnp.float32),
            pltpu.VMEM((levels, rows, lanes), jnp.float32),
            pltpu.VMEM((levels, rows, lanes), jnp.float32),
            pltpu.SemaphoreType.DMA((steps,)),
        ],
        compiler_params=pltpu.CompilerParams(vmem_limit_bytes=48 * 1024 * 1024),
    )(right, left, wind_x, wind_y, diffusivity, st_xh, mask, prior, tall)


def _pairs(axis):
    n = lax.axis_size(axis)
    return [(i, i + 1) for i in range(n - 1)], [(i + 1, i) for i in range(n - 1)]


def local(pixel_adjoint, pixel_owner, pixel_column, pixel_level, wind_x, wind_y,
          diffusivity, prior_emission, region_map):
    gx_n = lax.axis_size("gx")
    gy_n = lax.axis_size("gy")
    devices = gx_n * gy_n
    steps, rows, cols = wind_x.shape
    levels = diffusivity.shape[0] + 1
    species = prior_emission.shape[0]
    kernel = pixel_adjoint.shape[1] // species
    pixels = pixel_adjoint.shape[2]
    capacity = 2 * pixels // devices
    cells = rows * cols
    slots = devices * capacity
    halo = rows // 2
    assert steps <= halo
    lanes = 2 * cols
    ext_rows = 2 * rows

    n_s = 2 * steps + levels - 1
    group = cols // halo
    n_pad = -(-n_s // group) * group
    placed, st_lo, st_hi = pack_call(capacity, devices, n_pad, pixel_adjoint, pixel_owner,
                                     pixel_column, pixel_level, wind_x, wind_y, diffusivity)
    up_x, down_x = _pairs("gx")
    up_y, down_y = _pairs("gy")
    st_below = lax.ppermute(st_lo, "gx", down_x)
    st_above = lax.ppermute(st_hi, "gx", up_x)
    received = lax.all_to_all(placed, ("gx", "gy"), 0, 0, tiled=True)

    below = lax.ppermute(received, "gx", down_x)
    above = lax.ppermute(received, "gx", up_x)
    tall, right, left, st_xh = forcing_call(species, kernel, levels, n_s, received, below, above,
                                            wind_x, wind_y, diffusivity, st_below, st_above)
    right = lax.ppermute(right, "gy", down_y)
    left = lax.ppermute(left, "gy", up_y)

    gxi = lax.axis_index("gx")
    gyi = lax.axis_index("gy")
    r = jnp.arange(ext_rows, dtype=jnp.int32)[:, None]
    c = jnp.arange(lanes, dtype=jnp.int32)[None, :]
    grow = gxi * rows + jnp.where(r < rows + halo, r, r - ext_rows)
    ccol = jnp.where(c < cols + halo, c, c - lanes)
    gcol = gyi * cols + ccol
    inside = ((grow >= 0) & (grow < gx_n * rows) & (gcol >= 0) & (gcol < gy_n * cols)
              & ((c < cols + halo) | (c >= lanes - halo)))
    mask = inside.astype(jnp.float32)

    adjoint, surface_sum = steps_call(steps, species, levels, n_s, right, left, wind_x, wind_y,
                                      diffusivity, st_xh, mask, prior_emission, tall)

    nreg = REG_DEV * devices
    blocks = surface_sum.reshape(species, rows // 2, 2, cols // 4, 4).sum(axis=(2, 4))
    block_region = region_map[::2, ::4].reshape(-1)
    member = (block_region[:, None] == jnp.arange(nreg, dtype=jnp.int32)).astype(jnp.float32)
    partial = jnp.dot(blocks.reshape(species, -1), member, precision=HI)
    pieces = lax.all_to_all(partial.reshape(species, devices, nreg // devices), ("gx", "gy"), 1, 1,
                            tiled=True)
    gradient = jnp.sum(pieces, axis=1)
    return adjoint, gradient


def solution(mesh):
    in_specs = (
        P(None, None, ("gx", "gy")),
        P(None, ("gx", "gy"), None),
        P(None, ("gx", "gy")),
        P(None, ("gx", "gy")),
        P(None, "gx", "gy"),
        P(None, "gx", "gy"),
        P(None, "gx", "gy"),
        P(None, "gx", "gy"),
        P("gx", "gy"),
    )
    out_specs = (P(None, None, "gx", "gy"), P(None, ("gx", "gy")))
    return jax.shard_map(local, mesh=mesh, in_specs=in_specs, out_specs=out_specs, check_vma=False)
```

```python
import functools

import jax
import jax.numpy as jnp
from jax import lax
from jax.experimental import pallas as pl
from jax.experimental.pallas import tpu as pltpu
from jax.sharding import PartitionSpec as P

HI = lax.Precision.HIGHEST
REG_DEV = 8


def _full(shape):
    nd = len(shape)
    return pl.BlockSpec(shape, lambda i, _n=nd: (0,) * _n)


def _unpack(r, l, q, cols, half):
    lane = lax.broadcasted_iota(jnp.int32, r.shape, 1)
    rs = (cols - half * q) % cols
    ls = (cols - half - half * q) % cols
    return jnp.where(lane < half, pltpu.roll(r, rs, 1) if rs else r,
                     jnp.where(lane >= cols - half, pltpu.roll(l, ls, 1) if ls else l, 0.0))


def _static_plane(c, refs):
    for ref in refs:
        if c < ref.shape[0]:
            return ref[c]
        c -= ref.shape[0]
    return jnp.zeros(refs[0].shape[1:], jnp.float32)


def _pack_kernel(capacity, adj_ref, owner_ref, col_ref, lev_ref, wx_ref, wy_ref, diff_ref,
                 out_ref, lo_ref, hi_ref, rows_ref, tbuf_ref):
    steps, n_pay, pixels = adj_ref.shape
    devices, width = out_ref.shape
    block = width // (steps * capacity)
    row = lax.broadcasted_iota(jnp.int32, (pixels, pixels), 0)
    lane = lax.broadcasted_iota(jnp.int32, (pixels, pixels), 1)
    dest = lax.broadcasted_iota(jnp.int32, (pixels, devices), 1).astype(jnp.float32)
    tbuf_ref[...] = jnp.zeros(tbuf_ref.shape, jnp.float32)
    for k in range(steps):
        across = jnp.broadcast_to(owner_ref[k:k + 1].astype(jnp.float32), (pixels, pixels))
        down = jnp.transpose(across)
        same = (down == across) & (lane < row)
        rank = jnp.sum(jnp.where(same, 1.0, 0.0), axis=1, keepdims=True)
        owner = down[:, :devices]
        rows_ref[:n_pay] = adj_ref[k]
        rows_ref[n_pay:n_pay + 1] = col_ref[k:k + 1].astype(jnp.float32)
        rows_ref[n_pay + 1:n_pay + 2] = lev_ref[k:k + 1].astype(jnp.float32)
        for j in range(capacity):
            pick = jnp.where((owner == dest) & (rank[:, :1] == j), 1.0, 0.0)
            at = (k * capacity + j) * block
            tbuf_ref[at:at + n_pay + 2] = _exact_dot(
                rows_ref[...], pick.astype(jnp.bfloat16), (((1,), (0,)), ((), ())))
    out_ref[...] = jnp.transpose(tbuf_ref[...])
    statics = (wx_ref, wy_ref, diff_ref)
    tr = wx_ref.shape[1]
    half = tr // 2
    trow = lax.broadcasted_iota(jnp.int32, wx_ref.shape[1:], 0)
    for i in range(lo_ref.shape[0]):
        a = _static_plane(2 * i, statics)
        b = _static_plane(2 * i + 1, statics)
        lo_ref[i] = jnp.where(trow < half, a, pltpu.roll(b, half, 0))
        hi_ref[i] = jnp.where(trow < half, pltpu.roll(a, half, 0), b)


def pack_call(capacity, devices, n_pad, pixel_adjoint, pixel_owner, pixel_column, pixel_level,
              wind_x, wind_y, diffusivity):
    steps, n_pay, pixels = pixel_adjoint.shape
    rows, cols = wind_x.shape[1:]
    block = -(-(n_pay + 2) // 16) * 16
    width = steps * capacity * block
    pairs = jax.ShapeDtypeStruct((n_pad // 2, rows, cols), jnp.float32)
    vmem = pl.BlockSpec(memory_space=pltpu.VMEM)
    return pl.pallas_call(
        functools.partial(_pack_kernel, capacity),
        in_specs=[vmem] * 7,
        out_specs=[vmem] * 3,
        out_shape=[jax.ShapeDtypeStruct((devices, width), jnp.float32), pairs, pairs],
        scratch_shapes=[pltpu.VMEM((n_pay + 2, pixels), jnp.float32),
                        pltpu.VMEM((width, devices), jnp.float32)],
    )(pixel_adjoint, pixel_owner.reshape(steps, pixels), pixel_column, pixel_level, wind_x,
      wind_y, diffusivity)


def _exact_dot(a, b, dims=(((1,), (1,)), ((), ()))):
    hi = a.astype(jnp.bfloat16)
    rest = a - hi.astype(jnp.float32)
    mid = rest.astype(jnp.bfloat16)
    lo = (rest - mid.astype(jnp.float32)).astype(jnp.bfloat16)
    out = lax.dot_general(hi, b, dims, preferred_element_type=jnp.float32)
    out = out + lax.dot_general(mid, b, dims, preferred_element_type=jnp.float32)
    return out + lax.dot_general(lo, b, dims, preferred_element_type=jnp.float32)


def _forcing_kernel(species, kernel, levels, n_statics, own_ref, below_ref, above_ref, wx_ref,
                    wy_ref, diff_ref, sb_ref, sa_ref,
                    tall_ref, right_ref, left_ref, st_xh_ref, lown_ref, lnb_ref, *trans):
    steps = tall_ref.shape[0]
    devices, width = own_ref.shape
    capacity = 2
    block = width // (steps * capacity)
    slots = devices * capacity
    tr2, tc = tall_ref.shape[2:]
    tr = tr2 // 2
    half = tr // 2
    group = tc // half
    n_pay = species * kernel
    lane_t = lax.broadcasted_iota(jnp.int32, (tc, slots), 0)
    row_i = lax.broadcasted_iota(jnp.int32, (tr, slots), 0)
    lev_i = lax.broadcasted_iota(jnp.int32, (levels, slots), 0)
    lane16 = lax.broadcasted_iota(jnp.int32, (tr2, tc), 1)
    right_ref[...] = jnp.zeros(right_ref.shape, jnp.float32)
    left_ref[...] = jnp.zeros(left_ref.shape, jnp.float32)
    for tref, ref in zip(trans, (own_ref, below_ref, above_ref)):
        tref[...] = jnp.transpose(ref[...])
    for k in range(steps):
        hts = []
        for src, tref in enumerate(trans):
            at = k * capacity * block
            blk = jnp.concatenate(
                [tref[at + j * block:at + j * block + n_pay + 2] for j in range(capacity)], axis=1)
            col = blk[n_pay:n_pay + 1].astype(jnp.int32)
            lev = blk[n_pay + 1:n_pay + 2].astype(jnp.int32)
            row_q = col // tc
            lane_q = col % tc
            if src == 1:
                row_q = jnp.where(row_q < half, row_q, -1)
            elif src == 2:
                row_q = jnp.where(row_q >= half, row_q, -1)
            rmask = row_i == row_q
            hts.append((lane_t == lane_q).astype(jnp.bfloat16))
            offset = lev_i - lev
            dst = lown_ref if src == 0 else lnb_ref
            c0 = 0 if src < 2 else slots
            for s in range(species):
                prof = jnp.zeros((levels, slots), jnp.float32)
                for j in range(kernel):
                    prof = prof + jnp.where(offset == j, blk[s * kernel + j:s * kernel + j + 1], 0.0)
                for l in range(levels):
                    c = s * levels + l
                    dst[c * tr:(c + 1) * tr, c0:c0 + slots] = jnp.where(
                        rmask, jnp.broadcast_to(prof[l:l + 1], (tr, slots)), 0.0)
        own = _exact_dot(lown_ref[...], hts[0])
        xh = _exact_dot(lnb_ref[...], jnp.concatenate([hts[1], hts[2]], axis=1))
        planes = own.shape[0] // tr
        tall_ref[k, :, :tr, :] = own.reshape(planes, tr, tc)
        tall_ref[k, :, tr:, :] = xh.reshape(planes, tr, tc)
        for c in range(planes):
            g, q = divmod(k * planes + c, group)
            plane = tall_ref[k, c]
            sel = (lane16 >= half * q) & (lane16 < half * q + half)
            rs = (half * q) % tc
            ls = (half * q + half) % tc
            right_ref[g] = jnp.where(sel, pltpu.roll(plane, rs, 1) if rs else plane, right_ref[g])
            left_ref[g] = jnp.where(sel, pltpu.roll(plane, ls, 1) if ls else plane, left_ref[g])
    statics = (wx_ref, wy_ref, diff_ref)
    trow = lax.broadcasted_iota(jnp.int32, (tr, tc), 0)
    base = steps * species * levels
    for i in range(sb_ref.shape[0]):
        b = sb_ref[i]
        a = sa_ref[i]
        xhs = (jnp.where(trow < half, b, pltpu.roll(a, half, 0)),
               jnp.where(trow < half, pltpu.roll(b, half, 0), a))
        for off in range(2):
            c = 2 * i + off
            st_xh_ref[c] = xhs[off]
            if c >= n_statics:
                continue
            g, q = divmod(base + c, group)
            sel = (lane16 >= half * q) & (lane16 < half * q + half)
            rs = (half * q) % tc
            ls = (half * q + half) % tc
            for part, plane in ((slice(0, tr), _static_plane(c, statics)),
                                (slice(tr, tr2), xhs[off])):
                selp = sel[part]
                right_ref[g, part] = jnp.where(
                    selp, pltpu.roll(plane, rs, 1) if rs else plane, right_ref[g, part])
                left_ref[g, part] = jnp.where(
                    selp, pltpu.roll(plane, ls, 1) if ls else plane, left_ref[g, part])


def forcing_call(species, kernel, levels, n_statics, own, below, above, wind_x, wind_y,
                 diffusivity, st_below, st_above):
    steps = wind_x.shape[0]
    devices, width = own.shape
    slots = 2 * devices
    tr, cols = wind_x.shape[1:]
    planes = species * levels
    group = cols // (tr // 2)
    n_groups = -(-(steps * planes + n_statics) // group)
    packed = jax.ShapeDtypeStruct((n_groups, 2 * tr, cols), jnp.float32)
    vmem = pl.BlockSpec(memory_space=pltpu.VMEM)
    return pl.pallas_call(
        functools.partial(_forcing_kernel, species, kernel, levels, n_statics),
        in_specs=[vmem] * 8,
        out_specs=[vmem] * 4,
        out_shape=[jax.ShapeDtypeStruct((steps, planes, 2 * tr, cols), jnp.float32), packed,
                   packed, jax.ShapeDtypeStruct((2 * st_below.shape[0], tr, cols), jnp.float32)],
        scratch_shapes=[pltpu.VMEM((planes * tr, slots), jnp.float32),
                        pltpu.VMEM((planes * tr, 2 * slots), jnp.float32)]
        + [pltpu.VMEM((width, devices), jnp.float32)] * 3,
    )(own, below, above, wind_x, wind_y, diffusivity, st_below, st_above)


def _steps_kernel(steps, species, levels, n_statics,
                  right_ref, left_ref, wx_ref, wy_ref, diff_ref, st_xh, mask_ref, prior_ref,
                  tall_hbm, adj_ref, ss_ref,
                  tall_buf, yh_buf, se_ref, state_ref, red_ref, ratio_ref, inv_ref, sems):
    planes = species * levels
    rows, lanes = mask_ref.shape
    tr, tc = adj_ref.shape[2:]
    half = tr // 2
    group = tc // half
    d0 = 2 * steps

    loads = {}
    for k in reversed(range(steps)):
        copy = pltpu.make_async_copy(tall_hbm.at[k], tall_buf.at[k], sems.at[k])
        copy.start()
        loads[k] = copy

    n_fgroups = steps * planes // group

    def unpack_group(g, carry):
        r = right_ref[g]
        l = left_ref[g]
        for q in range(group):
            yh_buf[g * group + q] = _unpack(r, l, q, tc, half)
        return carry

    lax.fori_loop(0, n_fgroups, unpack_group, 0)
    for c in range(n_statics):
        g, q = divmod(n_fgroups * group + c, group)
        se_ref[c, :, tc:] = _unpack(right_ref[g], left_ref[g], q, tc, half)

    for c in range(n_statics):
        se_ref[c, :tr, :tc] = _static_plane(c, (wx_ref, wy_ref, diff_ref))
        se_ref[c, tr:, :tc] = st_xh[c]

    zero = jnp.zeros((rows, lanes), jnp.float32)
    inside = mask_ref[...] > 0.5
    carried = zero
    for l in range(levels):
        below = se_ref[d0 + l - 1] if l > 0 else zero
        above = se_ref[d0 + l] if l < levels - 1 else zero
        inverse = 1.0 / (1.0 + below + above + below * carried)
        ratio = -above * inverse
        ratio_ref[l] = ratio
        inv_ref[l] = inverse
        carried = ratio

    for k in reversed(range(steps)):
        first = k == steps - 1
        last = k == 0
        if first:
            loads[k].wait()
            for s in range(species):

                def assemble(l, carry, s=s, k=k):
                    c = s * levels + l
                    state_ref[s, l, :, :tc] = tall_buf[k, c]
                    state_ref[s, l, :, tc:] = yh_buf[k * planes + c]
                    state_ref[s, l] = jnp.where(inside, state_ref[s, l], 0.0)
                    return carry

                lax.fori_loop(0, levels, assemble, 0, unroll=4)
        if not last:
            loads[k - 1].wait()

        wx = se_ref[k]
        wy = se_ref[steps + k]
        east = jnp.maximum(wx, 0.0)
        west = jnp.maximum(-wx, 0.0)
        north = jnp.maximum(wy, 0.0)
        south = jnp.maximum(-wy, 0.0)
        remain = 1.0 - (east + west + north + south)
        if last:
            _last_step(species, levels, tr, tc, state_ref, east, west, north, south, remain,
                       se_ref, d0, inv_ref, ratio_ref, red_ref, adj_ref, ss_ref, prior_ref)
            continue

        def forward(l, reduced):
            below = jnp.where(l > 0, se_ref[d0 + jnp.maximum(l - 1, 0)], zero)
            inverse = inv_ref[l]
            out = []
            for s in range(species):
                f = state_ref[s, l]
                from_east = pltpu.roll(east * f, rows - 1, 0)
                from_west = pltpu.roll(west * f, 1, 0)
                from_north = pltpu.roll(north * f, lanes - 1, 1)
                from_south = pltpu.roll(south * f, 1, 1)
                moved = f * remain
                moved = moved + from_east + from_west
                moved = moved + from_north + from_south
                r = (moved + below * reduced[s]) * inverse
                red_ref[s, l] = r
                out.append(r)
            return tuple(out)

        lax.fori_loop(0, levels, forward, (zero,) * species, unroll=8)

        def backward(i, result, k=k):
            l = levels - 1 - i
            ratio = ratio_ref[l]
            out = []
            for s in range(species):
                c = s * levels + l
                r = red_ref[s, l] - ratio * result[s]
                state_ref[s, l, :, :tc] = jnp.where(
                    inside[:, :tc], r[:, :tc] + tall_buf[k - 1, c], 0.0)
                state_ref[s, l, :, tc:] = jnp.where(
                    inside[:, tc:], r[:, tc:] + yh_buf[(k - 1) * planes + c], 0.0)
                out.append(r)
            return tuple(out)

        surface = lax.fori_loop(0, levels, backward, (zero,) * species, unroll=8)
        for s in range(species):
            if first:
                ss_ref[s] = prior_ref[s] * surface[s][:tr, :tc]
            else:
                ss_ref[s] = ss_ref[s] + prior_ref[s] * surface[s][:tr, :tc]


def _last_step(species, levels, tr, tc, forced_ref, east, west, north, south, remain, se_ref,
               d0, inv_ref, ratio_ref, red_ref, out_ref, ss_ref, prior_ref):
    row = lax.broadcasted_iota(jnp.int32, (tr, tc), 0)
    lane = lax.broadcasted_iota(jnp.int32, (tr, tc), 1)
    last_row = row == tr - 1
    first_row = row == 0
    last_lane = lane == tc - 1
    first_lane = lane == 0
    e_a, e_b = east[:tr, :tc], east[tr:, :tc]
    w_a, w_b = west[:tr, :tc], west[tr:, :tc]
    n_a, n_c = north[:tr, :tc], north[:tr, tc:]
    s_a, s_c = south[:tr, :tc], south[:tr, tc:]
    rem = remain[:tr, :tc]
    zero = jnp.zeros((tr, tc), jnp.float32)
    def forward(l, reduced):
        below = jnp.where(l > 0, se_ref[d0 + jnp.maximum(l - 1, 0), :tr, :tc], zero)
        inverse = inv_ref[l, :tr, :tc]
        out = []
        for s in range(species):
            f_a = forced_ref[s, l, :tr, :tc]
            f_b = forced_ref[s, l, tr:, :tc]
            f_c = forced_ref[s, l, :tr, tc:]
            from_east = jnp.where(last_row, pltpu.roll(e_b * f_b, tr - 1, 0),
                                  pltpu.roll(e_a * f_a, tr - 1, 0))
            from_west = jnp.where(first_row, pltpu.roll(w_b * f_b, 1, 0),
                                  pltpu.roll(w_a * f_a, 1, 0))
            from_north = jnp.where(last_lane, pltpu.roll(n_c * f_c, tc - 1, 1),
                                   pltpu.roll(n_a * f_a, tc - 1, 1))
            from_south = jnp.where(first_lane, pltpu.roll(s_c * f_c, 1, 1),
                                   pltpu.roll(s_a * f_a, 1, 1))
            moved = f_a * rem
            moved = moved + from_east + from_west
            moved = moved + from_north + from_south
            r = (moved + below * reduced[s]) * inverse
            red_ref[s, l, :tr, :tc] = r
            out.append(r)
        return tuple(out)

    lax.fori_loop(0, levels, forward, (zero,) * species, unroll=4)

    def backward(i, result):
        l = levels - 1 - i
        ratio = ratio_ref[l, :tr, :tc]
        out = []
        for s in range(species):
            r = red_ref[s, l, :tr, :tc] - ratio * result[s]
            out_ref[s, l] = r
            out.append(r)
        return tuple(out)

    surface = lax.fori_loop(0, levels, backward, (zero,) * species, unroll=4)
    for s in range(species):
        ss_ref[s] = ss_ref[s] + prior_ref[s] * surface[s]


def steps_call(steps, species, levels, n_statics, right, left, wind_x, wind_y, diffusivity,
               st_xh, mask, prior, tall):
    _, planes, rows, tc = tall.shape
    tr = rows // 2
    lanes = mask.shape[1]
    vmem = pl.BlockSpec(memory_space=pltpu.VMEM)
    anyspace = pl.BlockSpec(memory_space=pl.ANY)
    return pl.pallas_call(
        functools.partial(_steps_kernel, steps, species, levels, n_statics),
        in_specs=[vmem] * 8 + [anyspace],
        out_specs=[vmem, vmem],
        out_shape=[jax.ShapeDtypeStruct((species, levels, tr, tc), jnp.float32),
                   jax.ShapeDtypeStruct(prior.shape, jnp.float32)],
        scratch_shapes=[
            pltpu.VMEM((steps, planes, rows, tc), jnp.float32),
            pltpu.VMEM((steps * planes, rows, tc), jnp.float32),
            pltpu.VMEM((n_statics, rows, lanes), jnp.float32),
            pltpu.VMEM((species, levels, rows, lanes), jnp.float32),
            pltpu.VMEM((species, levels, rows, lanes), jnp.float32),
            pltpu.VMEM((levels, rows, lanes), jnp.float32),
            pltpu.VMEM((levels, rows, lanes), jnp.float32),
            pltpu.SemaphoreType.DMA((steps,)),
        ],
        compiler_params=pltpu.CompilerParams(vmem_limit_bytes=48 * 1024 * 1024),
    )(right, left, wind_x, wind_y, diffusivity, st_xh, mask, prior, tall)


def _pairs(axis):
    n = lax.axis_size(axis)
    return [(i, i + 1) for i in range(n - 1)], [(i + 1, i) for i in range(n - 1)]


def local(pixel_adjoint, pixel_owner, pixel_column, pixel_level, wind_x, wind_y,
          diffusivity, prior_emission, region_map):
    gx_n = lax.axis_size("gx")
    gy_n = lax.axis_size("gy")
    devices = gx_n * gy_n
    steps, rows, cols = wind_x.shape
    levels = diffusivity.shape[0] + 1
    species = prior_emission.shape[0]
    kernel = pixel_adjoint.shape[1] // species
    pixels = pixel_adjoint.shape[2]
    capacity = 2 * pixels // devices
    cells = rows * cols
    slots = devices * capacity
    halo = rows // 2
    assert steps <= halo
    lanes = 2 * cols
    ext_rows = 2 * rows

    n_s = 2 * steps + levels - 1
    group = cols // halo
    n_pad = -(-n_s // group) * group
    placed, st_lo, st_hi = pack_call(capacity, devices, n_pad, pixel_adjoint, pixel_owner,
                                     pixel_column, pixel_level, wind_x, wind_y, diffusivity)
    up_x, down_x = _pairs("gx")
    up_y, down_y = _pairs("gy")
    st_below = lax.ppermute(st_lo, "gx", down_x)
    st_above = lax.ppermute(st_hi, "gx", up_x)
    received = lax.all_to_all(placed, ("gx", "gy"), 0, 0, tiled=True)

    below = lax.ppermute(received, "gx", down_x)
    above = lax.ppermute(received, "gx", up_x)
    tall, right, left, st_xh = forcing_call(species, kernel, levels, n_s, received, below, above,
                                            wind_x, wind_y, diffusivity, st_below, st_above)
    right = lax.ppermute(right, "gy", down_y)
    left = lax.ppermute(left, "gy", up_y)

    gxi = lax.axis_index("gx")
    gyi = lax.axis_index("gy")
    r = jnp.arange(ext_rows, dtype=jnp.int32)[:, None]
    c = jnp.arange(lanes, dtype=jnp.int32)[None, :]
    grow = gxi * rows + jnp.where(r < rows + halo, r, r - ext_rows)
    ccol = jnp.where(c < cols + halo, c, c - lanes)
    gcol = gyi * cols + ccol
    inside = ((grow >= 0) & (grow < gx_n * rows) & (gcol >= 0) & (gcol < gy_n * cols)
              & ((c < cols + halo) | (c >= lanes - halo)))
    mask = inside.astype(jnp.float32)

    adjoint, surface_sum = steps_call(steps, species, levels, n_s, right, left, wind_x, wind_y,
                                      diffusivity, st_xh, mask, prior_emission, tall)

    nreg = REG_DEV * devices
    blocks = surface_sum.reshape(species, rows // 2, 2, cols // 4, 4).sum(axis=(2, 4))
    block_region = region_map[::2, ::4].reshape(-1)
    member = (block_region[:, None] == jnp.arange(nreg, dtype=jnp.int32)).astype(jnp.float32)
    partial = jnp.dot(blocks.reshape(species, -1), member, precision=HI)
    pieces = lax.all_to_all(partial.reshape(species, devices, nreg // devices), ("gx", "gy"), 1, 1,
                            tiled=True)
    gradient = jnp.sum(pieces, axis=1)
    return adjoint, gradient


def solution(mesh):
    in_specs = (
        P(None, None, ("gx", "gy")),
        P(None, ("gx", "gy"), None),
        P(None, ("gx", "gy")),
        P(None, ("gx", "gy")),
        P(None, "gx", "gy"),
        P(None, "gx", "gy"),
        P(None, "gx", "gy"),
        P(None, "gx", "gy"),
        P("gx", "gy"),
    )
    out_specs = (P(None, None, "gx", "gy"), P(None, ("gx", "gy")))
    return jax.shard_map(local, mesh=mesh, in_specs=in_specs, out_specs=out_specs, check_vma=False)
```

```python
import functools

import jax
import jax.numpy as jnp
from jax import lax
from jax.experimental import pallas as pl
from jax.experimental.pallas import tpu as pltpu
from jax.sharding import PartitionSpec as P

HI = lax.Precision.HIGHEST
REG_DEV = 8


def _full(shape):
    nd = len(shape)
    return pl.BlockSpec(shape, lambda i, _n=nd: (0,) * _n)


def _unpack(r, l, q, cols, half):
    lane = lax.broadcasted_iota(jnp.int32, r.shape, 1)
    rs = (cols - half * q) % cols
    ls = (cols - half - half * q) % cols
    return jnp.where(lane < half, pltpu.roll(r, rs, 1) if rs else r,
                     jnp.where(lane >= cols - half, pltpu.roll(l, ls, 1) if ls else l, 0.0))


def _static_plane(c, refs):
    for ref in refs:
        if c < ref.shape[0]:
            return ref[c]
        c -= ref.shape[0]
    return jnp.zeros(refs[0].shape[1:], jnp.float32)


def _pack_kernel(capacity, adj_ref, owner_ref, col_ref, lev_ref, wx_ref, wy_ref, diff_ref,
                 out_ref, lo_ref, hi_ref, rows_ref, tbuf_ref):
    steps, n_pay, pixels = adj_ref.shape
    devices, width = out_ref.shape
    block = width // (steps * capacity)
    row = lax.broadcasted_iota(jnp.int32, (pixels, pixels), 0)
    lane = lax.broadcasted_iota(jnp.int32, (pixels, pixels), 1)
    dest = lax.broadcasted_iota(jnp.int32, (pixels, devices), 1).astype(jnp.float32)
    tbuf_ref[...] = jnp.zeros(tbuf_ref.shape, jnp.float32)
    for k in range(steps):
        across = jnp.broadcast_to(owner_ref[k:k + 1].astype(jnp.float32), (pixels, pixels))
        down = jnp.transpose(across)
        same = (down == across) & (lane < row)
        rank = jnp.sum(jnp.where(same, 1.0, 0.0), axis=1, keepdims=True)
        owner = down[:, :devices]
        rows_ref[:n_pay] = adj_ref[k]
        rows_ref[n_pay:n_pay + 1] = col_ref[k:k + 1].astype(jnp.float32)
        rows_ref[n_pay + 1:n_pay + 2] = lev_ref[k:k + 1].astype(jnp.float32)
        for j in range(capacity):
            pick = jnp.where((owner == dest) & (rank[:, :1] == j), 1.0, 0.0)
            at = (k * capacity + j) * block
            tbuf_ref[at:at + n_pay + 2] = _exact_dot(
                rows_ref[...], pick.astype(jnp.bfloat16), (((1,), (0,)), ((), ())))
    out_ref[...] = jnp.transpose(tbuf_ref[...])
    statics = (wx_ref, wy_ref, diff_ref)
    tr = wx_ref.shape[1]
    half = tr // 2
    trow = lax.broadcasted_iota(jnp.int32, wx_ref.shape[1:], 0)
    for i in range(lo_ref.shape[0]):
        a = _static_plane(2 * i, statics)
        b = _static_plane(2 * i + 1, statics)
        lo_ref[i] = jnp.where(trow < half, a, pltpu.roll(b, half, 0))
        hi_ref[i] = jnp.where(trow < half, pltpu.roll(a, half, 0), b)


def pack_call(capacity, devices, n_pad, pixel_adjoint, pixel_owner, pixel_column, pixel_level,
              wind_x, wind_y, diffusivity):
    steps, n_pay, pixels = pixel_adjoint.shape
    rows, cols = wind_x.shape[1:]
    block = -(-(n_pay + 2) // 16) * 16
    width = steps * capacity * block
    pairs = jax.ShapeDtypeStruct((n_pad // 2, rows, cols), jnp.float32)
    vmem = pl.BlockSpec(memory_space=pltpu.VMEM)
    return pl.pallas_call(
        functools.partial(_pack_kernel, capacity),
        in_specs=[vmem] * 7,
        out_specs=[vmem] * 3,
        out_shape=[jax.ShapeDtypeStruct((devices, width), jnp.float32), pairs, pairs],
        scratch_shapes=[pltpu.VMEM((n_pay + 2, pixels), jnp.float32),
                        pltpu.VMEM((width, devices), jnp.float32)],
    )(pixel_adjoint, pixel_owner.reshape(steps, pixels), pixel_column, pixel_level, wind_x,
      wind_y, diffusivity)


def _exact_dot(a, b, dims=(((1,), (1,)), ((), ()))):
    hi = a.astype(jnp.bfloat16)
    rest = a - hi.astype(jnp.float32)
    mid = rest.astype(jnp.bfloat16)
    lo = (rest - mid.astype(jnp.float32)).astype(jnp.bfloat16)
    out = lax.dot_general(hi, b, dims, preferred_element_type=jnp.float32)
    out = out + lax.dot_general(mid, b, dims, preferred_element_type=jnp.float32)
    return out + lax.dot_general(lo, b, dims, preferred_element_type=jnp.float32)


def _forcing_kernel(species, kernel, levels, n_statics, own_ref, below_ref, above_ref, wx_ref,
                    wy_ref, diff_ref, sb_ref, sa_ref,
                    tall_ref, right_ref, left_ref, st_xh_ref, lown_ref, lnb_ref, *trans):
    steps = tall_ref.shape[0]
    devices, width = own_ref.shape
    capacity = 2
    block = width // (steps * capacity)
    slots = devices * capacity
    tr2, tc = tall_ref.shape[2:]
    tr = tr2 // 2
    half = tr // 2
    group = tc // half
    n_pay = species * kernel
    lane_t = lax.broadcasted_iota(jnp.int32, (tc, slots), 0)
    row_i = lax.broadcasted_iota(jnp.int32, (tr, slots), 0)
    lev_i = lax.broadcasted_iota(jnp.int32, (levels, slots), 0)
    lane16 = lax.broadcasted_iota(jnp.int32, (tr2, tc), 1)
    right_ref[...] = jnp.zeros(right_ref.shape, jnp.float32)
    left_ref[...] = jnp.zeros(left_ref.shape, jnp.float32)
    for tref, ref in zip(trans, (own_ref, below_ref, above_ref)):
        tref[...] = jnp.transpose(ref[...])
    for k in range(steps):
        hts = []
        for src, tref in enumerate(trans):
            at = k * capacity * block
            blk = jnp.concatenate(
                [tref[at + j * block:at + j * block + n_pay + 2] for j in range(capacity)], axis=1)
            col = blk[n_pay:n_pay + 1].astype(jnp.int32)
            lev = blk[n_pay + 1:n_pay + 2].astype(jnp.int32)
            row_q = col // tc
            lane_q = col % tc
            if src == 1:
                row_q = jnp.where(row_q < half, row_q, -1)
            elif src == 2:
                row_q = jnp.where(row_q >= half, row_q, -1)
            rmask = row_i == row_q
            hts.append((lane_t == lane_q).astype(jnp.bfloat16))
            offset = lev_i - lev
            dst = lown_ref if src == 0 else lnb_ref
            c0 = 0 if src < 2 else slots
            for s in range(species):
                prof = jnp.zeros((levels, slots), jnp.float32)
                for j in range(kernel):
                    prof = prof + jnp.where(offset == j, blk[s * kernel + j:s * kernel + j + 1], 0.0)
                for l in range(levels):
                    c = s * levels + l
                    dst[c * tr:(c + 1) * tr, c0:c0 + slots] = jnp.where(
                        rmask, jnp.broadcast_to(prof[l:l + 1], (tr, slots)), 0.0)
        own = _exact_dot(lown_ref[...], hts[0])
        xh = _exact_dot(lnb_ref[...], jnp.concatenate([hts[1], hts[2]], axis=1))
        planes = own.shape[0] // tr
        tall_ref[k, :, :tr, :] = own.reshape(planes, tr, tc)
        tall_ref[k, :, tr:, :] = xh.reshape(planes, tr, tc)
        for c in range(planes):
            g, q = divmod(k * planes + c, group)
            plane = tall_ref[k, c]
            sel = (lane16 >= half * q) & (lane16 < half * q + half)
            rs = (half * q) % tc
            ls = (half * q + half) % tc
            right_ref[g] = jnp.where(sel, pltpu.roll(plane, rs, 1) if rs else plane, right_ref[g])
            left_ref[g] = jnp.where(sel, pltpu.roll(plane, ls, 1) if ls else plane, left_ref[g])
    statics = (wx_ref, wy_ref, diff_ref)
    trow = lax.broadcasted_iota(jnp.int32, (tr, tc), 0)
    base = steps * species * levels
    for i in range(sb_ref.shape[0]):
        b = sb_ref[i]
        a = sa_ref[i]
        xhs = (jnp.where(trow < half, b, pltpu.roll(a, half, 0)),
               jnp.where(trow < half, pltpu.roll(b, half, 0), a))
        for off in range(2):
            c = 2 * i + off
            st_xh_ref[c] = xhs[off]
            if c >= n_statics:
                continue
            g, q = divmod(base + c, group)
            sel = (lane16 >= half * q) & (lane16 < half * q + half)
            rs = (half * q) % tc
            ls = (half * q + half) % tc
            for part, plane in ((slice(0, tr), _static_plane(c, statics)),
                                (slice(tr, tr2), xhs[off])):
                selp = sel[part]
                right_ref[g, part] = jnp.where(
                    selp, pltpu.roll(plane, rs, 1) if rs else plane, right_ref[g, part])
                left_ref[g, part] = jnp.where(
                    selp, pltpu.roll(plane, ls, 1) if ls else plane, left_ref[g, part])


def forcing_call(species, kernel, levels, n_statics, own, below, above, wind_x, wind_y,
                 diffusivity, st_below, st_above):
    steps = wind_x.shape[0]
    devices, width = own.shape
    slots = 2 * devices
    tr, cols = wind_x.shape[1:]
    planes = species * levels
    group = cols // (tr // 2)
    n_groups = -(-(steps * planes + n_statics) // group)
    packed = jax.ShapeDtypeStruct((n_groups, 2 * tr, cols), jnp.float32)
    vmem = pl.BlockSpec(memory_space=pltpu.VMEM)
    return pl.pallas_call(
        functools.partial(_forcing_kernel, species, kernel, levels, n_statics),
        in_specs=[vmem] * 8,
        out_specs=[vmem] * 4,
        out_shape=[jax.ShapeDtypeStruct((steps, planes, 2 * tr, cols), jnp.float32), packed,
                   packed, jax.ShapeDtypeStruct((2 * st_below.shape[0], tr, cols), jnp.float32)],
        scratch_shapes=[pltpu.VMEM((planes * tr, slots), jnp.float32),
                        pltpu.VMEM((planes * tr, 2 * slots), jnp.float32)]
        + [pltpu.VMEM((width, devices), jnp.float32)] * 3,
    )(own, below, above, wind_x, wind_y, diffusivity, st_below, st_above)


def _steps_kernel(steps, species, levels, n_statics,
                  right_ref, left_ref, wx_ref, wy_ref, diff_ref, st_xh, mask_ref, prior_ref,
                  tall_hbm, adj_ref, ss_ref,
                  tall_buf, yh_buf, se_ref, state_ref, red_ref, ratio_ref, inv_ref, sems):
    planes = species * levels
    rows, lanes = mask_ref.shape
    tr, tc = adj_ref.shape[2:]
    half = tr // 2
    group = tc // half
    d0 = 2 * steps

    loads = {}
    for k in reversed(range(steps)):
        copy = pltpu.make_async_copy(tall_hbm.at[k], tall_buf.at[k], sems.at[k])
        copy.start()
        loads[k] = copy

    n_fgroups = steps * planes // group

    def unpack_group(g, carry):
        r = right_ref[g]
        l = left_ref[g]
        for q in range(group):
            yh_buf[g * group + q] = _unpack(r, l, q, tc, half)
        return carry

    lax.fori_loop(0, n_fgroups, unpack_group, 0)
    for c in range(n_statics):
        g, q = divmod(n_fgroups * group + c, group)
        se_ref[c, :, tc:] = _unpack(right_ref[g], left_ref[g], q, tc, half)

    for c in range(n_statics):
        se_ref[c, :tr, :tc] = _static_plane(c, (wx_ref, wy_ref, diff_ref))
        se_ref[c, tr:, :tc] = st_xh[c]

    zero = jnp.zeros((rows, lanes), jnp.float32)
    inside = mask_ref[...] > 0.5
    carried = zero
    for l in range(levels):
        below = se_ref[d0 + l - 1] if l > 0 else zero
        above = se_ref[d0 + l] if l < levels - 1 else zero
        inverse = 1.0 / (1.0 + below + above + below * carried)
        ratio = -above * inverse
        ratio_ref[l] = ratio
        inv_ref[l] = inverse
        carried = ratio

    for k in reversed(range(steps)):
        first = k == steps - 1
        last = k == 0
        if first:
            loads[k].wait()
            for s in range(species):

                def assemble(l, carry, s=s, k=k):
                    c = s * levels + l
                    state_ref[s, l, :, :tc] = tall_buf[k, c]
                    state_ref[s, l, :, tc:] = yh_buf[k * planes + c]
                    state_ref[s, l] = jnp.where(inside, state_ref[s, l], 0.0)
                    return carry

                lax.fori_loop(0, levels, assemble, 0, unroll=4)
        if not last:
            loads[k - 1].wait()

        wx = se_ref[k]
        wy = se_ref[steps + k]
        east = jnp.maximum(wx, 0.0)
        west = jnp.maximum(-wx, 0.0)
        north = jnp.maximum(wy, 0.0)
        south = jnp.maximum(-wy, 0.0)
        remain = 1.0 - (east + west + north + south)
        if last:
            _last_step(species, levels, tr, tc, state_ref, east, west, north, south, remain,
                       se_ref, d0, inv_ref, ratio_ref, red_ref, adj_ref, ss_ref, prior_ref)
            continue

        def forward(l, reduced):
            below = jnp.where(l > 0, se_ref[d0 + jnp.maximum(l - 1, 0)], zero)
            inverse = inv_ref[l]
            out = []
            for s in range(species):
                f = state_ref[s, l]
                from_east = pltpu.roll(east * f, rows - 1, 0)
                from_west = pltpu.roll(west * f, 1, 0)
                from_north = pltpu.roll(north * f, lanes - 1, 1)
                from_south = pltpu.roll(south * f, 1, 1)
                moved = f * remain
                moved = moved + from_east + from_west
                moved = moved + from_north + from_south
                r = (moved + below * reduced[s]) * inverse
                red_ref[s, l] = r
                out.append(r)
            return tuple(out)

        lax.fori_loop(0, levels, forward, (zero,) * species, unroll=True)

        def backward(i, result, k=k):
            l = levels - 1 - i
            ratio = ratio_ref[l]
            out = []
            for s in range(species):
                c = s * levels + l
                r = red_ref[s, l] - ratio * result[s]
                state_ref[s, l, :, :tc] = jnp.where(
                    inside[:, :tc], r[:, :tc] + tall_buf[k - 1, c], 0.0)
                state_ref[s, l, :, tc:] = jnp.where(
                    inside[:, tc:], r[:, tc:] + yh_buf[(k - 1) * planes + c], 0.0)
                out.append(r)
            return tuple(out)

        surface = lax.fori_loop(0, levels, backward, (zero,) * species, unroll=True)
        for s in range(species):
            if first:
                ss_ref[s] = prior_ref[s] * surface[s][:tr, :tc]
            else:
                ss_ref[s] = ss_ref[s] + prior_ref[s] * surface[s][:tr, :tc]


def _last_step(species, levels, tr, tc, forced_ref, east, west, north, south, remain, se_ref,
               d0, inv_ref, ratio_ref, red_ref, out_ref, ss_ref, prior_ref):
    row = lax.broadcasted_iota(jnp.int32, (tr, tc), 0)
    lane = lax.broadcasted_iota(jnp.int32, (tr, tc), 1)
    last_row = row == tr - 1
    first_row = row == 0
    last_lane = lane == tc - 1
    first_lane = lane == 0
    e_a, e_b = east[:tr, :tc], east[tr:, :tc]
    w_a, w_b = west[:tr, :tc], west[tr:, :tc]
    n_a, n_c = north[:tr, :tc], north[:tr, tc:]
    s_a, s_c = south[:tr, :tc], south[:tr, tc:]
    rem = remain[:tr, :tc]
    zero = jnp.zeros((tr, tc), jnp.float32)
    def forward(l, reduced):
        below = jnp.where(l > 0, se_ref[d0 + jnp.maximum(l - 1, 0), :tr, :tc], zero)
        inverse = inv_ref[l, :tr, :tc]
        out = []
        for s in range(species):
            f_a = forced_ref[s, l, :tr, :tc]
            f_b = forced_ref[s, l, tr:, :tc]
            f_c = forced_ref[s, l, :tr, tc:]
            from_east = jnp.where(last_row, pltpu.roll(e_b * f_b, tr - 1, 0),
                                  pltpu.roll(e_a * f_a, tr - 1, 0))
            from_west = jnp.where(first_row, pltpu.roll(w_b * f_b, 1, 0),
                                  pltpu.roll(w_a * f_a, 1, 0))
            from_north = jnp.where(last_lane, pltpu.roll(n_c * f_c, tc - 1, 1),
                                   pltpu.roll(n_a * f_a, tc - 1, 1))
            from_south = jnp.where(first_lane, pltpu.roll(s_c * f_c, 1, 1),
                                   pltpu.roll(s_a * f_a, 1, 1))
            moved = f_a * rem
            moved = moved + from_east + from_west
            moved = moved + from_north + from_south
            r = (moved + below * reduced[s]) * inverse
            red_ref[s, l, :tr, :tc] = r
            out.append(r)
        return tuple(out)

    lax.fori_loop(0, levels, forward, (zero,) * species, unroll=4)

    def backward(i, result):
        l = levels - 1 - i
        ratio = ratio_ref[l, :tr, :tc]
        out = []
        for s in range(species):
            r = red_ref[s, l, :tr, :tc] - ratio * result[s]
            out_ref[s, l] = r
            out.append(r)
        return tuple(out)

    surface = lax.fori_loop(0, levels, backward, (zero,) * species, unroll=4)
    for s in range(species):
        ss_ref[s] = ss_ref[s] + prior_ref[s] * surface[s]


def steps_call(steps, species, levels, n_statics, right, left, wind_x, wind_y, diffusivity,
               st_xh, mask, prior, tall):
    _, planes, rows, tc = tall.shape
    tr = rows // 2
    lanes = mask.shape[1]
    vmem = pl.BlockSpec(memory_space=pltpu.VMEM)
    anyspace = pl.BlockSpec(memory_space=pl.ANY)
    return pl.pallas_call(
        functools.partial(_steps_kernel, steps, species, levels, n_statics),
        in_specs=[vmem] * 8 + [anyspace],
        out_specs=[vmem, vmem],
        out_shape=[jax.ShapeDtypeStruct((species, levels, tr, tc), jnp.float32),
                   jax.ShapeDtypeStruct(prior.shape, jnp.float32)],
        scratch_shapes=[
            pltpu.VMEM((steps, planes, rows, tc), jnp.float32),
            pltpu.VMEM((steps * planes, rows, tc), jnp.float32),
            pltpu.VMEM((n_statics, rows, lanes), jnp.float32),
            pltpu.VMEM((species, levels, rows, lanes), jnp.float32),
            pltpu.VMEM((species, levels, rows, lanes), jnp.float32),
            pltpu.VMEM((levels, rows, lanes), jnp.float32),
            pltpu.VMEM((levels, rows, lanes), jnp.float32),
            pltpu.SemaphoreType.DMA((steps,)),
        ],
        compiler_params=pltpu.CompilerParams(vmem_limit_bytes=48 * 1024 * 1024),
    )(right, left, wind_x, wind_y, diffusivity, st_xh, mask, prior, tall)


def _pairs(axis):
    n = lax.axis_size(axis)
    return [(i, i + 1) for i in range(n - 1)], [(i + 1, i) for i in range(n - 1)]


def local(pixel_adjoint, pixel_owner, pixel_column, pixel_level, wind_x, wind_y,
          diffusivity, prior_emission, region_map):
    gx_n = lax.axis_size("gx")
    gy_n = lax.axis_size("gy")
    devices = gx_n * gy_n
    steps, rows, cols = wind_x.shape
    levels = diffusivity.shape[0] + 1
    species = prior_emission.shape[0]
    kernel = pixel_adjoint.shape[1] // species
    pixels = pixel_adjoint.shape[2]
    capacity = 2 * pixels // devices
    cells = rows * cols
    slots = devices * capacity
    halo = rows // 2
    assert steps <= halo
    lanes = 2 * cols
    ext_rows = 2 * rows

    n_s = 2 * steps + levels - 1
    group = cols // halo
    n_pad = -(-n_s // group) * group
    placed, st_lo, st_hi = pack_call(capacity, devices, n_pad, pixel_adjoint, pixel_owner,
                                     pixel_column, pixel_level, wind_x, wind_y, diffusivity)
    up_x, down_x = _pairs("gx")
    up_y, down_y = _pairs("gy")
    st_below = lax.ppermute(st_lo, "gx", down_x)
    st_above = lax.ppermute(st_hi, "gx", up_x)
    received = lax.all_to_all(placed, ("gx", "gy"), 0, 0, tiled=True)

    below = lax.ppermute(received, "gx", down_x)
    above = lax.ppermute(received, "gx", up_x)
    tall, right, left, st_xh = forcing_call(species, kernel, levels, n_s, received, below, above,
                                            wind_x, wind_y, diffusivity, st_below, st_above)
    right = lax.ppermute(right, "gy", down_y)
    left = lax.ppermute(left, "gy", up_y)

    gxi = lax.axis_index("gx")
    gyi = lax.axis_index("gy")
    r = jnp.arange(ext_rows, dtype=jnp.int32)[:, None]
    c = jnp.arange(lanes, dtype=jnp.int32)[None, :]
    grow = gxi * rows + jnp.where(r < rows + halo, r, r - ext_rows)
    ccol = jnp.where(c < cols + halo, c, c - lanes)
    gcol = gyi * cols + ccol
    inside = ((grow >= 0) & (grow < gx_n * rows) & (gcol >= 0) & (gcol < gy_n * cols)
              & ((c < cols + halo) | (c >= lanes - halo)))
    mask = inside.astype(jnp.float32)

    adjoint, surface_sum = steps_call(steps, species, levels, n_s, right, left, wind_x, wind_y,
                                      diffusivity, st_xh, mask, prior_emission, tall)

    nreg = REG_DEV * devices
    blocks = surface_sum.reshape(species, rows // 2, 2, cols // 4, 4).sum(axis=(2, 4))
    block_region = region_map[::2, ::4].reshape(-1)
    member = (block_region[:, None] == jnp.arange(nreg, dtype=jnp.int32)).astype(jnp.float32)
    partial = jnp.dot(blocks.reshape(species, -1), member, precision=HI)
    pieces = lax.all_to_all(partial.reshape(species, devices, nreg // devices), ("gx", "gy"), 1, 1,
                            tiled=True)
    gradient = jnp.sum(pieces, axis=1)
    return adjoint, gradient


def solution(mesh):
    in_specs = (
        P(None, None, ("gx", "gy")),
        P(None, ("gx", "gy"), None),
        P(None, ("gx", "gy")),
        P(None, ("gx", "gy")),
        P(None, "gx", "gy"),
        P(None, "gx", "gy"),
        P(None, "gx", "gy"),
        P(None, "gx", "gy"),
        P("gx", "gy"),
    )
    out_specs = (P(None, None, "gx", "gy"), P(None, ("gx", "gy")))
    return jax.shard_map(local, mesh=mesh, in_specs=in_specs, out_specs=out_specs, check_vma=False)
```

```python
import functools

import jax
import jax.numpy as jnp
from jax import lax
from jax.experimental import pallas as pl
from jax.experimental.pallas import tpu as pltpu
from jax.sharding import PartitionSpec as P

HI = lax.Precision.HIGHEST
REG_DEV = 8


def _full(shape):
    nd = len(shape)
    return pl.BlockSpec(shape, lambda i, _n=nd: (0,) * _n)


def _unpack(r, l, q, cols, half):
    lane = lax.broadcasted_iota(jnp.int32, r.shape, 1)
    rs = (cols - half * q) % cols
    ls = (cols - half - half * q) % cols
    return jnp.where(lane < half, pltpu.roll(r, rs, 1) if rs else r,
                     jnp.where(lane >= cols - half, pltpu.roll(l, ls, 1) if ls else l, 0.0))


def _static_plane(c, refs):
    for ref in refs:
        if c < ref.shape[0]:
            return ref[c]
        c -= ref.shape[0]
    return jnp.zeros(refs[0].shape[1:], jnp.float32)


def _pack_kernel(capacity, adj_ref, owner_ref, col_ref, lev_ref, wx_ref, wy_ref, diff_ref,
                 out_ref, lo_ref, hi_ref, rows_ref, tbuf_ref):
    steps, n_pay, pixels = adj_ref.shape
    devices, width = out_ref.shape
    block = width // (steps * capacity)
    row = lax.broadcasted_iota(jnp.int32, (pixels, pixels), 0)
    lane = lax.broadcasted_iota(jnp.int32, (pixels, pixels), 1)
    dest = lax.broadcasted_iota(jnp.int32, (pixels, devices), 1).astype(jnp.float32)
    tbuf_ref[...] = jnp.zeros(tbuf_ref.shape, jnp.float32)
    for k in range(steps):
        across = jnp.broadcast_to(owner_ref[k:k + 1].astype(jnp.float32), (pixels, pixels))
        down = jnp.transpose(across)
        same = (down == across) & (lane < row)
        rank = jnp.sum(jnp.where(same, 1.0, 0.0), axis=1, keepdims=True)
        owner = down[:, :devices]
        rows_ref[:n_pay] = adj_ref[k]
        rows_ref[n_pay:n_pay + 1] = col_ref[k:k + 1].astype(jnp.float32)
        rows_ref[n_pay + 1:n_pay + 2] = lev_ref[k:k + 1].astype(jnp.float32)
        for j in range(capacity):
            pick = jnp.where((owner == dest) & (rank[:, :1] == j), 1.0, 0.0)
            at = (k * capacity + j) * block
            tbuf_ref[at:at + n_pay + 2] = _exact_dot(
                rows_ref[...], pick.astype(jnp.bfloat16), (((1,), (0,)), ((), ())))
    out_ref[...] = jnp.transpose(tbuf_ref[...])
    statics = (wx_ref, wy_ref, diff_ref)
    tr = wx_ref.shape[1]
    half = tr // 2
    trow = lax.broadcasted_iota(jnp.int32, wx_ref.shape[1:], 0)
    for i in range(lo_ref.shape[0]):
        a = _static_plane(2 * i, statics)
        b = _static_plane(2 * i + 1, statics)
        lo_ref[i] = jnp.where(trow < half, a, pltpu.roll(b, half, 0))
        hi_ref[i] = jnp.where(trow < half, pltpu.roll(a, half, 0), b)


def pack_call(capacity, devices, n_pad, pixel_adjoint, pixel_owner, pixel_column, pixel_level,
              wind_x, wind_y, diffusivity):
    steps, n_pay, pixels = pixel_adjoint.shape
    rows, cols = wind_x.shape[1:]
    block = -(-(n_pay + 2) // 16) * 16
    width = steps * capacity * block
    pairs = jax.ShapeDtypeStruct((n_pad // 2, rows, cols), jnp.float32)
    vmem = pl.BlockSpec(memory_space=pltpu.VMEM)
    return pl.pallas_call(
        functools.partial(_pack_kernel, capacity),
        in_specs=[vmem] * 7,
        out_specs=[vmem] * 3,
        out_shape=[jax.ShapeDtypeStruct((devices, width), jnp.float32), pairs, pairs],
        scratch_shapes=[pltpu.VMEM((n_pay + 2, pixels), jnp.float32),
                        pltpu.VMEM((width, devices), jnp.float32)],
    )(pixel_adjoint, pixel_owner.reshape(steps, pixels), pixel_column, pixel_level, wind_x,
      wind_y, diffusivity)


def _exact_dot(a, b, dims=(((1,), (1,)), ((), ()))):
    hi = a.astype(jnp.bfloat16)
    rest = a - hi.astype(jnp.float32)
    mid = rest.astype(jnp.bfloat16)
    lo = (rest - mid.astype(jnp.float32)).astype(jnp.bfloat16)
    out = lax.dot_general(hi, b, dims, preferred_element_type=jnp.float32)
    out = out + lax.dot_general(mid, b, dims, preferred_element_type=jnp.float32)
    return out + lax.dot_general(lo, b, dims, preferred_element_type=jnp.float32)


def _forcing_kernel(species, kernel, levels, n_statics, own_ref, below_ref, above_ref, wx_ref,
                    wy_ref, diff_ref, sb_ref, sa_ref,
                    tall_ref, right_ref, left_ref, st_xh_ref, lown_ref, lnb_ref, *trans):
    steps = tall_ref.shape[0]
    devices, width = own_ref.shape
    capacity = 2
    block = width // (steps * capacity)
    slots = devices * capacity
    tr2, tc = tall_ref.shape[2:]
    tr = tr2 // 2
    half = tr // 2
    group = tc // half
    n_pay = species * kernel
    lane_t = lax.broadcasted_iota(jnp.int32, (tc, slots), 0)
    row_i = lax.broadcasted_iota(jnp.int32, (tr, slots), 0)
    lev_i = lax.broadcasted_iota(jnp.int32, (levels, slots), 0)
    lane16 = lax.broadcasted_iota(jnp.int32, (tr2, tc), 1)
    right_ref[...] = jnp.zeros(right_ref.shape, jnp.float32)
    left_ref[...] = jnp.zeros(left_ref.shape, jnp.float32)
    for tref, ref in zip(trans, (own_ref, below_ref, above_ref)):
        tref[...] = jnp.transpose(ref[...])
    for k in range(steps):
        hts = []
        for src, tref in enumerate(trans):
            at = k * capacity * block
            blk = jnp.concatenate(
                [tref[at + j * block:at + j * block + n_pay + 2] for j in range(capacity)], axis=1)
            col = blk[n_pay:n_pay + 1].astype(jnp.int32)
            lev = blk[n_pay + 1:n_pay + 2].astype(jnp.int32)
            row_q = col // tc
            lane_q = col % tc
            if src == 1:
                row_q = jnp.where(row_q < half, row_q, -1)
            elif src == 2:
                row_q = jnp.where(row_q >= half, row_q, -1)
            rmask = row_i == row_q
            hts.append((lane_t == lane_q).astype(jnp.bfloat16))
            offset = lev_i - lev
            dst = lown_ref if src == 0 else lnb_ref
            c0 = 0 if src < 2 else slots
            for s in range(species):
                prof = jnp.zeros((levels, slots), jnp.float32)
                for j in range(kernel):
                    prof = prof + jnp.where(offset == j, blk[s * kernel + j:s * kernel + j + 1], 0.0)
                for l in range(levels):
                    c = s * levels + l
                    dst[c * tr:(c + 1) * tr, c0:c0 + slots] = jnp.where(
                        rmask, jnp.broadcast_to(prof[l:l + 1], (tr, slots)), 0.0)
        own = _exact_dot(lown_ref[...], hts[0])
        xh = _exact_dot(lnb_ref[...], jnp.concatenate([hts[1], hts[2]], axis=1))
        planes = own.shape[0] // tr
        tall_ref[k, :, :tr, :] = own.reshape(planes, tr, tc)
        tall_ref[k, :, tr:, :] = xh.reshape(planes, tr, tc)
        for c in range(planes):
            g, q = divmod(k * planes + c, group)
            plane = tall_ref[k, c]
            sel = (lane16 >= half * q) & (lane16 < half * q + half)
            rs = (half * q) % tc
            ls = (half * q + half) % tc
            right_ref[g] = jnp.where(sel, pltpu.roll(plane, rs, 1) if rs else plane, right_ref[g])
            left_ref[g] = jnp.where(sel, pltpu.roll(plane, ls, 1) if ls else plane, left_ref[g])
    statics = (wx_ref, wy_ref, diff_ref)
    trow = lax.broadcasted_iota(jnp.int32, (tr, tc), 0)
    base = steps * species * levels
    for i in range(sb_ref.shape[0]):
        b = sb_ref[i]
        a = sa_ref[i]
        xhs = (jnp.where(trow < half, b, pltpu.roll(a, half, 0)),
               jnp.where(trow < half, pltpu.roll(b, half, 0), a))
        for off in range(2):
            c = 2 * i + off
            st_xh_ref[c] = xhs[off]
            if c >= n_statics:
                continue
            g, q = divmod(base + c, group)
            sel = (lane16 >= half * q) & (lane16 < half * q + half)
            rs = (half * q) % tc
            ls = (half * q + half) % tc
            for part, plane in ((slice(0, tr), _static_plane(c, statics)),
                                (slice(tr, tr2), xhs[off])):
                selp = sel[part]
                right_ref[g, part] = jnp.where(
                    selp, pltpu.roll(plane, rs, 1) if rs else plane, right_ref[g, part])
                left_ref[g, part] = jnp.where(
                    selp, pltpu.roll(plane, ls, 1) if ls else plane, left_ref[g, part])


def forcing_call(species, kernel, levels, n_statics, own, below, above, wind_x, wind_y,
                 diffusivity, st_below, st_above):
    steps = wind_x.shape[0]
    devices, width = own.shape
    slots = 2 * devices
    tr, cols = wind_x.shape[1:]
    planes = species * levels
    group = cols // (tr // 2)
    n_groups = -(-(steps * planes + n_statics) // group)
    packed = jax.ShapeDtypeStruct((n_groups, 2 * tr, cols), jnp.float32)
    vmem = pl.BlockSpec(memory_space=pltpu.VMEM)
    return pl.pallas_call(
        functools.partial(_forcing_kernel, species, kernel, levels, n_statics),
        in_specs=[vmem] * 8,
        out_specs=[vmem] * 4,
        out_shape=[jax.ShapeDtypeStruct((steps, planes, 2 * tr, cols), jnp.float32), packed,
                   packed, jax.ShapeDtypeStruct((2 * st_below.shape[0], tr, cols), jnp.float32)],
        scratch_shapes=[pltpu.VMEM((planes * tr, slots), jnp.float32),
                        pltpu.VMEM((planes * tr, 2 * slots), jnp.float32)]
        + [pltpu.VMEM((width, devices), jnp.float32)] * 3,
    )(own, below, above, wind_x, wind_y, diffusivity, st_below, st_above)


def _steps_kernel(steps, species, levels, n_statics,
                  right_ref, left_ref, wx_ref, wy_ref, diff_ref, st_xh, mask_ref, prior_ref,
                  tall_hbm, adj_ref, ss_ref,
                  tall_buf, yh_buf, se_ref, state_ref, red_ref, ratio_ref, inv_ref, sems):
    planes = species * levels
    rows, lanes = mask_ref.shape
    tr, tc = adj_ref.shape[2:]
    half = tr // 2
    group = tc // half
    d0 = 2 * steps

    loads = {}
    for k in reversed(range(steps)):
        copy = pltpu.make_async_copy(tall_hbm.at[k], tall_buf.at[k], sems.at[k])
        copy.start()
        loads[k] = copy

    n_fgroups = steps * planes // group

    def unpack_group(g, carry):
        r = right_ref[g]
        l = left_ref[g]
        for q in range(group):
            yh_buf[g * group + q] = _unpack(r, l, q, tc, half)
        return carry

    lax.fori_loop(0, n_fgroups, unpack_group, 0)
    for c in range(n_statics):
        g, q = divmod(n_fgroups * group + c, group)
        se_ref[c, :, tc:] = _unpack(right_ref[g], left_ref[g], q, tc, half)

    for c in range(n_statics):
        se_ref[c, :tr, :tc] = _static_plane(c, (wx_ref, wy_ref, diff_ref))
        se_ref[c, tr:, :tc] = st_xh[c]

    zero = jnp.zeros((rows, lanes), jnp.float32)
    inside = mask_ref[...] > 0.5
    carried = zero
    for l in range(levels):
        below = se_ref[d0 + l - 1] if l > 0 else zero
        above = se_ref[d0 + l] if l < levels - 1 else zero
        inverse = 1.0 / (1.0 + below + above + below * carried)
        ratio = -above * inverse
        ratio_ref[l] = ratio
        inv_ref[l] = inverse
        carried = ratio

    for k in reversed(range(steps)):
        first = k == steps - 1
        last = k == 0
        if first:
            loads[k].wait()
            for s in range(species):

                def assemble(l, carry, s=s, k=k):
                    c = s * levels + l
                    state_ref[s, l, :, :tc] = tall_buf[k, c]
                    state_ref[s, l, :, tc:] = yh_buf[k * planes + c]
                    state_ref[s, l] = jnp.where(inside, state_ref[s, l], 0.0)
                    return carry

                lax.fori_loop(0, levels, assemble, 0, unroll=4)
        if not last:
            loads[k - 1].wait()

        wx = se_ref[k]
        wy = se_ref[steps + k]
        east = jnp.maximum(wx, 0.0)
        west = jnp.maximum(-wx, 0.0)
        north = jnp.maximum(wy, 0.0)
        south = jnp.maximum(-wy, 0.0)
        remain = 1.0 - (east + west + north + south)
        if last:
            _last_step(species, levels, tr, tc, state_ref, east, west, north, south, remain,
                       se_ref, d0, inv_ref, ratio_ref, red_ref, adj_ref, ss_ref, prior_ref)
            continue

        def forward(l, reduced):
            below = jnp.where(l > 0, se_ref[d0 + jnp.maximum(l - 1, 0)], zero)
            inverse = inv_ref[l]
            out = []
            for s in range(species):
                f = state_ref[s, l]
                from_east = pltpu.roll(east * f, rows - 1, 0)
                from_west = pltpu.roll(west * f, 1, 0)
                from_north = pltpu.roll(north * f, lanes - 1, 1)
                from_south = pltpu.roll(south * f, 1, 1)
                moved = f * remain
                moved = moved + from_east + from_west
                moved = moved + from_north + from_south
                r = (moved + below * reduced[s]) * inverse
                red_ref[s, l] = r
                out.append(r)
            return tuple(out)

        lax.fori_loop(0, levels, forward, (zero,) * species, unroll=True)

        def backward(i, result, k=k):
            l = levels - 1 - i
            ratio = ratio_ref[l]
            out = []
            for s in range(species):
                c = s * levels + l
                r = red_ref[s, l] - ratio * result[s]
                state_ref[s, l, :, :tc] = jnp.where(
                    inside[:, :tc], r[:, :tc] + tall_buf[k - 1, c], 0.0)
                state_ref[s, l, :, tc:] = jnp.where(
                    inside[:, tc:], r[:, tc:] + yh_buf[(k - 1) * planes + c], 0.0)
                out.append(r)
            return tuple(out)

        surface = lax.fori_loop(0, levels, backward, (zero,) * species, unroll=True)
        for s in range(species):
            if first:
                ss_ref[s] = prior_ref[s] * surface[s][:tr, :tc]
            else:
                ss_ref[s] = ss_ref[s] + prior_ref[s] * surface[s][:tr, :tc]


def _last_step(species, levels, tr, tc, forced_ref, east, west, north, south, remain, se_ref,
               d0, inv_ref, ratio_ref, red_ref, out_ref, ss_ref, prior_ref):
    row = lax.broadcasted_iota(jnp.int32, (tr, tc), 0)
    lane = lax.broadcasted_iota(jnp.int32, (tr, tc), 1)
    last_row = row == tr - 1
    first_row = row == 0
    last_lane = lane == tc - 1
    first_lane = lane == 0
    e_a, e_b = east[:tr, :tc], east[tr:, :tc]
    w_a, w_b = west[:tr, :tc], west[tr:, :tc]
    n_a, n_c = north[:tr, :tc], north[:tr, tc:]
    s_a, s_c = south[:tr, :tc], south[:tr, tc:]
    rem = remain[:tr, :tc]
    zero = jnp.zeros((tr, tc), jnp.float32)
    def forward(l, reduced):
        below = jnp.where(l > 0, se_ref[d0 + jnp.maximum(l - 1, 0), :tr, :tc], zero)
        inverse = inv_ref[l, :tr, :tc]
        out = []
        for s in range(species):
            f_a = forced_ref[s, l, :tr, :tc]
            f_b = forced_ref[s, l, tr:, :tc]
            f_c = forced_ref[s, l, :tr, tc:]
            from_east = jnp.where(last_row, pltpu.roll(e_b * f_b, tr - 1, 0),
                                  pltpu.roll(e_a * f_a, tr - 1, 0))
            from_west = jnp.where(first_row, pltpu.roll(w_b * f_b, 1, 0),
                                  pltpu.roll(w_a * f_a, 1, 0))
            from_north = jnp.where(last_lane, pltpu.roll(n_c * f_c, tc - 1, 1),
                                   pltpu.roll(n_a * f_a, tc - 1, 1))
            from_south = jnp.where(first_lane, pltpu.roll(s_c * f_c, 1, 1),
                                   pltpu.roll(s_a * f_a, 1, 1))
            moved = f_a * rem
            moved = moved + from_east + from_west
            moved = moved + from_north + from_south
            r = (moved + below * reduced[s]) * inverse
            red_ref[s, l, :tr, :tc] = r
            out.append(r)
        return tuple(out)

    lax.fori_loop(0, levels, forward, (zero,) * species, unroll=True)

    def backward(i, result):
        l = levels - 1 - i
        ratio = ratio_ref[l, :tr, :tc]
        out = []
        for s in range(species):
            r = red_ref[s, l, :tr, :tc] - ratio * result[s]
            out_ref[s, l] = r
            out.append(r)
        return tuple(out)

    surface = lax.fori_loop(0, levels, backward, (zero,) * species, unroll=True)
    for s in range(species):
        ss_ref[s] = ss_ref[s] + prior_ref[s] * surface[s]


def steps_call(steps, species, levels, n_statics, right, left, wind_x, wind_y, diffusivity,
               st_xh, mask, prior, tall):
    _, planes, rows, tc = tall.shape
    tr = rows // 2
    lanes = mask.shape[1]
    vmem = pl.BlockSpec(memory_space=pltpu.VMEM)
    anyspace = pl.BlockSpec(memory_space=pl.ANY)
    return pl.pallas_call(
        functools.partial(_steps_kernel, steps, species, levels, n_statics),
        in_specs=[vmem] * 8 + [anyspace],
        out_specs=[vmem, vmem],
        out_shape=[jax.ShapeDtypeStruct((species, levels, tr, tc), jnp.float32),
                   jax.ShapeDtypeStruct(prior.shape, jnp.float32)],
        scratch_shapes=[
            pltpu.VMEM((steps, planes, rows, tc), jnp.float32),
            pltpu.VMEM((steps * planes, rows, tc), jnp.float32),
            pltpu.VMEM((n_statics, rows, lanes), jnp.float32),
            pltpu.VMEM((species, levels, rows, lanes), jnp.float32),
            pltpu.VMEM((species, levels, rows, lanes), jnp.float32),
            pltpu.VMEM((levels, rows, lanes), jnp.float32),
            pltpu.VMEM((levels, rows, lanes), jnp.float32),
            pltpu.SemaphoreType.DMA((steps,)),
        ],
        compiler_params=pltpu.CompilerParams(vmem_limit_bytes=48 * 1024 * 1024),
    )(right, left, wind_x, wind_y, diffusivity, st_xh, mask, prior, tall)


def _pairs(axis):
    n = lax.axis_size(axis)
    return [(i, i + 1) for i in range(n - 1)], [(i + 1, i) for i in range(n - 1)]


def local(pixel_adjoint, pixel_owner, pixel_column, pixel_level, wind_x, wind_y,
          diffusivity, prior_emission, region_map):
    gx_n = lax.axis_size("gx")
    gy_n = lax.axis_size("gy")
    devices = gx_n * gy_n
    steps, rows, cols = wind_x.shape
    levels = diffusivity.shape[0] + 1
    species = prior_emission.shape[0]
    kernel = pixel_adjoint.shape[1] // species
    pixels = pixel_adjoint.shape[2]
    capacity = 2 * pixels // devices
    cells = rows * cols
    slots = devices * capacity
    halo = rows // 2
    assert steps <= halo
    lanes = 2 * cols
    ext_rows = 2 * rows

    n_s = 2 * steps + levels - 1
    group = cols // halo
    n_pad = -(-n_s // group) * group
    placed, st_lo, st_hi = pack_call(capacity, devices, n_pad, pixel_adjoint, pixel_owner,
                                     pixel_column, pixel_level, wind_x, wind_y, diffusivity)
    up_x, down_x = _pairs("gx")
    up_y, down_y = _pairs("gy")
    st_below = lax.ppermute(st_lo, "gx", down_x)
    st_above = lax.ppermute(st_hi, "gx", up_x)
    received = lax.all_to_all(placed, ("gx", "gy"), 0, 0, tiled=True)

    below = lax.ppermute(received, "gx", down_x)
    above = lax.ppermute(received, "gx", up_x)
    tall, right, left, st_xh = forcing_call(species, kernel, levels, n_s, received, below, above,
                                            wind_x, wind_y, diffusivity, st_below, st_above)
    right = lax.ppermute(right, "gy", down_y)
    left = lax.ppermute(left, "gy", up_y)

    gxi = lax.axis_index("gx")
    gyi = lax.axis_index("gy")
    r = jnp.arange(ext_rows, dtype=jnp.int32)[:, None]
    c = jnp.arange(lanes, dtype=jnp.int32)[None, :]
    grow = gxi * rows + jnp.where(r < rows + halo, r, r - ext_rows)
    ccol = jnp.where(c < cols + halo, c, c - lanes)
    gcol = gyi * cols + ccol
    inside = ((grow >= 0) & (grow < gx_n * rows) & (gcol >= 0) & (gcol < gy_n * cols)
              & ((c < cols + halo) | (c >= lanes - halo)))
    mask = inside.astype(jnp.float32)

    adjoint, surface_sum = steps_call(steps, species, levels, n_s, right, left, wind_x, wind_y,
                                      diffusivity, st_xh, mask, prior_emission, tall)

    nreg = REG_DEV * devices
    blocks = surface_sum.reshape(species, rows // 2, 2, cols // 4, 4).sum(axis=(2, 4))
    block_region = region_map[::2, ::4].reshape(-1)
    member = (block_region[:, None] == jnp.arange(nreg, dtype=jnp.int32)).astype(jnp.float32)
    partial = jnp.dot(blocks.reshape(species, -1), member, precision=HI)
    pieces = lax.all_to_all(partial.reshape(species, devices, nreg // devices), ("gx", "gy"), 1, 1,
                            tiled=True)
    gradient = jnp.sum(pieces, axis=1)
    return adjoint, gradient


def solution(mesh):
    in_specs = (
        P(None, None, ("gx", "gy")),
        P(None, ("gx", "gy"), None),
        P(None, ("gx", "gy")),
        P(None, ("gx", "gy")),
        P(None, "gx", "gy"),
        P(None, "gx", "gy"),
        P(None, "gx", "gy"),
        P(None, "gx", "gy"),
        P("gx", "gy"),
    )
    out_specs = (P(None, None, "gx", "gy"), P(None, ("gx", "gy")))
    return jax.shard_map(local, mesh=mesh, in_specs=in_specs, out_specs=out_specs, check_vma=False)
```

```python
import functools

import jax
import jax.numpy as jnp
from jax import lax
from jax.experimental import pallas as pl
from jax.experimental.pallas import tpu as pltpu
from jax.sharding import PartitionSpec as P

HI = lax.Precision.HIGHEST
REG_DEV = 8


def _full(shape):
    nd = len(shape)
    return pl.BlockSpec(shape, lambda i, _n=nd: (0,) * _n)


def _unpack(r, l, q, cols, half):
    lane = lax.broadcasted_iota(jnp.int32, r.shape, 1)
    rs = (cols - half * q) % cols
    ls = (cols - half - half * q) % cols
    return jnp.where(lane < half, pltpu.roll(r, rs, 1) if rs else r,
                     jnp.where(lane >= cols - half, pltpu.roll(l, ls, 1) if ls else l, 0.0))


def _static_plane(c, refs):
    for ref in refs:
        if c < ref.shape[0]:
            return ref[c]
        c -= ref.shape[0]
    return jnp.zeros(refs[0].shape[1:], jnp.float32)


def _pack_kernel(capacity, adj_ref, owner_ref, col_ref, lev_ref, wx_ref, wy_ref, diff_ref,
                 out_ref, lo_ref, hi_ref, rows_ref, tbuf_ref):
    steps, n_pay, pixels = adj_ref.shape
    devices, width = out_ref.shape
    block = width // (steps * capacity)
    row = lax.broadcasted_iota(jnp.int32, (pixels, pixels), 0)
    lane = lax.broadcasted_iota(jnp.int32, (pixels, pixels), 1)
    dest = lax.broadcasted_iota(jnp.int32, (pixels, devices), 1).astype(jnp.float32)
    tbuf_ref[...] = jnp.zeros(tbuf_ref.shape, jnp.float32)
    for k in range(steps):
        across = jnp.broadcast_to(owner_ref[k:k + 1].astype(jnp.float32), (pixels, pixels))
        down = jnp.transpose(across)
        same = (down == across) & (lane < row)
        rank = jnp.sum(jnp.where(same, 1.0, 0.0), axis=1, keepdims=True)
        owner = down[:, :devices]
        rows_ref[:n_pay] = adj_ref[k]
        rows_ref[n_pay:n_pay + 1] = col_ref[k:k + 1].astype(jnp.float32)
        rows_ref[n_pay + 1:n_pay + 2] = lev_ref[k:k + 1].astype(jnp.float32)
        for j in range(capacity):
            pick = jnp.where((owner == dest) & (rank[:, :1] == j), 1.0, 0.0)
            at = (k * capacity + j) * block
            tbuf_ref[at:at + n_pay + 2] = _exact_dot(
                rows_ref[...], pick.astype(jnp.bfloat16), (((1,), (0,)), ((), ())))
    out_ref[...] = jnp.transpose(tbuf_ref[...])
    statics = (wx_ref, wy_ref, diff_ref)
    tr = wx_ref.shape[1]
    half = tr // 2
    trow = lax.broadcasted_iota(jnp.int32, wx_ref.shape[1:], 0)
    for i in range(lo_ref.shape[0]):
        a = _static_plane(2 * i, statics)
        b = _static_plane(2 * i + 1, statics)
        lo_ref[i] = jnp.where(trow < half, a, pltpu.roll(b, half, 0))
        hi_ref[i] = jnp.where(trow < half, pltpu.roll(a, half, 0), b)


def pack_call(capacity, devices, n_pad, pixel_adjoint, pixel_owner, pixel_column, pixel_level,
              wind_x, wind_y, diffusivity):
    steps, n_pay, pixels = pixel_adjoint.shape
    rows, cols = wind_x.shape[1:]
    block = -(-(n_pay + 2) // 16) * 16
    width = steps * capacity * block
    pairs = jax.ShapeDtypeStruct((n_pad // 2, rows, cols), jnp.float32)
    vmem = pl.BlockSpec(memory_space=pltpu.VMEM)
    return pl.pallas_call(
        functools.partial(_pack_kernel, capacity),
        in_specs=[vmem] * 7,
        out_specs=[vmem] * 3,
        out_shape=[jax.ShapeDtypeStruct((devices, width), jnp.float32), pairs, pairs],
        scratch_shapes=[pltpu.VMEM((n_pay + 2, pixels), jnp.float32),
                        pltpu.VMEM((width, devices), jnp.float32)],
    )(pixel_adjoint, pixel_owner.reshape(steps, pixels), pixel_column, pixel_level, wind_x,
      wind_y, diffusivity)


def _exact_dot(a, b, dims=(((1,), (1,)), ((), ()))):
    hi = a.astype(jnp.bfloat16)
    rest = a - hi.astype(jnp.float32)
    mid = rest.astype(jnp.bfloat16)
    lo = (rest - mid.astype(jnp.float32)).astype(jnp.bfloat16)
    out = lax.dot_general(hi, b, dims, preferred_element_type=jnp.float32)
    out = out + lax.dot_general(mid, b, dims, preferred_element_type=jnp.float32)
    return out + lax.dot_general(lo, b, dims, preferred_element_type=jnp.float32)


def _forcing_kernel(species, kernel, levels, n_statics, own_ref, below_ref, above_ref, wx_ref,
                    wy_ref, diff_ref, sb_ref, sa_ref,
                    tall_ref, right_ref, left_ref, st_xh_ref, lown_ref, lnb_ref, *trans):
    steps = tall_ref.shape[0]
    devices, width = own_ref.shape
    capacity = 2
    block = width // (steps * capacity)
    slots = devices * capacity
    tr2, tc = tall_ref.shape[2:]
    tr = tr2 // 2
    half = tr // 2
    group = tc // half
    n_pay = species * kernel
    lane_t = lax.broadcasted_iota(jnp.int32, (tc, slots), 0)
    row_i = lax.broadcasted_iota(jnp.int32, (tr, slots), 0)
    lev_i = lax.broadcasted_iota(jnp.int32, (levels, slots), 0)
    lane16 = lax.broadcasted_iota(jnp.int32, (tr2, tc), 1)
    right_ref[...] = jnp.zeros(right_ref.shape, jnp.float32)
    left_ref[...] = jnp.zeros(left_ref.shape, jnp.float32)
    for tref, ref in zip(trans, (own_ref, below_ref, above_ref)):
        tref[...] = jnp.transpose(ref[...])
    for k in range(steps):
        hts = []
        for src, tref in enumerate(trans):
            at = k * capacity * block
            blk = jnp.concatenate(
                [tref[at + j * block:at + j * block + n_pay + 2] for j in range(capacity)], axis=1)
            col = blk[n_pay:n_pay + 1].astype(jnp.int32)
            lev = blk[n_pay + 1:n_pay + 2].astype(jnp.int32)
            row_q = col // tc
            lane_q = col % tc
            if src == 1:
                row_q = jnp.where(row_q < half, row_q, -1)
            elif src == 2:
                row_q = jnp.where(row_q >= half, row_q, -1)
            rmask = row_i == row_q
            hts.append((lane_t == lane_q).astype(jnp.bfloat16))
            offset = lev_i - lev
            dst = lown_ref if src == 0 else lnb_ref
            c0 = 0 if src < 2 else slots
            for s in range(species):
                prof = jnp.zeros((levels, slots), jnp.float32)
                for j in range(kernel):
                    prof = prof + jnp.where(offset == j, blk[s * kernel + j:s * kernel + j + 1], 0.0)
                for l in range(levels):
                    c = s * levels + l
                    dst[c * tr:(c + 1) * tr, c0:c0 + slots] = jnp.where(
                        rmask, jnp.broadcast_to(prof[l:l + 1], (tr, slots)), 0.0)
        own = _exact_dot(lown_ref[...], hts[0])
        xh = _exact_dot(lnb_ref[...], jnp.concatenate([hts[1], hts[2]], axis=1))
        planes = own.shape[0] // tr
        tall_ref[k, :, :tr, :] = own.reshape(planes, tr, tc)
        tall_ref[k, :, tr:, :] = xh.reshape(planes, tr, tc)
        for c in range(planes):
            g, q = divmod(k * planes + c, group)
            plane = tall_ref[k, c]
            sel = (lane16 >= half * q) & (lane16 < half * q + half)
            rs = (half * q) % tc
            ls = (half * q + half) % tc
            right_ref[g] = jnp.where(sel, pltpu.roll(plane, rs, 1) if rs else plane, right_ref[g])
            left_ref[g] = jnp.where(sel, pltpu.roll(plane, ls, 1) if ls else plane, left_ref[g])
    statics = (wx_ref, wy_ref, diff_ref)
    trow = lax.broadcasted_iota(jnp.int32, (tr, tc), 0)
    base = steps * species * levels
    for i in range(sb_ref.shape[0]):
        b = sb_ref[i]
        a = sa_ref[i]
        xhs = (jnp.where(trow < half, b, pltpu.roll(a, half, 0)),
               jnp.where(trow < half, pltpu.roll(b, half, 0), a))
        for off in range(2):
            c = 2 * i + off
            st_xh_ref[c] = xhs[off]
            if c >= n_statics:
                continue
            g, q = divmod(base + c, group)
            sel = (lane16 >= half * q) & (lane16 < half * q + half)
            rs = (half * q) % tc
            ls = (half * q + half) % tc
            for part, plane in ((slice(0, tr), _static_plane(c, statics)),
                                (slice(tr, tr2), xhs[off])):
                selp = sel[part]
                right_ref[g, part] = jnp.where(
                    selp, pltpu.roll(plane, rs, 1) if rs else plane, right_ref[g, part])
                left_ref[g, part] = jnp.where(
                    selp, pltpu.roll(plane, ls, 1) if ls else plane, left_ref[g, part])


def forcing_call(species, kernel, levels, n_statics, own, below, above, wind_x, wind_y,
                 diffusivity, st_below, st_above):
    steps = wind_x.shape[0]
    devices, width = own.shape
    slots = 2 * devices
    tr, cols = wind_x.shape[1:]
    planes = species * levels
    group = cols // (tr // 2)
    n_groups = -(-(steps * planes + n_statics) // group)
    packed = jax.ShapeDtypeStruct((n_groups, 2 * tr, cols), jnp.float32)
    vmem = pl.BlockSpec(memory_space=pltpu.VMEM)
    return pl.pallas_call(
        functools.partial(_forcing_kernel, species, kernel, levels, n_statics),
        in_specs=[vmem] * 8,
        out_specs=[vmem] * 4,
        out_shape=[jax.ShapeDtypeStruct((steps, planes, 2 * tr, cols), jnp.float32), packed,
                   packed, jax.ShapeDtypeStruct((2 * st_below.shape[0], tr, cols), jnp.float32)],
        scratch_shapes=[pltpu.VMEM((planes * tr, slots), jnp.float32),
                        pltpu.VMEM((planes * tr, 2 * slots), jnp.float32)]
        + [pltpu.VMEM((width, devices), jnp.float32)] * 3,
    )(own, below, above, wind_x, wind_y, diffusivity, st_below, st_above)


def _steps_kernel(steps, species, levels, n_statics,
                  right_ref, left_ref, wx_ref, wy_ref, diff_ref, st_xh, mask_ref, prior_ref,
                  tall_hbm, adj_ref, ss_ref,
                  tall_buf, yh_buf, se_ref, state_ref, red_ref, ratio_ref, inv_ref, sems):
    planes = species * levels
    rows, lanes = mask_ref.shape
    tr, tc = adj_ref.shape[2:]
    half = tr // 2
    group = tc // half
    d0 = 2 * steps

    loads = {}
    for k in reversed(range(steps)):
        copy = pltpu.make_async_copy(tall_hbm.at[k], tall_buf.at[k], sems.at[k])
        copy.start()
        loads[k] = copy

    n_fgroups = steps * planes // group

    def unpack_group(g, carry):
        r = right_ref[g]
        l = left_ref[g]
        for q in range(group):
            yh_buf[g * group + q] = _unpack(r, l, q, tc, half)
        return carry

    lax.fori_loop(0, n_fgroups, unpack_group, 0)
    for c in range(n_statics):
        g, q = divmod(n_fgroups * group + c, group)
        se_ref[c, :, tc:] = _unpack(right_ref[g], left_ref[g], q, tc, half)

    for c in range(n_statics):
        se_ref[c, :tr, :tc] = _static_plane(c, (wx_ref, wy_ref, diff_ref))
        se_ref[c, tr:, :tc] = st_xh[c]

    zero = jnp.zeros((rows, lanes), jnp.float32)
    inside = mask_ref[...] > 0.5
    carried = zero
    for l in range(levels):
        below = se_ref[d0 + l - 1] if l > 0 else zero
        above = se_ref[d0 + l] if l < levels - 1 else zero
        inverse = 1.0 / (1.0 + below + above + below * carried)
        ratio = -above * inverse
        ratio_ref[l] = ratio
        inv_ref[l] = inverse
        carried = ratio

    for k in reversed(range(steps)):
        first = k == steps - 1
        last = k == 0
        if first:
            loads[k].wait()
            for s in range(species):

                def assemble(l, carry, s=s, k=k):
                    c = s * levels + l
                    state_ref[s, l, :, :tc] = tall_buf[k, c]
                    state_ref[s, l, :, tc:] = yh_buf[k * planes + c]
                    state_ref[s, l] = jnp.where(inside, state_ref[s, l], 0.0)
                    return carry

                lax.fori_loop(0, levels, assemble, 0, unroll=True)
        if not last:
            loads[k - 1].wait()

        wx = se_ref[k]
        wy = se_ref[steps + k]
        east = jnp.maximum(wx, 0.0)
        west = jnp.maximum(-wx, 0.0)
        north = jnp.maximum(wy, 0.0)
        south = jnp.maximum(-wy, 0.0)
        remain = 1.0 - (east + west + north + south)
        if last:
            _last_step(species, levels, tr, tc, state_ref, east, west, north, south, remain,
                       se_ref, d0, inv_ref, ratio_ref, red_ref, adj_ref, ss_ref, prior_ref)
            continue

        def forward(l, reduced):
            below = jnp.where(l > 0, se_ref[d0 + jnp.maximum(l - 1, 0)], zero)
            inverse = inv_ref[l]
            out = []
            for s in range(species):
                f = state_ref[s, l]
                from_east = pltpu.roll(east * f, rows - 1, 0)
                from_west = pltpu.roll(west * f, 1, 0)
                from_north = pltpu.roll(north * f, lanes - 1, 1)
                from_south = pltpu.roll(south * f, 1, 1)
                moved = f * remain
                moved = moved + from_east + from_west
                moved = moved + from_north + from_south
                r = (moved + below * reduced[s]) * inverse
                red_ref[s, l] = r
                out.append(r)
            return tuple(out)

        lax.fori_loop(0, levels, forward, (zero,) * species, unroll=True)

        def backward(i, result, k=k):
            l = levels - 1 - i
            ratio = ratio_ref[l]
            out = []
            for s in range(species):
                c = s * levels + l
                r = red_ref[s, l] - ratio * result[s]
                state_ref[s, l, :, :tc] = jnp.where(
                    inside[:, :tc], r[:, :tc] + tall_buf[k - 1, c], 0.0)
                state_ref[s, l, :, tc:] = jnp.where(
                    inside[:, tc:], r[:, tc:] + yh_buf[(k - 1) * planes + c], 0.0)
                out.append(r)
            return tuple(out)

        surface = lax.fori_loop(0, levels, backward, (zero,) * species, unroll=True)
        for s in range(species):
            if first:
                ss_ref[s] = prior_ref[s] * surface[s][:tr, :tc]
            else:
                ss_ref[s] = ss_ref[s] + prior_ref[s] * surface[s][:tr, :tc]


def _last_step(species, levels, tr, tc, forced_ref, east, west, north, south, remain, se_ref,
               d0, inv_ref, ratio_ref, red_ref, out_ref, ss_ref, prior_ref):
    row = lax.broadcasted_iota(jnp.int32, (tr, tc), 0)
    lane = lax.broadcasted_iota(jnp.int32, (tr, tc), 1)
    last_row = row == tr - 1
    first_row = row == 0
    last_lane = lane == tc - 1
    first_lane = lane == 0
    e_a, e_b = east[:tr, :tc], east[tr:, :tc]
    w_a, w_b = west[:tr, :tc], west[tr:, :tc]
    n_a, n_c = north[:tr, :tc], north[:tr, tc:]
    s_a, s_c = south[:tr, :tc], south[:tr, tc:]
    rem = remain[:tr, :tc]
    zero = jnp.zeros((tr, tc), jnp.float32)
    def forward(l, reduced):
        below = jnp.where(l > 0, se_ref[d0 + jnp.maximum(l - 1, 0), :tr, :tc], zero)
        inverse = inv_ref[l, :tr, :tc]
        out = []
        for s in range(species):
            f_a = forced_ref[s, l, :tr, :tc]
            f_b = forced_ref[s, l, tr:, :tc]
            f_c = forced_ref[s, l, :tr, tc:]
            from_east = jnp.where(last_row, pltpu.roll(e_b * f_b, tr - 1, 0),
                                  pltpu.roll(e_a * f_a, tr - 1, 0))
            from_west = jnp.where(first_row, pltpu.roll(w_b * f_b, 1, 0),
                                  pltpu.roll(w_a * f_a, 1, 0))
            from_north = jnp.where(last_lane, pltpu.roll(n_c * f_c, tc - 1, 1),
                                   pltpu.roll(n_a * f_a, tc - 1, 1))
            from_south = jnp.where(first_lane, pltpu.roll(s_c * f_c, 1, 1),
                                   pltpu.roll(s_a * f_a, 1, 1))
            moved = f_a * rem
            moved = moved + from_east + from_west
            moved = moved + from_north + from_south
            r = (moved + below * reduced[s]) * inverse
            red_ref[s, l, :tr, :tc] = r
            out.append(r)
        return tuple(out)

    lax.fori_loop(0, levels, forward, (zero,) * species, unroll=True)

    def backward(i, result):
        l = levels - 1 - i
        ratio = ratio_ref[l, :tr, :tc]
        out = []
        for s in range(species):
            r = red_ref[s, l, :tr, :tc] - ratio * result[s]
            out_ref[s, l] = r
            out.append(r)
        return tuple(out)

    surface = lax.fori_loop(0, levels, backward, (zero,) * species, unroll=True)
    for s in range(species):
        ss_ref[s] = ss_ref[s] + prior_ref[s] * surface[s]


def steps_call(steps, species, levels, n_statics, right, left, wind_x, wind_y, diffusivity,
               st_xh, mask, prior, tall):
    _, planes, rows, tc = tall.shape
    tr = rows // 2
    lanes = mask.shape[1]
    vmem = pl.BlockSpec(memory_space=pltpu.VMEM)
    anyspace = pl.BlockSpec(memory_space=pl.ANY)
    return pl.pallas_call(
        functools.partial(_steps_kernel, steps, species, levels, n_statics),
        in_specs=[vmem] * 8 + [anyspace],
        out_specs=[vmem, vmem],
        out_shape=[jax.ShapeDtypeStruct((species, levels, tr, tc), jnp.float32),
                   jax.ShapeDtypeStruct(prior.shape, jnp.float32)],
        scratch_shapes=[
            pltpu.VMEM((steps, planes, rows, tc), jnp.float32),
            pltpu.VMEM((steps * planes, rows, tc), jnp.float32),
            pltpu.VMEM((n_statics, rows, lanes), jnp.float32),
            pltpu.VMEM((species, levels, rows, lanes), jnp.float32),
            pltpu.VMEM((species, levels, rows, lanes), jnp.float32),
            pltpu.VMEM((levels, rows, lanes), jnp.float32),
            pltpu.VMEM((levels, rows, lanes), jnp.float32),
            pltpu.SemaphoreType.DMA((steps,)),
        ],
        compiler_params=pltpu.CompilerParams(vmem_limit_bytes=48 * 1024 * 1024),
    )(right, left, wind_x, wind_y, diffusivity, st_xh, mask, prior, tall)


def _pairs(axis):
    n = lax.axis_size(axis)
    return [(i, i + 1) for i in range(n - 1)], [(i + 1, i) for i in range(n - 1)]


def local(pixel_adjoint, pixel_owner, pixel_column, pixel_level, wind_x, wind_y,
          diffusivity, prior_emission, region_map):
    gx_n = lax.axis_size("gx")
    gy_n = lax.axis_size("gy")
    devices = gx_n * gy_n
    steps, rows, cols = wind_x.shape
    levels = diffusivity.shape[0] + 1
    species = prior_emission.shape[0]
    kernel = pixel_adjoint.shape[1] // species
    pixels = pixel_adjoint.shape[2]
    capacity = 2 * pixels // devices
    cells = rows * cols
    slots = devices * capacity
    halo = rows // 2
    assert steps <= halo
    lanes = 2 * cols
    ext_rows = 2 * rows

    n_s = 2 * steps + levels - 1
    group = cols // halo
    n_pad = -(-n_s // group) * group
    placed, st_lo, st_hi = pack_call(capacity, devices, n_pad, pixel_adjoint, pixel_owner,
                                     pixel_column, pixel_level, wind_x, wind_y, diffusivity)
    up_x, down_x = _pairs("gx")
    up_y, down_y = _pairs("gy")
    st_below = lax.ppermute(st_lo, "gx", down_x)
    st_above = lax.ppermute(st_hi, "gx", up_x)
    received = lax.all_to_all(placed, ("gx", "gy"), 0, 0, tiled=True)

    below = lax.ppermute(received, "gx", down_x)
    above = lax.ppermute(received, "gx", up_x)
    tall, right, left, st_xh = forcing_call(species, kernel, levels, n_s, received, below, above,
                                            wind_x, wind_y, diffusivity, st_below, st_above)
    right = lax.ppermute(right, "gy", down_y)
    left = lax.ppermute(left, "gy", up_y)

    gxi = lax.axis_index("gx")
    gyi = lax.axis_index("gy")
    r = jnp.arange(ext_rows, dtype=jnp.int32)[:, None]
    c = jnp.arange(lanes, dtype=jnp.int32)[None, :]
    grow = gxi * rows + jnp.where(r < rows + halo, r, r - ext_rows)
    ccol = jnp.where(c < cols + halo, c, c - lanes)
    gcol = gyi * cols + ccol
    inside = ((grow >= 0) & (grow < gx_n * rows) & (gcol >= 0) & (gcol < gy_n * cols)
              & ((c < cols + halo) | (c >= lanes - halo)))
    mask = inside.astype(jnp.float32)

    adjoint, surface_sum = steps_call(steps, species, levels, n_s, right, left, wind_x, wind_y,
                                      diffusivity, st_xh, mask, prior_emission, tall)

    nreg = REG_DEV * devices
    blocks = surface_sum.reshape(species, rows // 2, 2, cols // 4, 4).sum(axis=(2, 4))
    block_region = region_map[::2, ::4].reshape(-1)
    member = (block_region[:, None] == jnp.arange(nreg, dtype=jnp.int32)).astype(jnp.float32)
    partial = jnp.dot(blocks.reshape(species, -1), member, precision=HI)
    pieces = lax.all_to_all(partial.reshape(species, devices, nreg // devices), ("gx", "gy"), 1, 1,
                            tiled=True)
    gradient = jnp.sum(pieces, axis=1)
    return adjoint, gradient


def solution(mesh):
    in_specs = (
        P(None, None, ("gx", "gy")),
        P(None, ("gx", "gy"), None),
        P(None, ("gx", "gy")),
        P(None, ("gx", "gy")),
        P(None, "gx", "gy"),
        P(None, "gx", "gy"),
        P(None, "gx", "gy"),
        P(None, "gx", "gy"),
        P("gx", "gy"),
    )
    out_specs = (P(None, None, "gx", "gy"), P(None, ("gx", "gy")))
    return jax.shard_map(local, mesh=mesh, in_specs=in_specs, out_specs=out_specs, check_vma=False)
```
